32 devices in a mesh: section: 4 (over z), dp: 8 (over y, x, core).
Axes of the slice: x: 2, y: 2, z: 4, core: 2. Of those that a mesh axis runs over, the one named last changes fastest.
Arguments:
- layer_inputs: bfloat16 [4, 8, 128, 2560], P('section', 'dp'), may hold values from -6 to 6
- w_bc: bfloat16 [4, 2560, 256], P('section'), may hold values from -0.125 to 0.125
- log_decay: float32 [4, 8, 128, 40], P('section', 'dp'), may hold values from -1.7 to 0, as said below
- top_grad: bfloat16 [8, 128, 2560], P('dp'), may hold values from -6 to 6
Outputs:
- grad_inputs: bfloat16 [4, 8, 128, 2560], P('section', 'dp')
- grad_w: float32 [4, 2560, 256], P('section', 'dp')
The draws below stay inside these ranges and needn't reach their ends.
Inputs may be any that keep to these rules, and one draw needn't show every extreme that they name: `log_decay`: every entry is negative.
All inputs are finite; a program needn't handle non-finite values.
Results may differ from the reference program's by a relative error of at most 0.0085.
Values may be sent and summed in bfloat16 or wider, within the bound.
No kernel may reach another device: no remote copies, remote signals or barrier semaphores. Data moves between devices by JAX's collectives and lax.ppermute only.
A program may use at most 64 MiB of HBM per device.

```python
import math
import jax
import jax.numpy as jnp
from jax import lax

D = 2560
RECURRENT_GROUPS = 40
STATE = 128
GROUP = 32
MICRO = 4
DEPTH_OF_STACK = 4
BATCH_STRINGS = 8
STRING_LENGTH = 128


def draw_log_decay(key, part):
    stochastic_seeds = jax.random.split(key, 7)
    head_shape = (DEPTH_OF_STACK, BATCH_STRINGS, 1, RECURRENT_GROUPS)
    fast_share = 0.5
    fast_mask = jax.random.uniform(stochastic_seeds[0], head_shape) < fast_share
    fast_rate = jnp.exp(jax.random.uniform(stochastic_seeds[1], head_shape, minval=math.log(0.05), maxval=math.log(0.12)))
    slow_rate = jnp.exp(jax.random.uniform(stochastic_seeds[2], head_shape, minval=math.log(0.0006), maxval=math.log(0.002)))
    drawn_frequency = jnp.where(fast_mask, fast_rate, slow_rate)
    device_magnitude = jax.random.uniform(stochastic_seeds[3], (DEPTH_OF_STACK, BATCH_STRINGS, 1, 1), minval=0.6, maxval=1.6)
    noise_amplitude = jax.random.uniform(stochastic_seeds[4], (DEPTH_OF_STACK, BATCH_STRINGS, STRING_LENGTH, RECURRENT_GROUPS), minval=0.5, maxval=1.5)
    spike_onset = jax.random.randint(stochastic_seeds[5], (DEPTH_OF_STACK, BATCH_STRINGS, 2, 1), 0, STRING_LENGTH)
    spike_duration = jax.random.uniform(stochastic_seeds[6], (DEPTH_OF_STACK, BATCH_STRINGS, 2, RECURRENT_GROUPS), minval=math.log(0.5), maxval=math.log(0.8))
    locations = jnp.arange(STRING_LENGTH)[None, None, None, :]
    match_number = (spike_onset == locations).astype(jnp.float32)
    spike_occurrences = jnp.sum(match_number[:, :, :, :, None] * spike_duration[:, :, :, None, :], axis=2)
    return (spike_occurrences - drawn_frequency * device_magnitude * noise_amplitude).astype(jnp.float32)


def raised(drawn, own_key, source, target, blocks, factor):
    def block_of(axis_at):
        return (jnp.arange(drawn.shape[axis_at]) // (drawn.shape[axis_at] // blocks)).reshape((-1,) + (1,) * (drawn.ndim - 1 - axis_at))

    one_side = jax.random.permutation(own_key, blocks)[block_of(target)]
    far = (block_of(target) + blocks // 2) % blocks
    return jnp.where((block_of(source) == one_side) | (block_of(source) == far), factor * drawn, drawn)


def block_scale(own_key, extent, cuts, low, top_value):
    gain = 1.0
    for dim, parts in cuts:
        draws = jax.random.uniform(jax.random.fold_in(jax.random.fold_in(own_key, 6), dim), (parts,), jnp.float32, low / len(cuts), top_value / len(cuts))
        gain = gain * jnp.repeat(jnp.exp(draws), extent[dim] // parts).reshape((-1,) + (1,) * (len(extent) - 1 - dim))
    return gain


def centred(stream_key, extent, width, bound, cuts=(), kind=jnp.bfloat16):
    entries = width * jax.random.normal(stream_key, extent, jnp.float32)
    if cuts:
        entries = entries * block_scale(stream_key, extent, cuts, -0.22, 0.18)
    return jnp.clip(entries, -bound, bound).astype(kind)


def heavy_noise(own_key, dims, width, limit, pieces, heavy, kind=jnp.bfloat16):
    array = width * jax.random.normal(own_key, dims, jnp.float32)
    if pieces:
        array = array * block_scale(own_key, dims, pieces, -0.22, 0.18)
    return jnp.clip(raised(array, jax.random.fold_in(own_key, 3), *heavy), -limit, limit).astype(kind)


def setup_inputs(seed: int = 0) -> dict:
    streams_of = jax.random.split(jax.random.key(seed), 5)
    return {
        "layer_inputs": heavy_noise(streams_of[0], (DEPTH_OF_STACK, BATCH_STRINGS, STRING_LENGTH, D), 1.0, 6.0, ((0, 4), (1, 8)), (1, 3, 8, 2.0)),
        "w_bc": centred(streams_of[1], (DEPTH_OF_STACK, D, 2 * STATE), D ** -0.5, 0.125, ((0, 4),)),
        "log_decay": draw_log_decay(jax.random.fold_in(streams_of[4], 71), 0),
        "top_grad": centred(streams_of[3], (BATCH_STRINGS, STRING_LENGTH, D), 1.0, 6.0, ((0, 8),)),
    }


def block_terms(inputs_b, in_b, out_b, rates, grads_b, carried, state_in, factor):
    length = inputs_b.shape[0]
    cumulative = jnp.cumsum(rates, axis=0)
    ending = cumulative[-1]
    locations = jnp.arange(length)
    lower_mask = (locations[:, None] >= locations[None, :])[:, :, None]
    spread = jnp.where(lower_mask, cumulative[:, None, :] - cumulative[None, :, :], 0.0)
    decays = jnp.where(lower_mask, jnp.exp(spread), 0.0)
    tail_decay = jnp.exp(ending[None, :] - cumulative)
    leading = jnp.exp(cumulative)
    scores = jnp.dot(out_b, in_b.T, preferred_element_type=jnp.float32)
    weighted = (factor * decays * scores[:, :, None]).astype(jnp.bfloat16)
    carried_b = carried.astype(jnp.bfloat16)
    state_b = state_in.astype(jnp.bfloat16)
    grad_feats = jnp.einsum('kjh,khp->jhp', weighted, grads_b, preferred_element_type=jnp.float32)
    grad_feats = grad_feats + tail_decay[:, :, None] * jnp.einsum('hpn,jn->jhp', carried_b, in_b, preferred_element_type=jnp.float32)
    pair_dots = jnp.einsum('khp,jhp->kjh', grads_b, inputs_b, preferred_element_type=jnp.float32)
    mixing = jnp.sum(decays * pair_dots, axis=2).astype(jnp.bfloat16)
    tail_inputs = (tail_decay[:, :, None] * inputs_b.astype(jnp.float32)).astype(jnp.bfloat16)
    lead_grads = (leading[:, :, None] * grads_b.astype(jnp.float32)).astype(jnp.bfloat16)
    grad_inmap = factor * jnp.dot(mixing.T, out_b, preferred_element_type=jnp.float32)
    grad_inmap = grad_inmap + jnp.einsum('jhp,hpn->jn', tail_inputs, carried_b, preferred_element_type=jnp.float32)
    grad_outmap = factor * (jnp.dot(mixing, in_b, preferred_element_type=jnp.float32) + jnp.einsum('ihp,hpn->in', lead_grads, state_b, preferred_element_type=jnp.float32))
    carry_out = factor * jnp.einsum('khp,kn->hpn', lead_grads, out_b, preferred_element_type=jnp.float32)
    carry_out = carry_out + jnp.exp(ending)[:, None, None] * carried
    return grad_feats, grad_inmap, grad_outmap, carry_out


def block_end(inputs_b, in_b, rates, state_in):
    cumulative = jnp.cumsum(rates, axis=0)
    ending = cumulative[-1]
    tail_decay = jnp.exp(ending[None, :] - cumulative)
    tail_inputs = (tail_decay[:, :, None] * inputs_b.astype(jnp.float32)).astype(jnp.bfloat16)
    fresh = jnp.einsum('jhp,jn->hpn', tail_inputs, in_b, preferred_element_type=jnp.float32)
    return jnp.exp(ending)[:, None, None] * state_in + fresh


def split_block(inputs_c, map_block, head_count):
    length, features = inputs_c.shape
    state_size = map_block.shape[1] // 2
    inputs_b = inputs_c.reshape(length, head_count, features // head_count)
    in_b = map_block[:, :state_size]
    out_b = map_block[:, state_size:]
    return inputs_b, in_b, out_b


def block_back(inputs_c, map_block, rates, grads_c, carried, state_in, weights):
    length, features = inputs_c.shape
    head_count = rates.shape[1]
    factor = 0.25 / (map_block.shape[1] // 2)
    inputs_b, in_b, out_b = split_block(inputs_c, map_block, head_count)
    grads_b = grads_c.reshape(length, head_count, features // head_count)
    grad_feats, grad_inmap, grad_outmap, carry_out = block_terms(inputs_b, in_b, out_b, rates, grads_b, carried, state_in, factor)
    grad_bc = jnp.concatenate([grad_inmap, grad_outmap], axis=1).astype(jnp.bfloat16)
    back_proj = lax.dot_general(grad_bc, weights, (((1,), (1,)), ((), ())), preferred_element_type=jnp.float32)
    summed = grads_c.astype(jnp.float32) + grad_feats.reshape(length, features) + back_proj
    return summed.astype(jnp.bfloat16), carry_out, grad_bc


def layer_starts(inputs_s, bc_s, rates_s):
    head_count = rates_s.shape[1]
    features = inputs_s.shape[1]
    state_size = bc_s.shape[1] // 2
    state_now = jnp.zeros((head_count, features // head_count, state_size), jnp.float32)
    saved = []
    for block_no in range(MICRO):
        lo_row = block_no * GROUP
        inputs_b, in_b, out_b = split_block(inputs_s[lo_row:lo_row + GROUP], bc_s[lo_row:lo_row + GROUP], head_count)
        saved.append(state_now)
        state_now = block_end(inputs_b, in_b, rates_s[lo_row:lo_row + GROUP], state_now)
    return jnp.stack(saved)


def layer_back(inputs_s, weights, rates_s, incoming):
    bc_s = jnp.dot(inputs_s, weights, preferred_element_type=jnp.float32).astype(jnp.bfloat16)
    starts = layer_starts(inputs_s, bc_s, rates_s)
    carried = jnp.zeros_like(starts[0])
    grad_list = [None] * MICRO
    map_list = [None] * MICRO
    for block_no in reversed(range(MICRO)):
        lo_row = block_no * GROUP
        hi_row = lo_row + GROUP
        grad_block, carried, grad_bc = block_back(inputs_s[lo_row:hi_row], bc_s[lo_row:hi_row], rates_s[lo_row:hi_row], incoming[lo_row:hi_row], carried, starts[block_no], weights)
        grad_list[block_no] = grad_block
        map_list[block_no] = grad_bc
    return jnp.concatenate(grad_list, axis=0), jnp.concatenate(map_list, axis=0)


def reference(layer_inputs, w_bc, log_decay, top_grad):
    def one_sequence(packed):
        inputs_q, rates_q, top_q = packed

        def descend(incoming, layer_data):
            level_inputs, level_weights, level_rates = layer_data
            level_grads, level_maps = layer_back(level_inputs, level_weights, level_rates, incoming)
            return level_grads, (level_grads, level_maps)

        final_grad, stacked = lax.scan(descend, top_q, (inputs_q, w_bc, rates_q), reverse=True)
        return stacked

    all_grads, all_maps = lax.map(one_sequence, (jnp.swapaxes(layer_inputs, 0, 1), jnp.swapaxes(log_decay, 0, 1), top_grad))
    grad_inputs = jnp.swapaxes(all_grads, 0, 1)
    map_grads = jnp.swapaxes(all_maps, 0, 1)

    def layer_weight(packed):
        level_inputs, level_maps = packed
        return jnp.dot(level_inputs.reshape(-1, D).T, level_maps.reshape(-1, 2 * STATE), preferred_element_type=jnp.float32)

    grad_w = lax.map(layer_weight, (layer_inputs, map_grads)) / BATCH_STRINGS
    return grad_inputs, grad_w
```

```python
import jax
import jax.numpy as jnp
from jax import lax
from jax.sharding import PartitionSpec as P

MICRO = 4


def shortened(value):
    return jax.tree.map(lambda a: a.astype(jnp.bfloat16) if a.dtype == jnp.float32 else a, value)


def passed_along(block, axis, distance):
    devices = range(lax.axis_size(axis))
    route = [(i - distance, i) for i in devices if i - distance in devices]
    return lax.ppermute(block, axis, route)


def block_terms(inputs_b, in_b, out_b, rates, grads_b, carried, state_in, factor):
    length = inputs_b.shape[0]
    cumulative = jnp.cumsum(rates, axis=0)
    ending = cumulative[-1]
    locations = jnp.arange(length)
    lower_mask = (locations[:, None] >= locations[None, :])[:, :, None]
    spread = jnp.where(lower_mask, cumulative[:, None, :] - cumulative[None, :, :], 0.0)
    decays = jnp.where(lower_mask, jnp.exp(spread), 0.0)
    tail_decay = jnp.exp(ending[None, :] - cumulative)
    leading = jnp.exp(cumulative)
    scores = jnp.dot(out_b, in_b.T, preferred_element_type=jnp.float32)
    weighted = (factor * decays * scores[:, :, None]).astype(jnp.bfloat16)
    carried_b = carried.astype(jnp.bfloat16)
    state_b = state_in.astype(jnp.bfloat16)
    grad_feats = jnp.einsum("kjh,khp->jhp", weighted, grads_b, preferred_element_type=jnp.float32)
    grad_feats = grad_feats + tail_decay[:, :, None] * jnp.einsum(
        "hpn,jn->jhp", carried_b, in_b, preferred_element_type=jnp.float32
    )
    pair_dots = jnp.einsum("khp,jhp->kjh", grads_b, inputs_b, preferred_element_type=jnp.float32)
    mixing = jnp.sum(decays * pair_dots, axis=2).astype(jnp.bfloat16)
    tail_inputs = (tail_decay[:, :, None] * inputs_b.astype(jnp.float32)).astype(jnp.bfloat16)
    lead_grads = (leading[:, :, None] * grads_b.astype(jnp.float32)).astype(jnp.bfloat16)
    grad_inmap = factor * jnp.dot(mixing.T, out_b, preferred_element_type=jnp.float32)
    grad_inmap = grad_inmap + jnp.einsum(
        "jhp,hpn->jn", tail_inputs, carried_b, preferred_element_type=jnp.float32
    )
    grad_outmap = factor * (
        jnp.dot(mixing, in_b, preferred_element_type=jnp.float32)
        + jnp.einsum("ihp,hpn->in", lead_grads, state_b, preferred_element_type=jnp.float32)
    )
    carry_out = factor * jnp.einsum(
        "khp,kn->hpn", lead_grads, out_b, preferred_element_type=jnp.float32
    )
    carry_out = carry_out + jnp.exp(ending)[:, None, None] * carried
    return (grad_feats, grad_inmap, grad_outmap, carry_out)


def block_end(inputs_b, in_b, rates, state_in):
    cumulative = jnp.cumsum(rates, axis=0)
    ending = cumulative[-1]
    tail_decay = jnp.exp(ending[None, :] - cumulative)
    tail_inputs = (tail_decay[:, :, None] * inputs_b.astype(jnp.float32)).astype(jnp.bfloat16)
    fresh = jnp.einsum("jhp,jn->hpn", tail_inputs, in_b, preferred_element_type=jnp.float32)
    return jnp.exp(ending)[:, None, None] * state_in + fresh


def split_block(inputs_c, map_block, head_count):
    length, features = inputs_c.shape
    state_size = map_block.shape[1] // 2
    inputs_b = inputs_c.reshape(length, head_count, features // head_count)
    in_b = map_block[:, :state_size]
    out_b = map_block[:, state_size:]
    return (inputs_b, in_b, out_b)


def block_back(inputs_c, map_block, rates, grads_c, carried, state_in, weights):
    length, features = inputs_c.shape
    head_count = rates.shape[1]
    factor = 0.25 / (map_block.shape[1] // 2)
    inputs_b, in_b, out_b = split_block(inputs_c, map_block, head_count)
    grads_b = grads_c.reshape(length, head_count, features // head_count)
    grad_feats, grad_inmap, grad_outmap, carry_out = block_terms(
        inputs_b, in_b, out_b, rates, grads_b, carried, state_in, factor
    )
    grad_bc = jnp.concatenate([grad_inmap, grad_outmap], axis=1).astype(jnp.bfloat16)
    back_proj = lax.dot_general(
        grad_bc, weights, (((1,), (1,)), ((), ())), preferred_element_type=jnp.float32
    )
    summed = grads_c.astype(jnp.float32) + grad_feats.reshape(length, features) + back_proj
    return (summed.astype(jnp.bfloat16), carry_out, grad_bc)


def layer_starts(inputs_s, bc_s, rates_s):
    head_count = rates_s.shape[1]
    features = inputs_s.shape[1]
    state_size = bc_s.shape[1] // 2
    block_len = inputs_s.shape[0] // MICRO
    state_now = jnp.zeros((head_count, features // head_count, state_size), jnp.float32)
    saved = []
    for block_no in range(MICRO):
        lo_row = block_no * block_len
        inputs_b, in_b, out_b = split_block(
            inputs_s[lo_row : lo_row + block_len], bc_s[lo_row : lo_row + block_len], head_count
        )
        saved.append(state_now)
        state_now = block_end(inputs_b, in_b, rates_s[lo_row : lo_row + block_len], state_now)
    return jnp.stack(saved)


def shards(layer_inputs, w_bc, log_decay, top_grad):
    sections = lax.axis_size("section")
    section_id = lax.axis_index("section")
    lay_dev, seq_dev, tok_len, features = layer_inputs.shape
    block_len = tok_len // MICRO
    bc_all = jnp.einsum(
        "lstd,ldc->lstc", layer_inputs, w_bc, preferred_element_type=jnp.float32
    ).astype(jnp.bfloat16)
    starts = jax.vmap(jax.vmap(layer_starts))(layer_inputs, bc_all, log_decay)
    is_top = section_id == sections - 1
    back_all = jax.vmap(block_back, in_axes=(0, 0, 0, 0, 0, 0, None))

    def advance(counter, loop_state):
        incoming, carried, grad_store, map_store = loop_state
        offset = counter - (sections - 1 - section_id)
        is_valid = (offset >= 0) & (offset < MICRO)
        block_no = jnp.clip(MICRO - 1 - offset, 0, MICRO - 1)
        row_start = block_no * block_len
        from_top = lax.dynamic_slice_in_dim(top_grad, row_start, block_len, 1)
        grad_block = jnp.where(is_top, from_top, incoming)

        def compute(stores):
            carried_in, grads_in, maps_in = stores
            current = grad_block
            for level_no in reversed(range(lay_dev)):
                inputs_c = lax.dynamic_slice_in_dim(layer_inputs[level_no], row_start, block_len, 1)
                map_block = lax.dynamic_slice_in_dim(bc_all[level_no], row_start, block_len, 1)
                rates = lax.dynamic_slice_in_dim(log_decay[level_no], row_start, block_len, 1)
                state_in = lax.dynamic_index_in_dim(starts[level_no], block_no, 1, keepdims=False)
                level_grads, carry_out, grad_bc = back_all(
                    inputs_c,
                    map_block,
                    rates,
                    current,
                    carried_in[level_no],
                    state_in,
                    w_bc[level_no],
                )
                carried_in = carried_in.at[level_no].set(carry_out)
                grads_in = grads_in.at[level_no].set(
                    lax.dynamic_update_slice_in_dim(grads_in[level_no], level_grads, row_start, 1)
                )
                maps_in = maps_in.at[level_no].set(
                    lax.dynamic_update_slice_in_dim(maps_in[level_no], grad_bc, row_start, 1)
                )
                current = level_grads
            return (current, (carried_in, grads_in, maps_in))

        def passing(stores):
            return (jnp.zeros_like(grad_block), stores)

        outgoing, updated = lax.cond(is_valid, compute, passing, (carried, grad_store, map_store))
        received = jax.tree.map(
            lambda part, own: part.astype(own.dtype),
            passed_along(shortened(outgoing), "section", -1),
            outgoing,
        )
        return (received, updated[0], updated[1], updated[2])

    initial = (
        jnp.zeros((seq_dev, block_len, features), jnp.bfloat16),
        jnp.zeros((lay_dev,) + starts.shape[1:2] + starts.shape[3:], jnp.float32),
        jnp.zeros(layer_inputs.shape, jnp.bfloat16),
        jnp.zeros(bc_all.shape, jnp.bfloat16),
    )
    final_state = lax.fori_loop(0, MICRO + sections - 1, advance, initial)
    grad_inputs = final_state[2]
    map_store = final_state[3]
    ways = lax.axis_size("dp")
    divisor = ways * seq_dev
    rows_here = layer_inputs.reshape(lay_dev, seq_dev * tok_len, features)
    rows_all = lax.all_to_all(rows_here, "dp", 2, 1, tiled=True)
    maps_here = map_store.reshape(lay_dev, seq_dev * tok_len, map_store.shape[-1])
    maps_all = lax.all_gather(maps_here, "dp", axis=1, tiled=True)
    grad_w = jnp.einsum(
        "lrd,lrc->ldc", rows_all, maps_all, preferred_element_type=jnp.float32
    ) / divisor
    return (grad_inputs, grad_w)


def solution(mesh):
    in_specs = (
        P("section", "dp", None, None),
        P("section", None, None),
        P("section", "dp", None, None),
        P("dp", None, None),
    )
    out_specs = (P("section", "dp", None, None), P("section", "dp", None))
    return jax.shard_map(shards, mesh=mesh, in_specs=in_specs, out_specs=out_specs, check_vma=False)
```

```python
import jax
import jax.numpy as jnp
from jax import lax
from jax.sharding import PartitionSpec as P

MICRO = 4


def shortened(value):
    return jax.tree.map(lambda a: a.astype(jnp.bfloat16) if a.dtype == jnp.float32 else a, value)


def passed_along(block, axis, distance):
    devices = range(lax.axis_size(axis))
    route = [(i - distance, i) for i in devices if i - distance in devices]
    return lax.ppermute(block, axis, route)


def block_terms(inputs_b, in_b, out_b, rates, grads_b, carried, state_in, factor):
    length = inputs_b.shape[0]
    cumulative = jnp.cumsum(rates, axis=0)
    ending = cumulative[-1]
    locations = jnp.arange(length)
    lower_mask = (locations[:, None] >= locations[None, :])[:, :, None]
    spread = jnp.where(lower_mask, cumulative[:, None, :] - cumulative[None, :, :], 0.0)
    decays = jnp.where(lower_mask, jnp.exp(spread), 0.0)
    tail_decay = jnp.exp(ending[None, :] - cumulative)
    leading = jnp.exp(cumulative)
    scores = jnp.dot(out_b, in_b.T, preferred_element_type=jnp.float32)
    weighted = (factor * decays * scores[:, :, None]).astype(jnp.bfloat16)
    carried_b = carried.astype(jnp.bfloat16)
    state_b = state_in.astype(jnp.bfloat16)
    grad_feats = jnp.einsum("kjh,khp->jhp", weighted, grads_b, preferred_element_type=jnp.float32)
    grad_feats = grad_feats + tail_decay[:, :, None] * jnp.einsum(
        "hpn,jn->jhp", carried_b, in_b, preferred_element_type=jnp.float32
    )
    pair_dots = jnp.einsum("khp,jhp->kjh", grads_b, inputs_b, preferred_element_type=jnp.float32)
    mixing = jnp.sum(decays * pair_dots, axis=2).astype(jnp.bfloat16)
    tail_inputs = (tail_decay[:, :, None] * inputs_b.astype(jnp.float32)).astype(jnp.bfloat16)
    lead_grads = (leading[:, :, None] * grads_b.astype(jnp.float32)).astype(jnp.bfloat16)
    grad_inmap = factor * jnp.dot(mixing.T, out_b, preferred_element_type=jnp.float32)
    grad_inmap = grad_inmap + jnp.einsum(
        "jhp,hpn->jn", tail_inputs, carried_b, preferred_element_type=jnp.float32
    )
    grad_outmap = factor * (
        jnp.dot(mixing, in_b, preferred_element_type=jnp.float32)
        + jnp.einsum("ihp,hpn->in", lead_grads, state_b, preferred_element_type=jnp.float32)
    )
    carry_out = factor * jnp.einsum(
        "khp,kn->hpn", lead_grads, out_b, preferred_element_type=jnp.float32
    )
    carry_out = carry_out + jnp.exp(ending)[:, None, None] * carried
    return (grad_feats, grad_inmap, grad_outmap, carry_out)


def block_end(inputs_b, in_b, rates, state_in):
    cumulative = jnp.cumsum(rates, axis=0)
    ending = cumulative[-1]
    tail_decay = jnp.exp(ending[None, :] - cumulative)
    tail_inputs = (tail_decay[:, :, None] * inputs_b.astype(jnp.float32)).astype(jnp.bfloat16)
    fresh = jnp.einsum("jhp,jn->hpn", tail_inputs, in_b, preferred_element_type=jnp.float32)
    return jnp.exp(ending)[:, None, None] * state_in + fresh


def split_block(inputs_c, map_block, head_count):
    length, features = inputs_c.shape
    state_size = map_block.shape[1] // 2
    inputs_b = inputs_c.reshape(length, head_count, features // head_count)
    in_b = map_block[:, :state_size]
    out_b = map_block[:, state_size:]
    return (inputs_b, in_b, out_b)


def block_back(inputs_c, map_block, rates, grads_c, carried, state_in, weights):
    length, features = inputs_c.shape
    head_count = rates.shape[1]
    factor = 0.25 / (map_block.shape[1] // 2)
    inputs_b, in_b, out_b = split_block(inputs_c, map_block, head_count)
    grads_b = grads_c.reshape(length, head_count, features // head_count)
    grad_feats, grad_inmap, grad_outmap, carry_out = block_terms(
        inputs_b, in_b, out_b, rates, grads_b, carried, state_in, factor
    )
    grad_bc = jnp.concatenate([grad_inmap, grad_outmap], axis=1).astype(jnp.bfloat16)
    back_proj = lax.dot_general(
        grad_bc, weights, (((1,), (1,)), ((), ())), preferred_element_type=jnp.float32
    )
    summed = grads_c.astype(jnp.float32) + grad_feats.reshape(length, features) + back_proj
    return (summed.astype(jnp.bfloat16), carry_out, grad_bc)


def layer_starts(inputs_s, bc_s, rates_s):
    head_count = rates_s.shape[1]
    features = inputs_s.shape[1]
    state_size = bc_s.shape[1] // 2
    block_len = inputs_s.shape[0] // MICRO
    state_now = jnp.zeros((head_count, features // head_count, state_size), jnp.float32)
    saved = []
    for block_no in range(MICRO):
        lo_row = block_no * block_len
        inputs_b, in_b, out_b = split_block(
            inputs_s[lo_row : lo_row + block_len], bc_s[lo_row : lo_row + block_len], head_count
        )
        saved.append(state_now)
        state_now = block_end(inputs_b, in_b, rates_s[lo_row : lo_row + block_len], state_now)
    return jnp.stack(saved)


def block_consts(inputs_b, in_b, out_b, rates, factor):
    length = inputs_b.shape[0]
    cumulative = jnp.cumsum(rates, axis=0)
    ending = cumulative[-1]
    locations = jnp.arange(length)
    lower_mask = (locations[:, None] >= locations[None, :])[:, :, None]
    spread = jnp.where(lower_mask, cumulative[:, None, :] - cumulative[None, :, :], 0.0)
    decays = jnp.where(lower_mask, jnp.exp(spread), 0.0)
    tail_decay = jnp.exp(ending[None, :] - cumulative)
    leading = jnp.exp(cumulative)
    scores = jnp.dot(out_b, in_b.T, preferred_element_type=jnp.float32)
    weighted = (factor * decays * scores[:, :, None]).astype(jnp.bfloat16)
    tail_inputs = (tail_decay[:, :, None] * inputs_b.astype(jnp.float32)).astype(jnp.bfloat16)
    fresh = jnp.einsum("jhp,jn->hpn", tail_inputs, in_b, preferred_element_type=jnp.float32)
    return dict(
        decays=decays,
        tail=tail_decay,
        lead=leading,
        weighted=weighted,
        tail_inputs=tail_inputs,
        fresh=fresh,
        ending=jnp.exp(ending),
    )


def block_step(consts, inputs_b, in_b, out_b, state_b, grads_c, carried, weights, factor):
    length, features = grads_c.shape
    head_count = consts["tail"].shape[1]
    grads_b = grads_c.reshape(length, head_count, features // head_count)
    carried_b = carried.astype(jnp.bfloat16)
    grad_feats = jnp.einsum(
        "kjh,khp->jhp", consts["weighted"], grads_b, preferred_element_type=jnp.float32
    )
    grad_feats = grad_feats + consts["tail"][:, :, None] * jnp.einsum(
        "hpn,jn->jhp", carried_b, in_b, preferred_element_type=jnp.float32
    )
    pair_dots = jnp.einsum("khp,jhp->kjh", grads_b, inputs_b, preferred_element_type=jnp.float32)
    mixing = jnp.sum(consts["decays"] * pair_dots, axis=2).astype(jnp.bfloat16)
    lead_grads = (consts["lead"][:, :, None] * grads_b.astype(jnp.float32)).astype(jnp.bfloat16)
    grad_inmap = factor * jnp.dot(mixing.T, out_b, preferred_element_type=jnp.float32)
    grad_inmap = grad_inmap + jnp.einsum(
        "jhp,hpn->jn", consts["tail_inputs"], carried_b, preferred_element_type=jnp.float32
    )
    grad_outmap = factor * (
        jnp.dot(mixing, in_b, preferred_element_type=jnp.float32)
        + jnp.einsum("ihp,hpn->in", lead_grads, state_b, preferred_element_type=jnp.float32)
    )
    carry_out = factor * jnp.einsum(
        "khp,kn->hpn", lead_grads, out_b, preferred_element_type=jnp.float32
    )
    carry_out = carry_out + consts["ending"][:, None, None] * carried
    grad_bc = jnp.concatenate([grad_inmap, grad_outmap], axis=1).astype(jnp.bfloat16)
    back_proj = lax.dot_general(
        grad_bc, weights, (((1,), (1,)), ((), ())), preferred_element_type=jnp.float32
    )
    summed = grads_c.astype(jnp.float32) + grad_feats.reshape(length, features) + back_proj
    return (summed.astype(jnp.bfloat16), carry_out, grad_bc)


def shards(layer_inputs, w_bc, log_decay, top_grad):
    sections = lax.axis_size("section")
    section_id = lax.axis_index("section")
    lay_dev, seq_dev, tok_len, features = layer_inputs.shape
    head_count = log_decay.shape[-1]
    block_len = tok_len // MICRO
    state_size = w_bc.shape[-1] // 2
    factor = 0.25 / state_size
    bc_all = jnp.einsum(
        "lstd,ldc->lstc", layer_inputs, w_bc, preferred_element_type=jnp.float32
    ).astype(jnp.bfloat16)

    def blocked(a):
        split = a.reshape(a.shape[:2] + (MICRO, block_len) + a.shape[3:])
        return jnp.moveaxis(split, 2, 0)

    x_blk = blocked(layer_inputs).reshape(
        (MICRO, lay_dev, seq_dev, block_len, head_count, features // head_count)
    )
    bc_blk = blocked(bc_all)
    in_blk = bc_blk[..., :state_size]
    out_blk = bc_blk[..., state_size:]
    rates_blk = blocked(log_decay)
    consts_fn = jax.vmap(jax.vmap(jax.vmap(lambda x, b, c, r: block_consts(x, b, c, r, factor))))
    consts = consts_fn(x_blk, in_blk, out_blk, rates_blk)

    state_now = jnp.zeros(consts["fresh"].shape[1:], jnp.float32)
    saved = []
    for block_no in range(MICRO):
        saved.append(state_now.astype(jnp.bfloat16))
        state_now = consts["ending"][block_no][..., None, None] * state_now + consts["fresh"][block_no]
    states_b = jnp.stack(saved)
    del consts["fresh"]

    top_blk = jnp.moveaxis(
        top_grad.reshape((seq_dev, MICRO, block_len, features)), 1, 0
    )
    is_top = section_id == sections - 1
    step_fn = jax.vmap(
        lambda k, x, b, c, sb, g, r, w: block_step(k, x, b, c, sb, g, r, w, factor),
        in_axes=(0, 0, 0, 0, 0, 0, 0, None),
    )

    def advance(counter, loop_state):
        incoming, carried, grad_store, map_store = loop_state
        offset = counter - (sections - 1 - section_id)
        is_valid = (offset >= 0) & (offset < MICRO)
        block_no = jnp.clip(MICRO - 1 - offset, 0, MICRO - 1)
        slot = jnp.where(is_valid, block_no, MICRO)
        from_top = lax.dynamic_index_in_dim(top_blk, block_no, 0, keepdims=False)
        current = jnp.where(is_top, from_top, incoming)
        picked = jax.tree.map(
            lambda a: lax.dynamic_index_in_dim(a, block_no, 0, keepdims=False), consts
        )
        x_now = lax.dynamic_index_in_dim(x_blk, block_no, 0, keepdims=False)
        in_now = lax.dynamic_index_in_dim(in_blk, block_no, 0, keepdims=False)
        out_now = lax.dynamic_index_in_dim(out_blk, block_no, 0, keepdims=False)
        st_now = lax.dynamic_index_in_dim(states_b, block_no, 0, keepdims=False)
        new_carried = []
        for level_no in reversed(range(lay_dev)):
            level_grads, carry_out, grad_bc = step_fn(
                jax.tree.map(lambda a: a[level_no], picked),
                x_now[level_no],
                in_now[level_no],
                out_now[level_no],
                st_now[level_no],
                current,
                carried[level_no],
                w_bc[level_no],
            )
            new_carried.append(carry_out)
            grad_store = lax.dynamic_update_slice(
                grad_store, level_grads[None, None], (slot, level_no, 0, 0, 0)
            )
            map_store = lax.dynamic_update_slice(
                map_store, grad_bc[None, None], (slot, level_no, 0, 0, 0)
            )
            current = level_grads
        carried = jnp.stack(new_carried[::-1])
        received = passed_along(current, "section", -1)
        return (received, carried, grad_store, map_store)

    initial = (
        jnp.zeros((seq_dev, block_len, features), jnp.bfloat16),
        jnp.zeros((lay_dev,) + states_b.shape[2:], jnp.float32),
        jnp.zeros((MICRO + 1, lay_dev, seq_dev, block_len, features), jnp.bfloat16),
        jnp.zeros((MICRO + 1, lay_dev, seq_dev, block_len, 2 * state_size), jnp.bfloat16),
    )
    final_state = lax.fori_loop(0, MICRO + sections - 1, advance, initial)
    grad_store = final_state[2]
    map_store = final_state[3]

    grad_inputs = jnp.moveaxis(grad_store[:MICRO], 0, 2).reshape(layer_inputs.shape)
    map_store = jnp.moveaxis(map_store[:MICRO], 0, 2).reshape(bc_all.shape)
    ways = lax.axis_size("dp")
    divisor = ways * seq_dev
    rows_here = layer_inputs.reshape(lay_dev, seq_dev * tok_len, features)
    rows_all = lax.all_to_all(rows_here, "dp", 2, 1, tiled=True)
    maps_here = map_store.reshape(lay_dev, seq_dev * tok_len, map_store.shape[-1])
    maps_all = lax.all_gather(maps_here, "dp", axis=1, tiled=True)
    grad_w = jnp.einsum(
        "lrd,lrc->ldc", rows_all, maps_all, preferred_element_type=jnp.float32
    ) / divisor
    return (grad_inputs, grad_w)


def solution(mesh):
    in_specs = (
        P("section", "dp", None, None),
        P("section", None, None),
        P("section", "dp", None, None),
        P("dp", None, None),
    )
    out_specs = (P("section", "dp", None, None), P("section", "dp", None))
    return jax.shard_map(shards, mesh=mesh, in_specs=in_specs, out_specs=out_specs, check_vma=False)
```

```python
import functools

import jax
import jax.numpy as jnp
from jax import lax
from jax.experimental import pallas as pl
from jax.experimental.pallas import tpu as pltpu
from jax.sharding import PartitionSpec as P

MICRO = 4


def shortened(value):
    return jax.tree.map(lambda a: a.astype(jnp.bfloat16) if a.dtype == jnp.float32 else a, value)


def passed_along(block, axis, distance):
    devices = range(lax.axis_size(axis))
    route = [(i - distance, i) for i in devices if i - distance in devices]
    return lax.ppermute(block, axis, route)


def block_terms(inputs_b, in_b, out_b, rates, grads_b, carried, state_in, factor):
    length = inputs_b.shape[0]
    cumulative = jnp.cumsum(rates, axis=0)
    ending = cumulative[-1]
    locations = jnp.arange(length)
    lower_mask = (locations[:, None] >= locations[None, :])[:, :, None]
    spread = jnp.where(lower_mask, cumulative[:, None, :] - cumulative[None, :, :], 0.0)
    decays = jnp.where(lower_mask, jnp.exp(spread), 0.0)
    tail_decay = jnp.exp(ending[None, :] - cumulative)
    leading = jnp.exp(cumulative)
    scores = jnp.dot(out_b, in_b.T, preferred_element_type=jnp.float32)
    weighted = (factor * decays * scores[:, :, None]).astype(jnp.bfloat16)
    carried_b = carried.astype(jnp.bfloat16)
    state_b = state_in.astype(jnp.bfloat16)
    grad_feats = jnp.einsum("kjh,khp->jhp", weighted, grads_b, preferred_element_type=jnp.float32)
    grad_feats = grad_feats + tail_decay[:, :, None] * jnp.einsum(
        "hpn,jn->jhp", carried_b, in_b, preferred_element_type=jnp.float32
    )
    pair_dots = jnp.einsum("khp,jhp->kjh", grads_b, inputs_b, preferred_element_type=jnp.float32)
    mixing = jnp.sum(decays * pair_dots, axis=2).astype(jnp.bfloat16)
    tail_inputs = (tail_decay[:, :, None] * inputs_b.astype(jnp.float32)).astype(jnp.bfloat16)
    lead_grads = (leading[:, :, None] * grads_b.astype(jnp.float32)).astype(jnp.bfloat16)
    grad_inmap = factor * jnp.dot(mixing.T, out_b, preferred_element_type=jnp.float32)
    grad_inmap = grad_inmap + jnp.einsum(
        "jhp,hpn->jn", tail_inputs, carried_b, preferred_element_type=jnp.float32
    )
    grad_outmap = factor * (
        jnp.dot(mixing, in_b, preferred_element_type=jnp.float32)
        + jnp.einsum("ihp,hpn->in", lead_grads, state_b, preferred_element_type=jnp.float32)
    )
    carry_out = factor * jnp.einsum(
        "khp,kn->hpn", lead_grads, out_b, preferred_element_type=jnp.float32
    )
    carry_out = carry_out + jnp.exp(ending)[:, None, None] * carried
    return (grad_feats, grad_inmap, grad_outmap, carry_out)


def block_end(inputs_b, in_b, rates, state_in):
    cumulative = jnp.cumsum(rates, axis=0)
    ending = cumulative[-1]
    tail_decay = jnp.exp(ending[None, :] - cumulative)
    tail_inputs = (tail_decay[:, :, None] * inputs_b.astype(jnp.float32)).astype(jnp.bfloat16)
    fresh = jnp.einsum("jhp,jn->hpn", tail_inputs, in_b, preferred_element_type=jnp.float32)
    return jnp.exp(ending)[:, None, None] * state_in + fresh


def split_block(inputs_c, map_block, head_count):
    length, features = inputs_c.shape
    state_size = map_block.shape[1] // 2
    inputs_b = inputs_c.reshape(length, head_count, features // head_count)
    in_b = map_block[:, :state_size]
    out_b = map_block[:, state_size:]
    return (inputs_b, in_b, out_b)


def block_back(inputs_c, map_block, rates, grads_c, carried, state_in, weights):
    length, features = inputs_c.shape
    head_count = rates.shape[1]
    factor = 0.25 / (map_block.shape[1] // 2)
    inputs_b, in_b, out_b = split_block(inputs_c, map_block, head_count)
    grads_b = grads_c.reshape(length, head_count, features // head_count)
    grad_feats, grad_inmap, grad_outmap, carry_out = block_terms(
        inputs_b, in_b, out_b, rates, grads_b, carried, state_in, factor
    )
    grad_bc = jnp.concatenate([grad_inmap, grad_outmap], axis=1).astype(jnp.bfloat16)
    back_proj = lax.dot_general(
        grad_bc, weights, (((1,), (1,)), ((), ())), preferred_element_type=jnp.float32
    )
    summed = grads_c.astype(jnp.float32) + grad_feats.reshape(length, features) + back_proj
    return (summed.astype(jnp.bfloat16), carry_out, grad_bc)


def layer_starts(inputs_s, bc_s, rates_s):
    head_count = rates_s.shape[1]
    features = inputs_s.shape[1]
    state_size = bc_s.shape[1] // 2
    block_len = inputs_s.shape[0] // MICRO
    state_now = jnp.zeros((head_count, features // head_count, state_size), jnp.float32)
    saved = []
    for block_no in range(MICRO):
        lo_row = block_no * block_len
        inputs_b, in_b, out_b = split_block(
            inputs_s[lo_row : lo_row + block_len], bc_s[lo_row : lo_row + block_len], head_count
        )
        saved.append(state_now)
        state_now = block_end(inputs_b, in_b, rates_s[lo_row : lo_row + block_len], state_now)
    return jnp.stack(saved)


def block_consts(inputs_b, in_b, out_b, rates, factor):
    length = inputs_b.shape[0]
    cumulative = jnp.cumsum(rates, axis=0)
    ending = cumulative[-1]
    locations = jnp.arange(length)
    lower_mask = (locations[:, None] >= locations[None, :])[:, :, None]
    spread = jnp.where(lower_mask, cumulative[:, None, :] - cumulative[None, :, :], 0.0)
    decays = jnp.where(lower_mask, jnp.exp(spread), 0.0)
    tail_decay = jnp.exp(ending[None, :] - cumulative)
    leading = jnp.exp(cumulative)
    scores = jnp.dot(out_b, in_b.T, preferred_element_type=jnp.float32)
    weighted = (factor * decays * scores[:, :, None]).astype(jnp.bfloat16)
    tail_inputs = (tail_decay[:, :, None] * inputs_b.astype(jnp.float32)).astype(jnp.bfloat16)
    fresh = jnp.einsum("jhp,jn->hpn", tail_inputs, in_b, preferred_element_type=jnp.float32)
    return dict(
        decays=decays,
        tail=tail_decay,
        lead=leading,
        weighted=weighted,
        tail_inputs=tail_inputs,
        fresh=fresh,
        ending=jnp.exp(ending),
    )


def step_kernel(
    wt_ref, dec_ref, v_ref, x_ref, b_ref, c_ref, tail_ref, lead_ref, xt_ref, sb_ref, r_ref, end_ref,
    w_ref, out_ref, rnew_ref, dbc_ref, gx_ref, *, factor, width
):
    f32 = jnp.float32
    bf16 = jnp.bfloat16
    length, features = v_ref.shape
    lanes = 128
    per_pair = lanes // width
    nt = (((1,), (1,)), ((), ()))
    tn = (((0,), (0,)), ((), ()))
    rb_t = r_ref[...].astype(bf16)
    in_map = b_ref[...]
    out_map = c_ref[...]
    lane_id = lax.broadcasted_iota(jnp.int32, (length, lanes), 1)
    masks = [(lane_id >= e * width) & (lane_id < (e + 1) * width) for e in range(per_pair)]
    mix_acc = jnp.zeros((per_pair * length, length), f32)
    for q in range(features // lanes):
        cols = slice(q * lanes, (q + 1) * lanes)
        v_q = v_ref[:, cols]
        x_q = x_ref[:, cols]
        stacked = jnp.concatenate([jnp.where(m, v_q, jnp.zeros_like(v_q)) for m in masks], axis=0)
        gx_q = jnp.dot(wt_ref[q], stacked, preferred_element_type=f32)
        rbb_q = jnp.dot(in_map, rb_t[:, cols], preferred_element_type=f32)
        gx_ref[:, cols] = gx_q + tail_ref[:, cols] * rbb_q
        pair_dots = lax.dot_general(stacked, x_q, nt, preferred_element_type=f32)
        mix_acc = mix_acc + dec_ref[q] * pair_dots
    mixing = mix_acc[0:length]
    for e in range(1, per_pair):
        mixing = mixing + mix_acc[e * length:(e + 1) * length]
    mixing = mixing.astype(bf16)
    v = v_ref[...]
    lead_grads = (lead_ref[...] * v.astype(f32)).astype(bf16)
    grad_inmap = factor * lax.dot_general(mixing, out_map, tn, preferred_element_type=f32)
    grad_inmap = grad_inmap + lax.dot_general(xt_ref[...], rb_t, nt, preferred_element_type=f32)
    grad_outmap = factor * (
        jnp.dot(mixing, in_map, preferred_element_type=f32)
        + lax.dot_general(lead_grads, sb_ref[...], nt, preferred_element_type=f32)
    )
    carry = factor * lax.dot_general(out_map, lead_grads, tn, preferred_element_type=f32)
    rnew_ref[...] = carry + end_ref[...] * r_ref[...]
    grad_bc = jnp.concatenate([grad_inmap, grad_outmap], axis=1).astype(bf16)
    dbc_ref[...] = grad_bc
    back = lax.dot_general(grad_bc, w_ref[...], nt, preferred_element_type=f32)
    out_ref[...] = (v.astype(f32) + gx_ref[...] + back).astype(out_ref.dtype)


def fused_step(wt, dec, v, x, in_map, out_map, tail, lead, xt, sb_t, r_t, end_col, w, factor, width):
    length, features = v.shape
    state_size = in_map.shape[1]
    vmem = pl.BlockSpec(memory_space=pltpu.VMEM)
    flops = 2 * length * features * (6 * state_size + 4 * length)
    moved = 2 * (4 * features * state_size * 2 + 6 * length * features) + 4 * 4 * length * features
    return pl.pallas_call(
        functools.partial(step_kernel, factor=factor, width=width),
        out_shape=(
            jax.ShapeDtypeStruct((length, features), jnp.bfloat16),
            jax.ShapeDtypeStruct(r_t.shape, jnp.float32),
            jax.ShapeDtypeStruct((length, 2 * state_size), jnp.bfloat16),
        ),
        in_specs=[vmem] * 13,
        out_specs=(vmem, vmem, vmem),
        scratch_shapes=[pltpu.VMEM((length, features), jnp.float32)],
        cost_estimate=pl.CostEstimate(flops=flops, bytes_accessed=moved, transcendentals=0),
    )(wt, dec, v, x, in_map, out_map, tail, lead, xt, sb_t, r_t, end_col, w)


def shards(layer_inputs, w_bc, log_decay, top_grad):
    sections = lax.axis_size("section")
    section_id = lax.axis_index("section")
    lay_dev, seq_dev, tok_len, features = layer_inputs.shape
    head_count = log_decay.shape[-1]
    block_len = tok_len // MICRO
    state_size = w_bc.shape[-1] // 2
    factor = 0.25 / state_size
    bc_all = jnp.einsum(
        "lstd,ldc->lstc", layer_inputs, w_bc, preferred_element_type=jnp.float32
    ).astype(jnp.bfloat16)

    def blocked(a):
        split = a.reshape(a.shape[:2] + (MICRO, block_len) + a.shape[3:])
        return jnp.moveaxis(split, 2, 0)

    x_blk = blocked(layer_inputs).reshape(
        (MICRO, lay_dev, seq_dev, block_len, head_count, features // head_count)
    )
    bc_blk = blocked(bc_all)
    in_blk = bc_blk[..., :state_size]
    out_blk = bc_blk[..., state_size:]
    rates_blk = blocked(log_decay)
    consts_fn = jax.vmap(jax.vmap(jax.vmap(lambda x, b, c, r: block_consts(x, b, c, r, factor))))
    consts = consts_fn(x_blk, in_blk, out_blk, rates_blk)
    width = features // head_count
    lead_dims = consts["tail"].shape[:3]
    pairs = head_count * width // 128
    per_pair = 128 // width
    weighted = jnp.swapaxes(consts["weighted"], -1, -3)
    weighted = weighted.reshape(lead_dims + (pairs, per_pair, block_len, block_len))
    wt2 = jnp.swapaxes(weighted, -3, -2).reshape(lead_dims + (pairs, block_len, per_pair * block_len))
    dec2 = jnp.moveaxis(consts["decays"], -1, -3).reshape(
        lead_dims + (pairs, per_pair * block_len, block_len)
    )
    tail_full = jnp.repeat(consts["tail"], width, axis=-1)
    lead_full = jnp.repeat(consts["lead"], width, axis=-1)
    xt_full = consts["tail_inputs"].reshape(lead_dims + (block_len, features))
    end_row = jnp.repeat(consts["ending"], width, axis=-1)[..., None, :]
    fresh_t = jnp.einsum(
        "mlsjn,mlsjd->mlsnd", in_blk, xt_full, preferred_element_type=jnp.float32
    )
    state_now = jnp.zeros(fresh_t.shape[1:], jnp.float32)
    saved = []
    for block_no in range(MICRO):
        saved.append(state_now.astype(jnp.bfloat16))
        state_now = end_row[block_no] * state_now + fresh_t[block_no]
    states_t = jnp.stack(saved)
    x_flat = x_blk.reshape(lead_dims + (block_len, features))
    per_block = (wt2, dec2, x_flat, in_blk, out_blk, tail_full, lead_full, xt_full, states_t, end_row)

    top_blk = jnp.moveaxis(
        top_grad.reshape((seq_dev, MICRO, block_len, features)), 1, 0
    )
    is_top = section_id == sections - 1

    def advance(counter, loop_state):
        incoming, carried, grad_store, map_store = loop_state
        offset = counter - (sections - 1 - section_id)
        is_valid = (offset >= 0) & (offset < MICRO)
        block_no = jnp.clip(MICRO - 1 - offset, 0, MICRO - 1)
        slot = jnp.where(is_valid, block_no, MICRO)
        from_top = lax.dynamic_index_in_dim(top_blk, block_no, 0, keepdims=False)
        current = jnp.where(is_top, from_top, incoming)
        picked = [lax.dynamic_index_in_dim(a, block_no, 0, keepdims=False) for a in per_block]
        new_carried = [[None] * seq_dev for _ in range(lay_dev)]
        for level_no in reversed(range(lay_dev)):
            level_out = []
            for seq_no in range(seq_dev):
                wt_b, dec_b, x_b, in_b, out_b, tail_b, lead_b, xt_b, st_b, end_b = [
                    a[level_no, seq_no] for a in picked
                ]
                level_grads, carry_out, grad_bc = fused_step(
                    wt_b, dec_b, current[seq_no], x_b, in_b, out_b, tail_b, lead_b, xt_b, st_b,
                    carried[level_no, seq_no], end_b, w_bc[level_no], factor, width,
                )
                new_carried[level_no][seq_no] = carry_out
                grad_store = lax.dynamic_update_slice(
                    grad_store, level_grads[None, None, None], (slot, level_no, seq_no, 0, 0)
                )
                map_store = lax.dynamic_update_slice(
                    map_store, grad_bc[None, None, None], (slot, level_no, seq_no, 0, 0)
                )
                level_out.append(level_grads)
            current = jnp.stack(level_out)
        carried = jnp.stack([jnp.stack(row) for row in new_carried])
        received = passed_along(current, "section", -1)
        return (received, carried, grad_store, map_store)

    initial = (
        jnp.zeros((seq_dev, block_len, features), jnp.bfloat16),
        jnp.zeros(states_t.shape[1:], jnp.float32),
        jnp.zeros((MICRO + 1, lay_dev, seq_dev, block_len, features), jnp.bfloat16),
        jnp.zeros((MICRO + 1, lay_dev, seq_dev, block_len, 2 * state_size), jnp.bfloat16),
    )
    final_state = lax.fori_loop(0, MICRO + sections - 1, advance, initial)
    grad_store = final_state[2]
    map_store = final_state[3]

    grad_inputs = jnp.moveaxis(grad_store[:MICRO], 0, 2).reshape(layer_inputs.shape)
    map_store = jnp.moveaxis(map_store[:MICRO], 0, 2).reshape(bc_all.shape)
    ways = lax.axis_size("dp")
    divisor = ways * seq_dev
    rows_here = layer_inputs.reshape(lay_dev, seq_dev * tok_len, features)
    rows_all = lax.all_to_all(rows_here, "dp", 2, 1, tiled=True)
    maps_here = map_store.reshape(lay_dev, seq_dev * tok_len, map_store.shape[-1])
    maps_all = lax.all_gather(maps_here, "dp", axis=1, tiled=True)
    grad_w = jnp.einsum(
        "lrd,lrc->ldc", rows_all, maps_all, preferred_element_type=jnp.float32
    ) / divisor
    return (grad_inputs, grad_w)


def solution(mesh):
    in_specs = (
        P("section", "dp", None, None),
        P("section", None, None),
        P("section", "dp", None, None),
        P("dp", None, None),
    )
    out_specs = (P("section", "dp", None, None), P("section", "dp", None))
    return jax.shard_map(shards, mesh=mesh, in_specs=in_specs, out_specs=out_specs, check_vma=False)
```

```python
import functools

import jax
import jax.numpy as jnp
from jax import lax
from jax.experimental import pallas as pl
from jax.experimental.pallas import tpu as pltpu
from jax.sharding import PartitionSpec as P

MICRO = 4


def shortened(value):
    return jax.tree.map(lambda a: a.astype(jnp.bfloat16) if a.dtype == jnp.float32 else a, value)


def passed_along(block, axis, distance):
    devices = range(lax.axis_size(axis))
    route = [(i - distance, i) for i in devices if i - distance in devices]
    return lax.ppermute(block, axis, route)


def block_terms(inputs_b, in_b, out_b, rates, grads_b, carried, state_in, factor):
    length = inputs_b.shape[0]
    cumulative = jnp.cumsum(rates, axis=0)
    ending = cumulative[-1]
    locations = jnp.arange(length)
    lower_mask = (locations[:, None] >= locations[None, :])[:, :, None]
    spread = jnp.where(lower_mask, cumulative[:, None, :] - cumulative[None, :, :], 0.0)
    decays = jnp.where(lower_mask, jnp.exp(spread), 0.0)
    tail_decay = jnp.exp(ending[None, :] - cumulative)
    leading = jnp.exp(cumulative)
    scores = jnp.dot(out_b, in_b.T, preferred_element_type=jnp.float32)
    weighted = (factor * decays * scores[:, :, None]).astype(jnp.bfloat16)
    carried_b = carried.astype(jnp.bfloat16)
    state_b = state_in.astype(jnp.bfloat16)
    grad_feats = jnp.einsum("kjh,khp->jhp", weighted, grads_b, preferred_element_type=jnp.float32)
    grad_feats = grad_feats + tail_decay[:, :, None] * jnp.einsum(
        "hpn,jn->jhp", carried_b, in_b, preferred_element_type=jnp.float32
    )
    pair_dots = jnp.einsum("khp,jhp->kjh", grads_b, inputs_b, preferred_element_type=jnp.float32)
    mixing = jnp.sum(decays * pair_dots, axis=2).astype(jnp.bfloat16)
    tail_inputs = (tail_decay[:, :, None] * inputs_b.astype(jnp.float32)).astype(jnp.bfloat16)
    lead_grads = (leading[:, :, None] * grads_b.astype(jnp.float32)).astype(jnp.bfloat16)
    grad_inmap = factor * jnp.dot(mixing.T, out_b, preferred_element_type=jnp.float32)
    grad_inmap = grad_inmap + jnp.einsum(
        "jhp,hpn->jn", tail_inputs, carried_b, preferred_element_type=jnp.float32
    )
    grad_outmap = factor * (
        jnp.dot(mixing, in_b, preferred_element_type=jnp.float32)
        + jnp.einsum("ihp,hpn->in", lead_grads, state_b, preferred_element_type=jnp.float32)
    )
    carry_out = factor * jnp.einsum(
        "khp,kn->hpn", lead_grads, out_b, preferred_element_type=jnp.float32
    )
    carry_out = carry_out + jnp.exp(ending)[:, None, None] * carried
    return (grad_feats, grad_inmap, grad_outmap, carry_out)


def block_end(inputs_b, in_b, rates, state_in):
    cumulative = jnp.cumsum(rates, axis=0)
    ending = cumulative[-1]
    tail_decay = jnp.exp(ending[None, :] - cumulative)
    tail_inputs = (tail_decay[:, :, None] * inputs_b.astype(jnp.float32)).astype(jnp.bfloat16)
    fresh = jnp.einsum("jhp,jn->hpn", tail_inputs, in_b, preferred_element_type=jnp.float32)
    return jnp.exp(ending)[:, None, None] * state_in + fresh


def split_block(inputs_c, map_block, head_count):
    length, features = inputs_c.shape
    state_size = map_block.shape[1] // 2
    inputs_b = inputs_c.reshape(length, head_count, features // head_count)
    in_b = map_block[:, :state_size]
    out_b = map_block[:, state_size:]
    return (inputs_b, in_b, out_b)


def block_back(inputs_c, map_block, rates, grads_c, carried, state_in, weights):
    length, features = inputs_c.shape
    head_count = rates.shape[1]
    factor = 0.25 / (map_block.shape[1] // 2)
    inputs_b, in_b, out_b = split_block(inputs_c, map_block, head_count)
    grads_b = grads_c.reshape(length, head_count, features // head_count)
    grad_feats, grad_inmap, grad_outmap, carry_out = block_terms(
        inputs_b, in_b, out_b, rates, grads_b, carried, state_in, factor
    )
    grad_bc = jnp.concatenate([grad_inmap, grad_outmap], axis=1).astype(jnp.bfloat16)
    back_proj = lax.dot_general(
        grad_bc, weights, (((1,), (1,)), ((), ())), preferred_element_type=jnp.float32
    )
    summed = grads_c.astype(jnp.float32) + grad_feats.reshape(length, features) + back_proj
    return (summed.astype(jnp.bfloat16), carry_out, grad_bc)


def layer_starts(inputs_s, bc_s, rates_s):
    head_count = rates_s.shape[1]
    features = inputs_s.shape[1]
    state_size = bc_s.shape[1] // 2
    block_len = inputs_s.shape[0] // MICRO
    state_now = jnp.zeros((head_count, features // head_count, state_size), jnp.float32)
    saved = []
    for block_no in range(MICRO):
        lo_row = block_no * block_len
        inputs_b, in_b, out_b = split_block(
            inputs_s[lo_row : lo_row + block_len], bc_s[lo_row : lo_row + block_len], head_count
        )
        saved.append(state_now)
        state_now = block_end(inputs_b, in_b, rates_s[lo_row : lo_row + block_len], state_now)
    return jnp.stack(saved)


def block_consts(inputs_b, in_b, out_b, rates, factor):
    length = inputs_b.shape[0]
    cumulative = jnp.cumsum(rates, axis=0)
    ending = cumulative[-1]
    locations = jnp.arange(length)
    lower_mask = (locations[:, None] >= locations[None, :])[:, :, None]
    spread = jnp.where(lower_mask, cumulative[:, None, :] - cumulative[None, :, :], 0.0)
    decays = jnp.where(lower_mask, jnp.exp(spread), 0.0)
    tail_decay = jnp.exp(ending[None, :] - cumulative)
    leading = jnp.exp(cumulative)
    scores = jnp.dot(out_b, in_b.T, preferred_element_type=jnp.float32)
    weighted = (factor * decays * scores[:, :, None]).astype(jnp.bfloat16)
    tail_inputs = (tail_decay[:, :, None] * inputs_b.astype(jnp.float32)).astype(jnp.bfloat16)
    fresh = jnp.einsum("jhp,jn->hpn", tail_inputs, in_b, preferred_element_type=jnp.float32)
    return dict(
        decays=decays,
        tail=tail_decay,
        lead=leading,
        weighted=weighted,
        tail_inputs=tail_inputs,
        fresh=fresh,
        ending=jnp.exp(ending),
    )


def step_kernel(
    picks_ref, wt_ref, dec_ref, inc_ref, top_ref, x_ref, b_ref, c_ref, tail_ref, lead_ref, xt_ref,
    sb_ref, r_ref, end_ref, w_ref, gs_ref, ms_ref, out_ref, rnew_ref, dbc_ref, gstore_ref, mstore_ref,
    v_ref, gx_ref, *, factor, width
):
    f32 = jnp.float32
    bf16 = jnp.bfloat16
    length, features = v_ref.shape
    lanes = 128
    per_pair = lanes // width
    nt = (((1,), (1,)), ((), ()))
    tn = (((0,), (0,)), ((), ()))
    v_ref[...] = jnp.where(picks_ref[1] > 0, top_ref[...], inc_ref[...])
    rb_t = r_ref[...].astype(bf16)
    in_map = b_ref[...]
    out_map = c_ref[...]
    lane_id = lax.broadcasted_iota(jnp.int32, (length, lanes), 1)
    masks = [(lane_id >= e * width) & (lane_id < (e + 1) * width) for e in range(per_pair)]
    mix_acc = jnp.zeros((per_pair * length, length), f32)
    for q in range(features // lanes):
        cols = slice(q * lanes, (q + 1) * lanes)
        v_q = v_ref[:, cols]
        x_q = x_ref[:, cols]
        stacked = jnp.concatenate([jnp.where(m, v_q, jnp.zeros_like(v_q)) for m in masks], axis=0)
        gx_q = jnp.dot(wt_ref[q], stacked, preferred_element_type=f32)
        rbb_q = jnp.dot(in_map, rb_t[:, cols], preferred_element_type=f32)
        gx_ref[:, cols] = gx_q + tail_ref[:, cols] * rbb_q
        pair_dots = lax.dot_general(stacked, x_q, nt, preferred_element_type=f32)
        mix_acc = mix_acc + dec_ref[q] * pair_dots
    mixing = mix_acc[0:length]
    for e in range(1, per_pair):
        mixing = mixing + mix_acc[e * length:(e + 1) * length]
    mixing = mixing.astype(bf16)
    v = v_ref[...]
    lead_grads = (lead_ref[...] * v.astype(f32)).astype(bf16)
    grad_inmap = factor * lax.dot_general(mixing, out_map, tn, preferred_element_type=f32)
    grad_inmap = grad_inmap + lax.dot_general(xt_ref[...], rb_t, nt, preferred_element_type=f32)
    grad_outmap = factor * (
        jnp.dot(mixing, in_map, preferred_element_type=f32)
        + lax.dot_general(lead_grads, sb_ref[...], nt, preferred_element_type=f32)
    )
    carry = factor * lax.dot_general(out_map, lead_grads, tn, preferred_element_type=f32)
    rnew_ref[...] = carry + end_ref[...] * r_ref[...]
    grad_bc = jnp.concatenate([grad_inmap, grad_outmap], axis=1).astype(bf16)
    dbc_ref[...] = grad_bc
    mstore_ref[...] = grad_bc
    back = lax.dot_general(grad_bc, w_ref[...], nt, preferred_element_type=f32)
    summed = (v.astype(f32) + gx_ref[...] + back).astype(out_ref.dtype)
    out_ref[...] = summed
    gstore_ref[...] = summed


def fused_step(picks, per_block, incoming, top_blk, carried, w_bc, grad_store, map_store, level_no, seq_no, factor, width):
    wt2, dec2, x_flat, in_blk, out_blk, tail_full, lead_full, xt_full, states_t, end_row = per_block
    length, features = incoming.shape[1:]
    state_size = in_blk.shape[-1]

    def lead_block(a):
        shape = (None, None, None) + a.shape[3:]
        tail = (0,) * (a.ndim - 3)
        return pl.BlockSpec(shape, lambda i, p: (p[0], level_no, seq_no) + tail)

    in_specs = [lead_block(a) for a in (wt2, dec2)]
    in_specs.append(pl.BlockSpec((None, length, features), lambda i, p: (seq_no, 0, 0)))
    in_specs.append(pl.BlockSpec((None, None, length, features), lambda i, p: (p[0], seq_no, 0, 0)))
    in_specs += [lead_block(a) for a in (x_flat, in_blk, out_blk, tail_full, lead_full, xt_full, states_t)]
    in_specs.append(pl.BlockSpec((None, None) + carried.shape[2:], lambda i, p: (level_no, seq_no, 0, 0)))
    in_specs.append(lead_block(end_row))
    in_specs.append(pl.BlockSpec((None,) + w_bc.shape[1:], lambda i, p: (level_no, 0, 0)))
    store_g = pl.BlockSpec((None, None, None, length, features), lambda i, p: (p[2], level_no, seq_no, 0, 0))
    store_m = pl.BlockSpec((None, None, None, length, 2 * state_size), lambda i, p: (p[2], level_no, seq_no, 0, 0))
    in_specs += [store_g, store_m]
    out_specs = (
        pl.BlockSpec((length, features), lambda i, p: (0, 0)),
        pl.BlockSpec((None, None) + carried.shape[2:], lambda i, p: (level_no, seq_no, 0, 0)),
        pl.BlockSpec((length, 2 * state_size), lambda i, p: (0, 0)),
        store_g,
        store_m,
    )
    flops = 2 * length * features * (6 * state_size + 4 * length)
    moved = 2 * (4 * features * state_size * 2 + 6 * length * features) + 4 * 4 * length * features
    return pl.pallas_call(
        functools.partial(step_kernel, factor=factor, width=width),
        out_shape=(
            jax.ShapeDtypeStruct((length, features), jnp.bfloat16),
            jax.ShapeDtypeStruct(carried.shape, jnp.float32),
            jax.ShapeDtypeStruct((length, 2 * state_size), jnp.bfloat16),
            jax.ShapeDtypeStruct(grad_store.shape, grad_store.dtype),
            jax.ShapeDtypeStruct(map_store.shape, map_store.dtype),
        ),
        grid_spec=pltpu.PrefetchScalarGridSpec(
            num_scalar_prefetch=1,
            grid=(1,),
            in_specs=in_specs,
            out_specs=out_specs,
            scratch_shapes=[
                pltpu.VMEM((length, features), jnp.bfloat16),
                pltpu.VMEM((length, features), jnp.float32),
            ],
        ),
        input_output_aliases={12: 1, 15: 3, 16: 4},
        cost_estimate=pl.CostEstimate(flops=flops, bytes_accessed=moved, transcendentals=0),
    )(picks, wt2, dec2, incoming, top_blk, x_flat, in_blk, out_blk, tail_full, lead_full, xt_full, states_t, carried, end_row, w_bc, grad_store, map_store)


def shards(layer_inputs, w_bc, log_decay, top_grad):
    sections = lax.axis_size("section")
    section_id = lax.axis_index("section")
    lay_dev, seq_dev, tok_len, features = layer_inputs.shape
    head_count = log_decay.shape[-1]
    block_len = tok_len // MICRO
    state_size = w_bc.shape[-1] // 2
    factor = 0.25 / state_size
    bc_all = jnp.einsum(
        "lstd,ldc->lstc", layer_inputs, w_bc, preferred_element_type=jnp.float32
    ).astype(jnp.bfloat16)

    def blocked(a):
        split = a.reshape(a.shape[:2] + (MICRO, block_len) + a.shape[3:])
        return jnp.moveaxis(split, 2, 0)

    x_blk = blocked(layer_inputs).reshape(
        (MICRO, lay_dev, seq_dev, block_len, head_count, features // head_count)
    )
    bc_blk = blocked(bc_all)
    in_blk = bc_blk[..., :state_size]
    out_blk = bc_blk[..., state_size:]
    rates_blk = blocked(log_decay)
    consts_fn = jax.vmap(jax.vmap(jax.vmap(lambda x, b, c, r: block_consts(x, b, c, r, factor))))
    consts = consts_fn(x_blk, in_blk, out_blk, rates_blk)
    width = features // head_count
    lead_dims = consts["tail"].shape[:3]
    pairs = head_count * width // 128
    per_pair = 128 // width
    weighted = jnp.swapaxes(consts["weighted"], -1, -3)
    weighted = weighted.reshape(lead_dims + (pairs, per_pair, block_len, block_len))
    wt2 = jnp.swapaxes(weighted, -3, -2).reshape(lead_dims + (pairs, block_len, per_pair * block_len))
    dec2 = jnp.moveaxis(consts["decays"], -1, -3).reshape(
        lead_dims + (pairs, per_pair * block_len, block_len)
    )
    tail_full = jnp.repeat(consts["tail"], width, axis=-1)
    lead_full = jnp.repeat(consts["lead"], width, axis=-1)
    xt_full = consts["tail_inputs"].reshape(lead_dims + (block_len, features))
    end_row = jnp.repeat(consts["ending"], width, axis=-1)[..., None, :]
    fresh_t = jnp.einsum(
        "mlsjn,mlsjd->mlsnd", in_blk, xt_full, preferred_element_type=jnp.float32
    )
    state_now = jnp.zeros(fresh_t.shape[1:], jnp.float32)
    saved = []
    for block_no in range(MICRO):
        saved.append(state_now.astype(jnp.bfloat16))
        state_now = end_row[block_no] * state_now + fresh_t[block_no]
    states_t = jnp.stack(saved)
    x_flat = x_blk.reshape(lead_dims + (block_len, features))
    per_block = (wt2, dec2, x_flat, in_blk, out_blk, tail_full, lead_full, xt_full, states_t, end_row)

    top_blk = jnp.moveaxis(
        top_grad.reshape((seq_dev, MICRO, block_len, features)), 1, 0
    )
    is_top = section_id == sections - 1

    def advance(counter, loop_state):
        incoming, carried, grad_store, map_store = loop_state
        offset = counter - (sections - 1 - section_id)
        is_valid = (offset >= 0) & (offset < MICRO)
        block_no = jnp.clip(MICRO - 1 - offset, 0, MICRO - 1)
        slot = jnp.where(is_valid, block_no, MICRO)
        picks = jnp.stack([block_no, is_top.astype(jnp.int32), slot]).astype(jnp.int32)
        for level_no in reversed(range(lay_dev)):
            level_out = []
            for seq_no in range(seq_dev):
                level_grads, carried, grad_bc, grad_store, map_store = fused_step(
                    picks, per_block, incoming, top_blk, carried, w_bc, grad_store, map_store,
                    level_no, seq_no, factor, width,
                )
                level_out.append(level_grads)
            incoming = jnp.stack(level_out)
            picks = picks.at[1].set(0)
        received = passed_along(incoming, "section", -1)
        return (received, carried, grad_store, map_store)

    initial = (
        jnp.zeros((seq_dev, block_len, features), jnp.bfloat16),
        jnp.zeros(states_t.shape[1:], jnp.float32),
        jnp.zeros((MICRO + 1, lay_dev, seq_dev, block_len, features), jnp.bfloat16),
        jnp.zeros((MICRO + 1, lay_dev, seq_dev, block_len, 2 * state_size), jnp.bfloat16),
    )
    final_state = lax.fori_loop(0, MICRO + sections - 1, advance, initial)
    grad_store = final_state[2]
    map_store = final_state[3]

    grad_inputs = jnp.moveaxis(grad_store[:MICRO], 0, 2).reshape(layer_inputs.shape)
    map_store = jnp.moveaxis(map_store[:MICRO], 0, 2).reshape(bc_all.shape)
    ways = lax.axis_size("dp")
    divisor = ways * seq_dev
    rows_here = layer_inputs.reshape(lay_dev, seq_dev * tok_len, features)
    rows_all = lax.all_to_all(rows_here, "dp", 2, 1, tiled=True)
    maps_here = map_store.reshape(lay_dev, seq_dev * tok_len, map_store.shape[-1])
    maps_all = lax.all_gather(maps_here, "dp", axis=1, tiled=True)
    grad_w = jnp.einsum(
        "lrd,lrc->ldc", rows_all, maps_all, preferred_element_type=jnp.float32
    ) / divisor
    return (grad_inputs, grad_w)


def solution(mesh):
    in_specs = (
        P("section", "dp", None, None),
        P("section", None, None),
        P("section", "dp", None, None),
        P("dp", None, None),
    )
    out_specs = (P("section", "dp", None, None), P("section", "dp", None))
    return jax.shard_map(shards, mesh=mesh, in_specs=in_specs, out_specs=out_specs, check_vma=False)
```

```python
import functools

import jax
import jax.numpy as jnp
from jax import lax
from jax.experimental import pallas as pl
from jax.experimental.pallas import tpu as pltpu
from jax.sharding import PartitionSpec as P

MICRO = 4


def shortened(value):
    return jax.tree.map(lambda a: a.astype(jnp.bfloat16) if a.dtype == jnp.float32 else a, value)


def passed_along(block, axis, distance):
    devices = range(lax.axis_size(axis))
    route = [(i - distance, i) for i in devices if i - distance in devices]
    return lax.ppermute(block, axis, route)


def block_terms(inputs_b, in_b, out_b, rates, grads_b, carried, state_in, factor):
    length = inputs_b.shape[0]
    cumulative = jnp.cumsum(rates, axis=0)
    ending = cumulative[-1]
    locations = jnp.arange(length)
    lower_mask = (locations[:, None] >= locations[None, :])[:, :, None]
    spread = jnp.where(lower_mask, cumulative[:, None, :] - cumulative[None, :, :], 0.0)
    decays = jnp.where(lower_mask, jnp.exp(spread), 0.0)
    tail_decay = jnp.exp(ending[None, :] - cumulative)
    leading = jnp.exp(cumulative)
    scores = jnp.dot(out_b, in_b.T, preferred_element_type=jnp.float32)
    weighted = (factor * decays * scores[:, :, None]).astype(jnp.bfloat16)
    carried_b = carried.astype(jnp.bfloat16)
    state_b = state_in.astype(jnp.bfloat16)
    grad_feats = jnp.einsum("kjh,khp->jhp", weighted, grads_b, preferred_element_type=jnp.float32)
    grad_feats = grad_feats + tail_decay[:, :, None] * jnp.einsum(
        "hpn,jn->jhp", carried_b, in_b, preferred_element_type=jnp.float32
    )
    pair_dots = jnp.einsum("khp,jhp->kjh", grads_b, inputs_b, preferred_element_type=jnp.float32)
    mixing = jnp.sum(decays * pair_dots, axis=2).astype(jnp.bfloat16)
    tail_inputs = (tail_decay[:, :, None] * inputs_b.astype(jnp.float32)).astype(jnp.bfloat16)
    lead_grads = (leading[:, :, None] * grads_b.astype(jnp.float32)).astype(jnp.bfloat16)
    grad_inmap = factor * jnp.dot(mixing.T, out_b, preferred_element_type=jnp.float32)
    grad_inmap = grad_inmap + jnp.einsum(
        "jhp,hpn->jn", tail_inputs, carried_b, preferred_element_type=jnp.float32
    )
    grad_outmap = factor * (
        jnp.dot(mixing, in_b, preferred_element_type=jnp.float32)
        + jnp.einsum("ihp,hpn->in", lead_grads, state_b, preferred_element_type=jnp.float32)
    )
    carry_out = factor * jnp.einsum(
        "khp,kn->hpn", lead_grads, out_b, preferred_element_type=jnp.float32
    )
    carry_out = carry_out + jnp.exp(ending)[:, None, None] * carried
    return (grad_feats, grad_inmap, grad_outmap, carry_out)


def block_end(inputs_b, in_b, rates, state_in):
    cumulative = jnp.cumsum(rates, axis=0)
    ending = cumulative[-1]
    tail_decay = jnp.exp(ending[None, :] - cumulative)
    tail_inputs = (tail_decay[:, :, None] * inputs_b.astype(jnp.float32)).astype(jnp.bfloat16)
    fresh = jnp.einsum("jhp,jn->hpn", tail_inputs, in_b, preferred_element_type=jnp.float32)
    return jnp.exp(ending)[:, None, None] * state_in + fresh


def split_block(inputs_c, map_block, head_count):
    length, features = inputs_c.shape
    state_size = map_block.shape[1] // 2
    inputs_b = inputs_c.reshape(length, head_count, features // head_count)
    in_b = map_block[:, :state_size]
    out_b = map_block[:, state_size:]
    return (inputs_b, in_b, out_b)


def block_back(inputs_c, map_block, rates, grads_c, carried, state_in, weights):
    length, features = inputs_c.shape
    head_count = rates.shape[1]
    factor = 0.25 / (map_block.shape[1] // 2)
    inputs_b, in_b, out_b = split_block(inputs_c, map_block, head_count)
    grads_b = grads_c.reshape(length, head_count, features // head_count)
    grad_feats, grad_inmap, grad_outmap, carry_out = block_terms(
        inputs_b, in_b, out_b, rates, grads_b, carried, state_in, factor
    )
    grad_bc = jnp.concatenate([grad_inmap, grad_outmap], axis=1).astype(jnp.bfloat16)
    back_proj = lax.dot_general(
        grad_bc, weights, (((1,), (1,)), ((), ())), preferred_element_type=jnp.float32
    )
    summed = grads_c.astype(jnp.float32) + grad_feats.reshape(length, features) + back_proj
    return (summed.astype(jnp.bfloat16), carry_out, grad_bc)


def layer_starts(inputs_s, bc_s, rates_s):
    head_count = rates_s.shape[1]
    features = inputs_s.shape[1]
    state_size = bc_s.shape[1] // 2
    block_len = inputs_s.shape[0] // MICRO
    state_now = jnp.zeros((head_count, features // head_count, state_size), jnp.float32)
    saved = []
    for block_no in range(MICRO):
        lo_row = block_no * block_len
        inputs_b, in_b, out_b = split_block(
            inputs_s[lo_row : lo_row + block_len], bc_s[lo_row : lo_row + block_len], head_count
        )
        saved.append(state_now)
        state_now = block_end(inputs_b, in_b, rates_s[lo_row : lo_row + block_len], state_now)
    return jnp.stack(saved)


def block_consts(inputs_b, in_b, out_b, rates, factor):
    length = inputs_b.shape[0]
    cumulative = jnp.cumsum(rates, axis=0)
    ending = cumulative[-1]
    locations = jnp.arange(length)
    lower_mask = (locations[:, None] >= locations[None, :])[:, :, None]
    spread = jnp.where(lower_mask, cumulative[:, None, :] - cumulative[None, :, :], 0.0)
    decays = jnp.where(lower_mask, jnp.exp(spread), 0.0)
    tail_decay = jnp.exp(ending[None, :] - cumulative)
    leading = jnp.exp(cumulative)
    scores = jnp.dot(out_b, in_b.T, preferred_element_type=jnp.float32)
    weighted = (factor * decays * scores[:, :, None]).astype(jnp.bfloat16)
    tail_inputs = (tail_decay[:, :, None] * inputs_b.astype(jnp.float32)).astype(jnp.bfloat16)
    fresh = jnp.einsum("jhp,jn->hpn", tail_inputs, in_b, preferred_element_type=jnp.float32)
    return dict(
        decays=decays,
        tail=tail_decay,
        lead=leading,
        weighted=weighted,
        tail_inputs=tail_inputs,
        fresh=fresh,
        ending=jnp.exp(ending),
    )


def step_kernel(
    picks_ref, wt_ref, dec_ref, inc_ref, top_ref, x_ref, b_ref, c_ref, tail_ref, lead_ref, xt_ref,
    sb_ref, r_ref, end_ref, w_ref, gs_ref, ms_ref, out_ref, rnew_ref, dbc_ref, gstore_ref, mstore_ref,
    v_ref, gx_ref, *, factor, width
):
    f32 = jnp.float32
    bf16 = jnp.bfloat16
    length, features = v_ref.shape
    lanes = 128
    per_pair = lanes // width
    nt = (((1,), (1,)), ((), ()))
    tn = (((0,), (0,)), ((), ()))
    v_ref[...] = jnp.where(picks_ref[1] > 0, top_ref[...], inc_ref[...])
    rb_t = r_ref[...].astype(bf16)
    in_map = b_ref[...]
    out_map = c_ref[...]
    lane_id = lax.broadcasted_iota(jnp.int32, (length, lanes), 1)
    masks = [(lane_id >= e * width) & (lane_id < (e + 1) * width) for e in range(per_pair)]
    mix_acc = jnp.zeros((per_pair * length, length), f32)
    for q in range(features // lanes):
        cols = slice(q * lanes, (q + 1) * lanes)
        v_q = v_ref[:, cols]
        x_q = x_ref[:, cols]
        stacked = jnp.concatenate([jnp.where(m, v_q, jnp.zeros_like(v_q)) for m in masks], axis=0)
        gx_q = jnp.dot(wt_ref[q], stacked, preferred_element_type=f32)
        rbb_q = jnp.dot(in_map, rb_t[:, cols], preferred_element_type=f32)
        gx_ref[:, cols] = gx_q + tail_ref[:, cols] * rbb_q
        pair_dots = lax.dot_general(stacked, x_q, nt, preferred_element_type=f32)
        mix_acc = mix_acc + dec_ref[q] * pair_dots
    mixing = mix_acc[0:length]
    for e in range(1, per_pair):
        mixing = mixing + mix_acc[e * length:(e + 1) * length]
    mixing = mixing.astype(bf16)
    v = v_ref[...]
    lead_grads = (lead_ref[...] * v.astype(f32)).astype(bf16)
    grad_inmap = factor * lax.dot_general(mixing, out_map, tn, preferred_element_type=f32)
    grad_inmap = grad_inmap + lax.dot_general(xt_ref[...], rb_t, nt, preferred_element_type=f32)
    grad_outmap = factor * (
        jnp.dot(mixing, in_map, preferred_element_type=f32)
        + lax.dot_general(lead_grads, sb_ref[...], nt, preferred_element_type=f32)
    )
    carry = factor * lax.dot_general(out_map, lead_grads, tn, preferred_element_type=f32)
    rnew_ref[...] = carry + end_ref[...] * r_ref[...]
    grad_bc = jnp.concatenate([grad_inmap, grad_outmap], axis=1).astype(bf16)
    dbc_ref[...] = grad_bc
    mstore_ref[...] = grad_bc
    back = lax.dot_general(grad_bc, w_ref[...], nt, preferred_element_type=f32)
    summed = (v.astype(f32) + gx_ref[...] + back).astype(out_ref.dtype)
    out_ref[...] = summed
    gstore_ref[...] = summed


def fused_step(picks, per_block, incoming, top_blk, carried, w_bc, grad_store, map_store, level_no, seq_no, factor, width):
    wt2, dec2, x_flat, in_blk, out_blk, tail_full, lead_full, xt_full, states_t, end_row = per_block
    length, features = incoming.shape[1:]
    state_size = in_blk.shape[-1]

    def lead_block(a):
        shape = (None, None, None) + a.shape[3:]
        tail = (0,) * (a.ndim - 3)
        return pl.BlockSpec(shape, lambda i, p: (p[0], level_no, seq_no) + tail)

    in_specs = [lead_block(a) for a in (wt2, dec2)]
    in_specs.append(pl.BlockSpec((None, length, features), lambda i, p: (seq_no, 0, 0)))
    in_specs.append(pl.BlockSpec((None, None, length, features), lambda i, p: (p[0], seq_no, 0, 0)))
    in_specs += [lead_block(a) for a in (x_flat, in_blk, out_blk, tail_full, lead_full, xt_full, states_t)]
    in_specs.append(pl.BlockSpec((None, None) + carried.shape[2:], lambda i, p: (level_no, seq_no, 0, 0)))
    in_specs.append(lead_block(end_row))
    in_specs.append(pl.BlockSpec((None,) + w_bc.shape[1:], lambda i, p: (level_no, 0, 0)))
    store_g = pl.BlockSpec((None, None, None, length, features), lambda i, p: (p[2], level_no, seq_no, 0, 0))
    store_m = pl.BlockSpec((None, None, None, length, 2 * state_size), lambda i, p: (p[2], level_no, seq_no, 0, 0))
    in_specs += [store_g, store_m]
    out_specs = (
        pl.BlockSpec((length, features), lambda i, p: (0, 0)),
        pl.BlockSpec((None, None) + carried.shape[2:], lambda i, p: (level_no, seq_no, 0, 0)),
        pl.BlockSpec((length, 2 * state_size), lambda i, p: (0, 0)),
        store_g,
        store_m,
    )
    flops = 2 * length * features * (6 * state_size + 4 * length)
    moved = 2 * (4 * features * state_size * 2 + 6 * length * features) + 4 * 4 * length * features
    return pl.pallas_call(
        functools.partial(step_kernel, factor=factor, width=width),
        out_shape=(
            jax.ShapeDtypeStruct((length, features), jnp.bfloat16),
            jax.ShapeDtypeStruct(carried.shape, jnp.float32),
            jax.ShapeDtypeStruct((length, 2 * state_size), jnp.bfloat16),
            jax.ShapeDtypeStruct(grad_store.shape, grad_store.dtype),
            jax.ShapeDtypeStruct(map_store.shape, map_store.dtype),
        ),
        grid_spec=pltpu.PrefetchScalarGridSpec(
            num_scalar_prefetch=1,
            grid=(1,),
            in_specs=in_specs,
            out_specs=out_specs,
            scratch_shapes=[
                pltpu.VMEM((length, features), jnp.bfloat16),
                pltpu.VMEM((length, features), jnp.float32),
            ],
        ),
        input_output_aliases={12: 1, 15: 3, 16: 4},
        cost_estimate=pl.CostEstimate(flops=flops, bytes_accessed=moved, transcendentals=0),
    )(picks, wt2, dec2, incoming, top_blk, x_flat, in_blk, out_blk, tail_full, lead_full, xt_full, states_t, carried, end_row, w_bc, grad_store, map_store)


def shards(layer_inputs, w_bc, log_decay, top_grad):
    sections = lax.axis_size("section")
    section_id = lax.axis_index("section")
    lay_dev, seq_dev, tok_len, features = layer_inputs.shape
    head_count = log_decay.shape[-1]
    block_len = tok_len // MICRO
    state_size = w_bc.shape[-1] // 2
    factor = 0.25 / state_size
    bc_all = jnp.einsum(
        "lstd,ldc->lstc", layer_inputs, w_bc, preferred_element_type=jnp.float32
    ).astype(jnp.bfloat16)

    def blocked(a):
        split = a.reshape(a.shape[:2] + (MICRO, block_len) + a.shape[3:])
        return jnp.moveaxis(split, 2, 0)

    x_blk = blocked(layer_inputs).reshape(
        (MICRO, lay_dev, seq_dev, block_len, head_count, features // head_count)
    )
    bc_blk = blocked(bc_all)
    in_blk = bc_blk[..., :state_size]
    out_blk = bc_blk[..., state_size:]
    rates_blk = blocked(log_decay)
    consts_fn = jax.vmap(jax.vmap(jax.vmap(lambda x, b, c, r: block_consts(x, b, c, r, factor))))
    consts = consts_fn(x_blk, in_blk, out_blk, rates_blk)
    width = features // head_count
    lead_dims = consts["tail"].shape[:3]
    pairs = head_count * width // 128
    per_pair = 128 // width
    weighted = jnp.swapaxes(consts["weighted"], -1, -3)
    weighted = weighted.reshape(lead_dims + (pairs, per_pair, block_len, block_len))
    wt2 = jnp.swapaxes(weighted, -3, -2).reshape(lead_dims + (pairs, block_len, per_pair * block_len))
    dec2 = jnp.moveaxis(consts["decays"], -1, -3).reshape(
        lead_dims + (pairs, per_pair * block_len, block_len)
    )
    tail_full = jnp.repeat(consts["tail"], width, axis=-1)
    lead_full = jnp.repeat(consts["lead"], width, axis=-1)
    xt_full = consts["tail_inputs"].reshape(lead_dims + (block_len, features))
    end_row = jnp.repeat(consts["ending"], width, axis=-1)[..., None, :]
    fresh_t = jnp.einsum(
        "mlsjn,mlsjd->mlsnd", in_blk, xt_full, preferred_element_type=jnp.float32
    )
    state_now = jnp.zeros(fresh_t.shape[1:], jnp.float32)
    saved = []
    for block_no in range(MICRO):
        saved.append(state_now.astype(jnp.bfloat16))
        state_now = end_row[block_no] * state_now + fresh_t[block_no]
    states_t = jnp.stack(saved)
    x_flat = x_blk.reshape(lead_dims + (block_len, features))
    per_block = (wt2, dec2, x_flat, in_blk, out_blk, tail_full, lead_full, xt_full, states_t, end_row)
    per_block = lax.optimization_barrier(per_block)

    top_blk = jnp.moveaxis(
        top_grad.reshape((seq_dev, MICRO, block_len, features)), 1, 0
    )
    is_top = section_id == sections - 1

    def advance(counter, loop_state):
        incoming, carried, grad_store, map_store = loop_state
        offset = counter - (sections - 1 - section_id)
        is_valid = (offset >= 0) & (offset < MICRO)
        block_no = jnp.clip(MICRO - 1 - offset, 0, MICRO - 1)
        slot = jnp.where(is_valid, block_no, MICRO)
        picks = jnp.stack([block_no, is_top.astype(jnp.int32), slot]).astype(jnp.int32)
        for level_no in reversed(range(lay_dev)):
            level_out = []
            for seq_no in range(seq_dev):
                level_grads, carried, grad_bc, grad_store, map_store = fused_step(
                    picks, per_block, incoming, top_blk, carried, w_bc, grad_store, map_store,
                    level_no, seq_no, factor, width,
                )
                level_out.append(level_grads)
            incoming = jnp.stack(level_out)
            picks = picks.at[1].set(0)
        received = passed_along(incoming, "section", -1)
        return (received, carried, grad_store, map_store)

    initial = (
        jnp.zeros((seq_dev, block_len, features), jnp.bfloat16),
        jnp.zeros(states_t.shape[1:], jnp.float32),
        jnp.zeros((MICRO + 1, lay_dev, seq_dev, block_len, features), jnp.bfloat16),
        jnp.zeros((MICRO + 1, lay_dev, seq_dev, block_len, 2 * state_size), jnp.bfloat16),
    )
    final_state = lax.fori_loop(0, MICRO + sections - 1, advance, initial)
    grad_store = final_state[2]
    map_store = final_state[3]

    grad_inputs = jnp.moveaxis(grad_store[:MICRO], 0, 2).reshape(layer_inputs.shape)
    map_store = jnp.moveaxis(map_store[:MICRO], 0, 2).reshape(bc_all.shape)
    ways = lax.axis_size("dp")
    divisor = ways * seq_dev
    rows_here = layer_inputs.reshape(lay_dev, seq_dev * tok_len, features)
    rows_all = lax.all_to_all(rows_here, "dp", 2, 1, tiled=True)
    maps_here = map_store.reshape(lay_dev, seq_dev * tok_len, map_store.shape[-1])
    maps_all = lax.all_gather(maps_here, "dp", axis=1, tiled=True)
    grad_w = jnp.einsum(
        "lrd,lrc->ldc", rows_all, maps_all, preferred_element_type=jnp.float32
    ) / divisor
    return (grad_inputs, grad_w)


def solution(mesh):
    in_specs = (
        P("section", "dp", None, None),
        P("section", None, None),
        P("section", "dp", None, None),
        P("dp", None, None),
    )
    out_specs = (P("section", "dp", None, None), P("section", "dp", None))
    return jax.shard_map(shards, mesh=mesh, in_specs=in_specs, out_specs=out_specs, check_vma=False)
```

```python
import functools

import jax
import jax.numpy as jnp
from jax import lax
from jax.experimental import pallas as pl
from jax.experimental.pallas import tpu as pltpu
from jax.sharding import PartitionSpec as P

MICRO = 4


def shortened(value):
    return jax.tree.map(lambda a: a.astype(jnp.bfloat16) if a.dtype == jnp.float32 else a, value)


def passed_along(block, axis, distance):
    devices = range(lax.axis_size(axis))
    route = [(i - distance, i) for i in devices if i - distance in devices]
    return lax.ppermute(block, axis, route)


def block_terms(inputs_b, in_b, out_b, rates, grads_b, carried, state_in, factor):
    length = inputs_b.shape[0]
    cumulative = jnp.cumsum(rates, axis=0)
    ending = cumulative[-1]
    locations = jnp.arange(length)
    lower_mask = (locations[:, None] >= locations[None, :])[:, :, None]
    spread = jnp.where(lower_mask, cumulative[:, None, :] - cumulative[None, :, :], 0.0)
    decays = jnp.where(lower_mask, jnp.exp(spread), 0.0)
    tail_decay = jnp.exp(ending[None, :] - cumulative)
    leading = jnp.exp(cumulative)
    scores = jnp.dot(out_b, in_b.T, preferred_element_type=jnp.float32)
    weighted = (factor * decays * scores[:, :, None]).astype(jnp.bfloat16)
    carried_b = carried.astype(jnp.bfloat16)
    state_b = state_in.astype(jnp.bfloat16)
    grad_feats = jnp.einsum("kjh,khp->jhp", weighted, grads_b, preferred_element_type=jnp.float32)
    grad_feats = grad_feats + tail_decay[:, :, None] * jnp.einsum(
        "hpn,jn->jhp", carried_b, in_b, preferred_element_type=jnp.float32
    )
    pair_dots = jnp.einsum("khp,jhp->kjh", grads_b, inputs_b, preferred_element_type=jnp.float32)
    mixing = jnp.sum(decays * pair_dots, axis=2).astype(jnp.bfloat16)
    tail_inputs = (tail_decay[:, :, None] * inputs_b.astype(jnp.float32)).astype(jnp.bfloat16)
    lead_grads = (leading[:, :, None] * grads_b.astype(jnp.float32)).astype(jnp.bfloat16)
    grad_inmap = factor * jnp.dot(mixing.T, out_b, preferred_element_type=jnp.float32)
    grad_inmap = grad_inmap + jnp.einsum(
        "jhp,hpn->jn", tail_inputs, carried_b, preferred_element_type=jnp.float32
    )
    grad_outmap = factor * (
        jnp.dot(mixing, in_b, preferred_element_type=jnp.float32)
        + jnp.einsum("ihp,hpn->in", lead_grads, state_b, preferred_element_type=jnp.float32)
    )
    carry_out = factor * jnp.einsum(
        "khp,kn->hpn", lead_grads, out_b, preferred_element_type=jnp.float32
    )
    carry_out = carry_out + jnp.exp(ending)[:, None, None] * carried
    return (grad_feats, grad_inmap, grad_outmap, carry_out)


def block_end(inputs_b, in_b, rates, state_in):
    cumulative = jnp.cumsum(rates, axis=0)
    ending = cumulative[-1]
    tail_decay = jnp.exp(ending[None, :] - cumulative)
    tail_inputs = (tail_decay[:, :, None] * inputs_b.astype(jnp.float32)).astype(jnp.bfloat16)
    fresh = jnp.einsum("jhp,jn->hpn", tail_inputs, in_b, preferred_element_type=jnp.float32)
    return jnp.exp(ending)[:, None, None] * state_in + fresh


def split_block(inputs_c, map_block, head_count):
    length, features = inputs_c.shape
    state_size = map_block.shape[1] // 2
    inputs_b = inputs_c.reshape(length, head_count, features // head_count)
    in_b = map_block[:, :state_size]
    out_b = map_block[:, state_size:]
    return (inputs_b, in_b, out_b)


def block_back(inputs_c, map_block, rates, grads_c, carried, state_in, weights):
    length, features = inputs_c.shape
    head_count = rates.shape[1]
    factor = 0.25 / (map_block.shape[1] // 2)
    inputs_b, in_b, out_b = split_block(inputs_c, map_block, head_count)
    grads_b = grads_c.reshape(length, head_count, features // head_count)
    grad_feats, grad_inmap, grad_outmap, carry_out = block_terms(
        inputs_b, in_b, out_b, rates, grads_b, carried, state_in, factor
    )
    grad_bc = jnp.concatenate([grad_inmap, grad_outmap], axis=1).astype(jnp.bfloat16)
    back_proj = lax.dot_general(
        grad_bc, weights, (((1,), (1,)), ((), ())), preferred_element_type=jnp.float32
    )
    summed = grads_c.astype(jnp.float32) + grad_feats.reshape(length, features) + back_proj
    return (summed.astype(jnp.bfloat16), carry_out, grad_bc)


def layer_starts(inputs_s, bc_s, rates_s):
    head_count = rates_s.shape[1]
    features = inputs_s.shape[1]
    state_size = bc_s.shape[1] // 2
    block_len = inputs_s.shape[0] // MICRO
    state_now = jnp.zeros((head_count, features // head_count, state_size), jnp.float32)
    saved = []
    for block_no in range(MICRO):
        lo_row = block_no * block_len
        inputs_b, in_b, out_b = split_block(
            inputs_s[lo_row : lo_row + block_len], bc_s[lo_row : lo_row + block_len], head_count
        )
        saved.append(state_now)
        state_now = block_end(inputs_b, in_b, rates_s[lo_row : lo_row + block_len], state_now)
    return jnp.stack(saved)


def block_consts(inputs_b, in_b, out_b, rates, factor):
    length = inputs_b.shape[0]
    cumulative = jnp.cumsum(rates, axis=0)
    ending = cumulative[-1]
    locations = jnp.arange(length)
    lower_mask = (locations[:, None] >= locations[None, :])[:, :, None]
    spread = jnp.where(lower_mask, cumulative[:, None, :] - cumulative[None, :, :], 0.0)
    decays = jnp.where(lower_mask, jnp.exp(spread), 0.0)
    tail_decay = jnp.exp(ending[None, :] - cumulative)
    leading = jnp.exp(cumulative)
    scores = jnp.dot(out_b, in_b.T, preferred_element_type=jnp.float32)
    weighted = (factor * decays * scores[:, :, None]).astype(jnp.bfloat16)
    tail_inputs = (tail_decay[:, :, None] * inputs_b.astype(jnp.float32)).astype(jnp.bfloat16)
    fresh = jnp.einsum("jhp,jn->hpn", tail_inputs, in_b, preferred_element_type=jnp.float32)
    return dict(
        decays=decays,
        tail=tail_decay,
        lead=leading,
        weighted=weighted,
        tail_inputs=tail_inputs,
        fresh=fresh,
        ending=jnp.exp(ending),
    )


def step_kernel(
    picks_ref, wt_ref, dec_ref, inc_ref, top_ref, x_ref, b_ref, c_ref, tail_ref, lead_ref, xt_ref,
    sb_ref, r_ref, end_ref, w_ref, gs_ref, ms_ref, out_ref, rnew_ref, dbc_ref, gstore_ref, mstore_ref,
    v_ref, gx_ref, *, factor, width
):
    f32 = jnp.float32
    bf16 = jnp.bfloat16
    length, features = v_ref.shape
    lanes = 128
    per_pair = lanes // width
    nt = (((1,), (1,)), ((), ()))
    tn = (((0,), (0,)), ((), ()))
    v_ref[...] = jnp.where(picks_ref[1] > 0, top_ref[...], inc_ref[...])
    rb_t = r_ref[...].astype(bf16)
    in_map = b_ref[...]
    out_map = c_ref[...]
    lane_id = lax.broadcasted_iota(jnp.int32, (length, lanes), 1)
    masks = [(lane_id >= e * width) & (lane_id < (e + 1) * width) for e in range(per_pair)]
    mix_acc = jnp.zeros((per_pair * length, length), f32)
    for q in range(features // lanes):
        cols = slice(q * lanes, (q + 1) * lanes)
        v_q = v_ref[:, cols]
        x_q = x_ref[:, cols]
        stacked = jnp.concatenate([jnp.where(m, v_q, jnp.zeros_like(v_q)) for m in masks], axis=0)
        gx_q = jnp.dot(wt_ref[q], stacked, preferred_element_type=f32)
        rbb_q = jnp.dot(in_map, rb_t[:, cols], preferred_element_type=f32)
        gx_ref[:, cols] = gx_q + tail_ref[:, cols] * rbb_q
        pair_dots = lax.dot_general(stacked, x_q, nt, preferred_element_type=f32)
        mix_acc = mix_acc + dec_ref[q] * pair_dots
    mixing = mix_acc[0:length]
    for e in range(1, per_pair):
        mixing = mixing + mix_acc[e * length:(e + 1) * length]
    mixing = mixing.astype(bf16)
    v = v_ref[...]
    lead_grads = (lead_ref[...] * v.astype(f32)).astype(bf16)
    grad_inmap = factor * lax.dot_general(mixing, out_map, tn, preferred_element_type=f32)
    grad_inmap = grad_inmap + lax.dot_general(xt_ref[...], rb_t, nt, preferred_element_type=f32)
    grad_outmap = factor * (
        jnp.dot(mixing, in_map, preferred_element_type=f32)
        + lax.dot_general(lead_grads, sb_ref[...], nt, preferred_element_type=f32)
    )
    carry = factor * lax.dot_general(out_map, lead_grads, tn, preferred_element_type=f32)
    rnew_ref[...] = carry + end_ref[...] * r_ref[...]
    grad_bc = jnp.concatenate([grad_inmap, grad_outmap], axis=1).astype(bf16)
    dbc_ref[...] = grad_bc
    mstore_ref[...] = grad_bc
    back = lax.dot_general(grad_bc, w_ref[...], nt, preferred_element_type=f32)
    summed = (v.astype(f32) + gx_ref[...] + back).astype(out_ref.dtype)
    out_ref[...] = summed
    gstore_ref[...] = summed


def fused_step(picks, per_block, incoming, top_blk, carried, w_bc, grad_store, map_store, level_no, seq_no, factor, width):
    wt2, dec2, x_flat, in_blk, out_blk, tail_full, lead_full, xt_full, states_t, end_row = per_block
    length, features = incoming.shape[1:]
    state_size = in_blk.shape[-1]

    def lead_block(a):
        shape = (None, None, None) + a.shape[3:]
        tail = (0,) * (a.ndim - 3)
        return pl.BlockSpec(shape, lambda i, p: (p[0], level_no, seq_no) + tail)

    in_specs = [lead_block(a) for a in (wt2, dec2)]
    in_specs.append(pl.BlockSpec((None, length, features), lambda i, p: (seq_no, 0, 0)))
    in_specs.append(pl.BlockSpec((None, None, length, features), lambda i, p: (p[0], seq_no, 0, 0)))
    in_specs += [lead_block(a) for a in (x_flat, in_blk, out_blk, tail_full, lead_full, xt_full, states_t)]
    in_specs.append(pl.BlockSpec((None, None) + carried.shape[2:], lambda i, p: (level_no, seq_no, 0, 0)))
    in_specs.append(lead_block(end_row))
    in_specs.append(pl.BlockSpec((None,) + w_bc.shape[1:], lambda i, p: (level_no, 0, 0)))
    store_g = pl.BlockSpec((None, None, None, length, features), lambda i, p: (p[2], level_no, seq_no, 0, 0))
    store_m = pl.BlockSpec((None, None, None, length, 2 * state_size), lambda i, p: (p[2], level_no, seq_no, 0, 0))
    in_specs += [store_g, store_m]
    out_specs = (
        pl.BlockSpec((length, features), lambda i, p: (0, 0)),
        pl.BlockSpec((None, None) + carried.shape[2:], lambda i, p: (level_no, seq_no, 0, 0)),
        pl.BlockSpec((length, 2 * state_size), lambda i, p: (0, 0)),
        store_g,
        store_m,
    )
    flops = 2 * length * features * (6 * state_size + 4 * length)
    moved = 2 * (4 * features * state_size * 2 + 6 * length * features) + 4 * 4 * length * features
    return pl.pallas_call(
        functools.partial(step_kernel, factor=factor, width=width),
        out_shape=(
            jax.ShapeDtypeStruct((length, features), jnp.bfloat16),
            jax.ShapeDtypeStruct(carried.shape, jnp.float32),
            jax.ShapeDtypeStruct((length, 2 * state_size), jnp.bfloat16),
            jax.ShapeDtypeStruct(grad_store.shape, grad_store.dtype),
            jax.ShapeDtypeStruct(map_store.shape, map_store.dtype),
        ),
        grid_spec=pltpu.PrefetchScalarGridSpec(
            num_scalar_prefetch=1,
            grid=(1,),
            in_specs=in_specs,
            out_specs=out_specs,
            scratch_shapes=[
                pltpu.VMEM((length, features), jnp.bfloat16),
                pltpu.VMEM((length, features), jnp.float32),
            ],
        ),
        input_output_aliases={12: 1, 15: 3, 16: 4},
        cost_estimate=pl.CostEstimate(flops=flops, bytes_accessed=moved, transcendentals=0),
    )(picks, wt2, dec2, incoming, top_blk, x_flat, in_blk, out_blk, tail_full, lead_full, xt_full, states_t, carried, end_row, w_bc, grad_store, map_store)


def shards(layer_inputs, w_bc, log_decay, top_grad):
    sections = lax.axis_size("section")
    section_id = lax.axis_index("section")
    lay_dev, seq_dev, tok_len, features = layer_inputs.shape
    head_count = log_decay.shape[-1]
    block_len = tok_len // MICRO
    state_size = w_bc.shape[-1] // 2
    factor = 0.25 / state_size
    bc_all = jnp.einsum(
        "lstd,ldc->lstc", layer_inputs, w_bc, preferred_element_type=jnp.float32
    ).astype(jnp.bfloat16)

    def blocked(a):
        split = a.reshape(a.shape[:2] + (MICRO, block_len) + a.shape[3:])
        return jnp.moveaxis(split, 2, 0)

    x_blk = blocked(layer_inputs).reshape(
        (MICRO, lay_dev, seq_dev, block_len, head_count, features // head_count)
    )
    bc_blk = blocked(bc_all)
    in_blk = bc_blk[..., :state_size]
    out_blk = bc_blk[..., state_size:]
    rates_blk = blocked(log_decay)
    consts_fn = jax.vmap(jax.vmap(jax.vmap(lambda x, b, c, r: block_consts(x, b, c, r, factor))))
    consts = consts_fn(x_blk, in_blk, out_blk, rates_blk)
    width = features // head_count
    lead_dims = consts["tail"].shape[:3]
    pairs = head_count * width // 128
    per_pair = 128 // width
    weighted = jnp.swapaxes(consts["weighted"], -1, -3)
    weighted = weighted.reshape(lead_dims + (pairs, per_pair, block_len, block_len))
    wt2 = jnp.swapaxes(weighted, -3, -2).reshape(lead_dims + (pairs, block_len, per_pair * block_len))
    dec2 = jnp.moveaxis(consts["decays"], -1, -3).reshape(
        lead_dims + (pairs, per_pair * block_len, block_len)
    )
    tail_full = jnp.repeat(consts["tail"], width, axis=-1)
    lead_full = jnp.repeat(consts["lead"], width, axis=-1)
    xt_full = consts["tail_inputs"].reshape(lead_dims + (block_len, features))
    end_row = jnp.repeat(consts["ending"], width, axis=-1)[..., None, :]
    fresh_t = jnp.einsum(
        "mlsjn,mlsjd->mlsnd", in_blk, xt_full, preferred_element_type=jnp.float32
    )
    state_now = jnp.zeros(fresh_t.shape[1:], jnp.float32)
    saved = []
    for block_no in range(MICRO):
        saved.append(state_now.astype(jnp.bfloat16))
        state_now = end_row[block_no] * state_now + fresh_t[block_no]
    states_t = jnp.stack(saved)
    x_flat = x_blk.reshape(lead_dims + (block_len, features))
    per_block = (wt2, dec2, x_flat, in_blk, out_blk, tail_full, lead_full, xt_full, states_t, end_row)
    per_block = lax.optimization_barrier(per_block)

    top_blk = jnp.moveaxis(
        top_grad.reshape((seq_dev, MICRO, block_len, features)), 1, 0
    )
    is_top = section_id == sections - 1

    def advance(counter, loop_state):
        incoming, carried, grad_store, map_store = loop_state
        offset = counter - (sections - 1 - section_id)
        is_valid = (offset >= 0) & (offset < MICRO)
        block_no = jnp.clip(MICRO - 1 - offset, 0, MICRO - 1)
        slot = jnp.where(is_valid, block_no, MICRO)
        picks = jnp.stack([block_no, is_top.astype(jnp.int32), slot]).astype(jnp.int32)
        for level_no in reversed(range(lay_dev)):
            level_out = []
            for seq_no in range(seq_dev):
                level_grads, carried, grad_bc, grad_store, map_store = fused_step(
                    picks, per_block, incoming, top_blk, carried, w_bc, grad_store, map_store,
                    level_no, seq_no, factor, width,
                )
                level_out.append(level_grads)
            incoming = jnp.stack(level_out)
            picks = picks.at[1].set(0)
        received = passed_along(incoming, "section", -1)
        return (received, carried, grad_store, map_store)

    initial = (
        jnp.zeros((seq_dev, block_len, features), jnp.bfloat16),
        jnp.zeros(states_t.shape[1:], jnp.float32),
        jnp.zeros((MICRO + 1, lay_dev, seq_dev, block_len, features), jnp.bfloat16),
        jnp.zeros((MICRO + 1, lay_dev, seq_dev, block_len, 2 * state_size), jnp.bfloat16),
    )
    final_state = lax.fori_loop(0, MICRO + sections - 1, advance, initial)
    grad_store = final_state[2]
    map_store = final_state[3]

    grad_inputs = jnp.moveaxis(grad_store[:MICRO], 0, 2).reshape(layer_inputs.shape)
    map_store = jnp.moveaxis(map_store[:MICRO], 0, 2).reshape(bc_all.shape)
    ways = lax.axis_size("dp")
    divisor = ways * seq_dev
    rows_here = layer_inputs.reshape(lay_dev, seq_dev * tok_len, ways, features // ways)
    rows_here = jnp.transpose(rows_here, (2, 0, 1, 3))
    rows_all = lax.all_to_all(rows_here, "dp", 0, 0, tiled=True)
    maps_here = map_store.reshape(1, lay_dev, seq_dev * tok_len, map_store.shape[-1])
    maps_all = lax.all_gather(maps_here, "dp", axis=0, tiled=True)
    grad_w = jnp.einsum(
        "glrd,glrc->ldc", rows_all, maps_all, preferred_element_type=jnp.float32
    ) / divisor
    return (grad_inputs, grad_w)


def solution(mesh):
    in_specs = (
        P("section", "dp", None, None),
        P("section", None, None),
        P("section", "dp", None, None),
        P("dp", None, None),
    )
    out_specs = (P("section", "dp", None, None), P("section", "dp", None))
    return jax.shard_map(shards, mesh=mesh, in_specs=in_specs, out_specs=out_specs, check_vma=False)
```

```python
import functools

import jax
import jax.numpy as jnp
from jax import lax
from jax.experimental import pallas as pl
from jax.experimental.pallas import tpu as pltpu
from jax.sharding import PartitionSpec as P

MICRO = 4


def shortened(value):
    return jax.tree.map(lambda a: a.astype(jnp.bfloat16) if a.dtype == jnp.float32 else a, value)


def passed_along(block, axis, distance):
    devices = range(lax.axis_size(axis))
    route = [(i - distance, i) for i in devices if i - distance in devices]
    return lax.ppermute(block, axis, route)


def block_terms(inputs_b, in_b, out_b, rates, grads_b, carried, state_in, factor):
    length = inputs_b.shape[0]
    cumulative = jnp.cumsum(rates, axis=0)
    ending = cumulative[-1]
    locations = jnp.arange(length)
    lower_mask = (locations[:, None] >= locations[None, :])[:, :, None]
    spread = jnp.where(lower_mask, cumulative[:, None, :] - cumulative[None, :, :], 0.0)
    decays = jnp.where(lower_mask, jnp.exp(spread), 0.0)
    tail_decay = jnp.exp(ending[None, :] - cumulative)
    leading = jnp.exp(cumulative)
    scores = jnp.dot(out_b, in_b.T, preferred_element_type=jnp.float32)
    weighted = (factor * decays * scores[:, :, None]).astype(jnp.bfloat16)
    carried_b = carried.astype(jnp.bfloat16)
    state_b = state_in.astype(jnp.bfloat16)
    grad_feats = jnp.einsum("kjh,khp->jhp", weighted, grads_b, preferred_element_type=jnp.float32)
    grad_feats = grad_feats + tail_decay[:, :, None] * jnp.einsum(
        "hpn,jn->jhp", carried_b, in_b, preferred_element_type=jnp.float32
    )
    pair_dots = jnp.einsum("khp,jhp->kjh", grads_b, inputs_b, preferred_element_type=jnp.float32)
    mixing = jnp.sum(decays * pair_dots, axis=2).astype(jnp.bfloat16)
    tail_inputs = (tail_decay[:, :, None] * inputs_b.astype(jnp.float32)).astype(jnp.bfloat16)
    lead_grads = (leading[:, :, None] * grads_b.astype(jnp.float32)).astype(jnp.bfloat16)
    grad_inmap = factor * jnp.dot(mixing.T, out_b, preferred_element_type=jnp.float32)
    grad_inmap = grad_inmap + jnp.einsum(
        "jhp,hpn->jn", tail_inputs, carried_b, preferred_element_type=jnp.float32
    )
    grad_outmap = factor * (
        jnp.dot(mixing, in_b, preferred_element_type=jnp.float32)
        + jnp.einsum("ihp,hpn->in", lead_grads, state_b, preferred_element_type=jnp.float32)
    )
    carry_out = factor * jnp.einsum(
        "khp,kn->hpn", lead_grads, out_b, preferred_element_type=jnp.float32
    )
    carry_out = carry_out + jnp.exp(ending)[:, None, None] * carried
    return (grad_feats, grad_inmap, grad_outmap, carry_out)


def block_end(inputs_b, in_b, rates, state_in):
    cumulative = jnp.cumsum(rates, axis=0)
    ending = cumulative[-1]
    tail_decay = jnp.exp(ending[None, :] - cumulative)
    tail_inputs = (tail_decay[:, :, None] * inputs_b.astype(jnp.float32)).astype(jnp.bfloat16)
    fresh = jnp.einsum("jhp,jn->hpn", tail_inputs, in_b, preferred_element_type=jnp.float32)
    return jnp.exp(ending)[:, None, None] * state_in + fresh


def split_block(inputs_c, map_block, head_count):
    length, features = inputs_c.shape
    state_size = map_block.shape[1] // 2
    inputs_b = inputs_c.reshape(length, head_count, features // head_count)
    in_b = map_block[:, :state_size]
    out_b = map_block[:, state_size:]
    return (inputs_b, in_b, out_b)


def block_back(inputs_c, map_block, rates, grads_c, carried, state_in, weights):
    length, features = inputs_c.shape
    head_count = rates.shape[1]
    factor = 0.25 / (map_block.shape[1] // 2)
    inputs_b, in_b, out_b = split_block(inputs_c, map_block, head_count)
    grads_b = grads_c.reshape(length, head_count, features // head_count)
    grad_feats, grad_inmap, grad_outmap, carry_out = block_terms(
        inputs_b, in_b, out_b, rates, grads_b, carried, state_in, factor
    )
    grad_bc = jnp.concatenate([grad_inmap, grad_outmap], axis=1).astype(jnp.bfloat16)
    back_proj = lax.dot_general(
        grad_bc, weights, (((1,), (1,)), ((), ())), preferred_element_type=jnp.float32
    )
    summed = grads_c.astype(jnp.float32) + grad_feats.reshape(length, features) + back_proj
    return (summed.astype(jnp.bfloat16), carry_out, grad_bc)


def layer_starts(inputs_s, bc_s, rates_s):
    head_count = rates_s.shape[1]
    features = inputs_s.shape[1]
    state_size = bc_s.shape[1] // 2
    block_len = inputs_s.shape[0] // MICRO
    state_now = jnp.zeros((head_count, features // head_count, state_size), jnp.float32)
    saved = []
    for block_no in range(MICRO):
        lo_row = block_no * block_len
        inputs_b, in_b, out_b = split_block(
            inputs_s[lo_row : lo_row + block_len], bc_s[lo_row : lo_row + block_len], head_count
        )
        saved.append(state_now)
        state_now = block_end(inputs_b, in_b, rates_s[lo_row : lo_row + block_len], state_now)
    return jnp.stack(saved)


def block_consts(inputs_b, in_b, out_b, rates, factor):
    length = inputs_b.shape[0]
    cumulative = jnp.cumsum(rates, axis=0)
    ending = cumulative[-1]
    locations = jnp.arange(length)
    lower_mask = (locations[:, None] >= locations[None, :])[:, :, None]
    spread = jnp.where(lower_mask, cumulative[:, None, :] - cumulative[None, :, :], 0.0)
    decays = jnp.where(lower_mask, jnp.exp(spread), 0.0)
    tail_decay = jnp.exp(ending[None, :] - cumulative)
    leading = jnp.exp(cumulative)
    scores = jnp.dot(out_b, in_b.T, preferred_element_type=jnp.float32)
    cum_t = cumulative.T
    upper = (locations[:, None] <= locations[None, :])[None]
    spread_t = jnp.where(upper, cum_t[:, None, :] - cum_t[:, :, None], 0.0)
    decays_t = jnp.where(upper, jnp.exp(spread_t), 0.0)
    scores_t = jnp.dot(in_b, out_b.T, preferred_element_type=jnp.float32)
    weighted = (factor * decays_t * scores_t[None]).astype(jnp.bfloat16)
    tail_inputs = (tail_decay[:, :, None] * inputs_b.astype(jnp.float32)).astype(jnp.bfloat16)
    return dict(
        decays=decays,
        tail=tail_decay,
        lead=leading,
        weighted=weighted,
        tail_inputs=tail_inputs,
        ending=jnp.exp(ending),
    )


def step_kernel(
    picks_ref, wt_ref, dec_ref, inc_ref, top_ref, x_ref, b_ref, c_ref, tail_ref, lead_ref, xt_ref,
    sb_ref, r_ref, end_ref, w_ref, gs_ref, ms_ref, out_ref, rnew_ref, dbc_ref, gstore_ref, mstore_ref,
    v_ref, gx_ref, *, factor, width
):
    f32 = jnp.float32
    bf16 = jnp.bfloat16
    length, features = v_ref.shape
    lanes = 128
    per_pair = lanes // width
    nt = (((1,), (1,)), ((), ()))
    tn = (((0,), (0,)), ((), ()))
    v_ref[...] = jnp.where(picks_ref[1] > 0, top_ref[...], inc_ref[...])
    rb_t = r_ref[...].astype(bf16)
    in_map = b_ref[...]
    out_map = c_ref[...]
    lane_id = lax.broadcasted_iota(jnp.int32, (length, lanes), 1)
    masks = [(lane_id >= e * width) & (lane_id < (e + 1) * width) for e in range(per_pair)]
    mix_acc = jnp.zeros((per_pair * length, length), f32)
    for q in range(features // lanes):
        cols = slice(q * lanes, (q + 1) * lanes)
        v_q = v_ref[:, cols]
        x_q = x_ref[:, cols]
        stacked = jnp.concatenate([jnp.where(m, v_q, jnp.zeros_like(v_q)) for m in masks], axis=0)
        gx_q = jnp.dot(
            wt_ref[per_pair * q], stacked[0:length], preferred_element_type=f32
        )
        for e in range(1, per_pair):
            gx_q = gx_q + jnp.dot(
                wt_ref[per_pair * q + e],
                stacked[e * length:(e + 1) * length],
                preferred_element_type=f32,
            )
        rbb_q = jnp.dot(in_map, rb_t[:, cols], preferred_element_type=f32)
        gx_ref[:, cols] = gx_q + tail_ref[:, cols] * rbb_q
        pair_dots = lax.dot_general(stacked, x_q, nt, preferred_element_type=f32)
        mix_acc = mix_acc + dec_ref[q] * pair_dots
    mixing = mix_acc[0:length]
    for e in range(1, per_pair):
        mixing = mixing + mix_acc[e * length:(e + 1) * length]
    mixing = mixing.astype(bf16)
    v = v_ref[...]
    lead_grads = (lead_ref[...] * v.astype(f32)).astype(bf16)
    grad_inmap = factor * lax.dot_general(mixing, out_map, tn, preferred_element_type=f32)
    grad_inmap = grad_inmap + lax.dot_general(xt_ref[...], rb_t, nt, preferred_element_type=f32)
    grad_outmap = factor * (
        jnp.dot(mixing, in_map, preferred_element_type=f32)
        + lax.dot_general(lead_grads, sb_ref[...], nt, preferred_element_type=f32)
    )
    carry = factor * lax.dot_general(out_map, lead_grads, tn, preferred_element_type=f32)
    rnew_ref[...] = carry + end_ref[...] * r_ref[...]
    grad_bc = jnp.concatenate([grad_inmap, grad_outmap], axis=1).astype(bf16)
    dbc_ref[...] = grad_bc
    mstore_ref[...] = jnp.where(picks_ref[2] > 0, grad_bc, ms_ref[...])
    back = lax.dot_general(grad_bc, w_ref[...], nt, preferred_element_type=f32)
    summed = (v.astype(f32) + gx_ref[...] + back).astype(out_ref.dtype)
    out_ref[...] = summed
    gstore_ref[...] = jnp.where(picks_ref[2] > 0, summed, gs_ref[...])


def fused_step(picks, per_block, incoming, top_blk, carried, w_bc, grad_store, map_store, level_no, seq_no, factor, width):
    wt2, dec2, x_flat, in_blk, out_blk, tail_full, lead_full, xt_full, states_t, end_row = per_block
    length, features = incoming.shape[1:]
    state_size = in_blk.shape[-1]

    def lead_block(a):
        shape = (None, None, None) + a.shape[3:]
        tail = (0,) * (a.ndim - 3)
        return pl.BlockSpec(shape, lambda i, p: (p[0], level_no, seq_no) + tail)

    in_specs = [lead_block(a) for a in (wt2, dec2)]
    in_specs.append(pl.BlockSpec((None, length, features), lambda i, p: (seq_no, 0, 0)))
    in_specs.append(pl.BlockSpec((None, None, length, features), lambda i, p: (p[0], seq_no, 0, 0)))
    in_specs += [lead_block(a) for a in (x_flat, in_blk, out_blk, tail_full, lead_full, xt_full, states_t)]
    in_specs.append(pl.BlockSpec((None, None) + carried.shape[2:], lambda i, p: (level_no, seq_no, 0, 0)))
    in_specs.append(lead_block(end_row))
    in_specs.append(pl.BlockSpec((None,) + w_bc.shape[1:], lambda i, p: (level_no, 0, 0)))
    store_g = pl.BlockSpec((None, None, None, length, features), lambda i, p: (p[0], level_no, seq_no, 0, 0))
    store_m = pl.BlockSpec((None, None, None, length, 2 * state_size), lambda i, p: (p[0], level_no, seq_no, 0, 0))
    in_specs += [store_g, store_m]
    out_specs = (
        pl.BlockSpec((length, features), lambda i, p: (0, 0)),
        pl.BlockSpec((None, None) + carried.shape[2:], lambda i, p: (level_no, seq_no, 0, 0)),
        pl.BlockSpec((length, 2 * state_size), lambda i, p: (0, 0)),
        store_g,
        store_m,
    )
    flops = 2 * length * features * (6 * state_size + 4 * length)
    moved = 2 * (4 * features * state_size * 2 + 6 * length * features) + 4 * 4 * length * features
    return pl.pallas_call(
        functools.partial(step_kernel, factor=factor, width=width),
        out_shape=(
            jax.ShapeDtypeStruct((length, features), jnp.bfloat16),
            jax.ShapeDtypeStruct(carried.shape, jnp.float32),
            jax.ShapeDtypeStruct((length, 2 * state_size), jnp.bfloat16),
            jax.ShapeDtypeStruct(grad_store.shape, grad_store.dtype),
            jax.ShapeDtypeStruct(map_store.shape, map_store.dtype),
        ),
        grid_spec=pltpu.PrefetchScalarGridSpec(
            num_scalar_prefetch=1,
            grid=(1,),
            in_specs=in_specs,
            out_specs=out_specs,
            scratch_shapes=[
                pltpu.VMEM((length, features), jnp.bfloat16),
                pltpu.VMEM((length, features), jnp.float32),
            ],
        ),
        input_output_aliases={12: 1, 15: 3, 16: 4},
        cost_estimate=pl.CostEstimate(flops=flops, bytes_accessed=moved, transcendentals=0),
    )(picks, wt2, dec2, incoming, top_blk, x_flat, in_blk, out_blk, tail_full, lead_full, xt_full, states_t, carried, end_row, w_bc, grad_store, map_store)


def shards(layer_inputs, w_bc, log_decay, top_grad):
    sections = lax.axis_size("section")
    section_id = lax.axis_index("section")
    lay_dev, seq_dev, tok_len, features = layer_inputs.shape
    head_count = log_decay.shape[-1]
    block_len = tok_len // MICRO
    state_size = w_bc.shape[-1] // 2
    factor = 0.25 / state_size
    bc_all = jnp.einsum(
        "lstd,ldc->lstc", layer_inputs, w_bc, preferred_element_type=jnp.float32
    ).astype(jnp.bfloat16)

    def blocked(a):
        split = a.reshape(a.shape[:2] + (MICRO, block_len) + a.shape[3:])
        return jnp.moveaxis(split, 2, 0)

    x_blk = blocked(layer_inputs).reshape(
        (MICRO, lay_dev, seq_dev, block_len, head_count, features // head_count)
    )
    bc_blk = blocked(bc_all)
    in_blk = bc_blk[..., :state_size]
    out_blk = bc_blk[..., state_size:]
    rates_blk = blocked(log_decay)
    consts_fn = jax.vmap(jax.vmap(jax.vmap(lambda x, b, c, r: block_consts(x, b, c, r, factor))))
    consts = consts_fn(x_blk, in_blk, out_blk, rates_blk)
    width = features // head_count
    lead_dims = consts["tail"].shape[:3]
    pairs = head_count * width // 128
    per_pair = 128 // width
    wt2 = consts["weighted"]
    dec2 = jnp.moveaxis(consts["decays"], -1, -3).reshape(
        lead_dims + (pairs, per_pair * block_len, block_len)
    )
    tail_full = jnp.repeat(consts["tail"], width, axis=-1)
    lead_full = jnp.repeat(consts["lead"], width, axis=-1)
    xt_full = consts["tail_inputs"].reshape(lead_dims + (block_len, features))
    end_row = jnp.repeat(consts["ending"], width, axis=-1)[..., None, :]
    fresh_t = jnp.einsum(
        "mlsjn,mlsjd->mlsnd", in_blk, xt_full, preferred_element_type=jnp.float32
    )
    state_now = jnp.zeros(fresh_t.shape[1:], jnp.float32)
    saved = []
    for block_no in range(MICRO):
        saved.append(state_now.astype(jnp.bfloat16))
        state_now = end_row[block_no] * state_now + fresh_t[block_no]
    states_t = jnp.stack(saved)
    x_flat = x_blk.reshape(lead_dims + (block_len, features))
    per_block = (wt2, dec2, x_flat, in_blk, out_blk, tail_full, lead_full, xt_full, states_t, end_row)
    per_block = lax.optimization_barrier(per_block)

    top_blk = jnp.moveaxis(
        top_grad.reshape((seq_dev, MICRO, block_len, features)), 1, 0
    )
    is_top = section_id == sections - 1

    def advance(counter, loop_state, send=True):
        incoming, carried, grad_store, map_store = loop_state
        offset = counter - (sections - 1 - section_id)
        is_valid = (offset >= 0) & (offset < MICRO)
        block_no = jnp.clip(MICRO - 1 - offset, 0, MICRO - 1)
        picks = jnp.stack([block_no, is_top.astype(jnp.int32), is_valid.astype(jnp.int32)])
        picks = picks.astype(jnp.int32)
        for level_no in reversed(range(lay_dev)):
            level_out = []
            for seq_no in range(seq_dev):
                level_grads, carried, grad_bc, grad_store, map_store = fused_step(
                    picks, per_block, incoming, top_blk, carried, w_bc, grad_store, map_store,
                    level_no, seq_no, factor, width,
                )
                level_out.append(level_grads)
            incoming = jnp.stack(level_out)
            picks = picks.at[1].set(0)
        if send:
            incoming = passed_along(incoming, "section", -1)
        return (incoming, carried, grad_store, map_store)

    initial = (
        jnp.zeros((seq_dev, block_len, features), jnp.bfloat16),
        jnp.zeros(states_t.shape[1:], jnp.float32),
        jnp.zeros((MICRO, lay_dev, seq_dev, block_len, features), jnp.bfloat16),
        jnp.zeros((MICRO, lay_dev, seq_dev, block_len, 2 * state_size), jnp.bfloat16),
    )
    steps = MICRO + sections - 1
    final_state = lax.fori_loop(0, steps - 1, advance, initial)
    final_state = advance(steps - 1, final_state, send=False)
    grad_store = final_state[2]
    map_store = final_state[3]

    grad_inputs = jnp.moveaxis(grad_store, 0, 2).reshape(layer_inputs.shape)
    map_store = jnp.moveaxis(map_store, 0, 2).reshape(bc_all.shape)
    ways = lax.axis_size("dp")
    divisor = ways * seq_dev
    rows_here = layer_inputs.reshape(lay_dev, seq_dev * tok_len, ways, features // ways)
    rows_here = jnp.transpose(rows_here, (2, 0, 1, 3))
    rows_all = lax.all_to_all(rows_here, "dp", 0, 0, tiled=True)
    maps_here = map_store.reshape(1, lay_dev, seq_dev * tok_len, map_store.shape[-1])
    maps_all = lax.all_gather(maps_here, "dp", axis=0, tiled=True)
    grad_w = jnp.einsum(
        "glrd,glrc->ldc", rows_all, maps_all, preferred_element_type=jnp.float32
    ) / divisor
    return (grad_inputs, grad_w)


def solution(mesh):
    in_specs = (
        P("section", "dp", None, None),
        P("section", None, None),
        P("section", "dp", None, None),
        P("dp", None, None),
    )
    out_specs = (P("section", "dp", None, None), P("section", "dp", None))
    return jax.shard_map(shards, mesh=mesh, in_specs=in_specs, out_specs=out_specs, check_vma=False)
```

```python
import functools

import jax
import jax.numpy as jnp
from jax import lax
from jax.experimental import pallas as pl
from jax.experimental.pallas import tpu as pltpu
from jax.sharding import PartitionSpec as P

MICRO = 4


def shortened(value):
    return jax.tree.map(lambda a: a.astype(jnp.bfloat16) if a.dtype == jnp.float32 else a, value)


def passed_along(block, axis, distance):
    devices = range(lax.axis_size(axis))
    route = [(i - distance, i) for i in devices if i - distance in devices]
    return lax.ppermute(block, axis, route)


def block_terms(inputs_b, in_b, out_b, rates, grads_b, carried, state_in, factor):
    length = inputs_b.shape[0]
    cumulative = jnp.cumsum(rates, axis=0)
    ending = cumulative[-1]
    locations = jnp.arange(length)
    lower_mask = (locations[:, None] >= locations[None, :])[:, :, None]
    spread = jnp.where(lower_mask, cumulative[:, None, :] - cumulative[None, :, :], 0.0)
    decays = jnp.where(lower_mask, jnp.exp(spread), 0.0)
    tail_decay = jnp.exp(ending[None, :] - cumulative)
    leading = jnp.exp(cumulative)
    scores = jnp.dot(out_b, in_b.T, preferred_element_type=jnp.float32)
    weighted = (factor * decays * scores[:, :, None]).astype(jnp.bfloat16)
    carried_b = carried.astype(jnp.bfloat16)
    state_b = state_in.astype(jnp.bfloat16)
    grad_feats = jnp.einsum("kjh,khp->jhp", weighted, grads_b, preferred_element_type=jnp.float32)
    grad_feats = grad_feats + tail_decay[:, :, None] * jnp.einsum(
        "hpn,jn->jhp", carried_b, in_b, preferred_element_type=jnp.float32
    )
    pair_dots = jnp.einsum("khp,jhp->kjh", grads_b, inputs_b, preferred_element_type=jnp.float32)
    mixing = jnp.sum(decays * pair_dots, axis=2).astype(jnp.bfloat16)
    tail_inputs = (tail_decay[:, :, None] * inputs_b.astype(jnp.float32)).astype(jnp.bfloat16)
    lead_grads = (leading[:, :, None] * grads_b.astype(jnp.float32)).astype(jnp.bfloat16)
    grad_inmap = factor * jnp.dot(mixing.T, out_b, preferred_element_type=jnp.float32)
    grad_inmap = grad_inmap + jnp.einsum(
        "jhp,hpn->jn", tail_inputs, carried_b, preferred_element_type=jnp.float32
    )
    grad_outmap = factor * (
        jnp.dot(mixing, in_b, preferred_element_type=jnp.float32)
        + jnp.einsum("ihp,hpn->in", lead_grads, state_b, preferred_element_type=jnp.float32)
    )
    carry_out = factor * jnp.einsum(
        "khp,kn->hpn", lead_grads, out_b, preferred_element_type=jnp.float32
    )
    carry_out = carry_out + jnp.exp(ending)[:, None, None] * carried
    return (grad_feats, grad_inmap, grad_outmap, carry_out)


def block_end(inputs_b, in_b, rates, state_in):
    cumulative = jnp.cumsum(rates, axis=0)
    ending = cumulative[-1]
    tail_decay = jnp.exp(ending[None, :] - cumulative)
    tail_inputs = (tail_decay[:, :, None] * inputs_b.astype(jnp.float32)).astype(jnp.bfloat16)
    fresh = jnp.einsum("jhp,jn->hpn", tail_inputs, in_b, preferred_element_type=jnp.float32)
    return jnp.exp(ending)[:, None, None] * state_in + fresh


def split_block(inputs_c, map_block, head_count):
    length, features = inputs_c.shape
    state_size = map_block.shape[1] // 2
    inputs_b = inputs_c.reshape(length, head_count, features // head_count)
    in_b = map_block[:, :state_size]
    out_b = map_block[:, state_size:]
    return (inputs_b, in_b, out_b)


def block_back(inputs_c, map_block, rates, grads_c, carried, state_in, weights):
    length, features = inputs_c.shape
    head_count = rates.shape[1]
    factor = 0.25 / (map_block.shape[1] // 2)
    inputs_b, in_b, out_b = split_block(inputs_c, map_block, head_count)
    grads_b = grads_c.reshape(length, head_count, features // head_count)
    grad_feats, grad_inmap, grad_outmap, carry_out = block_terms(
        inputs_b, in_b, out_b, rates, grads_b, carried, state_in, factor
    )
    grad_bc = jnp.concatenate([grad_inmap, grad_outmap], axis=1).astype(jnp.bfloat16)
    back_proj = lax.dot_general(
        grad_bc, weights, (((1,), (1,)), ((), ())), preferred_element_type=jnp.float32
    )
    summed = grads_c.astype(jnp.float32) + grad_feats.reshape(length, features) + back_proj
    return (summed.astype(jnp.bfloat16), carry_out, grad_bc)


def layer_starts(inputs_s, bc_s, rates_s):
    head_count = rates_s.shape[1]
    features = inputs_s.shape[1]
    state_size = bc_s.shape[1] // 2
    block_len = inputs_s.shape[0] // MICRO
    state_now = jnp.zeros((head_count, features // head_count, state_size), jnp.float32)
    saved = []
    for block_no in range(MICRO):
        lo_row = block_no * block_len
        inputs_b, in_b, out_b = split_block(
            inputs_s[lo_row : lo_row + block_len], bc_s[lo_row : lo_row + block_len], head_count
        )
        saved.append(state_now)
        state_now = block_end(inputs_b, in_b, rates_s[lo_row : lo_row + block_len], state_now)
    return jnp.stack(saved)


def block_consts(inputs_b, in_b, out_b, rates, factor):
    length = inputs_b.shape[0]
    cumulative = jnp.cumsum(rates, axis=0)
    ending = cumulative[-1]
    locations = jnp.arange(length)
    lower_mask = (locations[:, None] >= locations[None, :])[:, :, None]
    spread = jnp.where(lower_mask, cumulative[:, None, :] - cumulative[None, :, :], 0.0)
    decays = jnp.where(lower_mask, jnp.exp(spread), 0.0)
    tail_decay = jnp.exp(ending[None, :] - cumulative)
    leading = jnp.exp(cumulative)
    scores = jnp.dot(out_b, in_b.T, preferred_element_type=jnp.float32)
    cum_t = cumulative.T
    upper = (locations[:, None] <= locations[None, :])[None]
    spread_t = jnp.where(upper, cum_t[:, None, :] - cum_t[:, :, None], 0.0)
    decays_t = jnp.where(upper, jnp.exp(spread_t), 0.0)
    scores_t = jnp.dot(in_b, out_b.T, preferred_element_type=jnp.float32)
    weighted = (factor * decays_t * scores_t[None]).astype(jnp.bfloat16)
    tail_inputs = (tail_decay[:, :, None] * inputs_b.astype(jnp.float32)).astype(jnp.bfloat16)
    return dict(
        decays=decays,
        tail=tail_decay,
        lead=leading,
        weighted=weighted,
        tail_inputs=tail_inputs,
        ending=jnp.exp(ending),
    )


def step_kernel(
    picks_ref, wt_ref, dec_ref, inc_ref, top_ref, x_ref, b_ref, c_ref, tail_ref, lead_ref, xt_ref,
    sb_ref, r_ref, end_ref, w_ref, gs_ref, ms_ref, out_ref, rnew_ref, dbc_ref, gstore_ref, mstore_ref,
    v_ref, gx_ref, *, factor, width
):
    f32 = jnp.float32
    bf16 = jnp.bfloat16
    length, features = v_ref.shape
    lanes = 128
    per_pair = lanes // width
    nt = (((1,), (1,)), ((), ()))
    tn = (((0,), (0,)), ((), ()))
    v_ref[...] = jnp.where(picks_ref[1] > 0, top_ref[...], inc_ref[...])
    rb_t = r_ref[...].astype(bf16)
    in_map = b_ref[...]
    out_map = c_ref[...]
    lane_id = lax.broadcasted_iota(jnp.int32, (length, lanes), 1)
    masks = [(lane_id >= e * width) & (lane_id < (e + 1) * width) for e in range(per_pair)]
    mix_acc = jnp.zeros((per_pair * length, length), f32)
    for q in range(features // lanes):
        cols = slice(q * lanes, (q + 1) * lanes)
        v_q = v_ref[:, cols]
        x_q = x_ref[:, cols]
        stacked = jnp.concatenate([jnp.where(m, v_q, jnp.zeros_like(v_q)) for m in masks], axis=0)
        gx_q = jnp.dot(
            wt_ref[per_pair * q], stacked[0:length], preferred_element_type=f32
        )
        for e in range(1, per_pair):
            gx_q = gx_q + jnp.dot(
                wt_ref[per_pair * q + e],
                stacked[e * length:(e + 1) * length],
                preferred_element_type=f32,
            )
        rbb_q = jnp.dot(in_map, rb_t[:, cols], preferred_element_type=f32)
        gx_ref[:, cols] = gx_q + tail_ref[:, cols] * rbb_q
        pair_dots = lax.dot_general(stacked, x_q, nt, preferred_element_type=f32)
        mix_acc = mix_acc + dec_ref[q] * pair_dots
    mixing = mix_acc[0:length]
    for e in range(1, per_pair):
        mixing = mixing + mix_acc[e * length:(e + 1) * length]
    mixing = mixing.astype(bf16)
    v = v_ref[...]
    lead_grads = (lead_ref[...] * v.astype(f32)).astype(bf16)
    grad_inmap = factor * lax.dot_general(mixing, out_map, tn, preferred_element_type=f32)
    grad_inmap = grad_inmap + lax.dot_general(xt_ref[...], rb_t, nt, preferred_element_type=f32)
    grad_outmap = factor * (
        jnp.dot(mixing, in_map, preferred_element_type=f32)
        + lax.dot_general(lead_grads, sb_ref[...], nt, preferred_element_type=f32)
    )
    carry = factor * lax.dot_general(out_map, lead_grads, tn, preferred_element_type=f32)
    rnew_ref[...] = carry + end_ref[...] * r_ref[...]
    grad_bc = jnp.concatenate([grad_inmap, grad_outmap], axis=1).astype(bf16)
    dbc_ref[...] = grad_bc
    mstore_ref[...] = jnp.where(picks_ref[2] > 0, grad_bc, ms_ref[...])
    back = lax.dot_general(grad_bc, w_ref[...], nt, preferred_element_type=f32)
    summed = (v.astype(f32) + gx_ref[...] + back).astype(out_ref.dtype)
    out_ref[...] = summed
    gstore_ref[...] = jnp.where(picks_ref[2] > 0, summed, gs_ref[...])


def fused_step(picks, per_block, incoming, top_blk, carried, w_bc, grad_store, map_store, level_no, seq_no, factor, width):
    wt2, dec2, x_flat, in_blk, out_blk, tail_full, lead_full, xt_full, states_t, end_row = per_block
    length, features = incoming.shape[1:]
    state_size = in_blk.shape[-1]

    def lead_block(a):
        shape = (None, None, None) + a.shape[3:]
        tail = (0,) * (a.ndim - 3)
        return pl.BlockSpec(shape, lambda i, p: (p[0], level_no, seq_no) + tail)

    in_specs = [lead_block(a) for a in (wt2, dec2)]
    in_specs.append(pl.BlockSpec((None, length, features), lambda i, p: (seq_no, 0, 0)))
    in_specs.append(pl.BlockSpec((None, None, length, features), lambda i, p: (p[0], seq_no, 0, 0)))
    in_specs += [lead_block(a) for a in (x_flat, in_blk, out_blk, tail_full, lead_full, xt_full, states_t)]
    in_specs.append(pl.BlockSpec((None, None) + carried.shape[2:], lambda i, p: (level_no, seq_no, 0, 0)))
    in_specs.append(lead_block(end_row))
    in_specs.append(pl.BlockSpec((None,) + w_bc.shape[1:], lambda i, p: (level_no, 0, 0)))
    store_g = pl.BlockSpec((None, None, None, length, features), lambda i, p: (p[0], level_no, seq_no, 0, 0))
    store_m = pl.BlockSpec((None, None, None, length, 2 * state_size), lambda i, p: (p[0], level_no, seq_no, 0, 0))
    in_specs += [store_g, store_m]
    out_specs = (
        pl.BlockSpec((length, features), lambda i, p: (0, 0)),
        pl.BlockSpec((None, None) + carried.shape[2:], lambda i, p: (level_no, seq_no, 0, 0)),
        pl.BlockSpec((length, 2 * state_size), lambda i, p: (0, 0)),
        store_g,
        store_m,
    )
    flops = 2 * length * features * (6 * state_size + 4 * length)
    moved = 2 * (4 * features * state_size * 2 + 6 * length * features) + 4 * 4 * length * features
    return pl.pallas_call(
        functools.partial(step_kernel, factor=factor, width=width),
        out_shape=(
            jax.ShapeDtypeStruct((length, features), jnp.bfloat16),
            jax.ShapeDtypeStruct(carried.shape, jnp.float32),
            jax.ShapeDtypeStruct((length, 2 * state_size), jnp.bfloat16),
            jax.ShapeDtypeStruct(grad_store.shape, grad_store.dtype),
            jax.ShapeDtypeStruct(map_store.shape, map_store.dtype),
        ),
        grid_spec=pltpu.PrefetchScalarGridSpec(
            num_scalar_prefetch=1,
            grid=(1,),
            in_specs=in_specs,
            out_specs=out_specs,
            scratch_shapes=[
                pltpu.VMEM((length, features), jnp.bfloat16),
                pltpu.VMEM((length, features), jnp.float32),
            ],
        ),
        input_output_aliases={12: 1, 15: 3, 16: 4},
        cost_estimate=pl.CostEstimate(flops=flops, bytes_accessed=moved, transcendentals=0),
    )(picks, wt2, dec2, incoming, top_blk, x_flat, in_blk, out_blk, tail_full, lead_full, xt_full, states_t, carried, end_row, w_bc, grad_store, map_store)


def shards(layer_inputs, w_bc, log_decay, top_grad):
    sections = lax.axis_size("section")
    section_id = lax.axis_index("section")
    lay_dev, seq_dev, tok_len, features = layer_inputs.shape
    head_count = log_decay.shape[-1]
    block_len = tok_len // MICRO
    state_size = w_bc.shape[-1] // 2
    factor = 0.25 / state_size
    bc_all = jnp.einsum(
        "lstd,ldc->lstc", layer_inputs, w_bc, preferred_element_type=jnp.float32
    ).astype(jnp.bfloat16)

    def blocked(a):
        split = a.reshape(a.shape[:2] + (MICRO, block_len) + a.shape[3:])
        return jnp.moveaxis(split, 2, 0)

    x_blk = blocked(layer_inputs).reshape(
        (MICRO, lay_dev, seq_dev, block_len, head_count, features // head_count)
    )
    bc_blk = blocked(bc_all)
    in_blk = bc_blk[..., :state_size]
    out_blk = bc_blk[..., state_size:]
    rates_blk = blocked(log_decay)
    consts_fn = jax.vmap(jax.vmap(jax.vmap(lambda x, b, c, r: block_consts(x, b, c, r, factor))))
    consts = consts_fn(x_blk, in_blk, out_blk, rates_blk)
    width = features // head_count
    lead_dims = consts["tail"].shape[:3]
    pairs = head_count * width // 128
    per_pair = 128 // width
    wt2 = consts["weighted"]
    dec2 = jnp.moveaxis(consts["decays"], -1, -3).reshape(
        lead_dims + (pairs, per_pair * block_len, block_len)
    )
    spread_heads = (
        jnp.arange(features)[None, :] // width == jnp.arange(head_count)[:, None]
    ).astype(jnp.float32)

    def per_lane(a):
        return jnp.einsum(
            "...h,hd->...d", a, spread_heads, precision=lax.Precision.HIGHEST,
            preferred_element_type=jnp.float32,
        )

    tail_full = per_lane(consts["tail"])
    lead_full = per_lane(consts["lead"])
    xt_full = consts["tail_inputs"].reshape(lead_dims + (block_len, features))
    end_row = per_lane(consts["ending"])[..., None, :]
    fresh_t = jnp.einsum(
        "mlsjn,mlsjd->mlsnd", in_blk, xt_full, preferred_element_type=jnp.float32
    )
    state_now = jnp.zeros(fresh_t.shape[1:], jnp.float32)
    saved = []
    for block_no in range(MICRO):
        saved.append(state_now.astype(jnp.bfloat16))
        state_now = end_row[block_no] * state_now + fresh_t[block_no]
    states_t = jnp.stack(saved)
    x_flat = x_blk.reshape(lead_dims + (block_len, features))
    per_block = (wt2, dec2, x_flat, in_blk, out_blk, tail_full, lead_full, xt_full, states_t, end_row)
    per_block = lax.optimization_barrier(per_block)

    top_blk = jnp.moveaxis(
        top_grad.reshape((seq_dev, MICRO, block_len, features)), 1, 0
    )
    is_top = section_id == sections - 1

    def advance(counter, loop_state, send=True):
        incoming, carried, grad_store, map_store = loop_state
        offset = counter - (sections - 1 - section_id)
        is_valid = (offset >= 0) & (offset < MICRO)
        block_no = jnp.clip(MICRO - 1 - offset, 0, MICRO - 1)
        picks = jnp.stack([block_no, is_top.astype(jnp.int32), is_valid.astype(jnp.int32)])
        picks = picks.astype(jnp.int32)
        for level_no in reversed(range(lay_dev)):
            level_out = []
            for seq_no in range(seq_dev):
                level_grads, carried, grad_bc, grad_store, map_store = fused_step(
                    picks, per_block, incoming, top_blk, carried, w_bc, grad_store, map_store,
                    level_no, seq_no, factor, width,
                )
                level_out.append(level_grads)
            incoming = jnp.stack(level_out)
            picks = picks.at[1].set(0)
        if send:
            incoming = passed_along(incoming, "section", -1)
        return (incoming, carried, grad_store, map_store)

    initial = (
        jnp.zeros((seq_dev, block_len, features), jnp.bfloat16),
        jnp.zeros(states_t.shape[1:], jnp.float32),
        jnp.zeros((MICRO, lay_dev, seq_dev, block_len, features), jnp.bfloat16),
        jnp.zeros((MICRO, lay_dev, seq_dev, block_len, 2 * state_size), jnp.bfloat16),
    )
    steps = MICRO + sections - 1
    final_state = lax.fori_loop(0, steps - 1, advance, initial)
    final_state = advance(steps - 1, final_state, send=False)
    grad_store = final_state[2]
    map_store = final_state[3]

    grad_inputs = jnp.moveaxis(grad_store, 0, 2).reshape(layer_inputs.shape)
    map_store = jnp.moveaxis(map_store, 0, 2).reshape(bc_all.shape)
    ways = lax.axis_size("dp")
    divisor = ways * seq_dev
    rows_here = layer_inputs.reshape(lay_dev, seq_dev * tok_len, ways, features // ways)
    rows_here = jnp.transpose(rows_here, (2, 0, 1, 3))
    rows_all = lax.all_to_all(rows_here, "dp", 0, 0, tiled=True)
    maps_here = map_store.reshape(1, lay_dev, seq_dev * tok_len, map_store.shape[-1])
    maps_all = lax.all_gather(maps_here, "dp", axis=0, tiled=True)
    grad_w = jnp.einsum(
        "glrd,glrc->ldc", rows_all, maps_all, preferred_element_type=jnp.float32
    ) / divisor
    return (grad_inputs, grad_w)


def solution(mesh):
    in_specs = (
        P("section", "dp", None, None),
        P("section", None, None),
        P("section", "dp", None, None),
        P("dp", None, None),
    )
    out_specs = (P("section", "dp", None, None), P("section", "dp", None))
    return jax.shard_map(shards, mesh=mesh, in_specs=in_specs, out_specs=out_specs, check_vma=False)
```

```python
import functools

import jax
import jax.numpy as jnp
from jax import lax
from jax.experimental import pallas as pl
from jax.experimental.pallas import tpu as pltpu
from jax.sharding import PartitionSpec as P

MICRO = 4


def shortened(value):
    return jax.tree.map(lambda a: a.astype(jnp.bfloat16) if a.dtype == jnp.float32 else a, value)


def passed_along(block, axis, distance):
    devices = range(lax.axis_size(axis))
    route = [(i - distance, i) for i in devices if i - distance in devices]
    return lax.ppermute(block, axis, route)


def block_terms(inputs_b, in_b, out_b, rates, grads_b, carried, state_in, factor):
    length = inputs_b.shape[0]
    cumulative = jnp.cumsum(rates, axis=0)
    ending = cumulative[-1]
    locations = jnp.arange(length)
    lower_mask = (locations[:, None] >= locations[None, :])[:, :, None]
    spread = jnp.where(lower_mask, cumulative[:, None, :] - cumulative[None, :, :], 0.0)
    decays = jnp.where(lower_mask, jnp.exp(spread), 0.0)
    tail_decay = jnp.exp(ending[None, :] - cumulative)
    leading = jnp.exp(cumulative)
    scores = jnp.dot(out_b, in_b.T, preferred_element_type=jnp.float32)
    weighted = (factor * decays * scores[:, :, None]).astype(jnp.bfloat16)
    carried_b = carried.astype(jnp.bfloat16)
    state_b = state_in.astype(jnp.bfloat16)
    grad_feats = jnp.einsum("kjh,khp->jhp", weighted, grads_b, preferred_element_type=jnp.float32)
    grad_feats = grad_feats + tail_decay[:, :, None] * jnp.einsum(
        "hpn,jn->jhp", carried_b, in_b, preferred_element_type=jnp.float32
    )
    pair_dots = jnp.einsum("khp,jhp->kjh", grads_b, inputs_b, preferred_element_type=jnp.float32)
    mixing = jnp.sum(decays * pair_dots, axis=2).astype(jnp.bfloat16)
    tail_inputs = (tail_decay[:, :, None] * inputs_b.astype(jnp.float32)).astype(jnp.bfloat16)
    lead_grads = (leading[:, :, None] * grads_b.astype(jnp.float32)).astype(jnp.bfloat16)
    grad_inmap = factor * jnp.dot(mixing.T, out_b, preferred_element_type=jnp.float32)
    grad_inmap = grad_inmap + jnp.einsum(
        "jhp,hpn->jn", tail_inputs, carried_b, preferred_element_type=jnp.float32
    )
    grad_outmap = factor * (
        jnp.dot(mixing, in_b, preferred_element_type=jnp.float32)
        + jnp.einsum("ihp,hpn->in", lead_grads, state_b, preferred_element_type=jnp.float32)
    )
    carry_out = factor * jnp.einsum(
        "khp,kn->hpn", lead_grads, out_b, preferred_element_type=jnp.float32
    )
    carry_out = carry_out + jnp.exp(ending)[:, None, None] * carried
    return (grad_feats, grad_inmap, grad_outmap, carry_out)


def block_end(inputs_b, in_b, rates, state_in):
    cumulative = jnp.cumsum(rates, axis=0)
    ending = cumulative[-1]
    tail_decay = jnp.exp(ending[None, :] - cumulative)
    tail_inputs = (tail_decay[:, :, None] * inputs_b.astype(jnp.float32)).astype(jnp.bfloat16)
    fresh = jnp.einsum("jhp,jn->hpn", tail_inputs, in_b, preferred_element_type=jnp.float32)
    return jnp.exp(ending)[:, None, None] * state_in + fresh


def split_block(inputs_c, map_block, head_count):
    length, features = inputs_c.shape
    state_size = map_block.shape[1] // 2
    inputs_b = inputs_c.reshape(length, head_count, features // head_count)
    in_b = map_block[:, :state_size]
    out_b = map_block[:, state_size:]
    return (inputs_b, in_b, out_b)


def block_back(inputs_c, map_block, rates, grads_c, carried, state_in, weights):
    length, features = inputs_c.shape
    head_count = rates.shape[1]
    factor = 0.25 / (map_block.shape[1] // 2)
    inputs_b, in_b, out_b = split_block(inputs_c, map_block, head_count)
    grads_b = grads_c.reshape(length, head_count, features // head_count)
    grad_feats, grad_inmap, grad_outmap, carry_out = block_terms(
        inputs_b, in_b, out_b, rates, grads_b, carried, state_in, factor
    )
    grad_bc = jnp.concatenate([grad_inmap, grad_outmap], axis=1).astype(jnp.bfloat16)
    back_proj = lax.dot_general(
        grad_bc, weights, (((1,), (1,)), ((), ())), preferred_element_type=jnp.float32
    )
    summed = grads_c.astype(jnp.float32) + grad_feats.reshape(length, features) + back_proj
    return (summed.astype(jnp.bfloat16), carry_out, grad_bc)


def layer_starts(inputs_s, bc_s, rates_s):
    head_count = rates_s.shape[1]
    features = inputs_s.shape[1]
    state_size = bc_s.shape[1] // 2
    block_len = inputs_s.shape[0] // MICRO
    state_now = jnp.zeros((head_count, features // head_count, state_size), jnp.float32)
    saved = []
    for block_no in range(MICRO):
        lo_row = block_no * block_len
        inputs_b, in_b, out_b = split_block(
            inputs_s[lo_row : lo_row + block_len], bc_s[lo_row : lo_row + block_len], head_count
        )
        saved.append(state_now)
        state_now = block_end(inputs_b, in_b, rates_s[lo_row : lo_row + block_len], state_now)
    return jnp.stack(saved)


def block_consts(inputs_b, in_b, out_b, rates, factor):
    length = inputs_b.shape[0]
    cumulative = jnp.cumsum(rates, axis=0)
    ending = cumulative[-1]
    locations = jnp.arange(length)
    lower_mask = (locations[:, None] >= locations[None, :])[:, :, None]
    spread = jnp.where(lower_mask, cumulative[:, None, :] - cumulative[None, :, :], 0.0)
    decays = jnp.where(lower_mask, jnp.exp(spread), 0.0)
    tail_decay = jnp.exp(ending[None, :] - cumulative)
    leading = jnp.exp(cumulative)
    scores = jnp.dot(out_b, in_b.T, preferred_element_type=jnp.float32)
    cum_t = cumulative.T
    upper = (locations[:, None] <= locations[None, :])[None]
    spread_t = jnp.where(upper, cum_t[:, None, :] - cum_t[:, :, None], 0.0)
    decays_t = jnp.where(upper, jnp.exp(spread_t), 0.0)
    scores_t = jnp.dot(in_b, out_b.T, preferred_element_type=jnp.float32)
    weighted = (factor * decays_t * scores_t[None]).astype(jnp.bfloat16)
    tail_inputs = (tail_decay[:, :, None] * inputs_b.astype(jnp.float32)).astype(jnp.bfloat16)
    return dict(
        decays=decays,
        tail=tail_decay,
        lead=leading,
        weighted=weighted,
        tail_inputs=tail_inputs,
        ending=jnp.exp(ending),
    )


def step_kernel(
    step_ref, tab_ref, wt_ref, dec_ref, inc_ref, top_ref, x_ref, b_ref, c_ref, tail_ref, lead_ref, xt_ref,
    sb_ref, r_ref, end_ref, w_ref, gs_ref, ms_ref, out_ref, rnew_ref, dbc_ref, gstore_ref, mstore_ref,
    v_ref, gx_ref, *, factor, width, level_pos, levels
):
    base = (step_ref[0] * levels + level_pos) * 3
    f32 = jnp.float32
    bf16 = jnp.bfloat16
    length, features = v_ref.shape
    lanes = 128
    per_pair = lanes // width
    nt = (((1,), (1,)), ((), ()))
    tn = (((0,), (0,)), ((), ()))
    v_ref[...] = jnp.where(tab_ref[base + 1] > 0, top_ref[...], inc_ref[...])
    rb_t = r_ref[...].astype(bf16)
    in_map = b_ref[...]
    out_map = c_ref[...]
    lane_id = lax.broadcasted_iota(jnp.int32, (length, lanes), 1)
    masks = [(lane_id >= e * width) & (lane_id < (e + 1) * width) for e in range(per_pair)]
    mix_acc = jnp.zeros((per_pair * length, length), f32)
    for q in range(features // lanes):
        cols = slice(q * lanes, (q + 1) * lanes)
        v_q = v_ref[:, cols]
        x_q = x_ref[:, cols]
        stacked = jnp.concatenate([jnp.where(m, v_q, jnp.zeros_like(v_q)) for m in masks], axis=0)
        gx_q = jnp.dot(
            wt_ref[per_pair * q], stacked[0:length], preferred_element_type=f32
        )
        for e in range(1, per_pair):
            gx_q = gx_q + jnp.dot(
                wt_ref[per_pair * q + e],
                stacked[e * length:(e + 1) * length],
                preferred_element_type=f32,
            )
        rbb_q = jnp.dot(in_map, rb_t[:, cols], preferred_element_type=f32)
        gx_ref[:, cols] = gx_q + tail_ref[:, cols] * rbb_q
        pair_dots = lax.dot_general(stacked, x_q, nt, preferred_element_type=f32)
        mix_acc = mix_acc + dec_ref[q] * pair_dots
    mixing = mix_acc[0:length]
    for e in range(1, per_pair):
        mixing = mixing + mix_acc[e * length:(e + 1) * length]
    mixing = mixing.astype(bf16)
    v = v_ref[...]
    lead_grads = (lead_ref[...] * v.astype(f32)).astype(bf16)
    grad_inmap = factor * lax.dot_general(mixing, out_map, tn, preferred_element_type=f32)
    grad_inmap = grad_inmap + lax.dot_general(xt_ref[...], rb_t, nt, preferred_element_type=f32)
    grad_outmap = factor * (
        jnp.dot(mixing, in_map, preferred_element_type=f32)
        + lax.dot_general(lead_grads, sb_ref[...], nt, preferred_element_type=f32)
    )
    carry = factor * lax.dot_general(out_map, lead_grads, tn, preferred_element_type=f32)
    rnew_ref[...] = carry + end_ref[...] * r_ref[...]
    grad_bc = jnp.concatenate([grad_inmap, grad_outmap], axis=1).astype(bf16)
    dbc_ref[...] = grad_bc
    mstore_ref[...] = jnp.where(tab_ref[base + 2] > 0, grad_bc, ms_ref[...])
    back = lax.dot_general(grad_bc, w_ref[...], nt, preferred_element_type=f32)
    summed = (v.astype(f32) + gx_ref[...] + back).astype(out_ref.dtype)
    out_ref[...] = summed
    gstore_ref[...] = jnp.where(tab_ref[base + 2] > 0, summed, gs_ref[...])


def fused_step(step_arr, table, level_pos, levels, per_block, incoming, top_blk, carried, w_bc, grad_store, map_store, level_no, seq_no, factor, width):
    wt2, dec2, x_flat, in_blk, out_blk, tail_full, lead_full, xt_full, states_t, end_row = per_block
    length, features = incoming.shape[1:]
    state_size = in_blk.shape[-1]

    def lead_block(a):
        shape = (None, None, None) + a.shape[3:]
        tail = (0,) * (a.ndim - 3)
        return pl.BlockSpec(shape, lambda i, c, t: (t[(c[0] * levels + level_pos) * 3], level_no, seq_no) + tail)

    in_specs = [lead_block(a) for a in (wt2, dec2)]
    in_specs.append(pl.BlockSpec((None, length, features), lambda i, c, t: (seq_no, 0, 0)))
    in_specs.append(pl.BlockSpec((None, None, length, features), lambda i, c, t: (t[(c[0] * levels + level_pos) * 3], seq_no, 0, 0)))
    in_specs += [lead_block(a) for a in (x_flat, in_blk, out_blk, tail_full, lead_full, xt_full, states_t)]
    in_specs.append(pl.BlockSpec((None, None) + carried.shape[2:], lambda i, c, t: (level_no, seq_no, 0, 0)))
    in_specs.append(lead_block(end_row))
    in_specs.append(pl.BlockSpec((None,) + w_bc.shape[1:], lambda i, c, t: (level_no, 0, 0)))
    store_g = pl.BlockSpec((None, None, None, length, features), lambda i, c, t: (t[(c[0] * levels + level_pos) * 3], level_no, seq_no, 0, 0))
    store_m = pl.BlockSpec((None, None, None, length, 2 * state_size), lambda i, c, t: (t[(c[0] * levels + level_pos) * 3], level_no, seq_no, 0, 0))
    in_specs += [store_g, store_m]
    out_specs = (
        pl.BlockSpec((length, features), lambda i, c, t: (0, 0)),
        pl.BlockSpec((None, None) + carried.shape[2:], lambda i, c, t: (level_no, seq_no, 0, 0)),
        pl.BlockSpec((length, 2 * state_size), lambda i, c, t: (0, 0)),
        store_g,
        store_m,
    )
    flops = 2 * length * features * (6 * state_size + 4 * length)
    moved = 2 * (4 * features * state_size * 2 + 6 * length * features) + 4 * 4 * length * features
    return pl.pallas_call(
        functools.partial(
            step_kernel, factor=factor, width=width, level_pos=level_pos, levels=levels
        ),
        out_shape=(
            jax.ShapeDtypeStruct((length, features), jnp.bfloat16),
            jax.ShapeDtypeStruct(carried.shape, jnp.float32),
            jax.ShapeDtypeStruct((length, 2 * state_size), jnp.bfloat16),
            jax.ShapeDtypeStruct(grad_store.shape, grad_store.dtype),
            jax.ShapeDtypeStruct(map_store.shape, map_store.dtype),
        ),
        grid_spec=pltpu.PrefetchScalarGridSpec(
            num_scalar_prefetch=2,
            grid=(1,),
            in_specs=in_specs,
            out_specs=out_specs,
            scratch_shapes=[
                pltpu.VMEM((length, features), jnp.bfloat16),
                pltpu.VMEM((length, features), jnp.float32),
            ],
        ),
        input_output_aliases={13: 1, 16: 3, 17: 4},
        cost_estimate=pl.CostEstimate(flops=flops, bytes_accessed=moved, transcendentals=0),
    )(step_arr, table, wt2, dec2, incoming, top_blk, x_flat, in_blk, out_blk, tail_full, lead_full, xt_full, states_t, carried, end_row, w_bc, grad_store, map_store)


def shards(layer_inputs, w_bc, log_decay, top_grad):
    sections = lax.axis_size("section")
    section_id = lax.axis_index("section")
    lay_dev, seq_dev, tok_len, features = layer_inputs.shape
    head_count = log_decay.shape[-1]
    block_len = tok_len // MICRO
    state_size = w_bc.shape[-1] // 2
    factor = 0.25 / state_size
    bc_all = jnp.einsum(
        "lstd,ldc->lstc", layer_inputs, w_bc, preferred_element_type=jnp.float32
    ).astype(jnp.bfloat16)

    def blocked(a):
        split = a.reshape(a.shape[:2] + (MICRO, block_len) + a.shape[3:])
        return jnp.moveaxis(split, 2, 0)

    x_blk = blocked(layer_inputs).reshape(
        (MICRO, lay_dev, seq_dev, block_len, head_count, features // head_count)
    )
    bc_blk = blocked(bc_all)
    in_blk = bc_blk[..., :state_size]
    out_blk = bc_blk[..., state_size:]
    rates_blk = blocked(log_decay)
    consts_fn = jax.vmap(jax.vmap(jax.vmap(lambda x, b, c, r: block_consts(x, b, c, r, factor))))
    consts = consts_fn(x_blk, in_blk, out_blk, rates_blk)
    width = features // head_count
    lead_dims = consts["tail"].shape[:3]
    pairs = head_count * width // 128
    per_pair = 128 // width
    wt2 = consts["weighted"]
    dec2 = jnp.moveaxis(consts["decays"], -1, -3).reshape(
        lead_dims + (pairs, per_pair * block_len, block_len)
    )
    spread_heads = (
        jnp.arange(features)[None, :] // width == jnp.arange(head_count)[:, None]
    ).astype(jnp.float32)

    def per_lane(a):
        return jnp.einsum(
            "...h,hd->...d", a, spread_heads, precision=lax.Precision.HIGHEST,
            preferred_element_type=jnp.float32,
        )

    tail_full = per_lane(consts["tail"])
    lead_full = per_lane(consts["lead"])
    xt_full = consts["tail_inputs"].reshape(lead_dims + (block_len, features))
    end_row = per_lane(consts["ending"])[..., None, :]
    fresh_t = jnp.einsum(
        "mlsjn,mlsjd->mlsnd", in_blk, xt_full, preferred_element_type=jnp.float32
    )
    state_now = jnp.zeros(fresh_t.shape[1:], jnp.float32)
    saved = []
    for block_no in range(MICRO):
        saved.append(state_now.astype(jnp.bfloat16))
        state_now = end_row[block_no] * state_now + fresh_t[block_no]
    states_t = jnp.stack(saved)
    x_flat = x_blk.reshape(lead_dims + (block_len, features))
    per_block = (wt2, dec2, x_flat, in_blk, out_blk, tail_full, lead_full, xt_full, states_t, end_row)
    per_block = lax.optimization_barrier(per_block)

    top_blk = jnp.moveaxis(
        top_grad.reshape((seq_dev, MICRO, block_len, features)), 1, 0
    )
    is_top = section_id == sections - 1

    steps = MICRO + sections - 1
    counters = jnp.arange(steps, dtype=jnp.int32)[:, None]
    offsets = counters - (sections - 1 - section_id)
    valid_tab = ((offsets >= 0) & (offsets < MICRO)).astype(jnp.int32)
    block_tab = jnp.clip(MICRO - 1 - offsets, 0, MICRO - 1).astype(jnp.int32)
    top_tab = (jnp.arange(lay_dev)[None, ::-1] == lay_dev - 1) & is_top
    table = jnp.stack(
        jnp.broadcast_arrays(block_tab, top_tab.astype(jnp.int32), valid_tab), axis=-1
    ).reshape(-1).astype(jnp.int32)

    def advance(counter, loop_state, send=True):
        incoming, carried, grad_store, map_store = loop_state
        step_arr = jnp.reshape(counter, (1,)).astype(jnp.int32)
        for level_pos, level_no in enumerate(reversed(range(lay_dev))):
            level_out = []
            for seq_no in range(seq_dev):
                level_grads, carried, grad_bc, grad_store, map_store = fused_step(
                    step_arr, table, level_pos, lay_dev, per_block, incoming, top_blk, carried,
                    w_bc, grad_store, map_store, level_no, seq_no, factor, width,
                )
                level_out.append(level_grads)
            incoming = jnp.stack(level_out)
        if send:
            incoming = passed_along(incoming, "section", -1)
        return (incoming, carried, grad_store, map_store)

    initial = (
        jnp.zeros((seq_dev, block_len, features), jnp.bfloat16),
        jnp.zeros(states_t.shape[1:], jnp.float32),
        jnp.zeros((MICRO, lay_dev, seq_dev, block_len, features), jnp.bfloat16),
        jnp.zeros((MICRO, lay_dev, seq_dev, block_len, 2 * state_size), jnp.bfloat16),
    )
    final_state = lax.fori_loop(0, steps - 1, advance, initial)
    final_state = advance(steps - 1, final_state, send=False)
    grad_store = final_state[2]
    map_store = final_state[3]

    grad_inputs = jnp.moveaxis(grad_store, 0, 2).reshape(layer_inputs.shape)
    map_store = jnp.moveaxis(map_store, 0, 2).reshape(bc_all.shape)
    ways = lax.axis_size("dp")
    divisor = ways * seq_dev
    rows_here = layer_inputs.reshape(lay_dev, seq_dev * tok_len, ways, features // ways)
    rows_here = jnp.transpose(rows_here, (2, 0, 1, 3))
    rows_all = lax.all_to_all(rows_here, "dp", 0, 0, tiled=True)
    maps_here = map_store.reshape(1, lay_dev, seq_dev * tok_len, map_store.shape[-1])
    maps_all = lax.all_gather(maps_here, "dp", axis=0, tiled=True)
    grad_w = jnp.einsum(
        "glrd,glrc->ldc", rows_all, maps_all, preferred_element_type=jnp.float32
    ) / divisor
    return (grad_inputs, grad_w)


def solution(mesh):
    in_specs = (
        P("section", "dp", None, None),
        P("section", None, None),
        P("section", "dp", None, None),
        P("dp", None, None),
    )
    out_specs = (P("section", "dp", None, None), P("section", "dp", None))
    return jax.shard_map(shards, mesh=mesh, in_specs=in_specs, out_specs=out_specs, check_vma=False)
```

```python
import functools

import jax
import jax.numpy as jnp
from jax import lax
from jax.experimental import pallas as pl
from jax.experimental.pallas import tpu as pltpu
from jax.sharding import PartitionSpec as P

MICRO = 4


def shortened(value):
    return jax.tree.map(lambda a: a.astype(jnp.bfloat16) if a.dtype == jnp.float32 else a, value)


def passed_along(block, axis, distance):
    devices = range(lax.axis_size(axis))
    route = [(i - distance, i) for i in devices if i - distance in devices]
    return lax.ppermute(block, axis, route)


def block_terms(inputs_b, in_b, out_b, rates, grads_b, carried, state_in, factor):
    length = inputs_b.shape[0]
    cumulative = jnp.cumsum(rates, axis=0)
    ending = cumulative[-1]
    locations = jnp.arange(length)
    lower_mask = (locations[:, None] >= locations[None, :])[:, :, None]
    spread = jnp.where(lower_mask, cumulative[:, None, :] - cumulative[None, :, :], 0.0)
    decays = jnp.where(lower_mask, jnp.exp(spread), 0.0)
    tail_decay = jnp.exp(ending[None, :] - cumulative)
    leading = jnp.exp(cumulative)
    scores = jnp.dot(out_b, in_b.T, preferred_element_type=jnp.float32)
    weighted = (factor * decays * scores[:, :, None]).astype(jnp.bfloat16)
    carried_b = carried.astype(jnp.bfloat16)
    state_b = state_in.astype(jnp.bfloat16)
    grad_feats = jnp.einsum("kjh,khp->jhp", weighted, grads_b, preferred_element_type=jnp.float32)
    grad_feats = grad_feats + tail_decay[:, :, None] * jnp.einsum(
        "hpn,jn->jhp", carried_b, in_b, preferred_element_type=jnp.float32
    )
    pair_dots = jnp.einsum("khp,jhp->kjh", grads_b, inputs_b, preferred_element_type=jnp.float32)
    mixing = jnp.sum(decays * pair_dots, axis=2).astype(jnp.bfloat16)
    tail_inputs = (tail_decay[:, :, None] * inputs_b.astype(jnp.float32)).astype(jnp.bfloat16)
    lead_grads = (leading[:, :, None] * grads_b.astype(jnp.float32)).astype(jnp.bfloat16)
    grad_inmap = factor * jnp.dot(mixing.T, out_b, preferred_element_type=jnp.float32)
    grad_inmap = grad_inmap + jnp.einsum(
        "jhp,hpn->jn", tail_inputs, carried_b, preferred_element_type=jnp.float32
    )
    grad_outmap = factor * (
        jnp.dot(mixing, in_b, preferred_element_type=jnp.float32)
        + jnp.einsum("ihp,hpn->in", lead_grads, state_b, preferred_element_type=jnp.float32)
    )
    carry_out = factor * jnp.einsum(
        "khp,kn->hpn", lead_grads, out_b, preferred_element_type=jnp.float32
    )
    carry_out = carry_out + jnp.exp(ending)[:, None, None] * carried
    return (grad_feats, grad_inmap, grad_outmap, carry_out)


def block_end(inputs_b, in_b, rates, state_in):
    cumulative = jnp.cumsum(rates, axis=0)
    ending = cumulative[-1]
    tail_decay = jnp.exp(ending[None, :] - cumulative)
    tail_inputs = (tail_decay[:, :, None] * inputs_b.astype(jnp.float32)).astype(jnp.bfloat16)
    fresh = jnp.einsum("jhp,jn->hpn", tail_inputs, in_b, preferred_element_type=jnp.float32)
    return jnp.exp(ending)[:, None, None] * state_in + fresh


def split_block(inputs_c, map_block, head_count):
    length, features = inputs_c.shape
    state_size = map_block.shape[1] // 2
    inputs_b = inputs_c.reshape(length, head_count, features // head_count)
    in_b = map_block[:, :state_size]
    out_b = map_block[:, state_size:]
    return (inputs_b, in_b, out_b)


def block_back(inputs_c, map_block, rates, grads_c, carried, state_in, weights):
    length, features = inputs_c.shape
    head_count = rates.shape[1]
    factor = 0.25 / (map_block.shape[1] // 2)
    inputs_b, in_b, out_b = split_block(inputs_c, map_block, head_count)
    grads_b = grads_c.reshape(length, head_count, features // head_count)
    grad_feats, grad_inmap, grad_outmap, carry_out = block_terms(
        inputs_b, in_b, out_b, rates, grads_b, carried, state_in, factor
    )
    grad_bc = jnp.concatenate([grad_inmap, grad_outmap], axis=1).astype(jnp.bfloat16)
    back_proj = lax.dot_general(
        grad_bc, weights, (((1,), (1,)), ((), ())), preferred_element_type=jnp.float32
    )
    summed = grads_c.astype(jnp.float32) + grad_feats.reshape(length, features) + back_proj
    return (summed.astype(jnp.bfloat16), carry_out, grad_bc)


def layer_starts(inputs_s, bc_s, rates_s):
    head_count = rates_s.shape[1]
    features = inputs_s.shape[1]
    state_size = bc_s.shape[1] // 2
    block_len = inputs_s.shape[0] // MICRO
    state_now = jnp.zeros((head_count, features // head_count, state_size), jnp.float32)
    saved = []
    for block_no in range(MICRO):
        lo_row = block_no * block_len
        inputs_b, in_b, out_b = split_block(
            inputs_s[lo_row : lo_row + block_len], bc_s[lo_row : lo_row + block_len], head_count
        )
        saved.append(state_now)
        state_now = block_end(inputs_b, in_b, rates_s[lo_row : lo_row + block_len], state_now)
    return jnp.stack(saved)


def block_consts(inputs_b, in_b, out_b, rates, factor):
    length = inputs_b.shape[0]
    cumulative = jnp.cumsum(rates, axis=0)
    ending = cumulative[-1]
    locations = jnp.arange(length)
    lower_mask = (locations[:, None] >= locations[None, :])[:, :, None]
    spread = jnp.where(lower_mask, cumulative[:, None, :] - cumulative[None, :, :], 0.0)
    decays = jnp.where(lower_mask, jnp.exp(spread), 0.0)
    tail_decay = jnp.exp(ending[None, :] - cumulative)
    leading = jnp.exp(cumulative)
    scores = jnp.dot(out_b, in_b.T, preferred_element_type=jnp.float32)
    cum_t = cumulative.T
    upper = (locations[:, None] <= locations[None, :])[None]
    spread_t = jnp.where(upper, cum_t[:, None, :] - cum_t[:, :, None], 0.0)
    decays_t = jnp.where(upper, jnp.exp(spread_t), 0.0)
    scores_t = jnp.dot(in_b, out_b.T, preferred_element_type=jnp.float32)
    weighted = (factor * decays_t * scores_t[None]).astype(jnp.bfloat16)
    tail_inputs = (tail_decay[:, :, None] * inputs_b.astype(jnp.float32)).astype(jnp.bfloat16)
    return dict(
        decays=decays,
        tail=tail_decay,
        lead=leading,
        weighted=weighted,
        tail_inputs=tail_inputs,
        ending=jnp.exp(ending),
    )


def step_kernel(
    step_ref, tab_ref, wt_ref, dec_ref, inc_ref, top_ref, x_ref, b_ref, c_ref, tail_ref, lead_ref, xt_ref,
    sb_ref, r_ref, end_ref, w_ref, gs_ref, ms_ref, out_ref, rnew_ref, dbc_ref, gstore_ref, mstore_ref,
    v_ref, gx_ref, tail_buf, lead_buf, xt_buf, sb_buf, r_buf, w_buf, sems, *, factor, width,
    level_pos, levels, level_no, seq_no
):
    base = (step_ref[0] * levels + level_pos) * 3
    blk = tab_ref[base]
    fetches = [
        pltpu.make_async_copy(r_ref.at[level_no, seq_no], r_buf, sems.at[0]),
        pltpu.make_async_copy(tail_ref.at[blk, level_no, seq_no], tail_buf, sems.at[1]),
        pltpu.make_async_copy(xt_ref.at[blk, level_no, seq_no], xt_buf, sems.at[2]),
        pltpu.make_async_copy(lead_ref.at[blk, level_no, seq_no], lead_buf, sems.at[3]),
        pltpu.make_async_copy(sb_ref.at[blk, level_no, seq_no], sb_buf, sems.at[4]),
        pltpu.make_async_copy(w_ref.at[level_no], w_buf, sems.at[5]),
    ]
    for fetch in fetches:
        fetch.start()
    f32 = jnp.float32
    bf16 = jnp.bfloat16
    length, features = v_ref.shape
    lanes = 128
    per_pair = lanes // width
    nt = (((1,), (1,)), ((), ()))
    tn = (((0,), (0,)), ((), ()))
    v_ref[...] = jnp.where(tab_ref[base + 1] > 0, top_ref[...], inc_ref[...])
    in_map = b_ref[...]
    out_map = c_ref[...]
    lane_id = lax.broadcasted_iota(jnp.int32, (length, lanes), 1)
    masks = [(lane_id >= e * width) & (lane_id < (e + 1) * width) for e in range(per_pair)]
    mix_acc = jnp.zeros((per_pair * length, length), f32)
    for q in range(features // lanes):
        cols = slice(q * lanes, (q + 1) * lanes)
        v_q = v_ref[:, cols]
        x_q = x_ref[:, cols]
        stacked = jnp.concatenate([jnp.where(m, v_q, jnp.zeros_like(v_q)) for m in masks], axis=0)
        gx_q = jnp.dot(
            wt_ref[per_pair * q], stacked[0:length], preferred_element_type=f32
        )
        for e in range(1, per_pair):
            gx_q = gx_q + jnp.dot(
                wt_ref[per_pair * q + e],
                stacked[e * length:(e + 1) * length],
                preferred_element_type=f32,
            )
        gx_ref[:, cols] = gx_q
        pair_dots = lax.dot_general(stacked, x_q, nt, preferred_element_type=f32)
        mix_acc = mix_acc + dec_ref[q] * pair_dots
    mixing = mix_acc[0:length]
    for e in range(1, per_pair):
        mixing = mixing + mix_acc[e * length:(e + 1) * length]
    mixing = mixing.astype(bf16)
    fetches[0].wait()
    fetches[1].wait()
    rb_t = r_buf[...].astype(bf16)
    rbb = jnp.dot(in_map, rb_t, preferred_element_type=f32)
    gx_ref[...] = gx_ref[...] + tail_buf[...] * rbb
    v = v_ref[...]
    fetches[2].wait()
    grad_inmap = factor * lax.dot_general(mixing, out_map, tn, preferred_element_type=f32)
    grad_inmap = grad_inmap + lax.dot_general(xt_buf[...], rb_t, nt, preferred_element_type=f32)
    fetches[3].wait()
    fetches[4].wait()
    lead_grads = (lead_buf[...] * v.astype(f32)).astype(bf16)
    grad_outmap = factor * (
        jnp.dot(mixing, in_map, preferred_element_type=f32)
        + lax.dot_general(lead_grads, sb_buf[...], nt, preferred_element_type=f32)
    )
    carry = factor * lax.dot_general(out_map, lead_grads, tn, preferred_element_type=f32)
    rnew_ref[...] = carry + end_ref[...] * r_buf[...]
    grad_bc = jnp.concatenate([grad_inmap, grad_outmap], axis=1).astype(bf16)
    dbc_ref[...] = grad_bc
    mstore_ref[...] = jnp.where(tab_ref[base + 2] > 0, grad_bc, ms_ref[...])
    fetches[5].wait()
    back = lax.dot_general(grad_bc, w_buf[...], nt, preferred_element_type=f32)
    summed = (v.astype(f32) + gx_ref[...] + back).astype(out_ref.dtype)
    out_ref[...] = summed
    gstore_ref[...] = jnp.where(tab_ref[base + 2] > 0, summed, gs_ref[...])


def fused_step(step_arr, table, level_pos, levels, per_block, incoming, top_blk, carried, w_bc, grad_store, map_store, level_no, seq_no, factor, width):
    wt2, dec2, x_flat, in_blk, out_blk, tail_full, lead_full, xt_full, states_t, end_row = per_block
    length, features = incoming.shape[1:]
    state_size = in_blk.shape[-1]

    def lead_block(a):
        shape = (None, None, None) + a.shape[3:]
        tail = (0,) * (a.ndim - 3)
        return pl.BlockSpec(shape, lambda i, c, t: (t[(c[0] * levels + level_pos) * 3], level_no, seq_no) + tail)

    in_specs = [lead_block(a) for a in (wt2, dec2)]
    in_specs.append(pl.BlockSpec((None, length, features), lambda i, c, t: (seq_no, 0, 0)))
    in_specs.append(pl.BlockSpec((None, None, length, features), lambda i, c, t: (t[(c[0] * levels + level_pos) * 3], seq_no, 0, 0)))
    in_hbm = pl.BlockSpec(memory_space=pl.ANY)
    in_specs += [lead_block(a) for a in (x_flat, in_blk, out_blk)]
    in_specs += [in_hbm] * 5
    in_specs.append(lead_block(end_row))
    in_specs.append(in_hbm)
    store_g = pl.BlockSpec((None, None, None, length, features), lambda i, c, t: (t[(c[0] * levels + level_pos) * 3], level_no, seq_no, 0, 0))
    store_m = pl.BlockSpec((None, None, None, length, 2 * state_size), lambda i, c, t: (t[(c[0] * levels + level_pos) * 3], level_no, seq_no, 0, 0))
    in_specs += [store_g, store_m]
    out_specs = (
        pl.BlockSpec((length, features), lambda i, c, t: (0, 0)),
        pl.BlockSpec((None, None) + carried.shape[2:], lambda i, c, t: (level_no, seq_no, 0, 0)),
        pl.BlockSpec((length, 2 * state_size), lambda i, c, t: (0, 0)),
        store_g,
        store_m,
    )
    flops = 2 * length * features * (6 * state_size + 4 * length)
    moved = 2 * (4 * features * state_size * 2 + 6 * length * features) + 4 * 4 * length * features
    return pl.pallas_call(
        functools.partial(
            step_kernel, factor=factor, width=width, level_pos=level_pos, levels=levels,
            level_no=level_no, seq_no=seq_no,
        ),
        out_shape=(
            jax.ShapeDtypeStruct((length, features), jnp.bfloat16),
            jax.ShapeDtypeStruct(carried.shape, jnp.float32),
            jax.ShapeDtypeStruct((length, 2 * state_size), jnp.bfloat16),
            jax.ShapeDtypeStruct(grad_store.shape, grad_store.dtype),
            jax.ShapeDtypeStruct(map_store.shape, map_store.dtype),
        ),
        grid_spec=pltpu.PrefetchScalarGridSpec(
            num_scalar_prefetch=2,
            grid=(1,),
            in_specs=in_specs,
            out_specs=out_specs,
            scratch_shapes=[
                pltpu.VMEM((length, features), jnp.bfloat16),
                pltpu.VMEM((length, features), jnp.float32),
                pltpu.VMEM((length, features), jnp.float32),
                pltpu.VMEM((length, features), jnp.float32),
                pltpu.VMEM((length, features), jnp.bfloat16),
                pltpu.VMEM(states_t.shape[3:], states_t.dtype),
                pltpu.VMEM(carried.shape[2:], jnp.float32),
                pltpu.VMEM(w_bc.shape[1:], w_bc.dtype),
                pltpu.SemaphoreType.DMA((6,)),
            ],
        ),
        input_output_aliases={13: 1, 16: 3, 17: 4},
        cost_estimate=pl.CostEstimate(flops=flops, bytes_accessed=moved, transcendentals=0),
    )(step_arr, table, wt2, dec2, incoming, top_blk, x_flat, in_blk, out_blk, tail_full, lead_full, xt_full, states_t, carried, end_row, w_bc, grad_store, map_store)


def shards(layer_inputs, w_bc, log_decay, top_grad):
    sections = lax.axis_size("section")
    section_id = lax.axis_index("section")
    lay_dev, seq_dev, tok_len, features = layer_inputs.shape
    head_count = log_decay.shape[-1]
    block_len = tok_len // MICRO
    state_size = w_bc.shape[-1] // 2
    factor = 0.25 / state_size
    bc_all = jnp.einsum(
        "lstd,ldc->lstc", layer_inputs, w_bc, preferred_element_type=jnp.float32
    ).astype(jnp.bfloat16)

    def blocked(a):
        split = a.reshape(a.shape[:2] + (MICRO, block_len) + a.shape[3:])
        return jnp.moveaxis(split, 2, 0)

    x_blk = blocked(layer_inputs).reshape(
        (MICRO, lay_dev, seq_dev, block_len, head_count, features // head_count)
    )
    bc_blk = blocked(bc_all)
    in_blk = bc_blk[..., :state_size]
    out_blk = bc_blk[..., state_size:]
    rates_blk = blocked(log_decay)
    consts_fn = jax.vmap(jax.vmap(jax.vmap(lambda x, b, c, r: block_consts(x, b, c, r, factor))))
    consts = consts_fn(x_blk, in_blk, out_blk, rates_blk)
    width = features // head_count
    lead_dims = consts["tail"].shape[:3]
    pairs = head_count * width // 128
    per_pair = 128 // width
    wt2 = consts["weighted"]
    dec2 = jnp.moveaxis(consts["decays"], -1, -3).reshape(
        lead_dims + (pairs, per_pair * block_len, block_len)
    )
    spread_heads = (
        jnp.arange(features)[None, :] // width == jnp.arange(head_count)[:, None]
    ).astype(jnp.float32)

    def per_lane(a):
        return jnp.einsum(
            "...h,hd->...d", a, spread_heads, precision=lax.Precision.HIGHEST,
            preferred_element_type=jnp.float32,
        )

    tail_full = per_lane(consts["tail"])
    lead_full = per_lane(consts["lead"])
    xt_full = consts["tail_inputs"].reshape(lead_dims + (block_len, features))
    end_row = per_lane(consts["ending"])[..., None, :]
    fresh_t = jnp.einsum(
        "mlsjn,mlsjd->mlsnd", in_blk, xt_full, preferred_element_type=jnp.float32
    )
    state_now = jnp.zeros(fresh_t.shape[1:], jnp.float32)
    saved = []
    for block_no in range(MICRO):
        saved.append(state_now.astype(jnp.bfloat16))
        state_now = end_row[block_no] * state_now + fresh_t[block_no]
    states_t = jnp.stack(saved)
    x_flat = x_blk.reshape(lead_dims + (block_len, features))
    per_block = (wt2, dec2, x_flat, in_blk, out_blk, tail_full, lead_full, xt_full, states_t, end_row)
    per_block = lax.optimization_barrier(per_block)

    top_blk = jnp.moveaxis(
        top_grad.reshape((seq_dev, MICRO, block_len, features)), 1, 0
    )
    is_top = section_id == sections - 1

    steps = MICRO + sections - 1
    counters = jnp.arange(steps, dtype=jnp.int32)[:, None]
    offsets = counters - (sections - 1 - section_id)
    valid_tab = ((offsets >= 0) & (offsets < MICRO)).astype(jnp.int32)
    block_tab = jnp.clip(MICRO - 1 - offsets, 0, MICRO - 1).astype(jnp.int32)
    top_tab = (jnp.arange(lay_dev)[None, ::-1] == lay_dev - 1) & is_top
    table = jnp.stack(
        jnp.broadcast_arrays(block_tab, top_tab.astype(jnp.int32), valid_tab), axis=-1
    ).reshape(-1).astype(jnp.int32)

    def advance(counter, loop_state, send=True):
        incoming, carried, grad_store, map_store = loop_state
        step_arr = jnp.reshape(counter, (1,)).astype(jnp.int32)
        for level_pos, level_no in enumerate(reversed(range(lay_dev))):
            level_out = []
            for seq_no in range(seq_dev):
                level_grads, carried, grad_bc, grad_store, map_store = fused_step(
                    step_arr, table, level_pos, lay_dev, per_block, incoming, top_blk, carried,
                    w_bc, grad_store, map_store, level_no, seq_no, factor, width,
                )
                level_out.append(level_grads)
            incoming = jnp.stack(level_out)
        if send:
            incoming = passed_along(incoming, "section", -1)
        return (incoming, carried, grad_store, map_store)

    initial = (
        jnp.zeros((seq_dev, block_len, features), jnp.bfloat16),
        jnp.zeros(states_t.shape[1:], jnp.float32),
        jnp.zeros((MICRO, lay_dev, seq_dev, block_len, features), jnp.bfloat16),
        jnp.zeros((MICRO, lay_dev, seq_dev, block_len, 2 * state_size), jnp.bfloat16),
    )
    final_state = lax.fori_loop(0, steps - 1, advance, initial)
    final_state = advance(steps - 1, final_state, send=False)
    grad_store = final_state[2]
    map_store = final_state[3]

    grad_inputs = jnp.moveaxis(grad_store, 0, 2).reshape(layer_inputs.shape)
    map_store = jnp.moveaxis(map_store, 0, 2).reshape(bc_all.shape)
    ways = lax.axis_size("dp")
    divisor = ways * seq_dev
    rows_here = layer_inputs.reshape(lay_dev, seq_dev * tok_len, ways, features // ways)
    rows_here = jnp.transpose(rows_here, (2, 0, 1, 3))
    rows_all = lax.all_to_all(rows_here, "dp", 0, 0, tiled=True)
    maps_here = map_store.reshape(1, lay_dev, seq_dev * tok_len, map_store.shape[-1])
    maps_all = lax.all_gather(maps_here, "dp", axis=0, tiled=True)
    grad_w = jnp.einsum(
        "glrd,glrc->ldc", rows_all, maps_all, preferred_element_type=jnp.float32
    ) / divisor
    return (grad_inputs, grad_w)


def solution(mesh):
    in_specs = (
        P("section", "dp", None, None),
        P("section", None, None),
        P("section", "dp", None, None),
        P("dp", None, None),
    )
    out_specs = (P("section", "dp", None, None), P("section", "dp", None))
    return jax.shard_map(shards, mesh=mesh, in_specs=in_specs, out_specs=out_specs, check_vma=False)
```

```python
import functools

import jax
import jax.numpy as jnp
from jax import lax
from jax.experimental import pallas as pl
from jax.experimental.pallas import tpu as pltpu
from jax.sharding import PartitionSpec as P

MICRO = 4


def shortened(value):
    return jax.tree.map(lambda a: a.astype(jnp.bfloat16) if a.dtype == jnp.float32 else a, value)


def passed_along(block, axis, distance):
    devices = range(lax.axis_size(axis))
    route = [(i - distance, i) for i in devices if i - distance in devices]
    return lax.ppermute(block, axis, route)


def block_terms(inputs_b, in_b, out_b, rates, grads_b, carried, state_in, factor):
    length = inputs_b.shape[0]
    cumulative = jnp.cumsum(rates, axis=0)
    ending = cumulative[-1]
    locations = jnp.arange(length)
    lower_mask = (locations[:, None] >= locations[None, :])[:, :, None]
    spread = jnp.where(lower_mask, cumulative[:, None, :] - cumulative[None, :, :], 0.0)
    decays = jnp.where(lower_mask, jnp.exp(spread), 0.0)
    tail_decay = jnp.exp(ending[None, :] - cumulative)
    leading = jnp.exp(cumulative)
    scores = jnp.dot(out_b, in_b.T, preferred_element_type=jnp.float32)
    weighted = (factor * decays * scores[:, :, None]).astype(jnp.bfloat16)
    carried_b = carried.astype(jnp.bfloat16)
    state_b = state_in.astype(jnp.bfloat16)
    grad_feats = jnp.einsum("kjh,khp->jhp", weighted, grads_b, preferred_element_type=jnp.float32)
    grad_feats = grad_feats + tail_decay[:, :, None] * jnp.einsum(
        "hpn,jn->jhp", carried_b, in_b, preferred_element_type=jnp.float32
    )
    pair_dots = jnp.einsum("khp,jhp->kjh", grads_b, inputs_b, preferred_element_type=jnp.float32)
    mixing = jnp.sum(decays * pair_dots, axis=2).astype(jnp.bfloat16)
    tail_inputs = (tail_decay[:, :, None] * inputs_b.astype(jnp.float32)).astype(jnp.bfloat16)
    lead_grads = (leading[:, :, None] * grads_b.astype(jnp.float32)).astype(jnp.bfloat16)
    grad_inmap = factor * jnp.dot(mixing.T, out_b, preferred_element_type=jnp.float32)
    grad_inmap = grad_inmap + jnp.einsum(
        "jhp,hpn->jn", tail_inputs, carried_b, preferred_element_type=jnp.float32
    )
    grad_outmap = factor * (
        jnp.dot(mixing, in_b, preferred_element_type=jnp.float32)
        + jnp.einsum("ihp,hpn->in", lead_grads, state_b, preferred_element_type=jnp.float32)
    )
    carry_out = factor * jnp.einsum(
        "khp,kn->hpn", lead_grads, out_b, preferred_element_type=jnp.float32
    )
    carry_out = carry_out + jnp.exp(ending)[:, None, None] * carried
    return (grad_feats, grad_inmap, grad_outmap, carry_out)


def block_end(inputs_b, in_b, rates, state_in):
    cumulative = jnp.cumsum(rates, axis=0)
    ending = cumulative[-1]
    tail_decay = jnp.exp(ending[None, :] - cumulative)
    tail_inputs = (tail_decay[:, :, None] * inputs_b.astype(jnp.float32)).astype(jnp.bfloat16)
    fresh = jnp.einsum("jhp,jn->hpn", tail_inputs, in_b, preferred_element_type=jnp.float32)
    return jnp.exp(ending)[:, None, None] * state_in + fresh


def split_block(inputs_c, map_block, head_count):
    length, features = inputs_c.shape
    state_size = map_block.shape[1] // 2
    inputs_b = inputs_c.reshape(length, head_count, features // head_count)
    in_b = map_block[:, :state_size]
    out_b = map_block[:, state_size:]
    return (inputs_b, in_b, out_b)


def block_back(inputs_c, map_block, rates, grads_c, carried, state_in, weights):
    length, features = inputs_c.shape
    head_count = rates.shape[1]
    factor = 0.25 / (map_block.shape[1] // 2)
    inputs_b, in_b, out_b = split_block(inputs_c, map_block, head_count)
    grads_b = grads_c.reshape(length, head_count, features // head_count)
    grad_feats, grad_inmap, grad_outmap, carry_out = block_terms(
        inputs_b, in_b, out_b, rates, grads_b, carried, state_in, factor
    )
    grad_bc = jnp.concatenate([grad_inmap, grad_outmap], axis=1).astype(jnp.bfloat16)
    back_proj = lax.dot_general(
        grad_bc, weights, (((1,), (1,)), ((), ())), preferred_element_type=jnp.float32
    )
    summed = grads_c.astype(jnp.float32) + grad_feats.reshape(length, features) + back_proj
    return (summed.astype(jnp.bfloat16), carry_out, grad_bc)


def layer_starts(inputs_s, bc_s, rates_s):
    head_count = rates_s.shape[1]
    features = inputs_s.shape[1]
    state_size = bc_s.shape[1] // 2
    block_len = inputs_s.shape[0] // MICRO
    state_now = jnp.zeros((head_count, features // head_count, state_size), jnp.float32)
    saved = []
    for block_no in range(MICRO):
        lo_row = block_no * block_len
        inputs_b, in_b, out_b = split_block(
            inputs_s[lo_row : lo_row + block_len], bc_s[lo_row : lo_row + block_len], head_count
        )
        saved.append(state_now)
        state_now = block_end(inputs_b, in_b, rates_s[lo_row : lo_row + block_len], state_now)
    return jnp.stack(saved)


def block_consts(inputs_b, in_b, out_b, rates, factor):
    length = inputs_b.shape[0]
    cumulative = jnp.cumsum(rates, axis=0)
    ending = cumulative[-1]
    locations = jnp.arange(length)
    lower_mask = (locations[:, None] >= locations[None, :])[:, :, None]
    spread = jnp.where(lower_mask, cumulative[:, None, :] - cumulative[None, :, :], 0.0)
    decays = jnp.where(lower_mask, jnp.exp(spread), 0.0)
    tail_decay = jnp.exp(ending[None, :] - cumulative)
    leading = jnp.exp(cumulative)
    scores = jnp.dot(out_b, in_b.T, preferred_element_type=jnp.float32)
    cum_t = cumulative.T
    upper = (locations[:, None] <= locations[None, :])[None]
    spread_t = jnp.where(upper, cum_t[:, None, :] - cum_t[:, :, None], 0.0)
    decays_t = jnp.where(upper, jnp.exp(spread_t), 0.0)
    scores_t = jnp.dot(in_b, out_b.T, preferred_element_type=jnp.float32)
    weighted = (factor * decays_t * scores_t[None]).astype(jnp.bfloat16)
    return dict(
        decays=decays,
        tail=tail_decay,
        lead=leading,
        weighted=weighted,
        ending=jnp.exp(ending),
    )


def step_kernel(
    step_ref, tab_ref, wt_ref, dec_ref, inc_ref, top_ref, x_ref, b_ref, c_ref, tail_ref, lead_ref, xt_ref,
    sb_ref, r_ref, end_ref, w_ref, gs_ref, ms_ref, out_ref, rnew_ref, dbc_ref, gstore_ref, mstore_ref,
    v_ref, gx_ref, tail_buf, lead_buf, xt_buf, sb_buf, r_buf, w_buf, sems, *, factor, width,
    level_pos, levels, level_no, seq_no
):
    base = (step_ref[0] * levels + level_pos) * 3
    blk = tab_ref[base]
    fetches = [
        pltpu.make_async_copy(r_ref.at[level_no, seq_no], r_buf, sems.at[0]),
        pltpu.make_async_copy(tail_ref.at[blk, level_no, seq_no], tail_buf, sems.at[1]),
        pltpu.make_async_copy(xt_ref.at[blk, level_no, seq_no], xt_buf, sems.at[2]),
        pltpu.make_async_copy(lead_ref.at[blk, level_no, seq_no], lead_buf, sems.at[3]),
        pltpu.make_async_copy(sb_ref.at[blk, level_no, seq_no], sb_buf, sems.at[4]),
        pltpu.make_async_copy(w_ref.at[level_no], w_buf, sems.at[5]),
    ]
    for fetch in fetches:
        fetch.start()
    f32 = jnp.float32
    bf16 = jnp.bfloat16
    length, features = v_ref.shape
    lanes = 128
    per_pair = lanes // width
    nt = (((1,), (1,)), ((), ()))
    tn = (((0,), (0,)), ((), ()))
    v_ref[...] = jnp.where(tab_ref[base + 1] > 0, top_ref[...], inc_ref[...])
    in_map = b_ref[...]
    out_map = c_ref[...]
    lane_id = lax.broadcasted_iota(jnp.int32, (length, lanes), 1)
    masks = [(lane_id >= e * width) & (lane_id < (e + 1) * width) for e in range(per_pair)]
    mix_acc = jnp.zeros((per_pair * length, length), f32)
    for q in range(features // lanes):
        cols = slice(q * lanes, (q + 1) * lanes)
        v_q = v_ref[:, cols]
        x_q = x_ref[:, cols]
        stacked = jnp.concatenate([jnp.where(m, v_q, jnp.zeros_like(v_q)) for m in masks], axis=0)
        gx_q = jnp.dot(
            wt_ref[per_pair * q], stacked[0:length], preferred_element_type=f32
        )
        for e in range(1, per_pair):
            gx_q = gx_q + jnp.dot(
                wt_ref[per_pair * q + e],
                stacked[e * length:(e + 1) * length],
                preferred_element_type=f32,
            )
        gx_ref[:, cols] = gx_q
        pair_dots = lax.dot_general(stacked, x_q, nt, preferred_element_type=f32)
        mix_acc = mix_acc + dec_ref[q] * pair_dots
    mixing = mix_acc[0:length]
    for e in range(1, per_pair):
        mixing = mixing + mix_acc[e * length:(e + 1) * length]
    mixing = mixing.astype(bf16)
    fetches[0].wait()
    fetches[1].wait()
    rb_t = r_buf[...].astype(bf16)
    rbb = jnp.dot(in_map, rb_t, preferred_element_type=f32)
    gx_ref[...] = gx_ref[...] + tail_buf[...] * rbb
    v = v_ref[...]
    fetches[2].wait()
    grad_inmap = factor * lax.dot_general(mixing, out_map, tn, preferred_element_type=f32)
    grad_inmap = grad_inmap + lax.dot_general(xt_buf[...], rb_t, nt, preferred_element_type=f32)
    fetches[3].wait()
    fetches[4].wait()
    lead_grads = (lead_buf[...] * v.astype(f32)).astype(bf16)
    grad_outmap = factor * (
        jnp.dot(mixing, in_map, preferred_element_type=f32)
        + lax.dot_general(lead_grads, sb_buf[...], nt, preferred_element_type=f32)
    )
    carry = factor * lax.dot_general(out_map, lead_grads, tn, preferred_element_type=f32)
    rnew_ref[...] = carry + end_ref[...] * r_buf[...]
    grad_bc = jnp.concatenate([grad_inmap, grad_outmap], axis=1).astype(bf16)
    dbc_ref[...] = grad_bc
    mstore_ref[...] = jnp.where(tab_ref[base + 2] > 0, grad_bc, ms_ref[...])
    fetches[5].wait()
    back = lax.dot_general(grad_bc, w_buf[...], nt, preferred_element_type=f32)
    summed = (v.astype(f32) + gx_ref[...] + back).astype(out_ref.dtype)
    out_ref[...] = summed
    gstore_ref[...] = jnp.where(tab_ref[base + 2] > 0, summed, gs_ref[...])


def fused_step(step_arr, table, level_pos, levels, per_block, incoming, top_blk, carried, w_bc, grad_store, map_store, level_no, seq_no, factor, width):
    wt2, dec2, x_flat, in_blk, out_blk, tail_full, lead_full, xt_full, states_t, end_row = per_block
    length, features = incoming.shape[1:]
    state_size = in_blk.shape[-1]

    def lead_block(a):
        shape = (None, None, None) + a.shape[3:]
        tail = (0,) * (a.ndim - 3)
        return pl.BlockSpec(shape, lambda i, c, t: (t[(c[0] * levels + level_pos) * 3], level_no, seq_no) + tail)

    in_specs = [lead_block(a) for a in (wt2, dec2)]
    in_specs.append(pl.BlockSpec((None, length, features), lambda i, c, t: (seq_no, 0, 0)))
    in_specs.append(pl.BlockSpec((None, None, length, features), lambda i, c, t: (t[(c[0] * levels + level_pos) * 3], seq_no, 0, 0)))
    in_hbm = pl.BlockSpec(memory_space=pl.ANY)
    in_specs += [lead_block(a) for a in (x_flat, in_blk, out_blk)]
    in_specs += [in_hbm] * 5
    in_specs.append(lead_block(end_row))
    in_specs.append(in_hbm)
    store_g = pl.BlockSpec((None, None, None, length, features), lambda i, c, t: (t[(c[0] * levels + level_pos) * 3], level_no, seq_no, 0, 0))
    store_m = pl.BlockSpec((None, None, None, length, 2 * state_size), lambda i, c, t: (t[(c[0] * levels + level_pos) * 3], level_no, seq_no, 0, 0))
    in_specs += [store_g, store_m]
    out_specs = (
        pl.BlockSpec((length, features), lambda i, c, t: (0, 0)),
        pl.BlockSpec((None, None) + carried.shape[2:], lambda i, c, t: (level_no, seq_no, 0, 0)),
        pl.BlockSpec((length, 2 * state_size), lambda i, c, t: (0, 0)),
        store_g,
        store_m,
    )
    flops = 2 * length * features * (6 * state_size + 4 * length)
    moved = 2 * (4 * features * state_size * 2 + 6 * length * features) + 4 * 4 * length * features
    return pl.pallas_call(
        functools.partial(
            step_kernel, factor=factor, width=width, level_pos=level_pos, levels=levels,
            level_no=level_no, seq_no=seq_no,
        ),
        out_shape=(
            jax.ShapeDtypeStruct((length, features), jnp.bfloat16),
            jax.ShapeDtypeStruct(carried.shape, jnp.float32),
            jax.ShapeDtypeStruct((length, 2 * state_size), jnp.bfloat16),
            jax.ShapeDtypeStruct(grad_store.shape, grad_store.dtype),
            jax.ShapeDtypeStruct(map_store.shape, map_store.dtype),
        ),
        grid_spec=pltpu.PrefetchScalarGridSpec(
            num_scalar_prefetch=2,
            grid=(1,),
            in_specs=in_specs,
            out_specs=out_specs,
            scratch_shapes=[
                pltpu.VMEM((length, features), jnp.bfloat16),
                pltpu.VMEM((length, features), jnp.float32),
                pltpu.VMEM((length, features), jnp.float32),
                pltpu.VMEM((length, features), jnp.float32),
                pltpu.VMEM((length, features), jnp.bfloat16),
                pltpu.VMEM(states_t.shape[3:], states_t.dtype),
                pltpu.VMEM(carried.shape[2:], jnp.float32),
                pltpu.VMEM(w_bc.shape[1:], w_bc.dtype),
                pltpu.SemaphoreType.DMA((6,)),
            ],
        ),
        input_output_aliases={13: 1, 16: 3, 17: 4},
        cost_estimate=pl.CostEstimate(flops=flops, bytes_accessed=moved, transcendentals=0),
    )(step_arr, table, wt2, dec2, incoming, top_blk, x_flat, in_blk, out_blk, tail_full, lead_full, xt_full, states_t, carried, end_row, w_bc, grad_store, map_store)


def shards(layer_inputs, w_bc, log_decay, top_grad):
    sections = lax.axis_size("section")
    section_id = lax.axis_index("section")
    lay_dev, seq_dev, tok_len, features = layer_inputs.shape
    head_count = log_decay.shape[-1]
    block_len = tok_len // MICRO
    state_size = w_bc.shape[-1] // 2
    factor = 0.25 / state_size
    bc_all = jnp.einsum(
        "lstd,ldc->lstc", layer_inputs, w_bc, preferred_element_type=jnp.float32
    ).astype(jnp.bfloat16)

    def blocked(a):
        split = a.reshape(a.shape[:2] + (MICRO, block_len) + a.shape[3:])
        return jnp.moveaxis(split, 2, 0)

    x_blk = blocked(layer_inputs).reshape(
        (MICRO, lay_dev, seq_dev, block_len, head_count, features // head_count)
    )
    bc_blk = blocked(bc_all)
    in_blk = bc_blk[..., :state_size]
    out_blk = bc_blk[..., state_size:]
    rates_blk = blocked(log_decay)
    consts_fn = jax.vmap(jax.vmap(jax.vmap(lambda x, b, c, r: block_consts(x, b, c, r, factor))))
    consts = consts_fn(x_blk, in_blk, out_blk, rates_blk)
    width = features // head_count
    lead_dims = consts["tail"].shape[:3]
    pairs = head_count * width // 128
    per_pair = 128 // width
    wt2 = consts["weighted"]
    dec2 = jnp.moveaxis(consts["decays"], -1, -3).reshape(
        lead_dims + (pairs, per_pair * block_len, block_len)
    )
    spread_heads = (
        jnp.arange(features)[None, :] // width == jnp.arange(head_count)[:, None]
    ).astype(jnp.float32)

    def per_lane(a):
        return jnp.einsum(
            "...h,hd->...d", a, spread_heads, precision=lax.Precision.HIGHEST,
            preferred_element_type=jnp.float32,
        )

    tail_full = per_lane(consts["tail"])
    lead_full = per_lane(consts["lead"])
    x_flat = x_blk.reshape(lead_dims + (block_len, features))
    xt_full = (tail_full * x_flat.astype(jnp.float32)).astype(jnp.bfloat16)
    end_row = per_lane(consts["ending"])[..., None, :]
    fresh_t = jnp.einsum(
        "mlsjn,mlsjd->mlsnd", in_blk, xt_full, preferred_element_type=jnp.float32
    )
    state_now = jnp.zeros(fresh_t.shape[1:], jnp.float32)
    saved = []
    for block_no in range(MICRO):
        saved.append(state_now.astype(jnp.bfloat16))
        state_now = end_row[block_no] * state_now + fresh_t[block_no]
    states_t = jnp.stack(saved)
    per_block = (wt2, dec2, x_flat, in_blk, out_blk, tail_full, lead_full, xt_full, states_t, end_row)
    per_block = lax.optimization_barrier(per_block)

    top_blk = jnp.moveaxis(
        top_grad.reshape((seq_dev, MICRO, block_len, features)), 1, 0
    )
    is_top = section_id == sections - 1

    steps = MICRO + sections - 1
    counters = jnp.arange(steps, dtype=jnp.int32)[:, None]
    offsets = counters - (sections - 1 - section_id)
    valid_tab = ((offsets >= 0) & (offsets < MICRO)).astype(jnp.int32)
    block_tab = jnp.clip(MICRO - 1 - offsets, 0, MICRO - 1).astype(jnp.int32)
    top_tab = (jnp.arange(lay_dev)[None, ::-1] == lay_dev - 1) & is_top
    table = jnp.stack(
        jnp.broadcast_arrays(block_tab, top_tab.astype(jnp.int32), valid_tab), axis=-1
    ).reshape(-1).astype(jnp.int32)

    def advance(counter, loop_state, send=True):
        incoming, carried, grad_store, map_store = loop_state
        step_arr = jnp.reshape(counter, (1,)).astype(jnp.int32)
        for level_pos, level_no in enumerate(reversed(range(lay_dev))):
            level_out = []
            for seq_no in range(seq_dev):
                level_grads, carried, grad_bc, grad_store, map_store = fused_step(
                    step_arr, table, level_pos, lay_dev, per_block, incoming, top_blk, carried,
                    w_bc, grad_store, map_store, level_no, seq_no, factor, width,
                )
                level_out.append(level_grads)
            incoming = jnp.stack(level_out)
        if send:
            incoming = passed_along(incoming, "section", -1)
        return (incoming, carried, grad_store, map_store)

    initial = (
        jnp.zeros((seq_dev, block_len, features), jnp.bfloat16),
        jnp.zeros(states_t.shape[1:], jnp.float32),
        jnp.zeros((MICRO, lay_dev, seq_dev, block_len, features), jnp.bfloat16),
        jnp.zeros((MICRO, lay_dev, seq_dev, block_len, 2 * state_size), jnp.bfloat16),
    )
    final_state = lax.fori_loop(0, steps - 1, advance, initial)
    final_state = advance(steps - 1, final_state, send=False)
    grad_store = final_state[2]
    map_store = final_state[3]

    grad_inputs = jnp.moveaxis(grad_store, 0, 2).reshape(layer_inputs.shape)
    map_store = jnp.moveaxis(map_store, 0, 2).reshape(bc_all.shape)
    ways = lax.axis_size("dp")
    divisor = ways * seq_dev
    rows_here = layer_inputs.reshape(lay_dev, seq_dev * tok_len, ways, features // ways)
    rows_here = jnp.transpose(rows_here, (2, 0, 1, 3))
    rows_all = lax.all_to_all(rows_here, "dp", 0, 0, tiled=True)
    maps_here = map_store.reshape(1, lay_dev, seq_dev * tok_len, map_store.shape[-1])
    maps_all = lax.all_gather(maps_here, "dp", axis=0, tiled=True)
    grad_w = jnp.einsum(
        "glrd,glrc->ldc", rows_all, maps_all, preferred_element_type=jnp.float32
    ) / divisor
    return (grad_inputs, grad_w)


def solution(mesh):
    in_specs = (
        P("section", "dp", None, None),
        P("section", None, None),
        P("section", "dp", None, None),
        P("dp", None, None),
    )
    out_specs = (P("section", "dp", None, None), P("section", "dp", None))
    return jax.shard_map(shards, mesh=mesh, in_specs=in_specs, out_specs=out_specs, check_vma=False)
```

```python
import functools

import jax
import jax.numpy as jnp
from jax import lax
from jax.experimental import pallas as pl
from jax.experimental.pallas import tpu as pltpu
from jax.sharding import PartitionSpec as P

MICRO = 4


def shortened(value):
    return jax.tree.map(lambda a: a.astype(jnp.bfloat16) if a.dtype == jnp.float32 else a, value)


def passed_along(block, axis, distance):
    devices = range(lax.axis_size(axis))
    route = [(i - distance, i) for i in devices if i - distance in devices]
    return lax.ppermute(block, axis, route)


def block_terms(inputs_b, in_b, out_b, rates, grads_b, carried, state_in, factor):
    length = inputs_b.shape[0]
    cumulative = jnp.cumsum(rates, axis=0)
    ending = cumulative[-1]
    locations = jnp.arange(length)
    lower_mask = (locations[:, None] >= locations[None, :])[:, :, None]
    spread = jnp.where(lower_mask, cumulative[:, None, :] - cumulative[None, :, :], 0.0)
    decays = jnp.where(lower_mask, jnp.exp(spread), 0.0)
    tail_decay = jnp.exp(ending[None, :] - cumulative)
    leading = jnp.exp(cumulative)
    scores = jnp.dot(out_b, in_b.T, preferred_element_type=jnp.float32)
    weighted = (factor * decays * scores[:, :, None]).astype(jnp.bfloat16)
    carried_b = carried.astype(jnp.bfloat16)
    state_b = state_in.astype(jnp.bfloat16)
    grad_feats = jnp.einsum("kjh,khp->jhp", weighted, grads_b, preferred_element_type=jnp.float32)
    grad_feats = grad_feats + tail_decay[:, :, None] * jnp.einsum(
        "hpn,jn->jhp", carried_b, in_b, preferred_element_type=jnp.float32
    )
    pair_dots = jnp.einsum("khp,jhp->kjh", grads_b, inputs_b, preferred_element_type=jnp.float32)
    mixing = jnp.sum(decays * pair_dots, axis=2).astype(jnp.bfloat16)
    tail_inputs = (tail_decay[:, :, None] * inputs_b.astype(jnp.float32)).astype(jnp.bfloat16)
    lead_grads = (leading[:, :, None] * grads_b.astype(jnp.float32)).astype(jnp.bfloat16)
    grad_inmap = factor * jnp.dot(mixing.T, out_b, preferred_element_type=jnp.float32)
    grad_inmap = grad_inmap + jnp.einsum(
        "jhp,hpn->jn", tail_inputs, carried_b, preferred_element_type=jnp.float32
    )
    grad_outmap = factor * (
        jnp.dot(mixing, in_b, preferred_element_type=jnp.float32)
        + jnp.einsum("ihp,hpn->in", lead_grads, state_b, preferred_element_type=jnp.float32)
    )
    carry_out = factor * jnp.einsum(
        "khp,kn->hpn", lead_grads, out_b, preferred_element_type=jnp.float32
    )
    carry_out = carry_out + jnp.exp(ending)[:, None, None] * carried
    return (grad_feats, grad_inmap, grad_outmap, carry_out)


def block_end(inputs_b, in_b, rates, state_in):
    cumulative = jnp.cumsum(rates, axis=0)
    ending = cumulative[-1]
    tail_decay = jnp.exp(ending[None, :] - cumulative)
    tail_inputs = (tail_decay[:, :, None] * inputs_b.astype(jnp.float32)).astype(jnp.bfloat16)
    fresh = jnp.einsum("jhp,jn->hpn", tail_inputs, in_b, preferred_element_type=jnp.float32)
    return jnp.exp(ending)[:, None, None] * state_in + fresh


def split_block(inputs_c, map_block, head_count):
    length, features = inputs_c.shape
    state_size = map_block.shape[1] // 2
    inputs_b = inputs_c.reshape(length, head_count, features // head_count)
    in_b = map_block[:, :state_size]
    out_b = map_block[:, state_size:]
    return (inputs_b, in_b, out_b)


def block_back(inputs_c, map_block, rates, grads_c, carried, state_in, weights):
    length, features = inputs_c.shape
    head_count = rates.shape[1]
    factor = 0.25 / (map_block.shape[1] // 2)
    inputs_b, in_b, out_b = split_block(inputs_c, map_block, head_count)
    grads_b = grads_c.reshape(length, head_count, features // head_count)
    grad_feats, grad_inmap, grad_outmap, carry_out = block_terms(
        inputs_b, in_b, out_b, rates, grads_b, carried, state_in, factor
    )
    grad_bc = jnp.concatenate([grad_inmap, grad_outmap], axis=1).astype(jnp.bfloat16)
    back_proj = lax.dot_general(
        grad_bc, weights, (((1,), (1,)), ((), ())), preferred_element_type=jnp.float32
    )
    summed = grads_c.astype(jnp.float32) + grad_feats.reshape(length, features) + back_proj
    return (summed.astype(jnp.bfloat16), carry_out, grad_bc)


def layer_starts(inputs_s, bc_s, rates_s):
    head_count = rates_s.shape[1]
    features = inputs_s.shape[1]
    state_size = bc_s.shape[1] // 2
    block_len = inputs_s.shape[0] // MICRO
    state_now = jnp.zeros((head_count, features // head_count, state_size), jnp.float32)
    saved = []
    for block_no in range(MICRO):
        lo_row = block_no * block_len
        inputs_b, in_b, out_b = split_block(
            inputs_s[lo_row : lo_row + block_len], bc_s[lo_row : lo_row + block_len], head_count
        )
        saved.append(state_now)
        state_now = block_end(inputs_b, in_b, rates_s[lo_row : lo_row + block_len], state_now)
    return jnp.stack(saved)


def block_consts(inputs_b, in_b, out_b, rates, factor):
    length = inputs_b.shape[0]
    cumulative = jnp.cumsum(rates, axis=0)
    ending = cumulative[-1]
    locations = jnp.arange(length)
    lower_mask = (locations[:, None] >= locations[None, :])[:, :, None]
    spread = jnp.where(lower_mask, cumulative[:, None, :] - cumulative[None, :, :], 0.0)
    decays = jnp.where(lower_mask, jnp.exp(spread), 0.0)
    tail_decay = jnp.exp(ending[None, :] - cumulative)
    leading = jnp.exp(cumulative)
    scores = jnp.dot(out_b, in_b.T, preferred_element_type=jnp.float32)
    cum_t = cumulative.T
    upper = (locations[:, None] <= locations[None, :])[None]
    spread_t = jnp.where(upper, cum_t[:, None, :] - cum_t[:, :, None], 0.0)
    decays_t = jnp.where(upper, jnp.exp(spread_t), 0.0)
    scores_t = jnp.dot(in_b, out_b.T, preferred_element_type=jnp.float32)
    weighted = (factor * decays_t * scores_t[None]).astype(jnp.bfloat16)
    return dict(
        decays=decays,
        tail=tail_decay,
        lead=leading,
        weighted=weighted,
        ending=jnp.exp(ending),
    )


def step_kernel(
    step_ref, tab_ref, wt_ref, dec_ref, inc_ref, top_ref, x_ref, b_ref, c_ref, tail_ref, lead_ref, xt_ref,
    sb_ref, r_ref, end_ref, w_ref, gs_ref, ms_ref, out_ref, rnew_ref, dbc_ref, gstore_ref, mstore_ref,
    v_ref, gx_ref, tail_buf, lead_buf, xt_buf, sb_buf, r_buf, w_buf, sems, *, factor, width,
    level_pos, levels, level_no, seq_no
):
    base = (step_ref[0] * levels + level_pos) * 3
    blk = tab_ref[base]
    fetches = [
        pltpu.make_async_copy(r_ref.at[level_no, seq_no], r_buf, sems.at[0]),
        pltpu.make_async_copy(tail_ref.at[blk, level_no, seq_no], tail_buf, sems.at[1]),
        pltpu.make_async_copy(xt_ref.at[blk, level_no, seq_no], xt_buf, sems.at[2]),
        pltpu.make_async_copy(lead_ref.at[blk, level_no, seq_no], lead_buf, sems.at[3]),
        pltpu.make_async_copy(sb_ref.at[blk, level_no, seq_no], sb_buf, sems.at[4]),
        pltpu.make_async_copy(w_ref.at[level_no], w_buf, sems.at[5]),
    ]
    for fetch in fetches:
        fetch.start()
    f32 = jnp.float32
    bf16 = jnp.bfloat16
    length, features = v_ref.shape
    lanes = 128
    per_pair = lanes // width
    nt = (((1,), (1,)), ((), ()))
    tn = (((0,), (0,)), ((), ()))
    v_ref[...] = jnp.where(tab_ref[base + 1] > 0, top_ref[...], inc_ref[...])
    in_map = b_ref[...]
    out_map = c_ref[...]
    lane_id = lax.broadcasted_iota(jnp.int32, (length, lanes), 1)
    masks = [(lane_id >= e * width) & (lane_id < (e + 1) * width) for e in range(per_pair)]
    mix_acc = jnp.zeros((per_pair * length, length), f32)
    for q in range(features // lanes):
        cols = slice(q * lanes, (q + 1) * lanes)
        v_q = v_ref[:, cols]
        x_q = x_ref[:, cols]
        stacked = jnp.concatenate([jnp.where(m, v_q, jnp.zeros_like(v_q)) for m in masks], axis=0)
        gx_q = jnp.dot(
            wt_ref[per_pair * q], stacked[0:length], preferred_element_type=f32
        )
        for e in range(1, per_pair):
            gx_q = gx_q + jnp.dot(
                wt_ref[per_pair * q + e],
                stacked[e * length:(e + 1) * length],
                preferred_element_type=f32,
            )
        gx_ref[:, cols] = gx_q
        pair_dots = lax.dot_general(stacked, x_q, nt, preferred_element_type=f32)
        mix_acc = mix_acc + dec_ref[q] * pair_dots
    mixing = mix_acc[0:length]
    for e in range(1, per_pair):
        mixing = mixing + mix_acc[e * length:(e + 1) * length]
    mixing = mixing.astype(bf16)
    fetches[0].wait()
    fetches[1].wait()
    rb_t = r_buf[...].astype(bf16)
    rbb = jnp.dot(in_map, rb_t, preferred_element_type=f32)
    gx_ref[...] = gx_ref[...] + tail_buf[...] * rbb
    v = v_ref[...]
    fetches[2].wait()
    grad_inmap = factor * lax.dot_general(mixing, out_map, tn, preferred_element_type=f32)
    grad_inmap = grad_inmap + lax.dot_general(xt_buf[...], rb_t, nt, preferred_element_type=f32)
    fetches[3].wait()
    fetches[4].wait()
    lead_grads = (lead_buf[...] * v.astype(f32)).astype(bf16)
    grad_outmap = factor * (
        jnp.dot(mixing, in_map, preferred_element_type=f32)
        + lax.dot_general(lead_grads, sb_buf[...], nt, preferred_element_type=f32)
    )
    carry = factor * lax.dot_general(out_map, lead_grads, tn, preferred_element_type=f32)
    rnew_ref[...] = carry + end_ref[...] * r_buf[...]
    grad_bc = jnp.concatenate([grad_inmap, grad_outmap], axis=1).astype(bf16)
    dbc_ref[...] = grad_bc
    mstore_ref[...] = jnp.where(tab_ref[base + 2] > 0, grad_bc, ms_ref[...])
    fetches[5].wait()
    back = lax.dot_general(grad_bc, w_buf[...], nt, preferred_element_type=f32)
    summed = (v.astype(f32) + gx_ref[...] + back).astype(out_ref.dtype)
    out_ref[...] = summed
    gstore_ref[...] = jnp.where(tab_ref[base + 2] > 0, summed, gs_ref[...])


def fused_step(step_arr, table, level_pos, levels, per_block, incoming, top_blk, carried, w_bc, grad_store, map_store, level_no, seq_no, factor, width):
    wt2, dec2, x_flat, in_blk, out_blk, tail_full, lead_full, xt_full, states_t, end_row = per_block
    length, features = incoming.shape[1:]
    state_size = in_blk.shape[-1]

    def lead_block(a):
        shape = (None, None, None) + a.shape[3:]
        tail = (0,) * (a.ndim - 3)
        return pl.BlockSpec(shape, lambda i, c, t: (t[(c[0] * levels + level_pos) * 3], level_no, seq_no) + tail)

    in_specs = [lead_block(a) for a in (wt2, dec2)]
    in_specs.append(pl.BlockSpec((None, length, features), lambda i, c, t: (seq_no, 0, 0)))
    in_specs.append(pl.BlockSpec((None, None, length, features), lambda i, c, t: (t[(c[0] * levels + level_pos) * 3], seq_no, 0, 0)))
    in_hbm = pl.BlockSpec(memory_space=pl.ANY)
    in_specs += [lead_block(a) for a in (x_flat, in_blk, out_blk)]
    in_specs += [in_hbm] * 5
    in_specs.append(lead_block(end_row))
    in_specs.append(in_hbm)
    store_g = pl.BlockSpec((None, None, None, length, features), lambda i, c, t: (t[(c[0] * levels + level_pos) * 3], level_no, seq_no, 0, 0))
    store_m = pl.BlockSpec((None, None, None, length, 2 * state_size), lambda i, c, t: (t[(c[0] * levels + level_pos) * 3], level_no, seq_no, 0, 0))
    in_specs += [store_g, store_m]
    out_specs = (
        pl.BlockSpec((length, features), lambda i, c, t: (0, 0)),
        pl.BlockSpec((None, None) + carried.shape[2:], lambda i, c, t: (level_no, seq_no, 0, 0)),
        pl.BlockSpec((length, 2 * state_size), lambda i, c, t: (0, 0)),
        store_g,
        store_m,
    )
    flops = 2 * length * features * (6 * state_size + 4 * length)
    moved = 2 * (4 * features * state_size * 2 + 6 * length * features) + 4 * 4 * length * features
    return pl.pallas_call(
        functools.partial(
            step_kernel, factor=factor, width=width, level_pos=level_pos, levels=levels,
            level_no=level_no, seq_no=seq_no,
        ),
        out_shape=(
            jax.ShapeDtypeStruct((length, features), jnp.bfloat16),
            jax.ShapeDtypeStruct(carried.shape, jnp.float32),
            jax.ShapeDtypeStruct((length, 2 * state_size), jnp.bfloat16),
            jax.ShapeDtypeStruct(grad_store.shape, grad_store.dtype),
            jax.ShapeDtypeStruct(map_store.shape, map_store.dtype),
        ),
        grid_spec=pltpu.PrefetchScalarGridSpec(
            num_scalar_prefetch=2,
            grid=(1,),
            in_specs=in_specs,
            out_specs=out_specs,
            scratch_shapes=[
                pltpu.VMEM((length, features), jnp.bfloat16),
                pltpu.VMEM((length, features), jnp.float32),
                pltpu.VMEM((length, features), jnp.float32),
                pltpu.VMEM((length, features), jnp.float32),
                pltpu.VMEM((length, features), jnp.bfloat16),
                pltpu.VMEM(states_t.shape[3:], states_t.dtype),
                pltpu.VMEM(carried.shape[2:], jnp.float32),
                pltpu.VMEM(w_bc.shape[1:], w_bc.dtype),
                pltpu.SemaphoreType.DMA((6,)),
            ],
        ),
        input_output_aliases={13: 1, 16: 3, 17: 4},
        cost_estimate=pl.CostEstimate(flops=flops, bytes_accessed=moved, transcendentals=0),
    )(step_arr, table, wt2, dec2, incoming, top_blk, x_flat, in_blk, out_blk, tail_full, lead_full, xt_full, states_t, carried, end_row, w_bc, grad_store, map_store)


def shards(layer_inputs, w_bc, log_decay, top_grad):
    sections = lax.axis_size("section")
    section_id = lax.axis_index("section")
    lay_dev, seq_dev, tok_len, features = layer_inputs.shape
    head_count = log_decay.shape[-1]
    block_len = tok_len // MICRO
    state_size = w_bc.shape[-1] // 2
    factor = 0.25 / state_size
    bc_all = jnp.einsum(
        "lstd,ldc->lstc", layer_inputs, w_bc, preferred_element_type=jnp.float32
    ).astype(jnp.bfloat16)

    def blocked(a):
        split = a.reshape(a.shape[:2] + (MICRO, block_len) + a.shape[3:])
        return jnp.moveaxis(split, 2, 0)

    x_blk = blocked(layer_inputs).reshape(
        (MICRO, lay_dev, seq_dev, block_len, head_count, features // head_count)
    )
    bc_blk = blocked(bc_all)
    in_blk = bc_blk[..., :state_size]
    out_blk = bc_blk[..., state_size:]
    rates_blk = blocked(log_decay)
    consts_fn = jax.vmap(jax.vmap(jax.vmap(lambda x, b, c, r: block_consts(x, b, c, r, factor))))
    consts = consts_fn(x_blk, in_blk, out_blk, rates_blk)
    width = features // head_count
    lead_dims = consts["tail"].shape[:3]
    pairs = head_count * width // 128
    per_pair = 128 // width
    wt2 = consts["weighted"]
    dec2 = jnp.moveaxis(consts["decays"], -1, -3).reshape(
        lead_dims + (pairs, per_pair * block_len, block_len)
    )
    spread_heads = (
        jnp.arange(features)[None, :] // width == jnp.arange(head_count)[:, None]
    ).astype(jnp.float32)

    def per_lane(a):
        return jnp.einsum(
            "...h,hd->...d", a, spread_heads, precision=lax.Precision.HIGHEST,
            preferred_element_type=jnp.float32,
        )

    tail_full = per_lane(consts["tail"])
    lead_full = per_lane(consts["lead"])
    x_flat = x_blk.reshape(lead_dims + (block_len, features))
    xt_full = (tail_full * x_flat.astype(jnp.float32)).astype(jnp.bfloat16)
    end_row = per_lane(consts["ending"])[..., None, :]
    fresh_t = jnp.einsum(
        "mlsjn,mlsjd->mlsnd", in_blk, xt_full, preferred_element_type=jnp.float32
    )
    state_now = jnp.zeros(fresh_t.shape[1:], jnp.float32)
    saved = []
    for block_no in range(MICRO):
        saved.append(state_now.astype(jnp.bfloat16))
        state_now = end_row[block_no] * state_now + fresh_t[block_no]
    states_t = jnp.stack(saved)
    per_block = (wt2, dec2, x_flat, in_blk, out_blk, tail_full, lead_full, xt_full, states_t, end_row)
    per_block = lax.optimization_barrier(per_block)

    top_blk = jnp.moveaxis(
        top_grad.reshape((seq_dev, MICRO, block_len, features)), 1, 0
    )
    is_top = section_id == sections - 1

    steps = MICRO + sections - 1
    counters = jnp.arange(steps, dtype=jnp.int32)[:, None]
    offsets = counters - (sections - 1 - section_id)
    valid_tab = ((offsets >= 0) & (offsets < MICRO)).astype(jnp.int32)
    block_tab = jnp.clip(MICRO - 1 - offsets, 0, MICRO - 1).astype(jnp.int32)
    top_tab = (jnp.arange(lay_dev)[None, ::-1] == lay_dev - 1) & is_top
    table = jnp.stack(
        jnp.broadcast_arrays(block_tab, top_tab.astype(jnp.int32), valid_tab), axis=-1
    ).reshape(-1).astype(jnp.int32)

    def advance(counter, loop_state, send=True):
        incoming, carried, grad_store, map_store = loop_state
        step_arr = jnp.reshape(counter, (1,)).astype(jnp.int32)
        for level_pos, level_no in enumerate(reversed(range(lay_dev))):
            level_out = []
            for seq_no in range(seq_dev):
                level_grads, carried, grad_bc, grad_store, map_store = fused_step(
                    step_arr, table, level_pos, lay_dev, per_block, incoming, top_blk, carried,
                    w_bc, grad_store, map_store, level_no, seq_no, factor, width,
                )
                level_out.append(level_grads)
            incoming = jnp.stack(level_out)
        if send:
            incoming = passed_along(incoming, "section", -1)
        return (incoming, carried, grad_store, map_store)

    initial = (
        jnp.zeros((seq_dev, block_len, features), jnp.bfloat16),
        jnp.zeros(states_t.shape[1:], jnp.float32),
        jnp.zeros((MICRO, lay_dev, seq_dev, block_len, features), jnp.bfloat16),
        jnp.zeros((MICRO, lay_dev, seq_dev, block_len, 2 * state_size), jnp.bfloat16),
    )
    ways = lax.axis_size("dp")
    rows_here = layer_inputs.reshape(lay_dev, seq_dev * tok_len, ways, features // ways)
    rows_here = jnp.transpose(rows_here, (2, 0, 1, 3))
    final_state = initial
    for counter in range(steps):
        final_state = advance(
            jnp.full((), counter, jnp.int32), final_state, send=counter < steps - 1
        )
        if counter == min(1, steps - 1):
            rows_here, held = lax.optimization_barrier((rows_here, final_state[1]))
            final_state = (final_state[0], held) + final_state[2:]
    grad_store = final_state[2]
    map_store = final_state[3]

    grad_inputs = jnp.moveaxis(grad_store, 0, 2).reshape(layer_inputs.shape)
    map_store = jnp.moveaxis(map_store, 0, 2).reshape(bc_all.shape)
    divisor = ways * seq_dev
    rows_all = lax.all_to_all(rows_here, "dp", 0, 0, tiled=True)
    maps_here = map_store.reshape(1, lay_dev, seq_dev * tok_len, map_store.shape[-1])
    maps_all = lax.all_gather(maps_here, "dp", axis=0, tiled=True)
    grad_w = jnp.einsum(
        "glrd,glrc->ldc", rows_all, maps_all, preferred_element_type=jnp.float32
    ) / divisor
    return (grad_inputs, grad_w)


def solution(mesh):
    in_specs = (
        P("section", "dp", None, None),
        P("section", None, None),
        P("section", "dp", None, None),
        P("dp", None, None),
    )
    out_specs = (P("section", "dp", None, None), P("section", "dp", None))
    return jax.shard_map(shards, mesh=mesh, in_specs=in_specs, out_specs=out_specs, check_vma=False)
```

```python
import functools

import jax
import jax.numpy as jnp
from jax import lax
from jax.experimental import pallas as pl
from jax.experimental.pallas import tpu as pltpu
from jax.sharding import PartitionSpec as P

MICRO = 4


def shortened(value):
    return jax.tree.map(lambda a: a.astype(jnp.bfloat16) if a.dtype == jnp.float32 else a, value)


def passed_along(block, axis, distance):
    devices = range(lax.axis_size(axis))
    route = [(i - distance, i) for i in devices if i - distance in devices]
    return lax.ppermute(block, axis, route)


def block_terms(inputs_b, in_b, out_b, rates, grads_b, carried, state_in, factor):
    length = inputs_b.shape[0]
    cumulative = jnp.cumsum(rates, axis=0)
    ending = cumulative[-1]
    locations = jnp.arange(length)
    lower_mask = (locations[:, None] >= locations[None, :])[:, :, None]
    spread = jnp.where(lower_mask, cumulative[:, None, :] - cumulative[None, :, :], 0.0)
    decays = jnp.where(lower_mask, jnp.exp(spread), 0.0)
    tail_decay = jnp.exp(ending[None, :] - cumulative)
    leading = jnp.exp(cumulative)
    scores = jnp.dot(out_b, in_b.T, preferred_element_type=jnp.float32)
    weighted = (factor * decays * scores[:, :, None]).astype(jnp.bfloat16)
    carried_b = carried.astype(jnp.bfloat16)
    state_b = state_in.astype(jnp.bfloat16)
    grad_feats = jnp.einsum("kjh,khp->jhp", weighted, grads_b, preferred_element_type=jnp.float32)
    grad_feats = grad_feats + tail_decay[:, :, None] * jnp.einsum(
        "hpn,jn->jhp", carried_b, in_b, preferred_element_type=jnp.float32
    )
    pair_dots = jnp.einsum("khp,jhp->kjh", grads_b, inputs_b, preferred_element_type=jnp.float32)
    mixing = jnp.sum(decays * pair_dots, axis=2).astype(jnp.bfloat16)
    tail_inputs = (tail_decay[:, :, None] * inputs_b.astype(jnp.float32)).astype(jnp.bfloat16)
    lead_grads = (leading[:, :, None] * grads_b.astype(jnp.float32)).astype(jnp.bfloat16)
    grad_inmap = factor * jnp.dot(mixing.T, out_b, preferred_element_type=jnp.float32)
    grad_inmap = grad_inmap + jnp.einsum(
        "jhp,hpn->jn", tail_inputs, carried_b, preferred_element_type=jnp.float32
    )
    grad_outmap = factor * (
        jnp.dot(mixing, in_b, preferred_element_type=jnp.float32)
        + jnp.einsum("ihp,hpn->in", lead_grads, state_b, preferred_element_type=jnp.float32)
    )
    carry_out = factor * jnp.einsum(
        "khp,kn->hpn", lead_grads, out_b, preferred_element_type=jnp.float32
    )
    carry_out = carry_out + jnp.exp(ending)[:, None, None] * carried
    return (grad_feats, grad_inmap, grad_outmap, carry_out)


def block_end(inputs_b, in_b, rates, state_in):
    cumulative = jnp.cumsum(rates, axis=0)
    ending = cumulative[-1]
    tail_decay = jnp.exp(ending[None, :] - cumulative)
    tail_inputs = (tail_decay[:, :, None] * inputs_b.astype(jnp.float32)).astype(jnp.bfloat16)
    fresh = jnp.einsum("jhp,jn->hpn", tail_inputs, in_b, preferred_element_type=jnp.float32)
    return jnp.exp(ending)[:, None, None] * state_in + fresh


def split_block(inputs_c, map_block, head_count):
    length, features = inputs_c.shape
    state_size = map_block.shape[1] // 2
    inputs_b = inputs_c.reshape(length, head_count, features // head_count)
    in_b = map_block[:, :state_size]
    out_b = map_block[:, state_size:]
    return (inputs_b, in_b, out_b)


def block_back(inputs_c, map_block, rates, grads_c, carried, state_in, weights):
    length, features = inputs_c.shape
    head_count = rates.shape[1]
    factor = 0.25 / (map_block.shape[1] // 2)
    inputs_b, in_b, out_b = split_block(inputs_c, map_block, head_count)
    grads_b = grads_c.reshape(length, head_count, features // head_count)
    grad_feats, grad_inmap, grad_outmap, carry_out = block_terms(
        inputs_b, in_b, out_b, rates, grads_b, carried, state_in, factor
    )
    grad_bc = jnp.concatenate([grad_inmap, grad_outmap], axis=1).astype(jnp.bfloat16)
    back_proj = lax.dot_general(
        grad_bc, weights, (((1,), (1,)), ((), ())), preferred_element_type=jnp.float32
    )
    summed = grads_c.astype(jnp.float32) + grad_feats.reshape(length, features) + back_proj
    return (summed.astype(jnp.bfloat16), carry_out, grad_bc)


def layer_starts(inputs_s, bc_s, rates_s):
    head_count = rates_s.shape[1]
    features = inputs_s.shape[1]
    state_size = bc_s.shape[1] // 2
    block_len = inputs_s.shape[0] // MICRO
    state_now = jnp.zeros((head_count, features // head_count, state_size), jnp.float32)
    saved = []
    for block_no in range(MICRO):
        lo_row = block_no * block_len
        inputs_b, in_b, out_b = split_block(
            inputs_s[lo_row : lo_row + block_len], bc_s[lo_row : lo_row + block_len], head_count
        )
        saved.append(state_now)
        state_now = block_end(inputs_b, in_b, rates_s[lo_row : lo_row + block_len], state_now)
    return jnp.stack(saved)


def block_consts(inputs_b, in_b, out_b, rates, factor):
    length = inputs_b.shape[0]
    cumulative = jnp.cumsum(rates, axis=0)
    ending = cumulative[-1]
    locations = jnp.arange(length)
    lower_mask = (locations[:, None] >= locations[None, :])[:, :, None]
    spread = jnp.where(lower_mask, cumulative[:, None, :] - cumulative[None, :, :], 0.0)
    decays = jnp.where(lower_mask, jnp.exp(spread), 0.0)
    tail_decay = jnp.exp(ending[None, :] - cumulative)
    leading = jnp.exp(cumulative)
    scores = jnp.dot(out_b, in_b.T, preferred_element_type=jnp.float32)
    cum_t = cumulative.T
    upper = (locations[:, None] <= locations[None, :])[None]
    spread_t = jnp.where(upper, cum_t[:, None, :] - cum_t[:, :, None], 0.0)
    decays_t = jnp.where(upper, jnp.exp(spread_t), 0.0)
    scores_t = jnp.dot(in_b, out_b.T, preferred_element_type=jnp.float32)
    weighted = (factor * decays_t * scores_t[None]).astype(jnp.bfloat16)
    return dict(
        decays=decays,
        tail=tail_decay,
        lead=leading,
        weighted=weighted,
        ending=jnp.exp(ending),
    )


def step_kernel(
    step_ref, tab_ref, wt_ref, dec_ref, inc_ref, top_ref, x_ref, b_ref, c_ref, tail_ref, lead_ref, xt_ref,
    sb_ref, r_ref, end_ref, w_ref, gs_ref, ms_ref, out_ref, dbc_ref, gstore_ref, mstore_ref,
    v_ref, gx_ref, tail_buf, lead_buf, xt_buf, sb_buf, r_buf, w_buf, sems, *, factor, width,
    level_pos, levels, level_no, seq_no
):
    base = (step_ref[0] * levels + level_pos) * 3
    blk = tab_ref[base]
    fetches = [
        pltpu.make_async_copy(r_ref.at[level_no, seq_no], r_buf, sems.at[0]),
        pltpu.make_async_copy(tail_ref.at[blk, level_no, seq_no], tail_buf, sems.at[1]),
        pltpu.make_async_copy(xt_ref.at[blk, level_no, seq_no], xt_buf, sems.at[2]),
        pltpu.make_async_copy(lead_ref.at[blk, level_no, seq_no], lead_buf, sems.at[3]),
        pltpu.make_async_copy(sb_ref.at[blk, level_no, seq_no], sb_buf, sems.at[4]),
        pltpu.make_async_copy(w_ref.at[level_no], w_buf, sems.at[5]),
    ]
    for fetch in fetches:
        fetch.start()
    f32 = jnp.float32
    bf16 = jnp.bfloat16
    length, features = v_ref.shape
    lanes = 128
    per_pair = lanes // width
    nt = (((1,), (1,)), ((), ()))
    tn = (((0,), (0,)), ((), ()))
    v_ref[...] = jnp.where(tab_ref[base + 1] > 0, top_ref[...], inc_ref[...])
    in_map = b_ref[...]
    out_map = c_ref[...]
    lane_id = lax.broadcasted_iota(jnp.int32, (length, lanes), 1)
    masks = [(lane_id >= e * width) & (lane_id < (e + 1) * width) for e in range(per_pair)]
    mix_acc = jnp.zeros((per_pair * length, length), f32)
    for q in range(features // lanes):
        cols = slice(q * lanes, (q + 1) * lanes)
        v_q = v_ref[:, cols]
        x_q = x_ref[:, cols]
        stacked = jnp.concatenate([jnp.where(m, v_q, jnp.zeros_like(v_q)) for m in masks], axis=0)
        gx_q = jnp.dot(
            wt_ref[per_pair * q], stacked[0:length], preferred_element_type=f32
        )
        for e in range(1, per_pair):
            gx_q = gx_q + jnp.dot(
                wt_ref[per_pair * q + e],
                stacked[e * length:(e + 1) * length],
                preferred_element_type=f32,
            )
        gx_ref[:, cols] = gx_q
        pair_dots = lax.dot_general(stacked, x_q, nt, preferred_element_type=f32)
        mix_acc = mix_acc + dec_ref[q] * pair_dots
    mixing = mix_acc[0:length]
    for e in range(1, per_pair):
        mixing = mixing + mix_acc[e * length:(e + 1) * length]
    mixing = mixing.astype(bf16)
    fetches[0].wait()
    fetches[1].wait()
    rb_t = r_buf[...].astype(bf16)
    rbb = jnp.dot(in_map, rb_t, preferred_element_type=f32)
    gx_ref[...] = gx_ref[...] + tail_buf[...] * rbb
    v = v_ref[...]
    fetches[2].wait()
    grad_inmap = factor * lax.dot_general(mixing, out_map, tn, preferred_element_type=f32)
    grad_inmap = grad_inmap + lax.dot_general(xt_buf[...], rb_t, nt, preferred_element_type=f32)
    fetches[3].wait()
    fetches[4].wait()
    lead_grads = (lead_buf[...] * v.astype(f32)).astype(bf16)
    grad_outmap = factor * (
        jnp.dot(mixing, in_map, preferred_element_type=f32)
        + lax.dot_general(lead_grads, sb_buf[...], nt, preferred_element_type=f32)
    )
    grad_bc = jnp.concatenate([grad_inmap, grad_outmap], axis=1).astype(bf16)
    dbc_ref[...] = grad_bc
    mstore_ref[...] = jnp.where(tab_ref[base + 2] > 0, grad_bc, ms_ref[...])
    fetches[5].wait()
    back = lax.dot_general(grad_bc, w_buf[...], nt, preferred_element_type=f32)
    summed = (v.astype(f32) + gx_ref[...] + back).astype(out_ref.dtype)
    out_ref[...] = summed
    gstore_ref[...] = jnp.where(tab_ref[base + 2] > 0, summed, gs_ref[...])


def carry_kernel(
    step_ref, tab_ref, inc_ref, top_ref, c_ref, lead_ref, end_ref, r_ref, rnew_ref, *, factor,
    level_pos, levels
):
    base = (step_ref[0] * levels + level_pos) * 3
    tn = (((0,), (0,)), ((), ()))
    v = jnp.where(tab_ref[base + 1] > 0, top_ref[...], inc_ref[...])
    lead_grads = (lead_ref[...] * v.astype(jnp.float32)).astype(jnp.bfloat16)
    carry = factor * lax.dot_general(
        c_ref[...], lead_grads, tn, preferred_element_type=jnp.float32
    )
    rnew_ref[...] = carry + end_ref[...] * r_ref[...]


def fused_step(step_arr, table, level_pos, levels, per_block, incoming, top_blk, carried, w_bc, grad_store, map_store, level_no, seq_no, factor, width):
    wt2, dec2, x_flat, in_blk, out_blk, tail_full, lead_full, xt_full, states_t, end_row = per_block
    length, features = incoming.shape[1:]
    state_size = in_blk.shape[-1]

    def lead_block(a):
        shape = (None, None, None) + a.shape[3:]
        tail = (0,) * (a.ndim - 3)
        return pl.BlockSpec(shape, lambda i, c, t: (t[(c[0] * levels + level_pos) * 3], level_no, seq_no) + tail)

    in_specs = [lead_block(a) for a in (wt2, dec2)]
    in_specs.append(pl.BlockSpec((None, length, features), lambda i, c, t: (seq_no, 0, 0)))
    in_specs.append(pl.BlockSpec((None, None, length, features), lambda i, c, t: (t[(c[0] * levels + level_pos) * 3], seq_no, 0, 0)))
    in_hbm = pl.BlockSpec(memory_space=pl.ANY)
    in_specs += [lead_block(a) for a in (x_flat, in_blk, out_blk)]
    in_specs += [in_hbm] * 5
    in_specs.append(lead_block(end_row))
    in_specs.append(in_hbm)
    store_g = pl.BlockSpec((None, None, None, length, features), lambda i, c, t: (t[(c[0] * levels + level_pos) * 3], level_no, seq_no, 0, 0))
    store_m = pl.BlockSpec((None, None, None, length, 2 * state_size), lambda i, c, t: (t[(c[0] * levels + level_pos) * 3], level_no, seq_no, 0, 0))
    in_specs += [store_g, store_m]
    out_specs = (
        pl.BlockSpec((length, features), lambda i, c, t: (0, 0)),
        pl.BlockSpec((length, 2 * state_size), lambda i, c, t: (0, 0)),
        store_g,
        store_m,
    )
    flops = 2 * length * features * (6 * state_size + 4 * length)
    moved = 2 * (4 * features * state_size * 2 + 6 * length * features) + 4 * 4 * length * features
    outs = pl.pallas_call(
        functools.partial(
            step_kernel, factor=factor, width=width, level_pos=level_pos, levels=levels,
            level_no=level_no, seq_no=seq_no,
        ),
        out_shape=(
            jax.ShapeDtypeStruct((length, features), jnp.bfloat16),
            jax.ShapeDtypeStruct((length, 2 * state_size), jnp.bfloat16),
            jax.ShapeDtypeStruct(grad_store.shape, grad_store.dtype),
            jax.ShapeDtypeStruct(map_store.shape, map_store.dtype),
        ),
        grid_spec=pltpu.PrefetchScalarGridSpec(
            num_scalar_prefetch=2,
            grid=(1,),
            in_specs=in_specs,
            out_specs=out_specs,
            scratch_shapes=[
                pltpu.VMEM((length, features), jnp.bfloat16),
                pltpu.VMEM((length, features), jnp.float32),
                pltpu.VMEM((length, features), jnp.float32),
                pltpu.VMEM((length, features), jnp.float32),
                pltpu.VMEM((length, features), jnp.bfloat16),
                pltpu.VMEM(states_t.shape[3:], states_t.dtype),
                pltpu.VMEM(carried.shape[2:], jnp.float32),
                pltpu.VMEM(w_bc.shape[1:], w_bc.dtype),
                pltpu.SemaphoreType.DMA((6,)),
            ],
        ),
        input_output_aliases={16: 2, 17: 3},
        cost_estimate=pl.CostEstimate(flops=flops, bytes_accessed=moved, transcendentals=0),
    )(step_arr, table, wt2, dec2, incoming, top_blk, x_flat, in_blk, out_blk, tail_full, lead_full, xt_full, states_t, carried, end_row, w_bc, grad_store, map_store)
    carry_specs = [
        pl.BlockSpec((None, length, features), lambda i, c, t: (seq_no, 0, 0)),
        pl.BlockSpec((None, None, length, features), lambda i, c, t: (t[(c[0] * levels + level_pos) * 3], seq_no, 0, 0)),
        lead_block(out_blk),
        lead_block(lead_full),
        lead_block(end_row),
        pl.BlockSpec((None, None) + carried.shape[2:], lambda i, c, t: (level_no, seq_no, 0, 0)),
    ]
    carried = pl.pallas_call(
        functools.partial(carry_kernel, factor=factor, level_pos=level_pos, levels=levels),
        out_shape=jax.ShapeDtypeStruct(carried.shape, jnp.float32),
        grid_spec=pltpu.PrefetchScalarGridSpec(
            num_scalar_prefetch=2,
            grid=(1,),
            in_specs=carry_specs,
            out_specs=carry_specs[-1],
        ),
        input_output_aliases={7: 0},
        cost_estimate=pl.CostEstimate(
            flops=2 * length * features * state_size,
            bytes_accessed=8 * features * state_size + 10 * length * features,
            transcendentals=0,
        ),
    )(step_arr, table, incoming, top_blk, out_blk, lead_full, end_row, carried)
    return (outs[0], carried, outs[1], outs[2], outs[3])


def shards(layer_inputs, w_bc, log_decay, top_grad):
    sections = lax.axis_size("section")
    section_id = lax.axis_index("section")
    lay_dev, seq_dev, tok_len, features = layer_inputs.shape
    head_count = log_decay.shape[-1]
    block_len = tok_len // MICRO
    state_size = w_bc.shape[-1] // 2
    factor = 0.25 / state_size
    bc_all = jnp.einsum(
        "lstd,ldc->lstc", layer_inputs, w_bc, preferred_element_type=jnp.float32
    ).astype(jnp.bfloat16)

    def blocked(a):
        split = a.reshape(a.shape[:2] + (MICRO, block_len) + a.shape[3:])
        return jnp.moveaxis(split, 2, 0)

    x_blk = blocked(layer_inputs).reshape(
        (MICRO, lay_dev, seq_dev, block_len, head_count, features // head_count)
    )
    bc_blk = blocked(bc_all)
    in_blk = bc_blk[..., :state_size]
    out_blk = bc_blk[..., state_size:]
    rates_blk = blocked(log_decay)
    consts_fn = jax.vmap(jax.vmap(jax.vmap(lambda x, b, c, r: block_consts(x, b, c, r, factor))))
    consts = consts_fn(x_blk, in_blk, out_blk, rates_blk)
    width = features // head_count
    lead_dims = consts["tail"].shape[:3]
    pairs = head_count * width // 128
    per_pair = 128 // width
    wt2 = consts["weighted"]
    dec2 = jnp.moveaxis(consts["decays"], -1, -3).reshape(
        lead_dims + (pairs, per_pair * block_len, block_len)
    )
    spread_heads = (
        jnp.arange(features)[None, :] // width == jnp.arange(head_count)[:, None]
    ).astype(jnp.float32)

    def per_lane(a):
        return jnp.einsum(
            "...h,hd->...d", a, spread_heads, precision=lax.Precision.HIGHEST,
            preferred_element_type=jnp.float32,
        )

    tail_full = per_lane(consts["tail"])
    lead_full = per_lane(consts["lead"])
    x_flat = x_blk.reshape(lead_dims + (block_len, features))
    xt_full = (tail_full * x_flat.astype(jnp.float32)).astype(jnp.bfloat16)
    end_row = per_lane(consts["ending"])[..., None, :]
    fresh_t = jnp.einsum(
        "mlsjn,mlsjd->mlsnd", in_blk, xt_full, preferred_element_type=jnp.float32
    )
    state_now = jnp.zeros(fresh_t.shape[1:], jnp.float32)
    saved = []
    for block_no in range(MICRO):
        saved.append(state_now.astype(jnp.bfloat16))
        state_now = end_row[block_no] * state_now + fresh_t[block_no]
    states_t = jnp.stack(saved)
    per_block = (wt2, dec2, x_flat, in_blk, out_blk, tail_full, lead_full, xt_full, states_t, end_row)
    per_block = lax.optimization_barrier(per_block)

    top_blk = jnp.moveaxis(
        top_grad.reshape((seq_dev, MICRO, block_len, features)), 1, 0
    )
    is_top = section_id == sections - 1

    steps = MICRO + sections - 1
    counters = jnp.arange(steps, dtype=jnp.int32)[:, None]
    offsets = counters - (sections - 1 - section_id)
    valid_tab = ((offsets >= 0) & (offsets < MICRO)).astype(jnp.int32)
    block_tab = jnp.clip(MICRO - 1 - offsets, 0, MICRO - 1).astype(jnp.int32)
    top_tab = (jnp.arange(lay_dev)[None, ::-1] == lay_dev - 1) & is_top
    table = jnp.stack(
        jnp.broadcast_arrays(block_tab, top_tab.astype(jnp.int32), valid_tab), axis=-1
    ).reshape(-1).astype(jnp.int32)

    def advance(counter, loop_state, send=True):
        incoming, carried, grad_store, map_store = loop_state
        step_arr = jnp.reshape(counter, (1,)).astype(jnp.int32)
        for level_pos, level_no in enumerate(reversed(range(lay_dev))):
            level_out = []
            for seq_no in range(seq_dev):
                level_grads, carried, grad_bc, grad_store, map_store = fused_step(
                    step_arr, table, level_pos, lay_dev, per_block, incoming, top_blk, carried,
                    w_bc, grad_store, map_store, level_no, seq_no, factor, width,
                )
                level_out.append(level_grads)
            incoming = jnp.stack(level_out)
        if send:
            incoming = passed_along(incoming, "section", -1)
        return (incoming, carried, grad_store, map_store)

    initial = (
        jnp.zeros((seq_dev, block_len, features), jnp.bfloat16),
        jnp.zeros(states_t.shape[1:], jnp.float32),
        jnp.zeros((MICRO, lay_dev, seq_dev, block_len, features), jnp.bfloat16),
        jnp.zeros((MICRO, lay_dev, seq_dev, block_len, 2 * state_size), jnp.bfloat16),
    )
    final_state = lax.fori_loop(0, steps - 1, advance, initial)
    final_state = advance(steps - 1, final_state, send=False)
    grad_store = final_state[2]
    map_store = final_state[3]

    grad_inputs = jnp.moveaxis(grad_store, 0, 2).reshape(layer_inputs.shape)
    map_store = jnp.moveaxis(map_store, 0, 2).reshape(bc_all.shape)
    ways = lax.axis_size("dp")
    divisor = ways * seq_dev
    rows_here = layer_inputs.reshape(lay_dev, seq_dev * tok_len, ways, features // ways)
    rows_here = jnp.transpose(rows_here, (2, 0, 1, 3))
    rows_all = lax.all_to_all(rows_here, "dp", 0, 0, tiled=True)
    maps_here = map_store.reshape(1, lay_dev, seq_dev * tok_len, map_store.shape[-1])
    maps_all = lax.all_gather(maps_here, "dp", axis=0, tiled=True)
    grad_w = jnp.einsum(
        "glrd,glrc->ldc", rows_all, maps_all, preferred_element_type=jnp.float32
    ) / divisor
    return (grad_inputs, grad_w)


def solution(mesh):
    in_specs = (
        P("section", "dp", None, None),
        P("section", None, None),
        P("section", "dp", None, None),
        P("dp", None, None),
    )
    out_specs = (P("section", "dp", None, None), P("section", "dp", None))
    return jax.shard_map(shards, mesh=mesh, in_specs=in_specs, out_specs=out_specs, check_vma=False)
```

```python
import functools

import jax
import jax.numpy as jnp
from jax import lax
from jax.experimental import pallas as pl
from jax.experimental.pallas import tpu as pltpu
from jax.sharding import PartitionSpec as P

MICRO = 4


def shortened(value):
    return jax.tree.map(lambda a: a.astype(jnp.bfloat16) if a.dtype == jnp.float32 else a, value)


def passed_along(block, axis, distance):
    devices = range(lax.axis_size(axis))
    route = [(i - distance, i) for i in devices if i - distance in devices]
    return lax.ppermute(block, axis, route)


def block_terms(inputs_b, in_b, out_b, rates, grads_b, carried, state_in, factor):
    length = inputs_b.shape[0]
    cumulative = jnp.cumsum(rates, axis=0)
    ending = cumulative[-1]
    locations = jnp.arange(length)
    lower_mask = (locations[:, None] >= locations[None, :])[:, :, None]
    spread = jnp.where(lower_mask, cumulative[:, None, :] - cumulative[None, :, :], 0.0)
    decays = jnp.where(lower_mask, jnp.exp(spread), 0.0)
    tail_decay = jnp.exp(ending[None, :] - cumulative)
    leading = jnp.exp(cumulative)
    scores = jnp.dot(out_b, in_b.T, preferred_element_type=jnp.float32)
    weighted = (factor * decays * scores[:, :, None]).astype(jnp.bfloat16)
    carried_b = carried.astype(jnp.bfloat16)
    state_b = state_in.astype(jnp.bfloat16)
    grad_feats = jnp.einsum("kjh,khp->jhp", weighted, grads_b, preferred_element_type=jnp.float32)
    grad_feats = grad_feats + tail_decay[:, :, None] * jnp.einsum(
        "hpn,jn->jhp", carried_b, in_b, preferred_element_type=jnp.float32
    )
    pair_dots = jnp.einsum("khp,jhp->kjh", grads_b, inputs_b, preferred_element_type=jnp.float32)
    mixing = jnp.sum(decays * pair_dots, axis=2).astype(jnp.bfloat16)
    tail_inputs = (tail_decay[:, :, None] * inputs_b.astype(jnp.float32)).astype(jnp.bfloat16)
    lead_grads = (leading[:, :, None] * grads_b.astype(jnp.float32)).astype(jnp.bfloat16)
    grad_inmap = factor * jnp.dot(mixing.T, out_b, preferred_element_type=jnp.float32)
    grad_inmap = grad_inmap + jnp.einsum(
        "jhp,hpn->jn", tail_inputs, carried_b, preferred_element_type=jnp.float32
    )
    grad_outmap = factor * (
        jnp.dot(mixing, in_b, preferred_element_type=jnp.float32)
        + jnp.einsum("ihp,hpn->in", lead_grads, state_b, preferred_element_type=jnp.float32)
    )
    carry_out = factor * jnp.einsum(
        "khp,kn->hpn", lead_grads, out_b, preferred_element_type=jnp.float32
    )
    carry_out = carry_out + jnp.exp(ending)[:, None, None] * carried
    return (grad_feats, grad_inmap, grad_outmap, carry_out)


def block_end(inputs_b, in_b, rates, state_in):
    cumulative = jnp.cumsum(rates, axis=0)
    ending = cumulative[-1]
    tail_decay = jnp.exp(ending[None, :] - cumulative)
    tail_inputs = (tail_decay[:, :, None] * inputs_b.astype(jnp.float32)).astype(jnp.bfloat16)
    fresh = jnp.einsum("jhp,jn->hpn", tail_inputs, in_b, preferred_element_type=jnp.float32)
    return jnp.exp(ending)[:, None, None] * state_in + fresh


def split_block(inputs_c, map_block, head_count):
    length, features = inputs_c.shape
    state_size = map_block.shape[1] // 2
    inputs_b = inputs_c.reshape(length, head_count, features // head_count)
    in_b = map_block[:, :state_size]
    out_b = map_block[:, state_size:]
    return (inputs_b, in_b, out_b)


def block_back(inputs_c, map_block, rates, grads_c, carried, state_in, weights):
    length, features = inputs_c.shape
    head_count = rates.shape[1]
    factor = 0.25 / (map_block.shape[1] // 2)
    inputs_b, in_b, out_b = split_block(inputs_c, map_block, head_count)
    grads_b = grads_c.reshape(length, head_count, features // head_count)
    grad_feats, grad_inmap, grad_outmap, carry_out = block_terms(
        inputs_b, in_b, out_b, rates, grads_b, carried, state_in, factor
    )
    grad_bc = jnp.concatenate([grad_inmap, grad_outmap], axis=1).astype(jnp.bfloat16)
    back_proj = lax.dot_general(
        grad_bc, weights, (((1,), (1,)), ((), ())), preferred_element_type=jnp.float32
    )
    summed = grads_c.astype(jnp.float32) + grad_feats.reshape(length, features) + back_proj
    return (summed.astype(jnp.bfloat16), carry_out, grad_bc)


def layer_starts(inputs_s, bc_s, rates_s):
    head_count = rates_s.shape[1]
    features = inputs_s.shape[1]
    state_size = bc_s.shape[1] // 2
    block_len = inputs_s.shape[0] // MICRO
    state_now = jnp.zeros((head_count, features // head_count, state_size), jnp.float32)
    saved = []
    for block_no in range(MICRO):
        lo_row = block_no * block_len
        inputs_b, in_b, out_b = split_block(
            inputs_s[lo_row : lo_row + block_len], bc_s[lo_row : lo_row + block_len], head_count
        )
        saved.append(state_now)
        state_now = block_end(inputs_b, in_b, rates_s[lo_row : lo_row + block_len], state_now)
    return jnp.stack(saved)


def block_consts(inputs_b, in_b, out_b, rates, factor):
    length = inputs_b.shape[0]
    cumulative = jnp.cumsum(rates, axis=0)
    ending = cumulative[-1]
    locations = jnp.arange(length)
    lower_mask = (locations[:, None] >= locations[None, :])[:, :, None]
    spread = jnp.where(lower_mask, cumulative[:, None, :] - cumulative[None, :, :], 0.0)
    decays = jnp.where(lower_mask, jnp.exp(spread), 0.0)
    tail_decay = jnp.exp(ending[None, :] - cumulative)
    leading = jnp.exp(cumulative)
    scores = jnp.dot(out_b, in_b.T, preferred_element_type=jnp.float32)
    cum_t = cumulative.T
    upper = (locations[:, None] <= locations[None, :])[None]
    spread_t = jnp.where(upper, cum_t[:, None, :] - cum_t[:, :, None], 0.0)
    decays_t = jnp.where(upper, jnp.exp(spread_t), 0.0)
    scores_t = jnp.dot(in_b, out_b.T, preferred_element_type=jnp.float32)
    weighted = (factor * decays_t * scores_t[None]).astype(jnp.bfloat16)
    return dict(
        decays=decays,
        tail=tail_decay,
        lead=leading,
        weighted=weighted,
        ending=jnp.exp(ending),
    )


def step_kernel(
    step_ref, tab_ref, wt_ref, dec_ref, inc_ref, top_ref, x_ref, b_ref, c_ref, tail_ref, lead_ref, xt_ref,
    sb_ref, r_ref, end_ref, w_ref, gs_ref, ms_ref, out_ref, rnew_ref, dbc_ref, gstore_ref, mstore_ref,
    v_ref, gx_ref, tail_buf, lead_buf, xt_buf, sb_buf, r_buf, w_buf, sems, *, factor, width,
    level_pos, levels, level_no, seq_no
):
    base = (step_ref[0] * levels + level_pos) * 3
    blk = tab_ref[base]
    fetches = [
        pltpu.make_async_copy(r_ref.at[level_no, seq_no], r_buf, sems.at[0]),
        pltpu.make_async_copy(tail_ref.at[blk, level_no, seq_no], tail_buf, sems.at[1]),
        pltpu.make_async_copy(xt_ref.at[blk, level_no, seq_no], xt_buf, sems.at[2]),
        pltpu.make_async_copy(lead_ref.at[blk, level_no, seq_no], lead_buf, sems.at[3]),
        pltpu.make_async_copy(sb_ref.at[blk, level_no, seq_no], sb_buf, sems.at[4]),
        pltpu.make_async_copy(w_ref.at[level_no], w_buf, sems.at[5]),
    ]
    for fetch in fetches:
        fetch.start()
    f32 = jnp.float32
    bf16 = jnp.bfloat16
    length, features = v_ref.shape
    lanes = 128
    per_pair = lanes // width
    nt = (((1,), (1,)), ((), ()))
    tn = (((0,), (0,)), ((), ()))
    v_ref[...] = jnp.where(tab_ref[base + 1] > 0, top_ref[...], inc_ref[...])
    in_map = b_ref[...]
    out_map = c_ref[...]
    lane_id = lax.broadcasted_iota(jnp.int32, (length, lanes), 1)
    masks = [(lane_id >= e * width) & (lane_id < (e + 1) * width) for e in range(per_pair)]
    mix_acc = jnp.zeros((per_pair * length, length), f32)
    for q in range(features // lanes):
        cols = slice(q * lanes, (q + 1) * lanes)
        v_q = v_ref[:, cols]
        x_q = x_ref[:, cols]
        stacked = jnp.concatenate([jnp.where(m, v_q, jnp.zeros_like(v_q)) for m in masks], axis=0)
        gx_q = jnp.dot(
            wt_ref[per_pair * q], stacked[0:length], preferred_element_type=f32
        )
        for e in range(1, per_pair):
            gx_q = gx_q + jnp.dot(
                wt_ref[per_pair * q + e],
                stacked[e * length:(e + 1) * length],
                preferred_element_type=f32,
            )
        gx_ref[:, cols] = gx_q
        pair_dots = lax.dot_general(stacked, x_q, nt, preferred_element_type=f32)
        mix_acc = mix_acc + dec_ref[q] * pair_dots
    mixing = mix_acc[0:length]
    for e in range(1, per_pair):
        mixing = mixing + mix_acc[e * length:(e + 1) * length]
    mixing = mixing.astype(bf16)
    fetches[0].wait()
    fetches[1].wait()
    rb_t = r_buf[...].astype(bf16)
    rbb = jnp.dot(in_map, rb_t, preferred_element_type=f32)
    gx_ref[...] = gx_ref[...] + tail_buf[...] * rbb
    v = v_ref[...]
    fetches[2].wait()
    grad_inmap = factor * lax.dot_general(mixing, out_map, tn, preferred_element_type=f32)
    grad_inmap = grad_inmap + lax.dot_general(xt_buf[...], rb_t, nt, preferred_element_type=f32)
    fetches[3].wait()
    fetches[4].wait()
    lead_grads = (lead_buf[...] * v.astype(f32)).astype(bf16)
    grad_outmap = factor * (
        jnp.dot(mixing, in_map, preferred_element_type=f32)
        + lax.dot_general(lead_grads, sb_buf[...], nt, preferred_element_type=f32)
    )
    carry = factor * lax.dot_general(out_map, lead_grads, tn, preferred_element_type=f32)
    rnew_ref[...] = carry + end_ref[...] * r_buf[...]
    grad_bc = jnp.concatenate([grad_inmap, grad_outmap], axis=1).astype(bf16)
    dbc_ref[...] = grad_bc
    mstore_ref[...] = jnp.where(tab_ref[base + 2] > 0, grad_bc, ms_ref[...])
    fetches[5].wait()
    back = lax.dot_general(grad_bc, w_buf[...], nt, preferred_element_type=f32)
    summed = (v.astype(f32) + gx_ref[...] + back).astype(out_ref.dtype)
    out_ref[...] = summed
    gstore_ref[...] = jnp.where(tab_ref[base + 2] > 0, summed, gs_ref[...])


def fused_step(step_arr, table, level_pos, levels, per_block, incoming, top_blk, carried, w_bc, grad_store, map_store, level_no, seq_no, factor, width):
    wt2, dec2, x_flat, in_blk, out_blk, tail_full, lead_full, xt_full, states_t, end_row = per_block
    length, features = incoming.shape[1:]
    state_size = in_blk.shape[-1]

    def lead_block(a):
        shape = (None, None, None) + a.shape[3:]
        tail = (0,) * (a.ndim - 3)
        return pl.BlockSpec(shape, lambda i, c, t: (t[(c[0] * levels + level_pos) * 3], level_no, seq_no) + tail)

    in_specs = [lead_block(a) for a in (wt2, dec2)]
    in_specs.append(pl.BlockSpec((None, length, features), lambda i, c, t: (seq_no, 0, 0)))
    in_specs.append(pl.BlockSpec((None, None, length, features), lambda i, c, t: (t[(c[0] * levels + level_pos) * 3], seq_no, 0, 0)))
    in_hbm = pl.BlockSpec(memory_space=pl.ANY)
    in_specs += [lead_block(a) for a in (x_flat, in_blk, out_blk)]
    in_specs += [in_hbm] * 5
    in_specs.append(lead_block(end_row))
    in_specs.append(in_hbm)
    store_g = pl.BlockSpec((None, None, None, length, features), lambda i, c, t: (t[(c[0] * levels + level_pos) * 3], level_no, seq_no, 0, 0))
    store_m = pl.BlockSpec((None, None, None, length, 2 * state_size), lambda i, c, t: (t[(c[0] * levels + level_pos) * 3], level_no, seq_no, 0, 0))
    in_specs += [store_g, store_m]
    out_specs = (
        pl.BlockSpec((length, features), lambda i, c, t: (0, 0)),
        pl.BlockSpec((None, None) + carried.shape[2:], lambda i, c, t: (level_no, seq_no, 0, 0)),
        pl.BlockSpec((length, 2 * state_size), lambda i, c, t: (0, 0)),
        store_g,
        store_m,
    )
    flops = 2 * length * features * (6 * state_size + 4 * length)
    moved = 2 * (4 * features * state_size * 2 + 6 * length * features) + 4 * 4 * length * features
    return pl.pallas_call(
        functools.partial(
            step_kernel, factor=factor, width=width, level_pos=level_pos, levels=levels,
            level_no=level_no, seq_no=seq_no,
        ),
        out_shape=(
            jax.ShapeDtypeStruct((length, features), jnp.bfloat16),
            jax.ShapeDtypeStruct(carried.shape, jnp.float32),
            jax.ShapeDtypeStruct((length, 2 * state_size), jnp.bfloat16),
            jax.ShapeDtypeStruct(grad_store.shape, grad_store.dtype),
            jax.ShapeDtypeStruct(map_store.shape, map_store.dtype),
        ),
        grid_spec=pltpu.PrefetchScalarGridSpec(
            num_scalar_prefetch=2,
            grid=(1,),
            in_specs=in_specs,
            out_specs=out_specs,
            scratch_shapes=[
                pltpu.VMEM((length, features), jnp.bfloat16),
                pltpu.VMEM((length, features), jnp.float32),
                pltpu.VMEM((length, features), jnp.float32),
                pltpu.VMEM((length, features), jnp.float32),
                pltpu.VMEM((length, features), jnp.bfloat16),
                pltpu.VMEM(states_t.shape[3:], states_t.dtype),
                pltpu.VMEM(carried.shape[2:], jnp.float32),
                pltpu.VMEM(w_bc.shape[1:], w_bc.dtype),
                pltpu.SemaphoreType.DMA((6,)),
            ],
        ),
        input_output_aliases={13: 1, 16: 3, 17: 4},
        cost_estimate=pl.CostEstimate(flops=flops, bytes_accessed=moved, transcendentals=0),
    )(step_arr, table, wt2, dec2, incoming, top_blk, x_flat, in_blk, out_blk, tail_full, lead_full, xt_full, states_t, carried, end_row, w_bc, grad_store, map_store)


def shards(layer_inputs, w_bc, log_decay, top_grad):
    sections = lax.axis_size("section")
    section_id = lax.axis_index("section")
    lay_dev, seq_dev, tok_len, features = layer_inputs.shape
    head_count = log_decay.shape[-1]
    block_len = tok_len // MICRO
    state_size = w_bc.shape[-1] // 2
    factor = 0.25 / state_size
    bc_all = jnp.einsum(
        "lstd,ldc->lstc", layer_inputs, w_bc, preferred_element_type=jnp.float32
    ).astype(jnp.bfloat16)

    def blocked(a):
        split = a.reshape(a.shape[:2] + (MICRO, block_len) + a.shape[3:])
        return jnp.moveaxis(split, 2, 0)

    x_blk = blocked(layer_inputs).reshape(
        (MICRO, lay_dev, seq_dev, block_len, head_count, features // head_count)
    )
    bc_blk = blocked(bc_all)
    in_blk = bc_blk[..., :state_size]
    out_blk = bc_blk[..., state_size:]
    rates_blk = blocked(log_decay)
    consts_fn = jax.vmap(jax.vmap(jax.vmap(lambda x, b, c, r: block_consts(x, b, c, r, factor))))
    consts = consts_fn(x_blk, in_blk, out_blk, rates_blk)
    width = features // head_count
    lead_dims = consts["tail"].shape[:3]
    pairs = head_count * width // 128
    per_pair = 128 // width
    wt2 = consts["weighted"]
    dec2 = jnp.moveaxis(consts["decays"], -1, -3).reshape(
        lead_dims + (pairs, per_pair * block_len, block_len)
    )
    spread_heads = (
        jnp.arange(features)[None, :] // width == jnp.arange(head_count)[:, None]
    ).astype(jnp.float32)

    def per_lane(a):
        return jnp.einsum(
            "...h,hd->...d", a, spread_heads, precision=lax.Precision.HIGHEST,
            preferred_element_type=jnp.float32,
        )

    tail_full = per_lane(consts["tail"])
    lead_full = per_lane(consts["lead"])
    x_flat = x_blk.reshape(lead_dims + (block_len, features))
    xt_full = (tail_full * x_flat.astype(jnp.float32)).astype(jnp.bfloat16)
    end_row = per_lane(consts["ending"])[..., None, :]
    fresh_t = jnp.einsum(
        "mlsnj,mlsjd->mlsnd",
        jnp.swapaxes(in_blk[: MICRO - 1], -1, -2),
        xt_full[: MICRO - 1],
        preferred_element_type=jnp.float32,
    )
    state_now = jnp.zeros(fresh_t.shape[1:], jnp.float32)
    saved = [state_now.astype(jnp.bfloat16)[None]]
    for block_no in range(MICRO - 1):
        state_now = end_row[block_no] * state_now + fresh_t[block_no]
        saved.append(state_now.astype(jnp.bfloat16)[None])
    states_t = jnp.concatenate(saved, axis=0)
    per_block = (wt2, dec2, x_flat, in_blk, out_blk, tail_full, lead_full, xt_full, states_t, end_row)
    per_block = lax.optimization_barrier(per_block)

    top_blk = jnp.moveaxis(
        top_grad.reshape((seq_dev, MICRO, block_len, features)), 1, 0
    )
    is_top = section_id == sections - 1

    steps = MICRO + sections - 1
    counters = jnp.arange(steps, dtype=jnp.int32)[:, None]
    offsets = counters - (sections - 1 - section_id)
    valid_tab = ((offsets >= 0) & (offsets < MICRO)).astype(jnp.int32)
    block_tab = jnp.clip(MICRO - 1 - offsets, 0, MICRO - 1).astype(jnp.int32)
    top_tab = (jnp.arange(lay_dev)[None, ::-1] == lay_dev - 1) & is_top
    table = jnp.stack(
        jnp.broadcast_arrays(block_tab, top_tab.astype(jnp.int32), valid_tab), axis=-1
    ).reshape(-1).astype(jnp.int32)

    def advance(counter, loop_state, send=True):
        incoming, carried, grad_store, map_store = loop_state
        step_arr = jnp.reshape(counter, (1,)).astype(jnp.int32)
        for level_pos, level_no in enumerate(reversed(range(lay_dev))):
            level_out = []
            for seq_no in range(seq_dev):
                level_grads, carried, grad_bc, grad_store, map_store = fused_step(
                    step_arr, table, level_pos, lay_dev, per_block, incoming, top_blk, carried,
                    w_bc, grad_store, map_store, level_no, seq_no, factor, width,
                )
                level_out.append(level_grads)
            incoming = jnp.stack(level_out)
        if send:
            incoming = passed_along(incoming, "section", -1)
        return (incoming, carried, grad_store, map_store)

    initial = (
        jnp.zeros((seq_dev, block_len, features), jnp.bfloat16),
        jnp.zeros(states_t.shape[1:], jnp.float32),
        jnp.zeros((MICRO, lay_dev, seq_dev, block_len, features), jnp.bfloat16),
        jnp.zeros((MICRO, lay_dev, seq_dev, block_len, 2 * state_size), jnp.bfloat16),
    )
    final_state = lax.fori_loop(0, steps - 1, advance, initial)
    final_state = advance(steps - 1, final_state, send=False)
    grad_store = final_state[2]
    map_store = final_state[3]

    grad_inputs = jnp.moveaxis(grad_store, 0, 2).reshape(layer_inputs.shape)
    map_store = jnp.moveaxis(map_store, 0, 2).reshape(bc_all.shape)
    ways = lax.axis_size("dp")
    divisor = ways * seq_dev
    rows_here = layer_inputs.reshape(lay_dev, seq_dev * tok_len, ways, features // ways)
    rows_here = jnp.transpose(rows_here, (2, 0, 1, 3))
    rows_all = lax.all_to_all(rows_here, "dp", 0, 0, tiled=True)
    maps_here = map_store.reshape(1, lay_dev, seq_dev * tok_len, map_store.shape[-1])
    maps_all = lax.all_gather(maps_here, "dp", axis=0, tiled=True)
    grad_w = jnp.einsum(
        "glrd,glrc->ldc", rows_all, maps_all, preferred_element_type=jnp.float32
    ) / divisor
    return (grad_inputs, grad_w)


def solution(mesh):
    in_specs = (
        P("section", "dp", None, None),
        P("section", None, None),
        P("section", "dp", None, None),
        P("dp", None, None),
    )
    out_specs = (P("section", "dp", None, None), P("section", "dp", None))
    return jax.shard_map(shards, mesh=mesh, in_specs=in_specs, out_specs=out_specs, check_vma=False)
```

```python
import functools

import jax
import jax.numpy as jnp
from jax import lax
from jax.experimental import pallas as pl
from jax.experimental.pallas import tpu as pltpu
from jax.sharding import PartitionSpec as P

MICRO = 4


def shortened(value):
    return jax.tree.map(lambda a: a.astype(jnp.bfloat16) if a.dtype == jnp.float32 else a, value)


def passed_along(block, axis, distance):
    devices = range(lax.axis_size(axis))
    route = [(i - distance, i) for i in devices if i - distance in devices]
    return lax.ppermute(block, axis, route)


def block_terms(inputs_b, in_b, out_b, rates, grads_b, carried, state_in, factor):
    length = inputs_b.shape[0]
    cumulative = jnp.cumsum(rates, axis=0)
    ending = cumulative[-1]
    locations = jnp.arange(length)
    lower_mask = (locations[:, None] >= locations[None, :])[:, :, None]
    spread = jnp.where(lower_mask, cumulative[:, None, :] - cumulative[None, :, :], 0.0)
    decays = jnp.where(lower_mask, jnp.exp(spread), 0.0)
    tail_decay = jnp.exp(ending[None, :] - cumulative)
    leading = jnp.exp(cumulative)
    scores = jnp.dot(out_b, in_b.T, preferred_element_type=jnp.float32)
    weighted = (factor * decays * scores[:, :, None]).astype(jnp.bfloat16)
    carried_b = carried.astype(jnp.bfloat16)
    state_b = state_in.astype(jnp.bfloat16)
    grad_feats = jnp.einsum("kjh,khp->jhp", weighted, grads_b, preferred_element_type=jnp.float32)
    grad_feats = grad_feats + tail_decay[:, :, None] * jnp.einsum(
        "hpn,jn->jhp", carried_b, in_b, preferred_element_type=jnp.float32
    )
    pair_dots = jnp.einsum("khp,jhp->kjh", grads_b, inputs_b, preferred_element_type=jnp.float32)
    mixing = jnp.sum(decays * pair_dots, axis=2).astype(jnp.bfloat16)
    tail_inputs = (tail_decay[:, :, None] * inputs_b.astype(jnp.float32)).astype(jnp.bfloat16)
    lead_grads = (leading[:, :, None] * grads_b.astype(jnp.float32)).astype(jnp.bfloat16)
    grad_inmap = factor * jnp.dot(mixing.T, out_b, preferred_element_type=jnp.float32)
    grad_inmap = grad_inmap + jnp.einsum(
        "jhp,hpn->jn", tail_inputs, carried_b, preferred_element_type=jnp.float32
    )
    grad_outmap = factor * (
        jnp.dot(mixing, in_b, preferred_element_type=jnp.float32)
        + jnp.einsum("ihp,hpn->in", lead_grads, state_b, preferred_element_type=jnp.float32)
    )
    carry_out = factor * jnp.einsum(
        "khp,kn->hpn", lead_grads, out_b, preferred_element_type=jnp.float32
    )
    carry_out = carry_out + jnp.exp(ending)[:, None, None] * carried
    return (grad_feats, grad_inmap, grad_outmap, carry_out)


def block_end(inputs_b, in_b, rates, state_in):
    cumulative = jnp.cumsum(rates, axis=0)
    ending = cumulative[-1]
    tail_decay = jnp.exp(ending[None, :] - cumulative)
    tail_inputs = (tail_decay[:, :, None] * inputs_b.astype(jnp.float32)).astype(jnp.bfloat16)
    fresh = jnp.einsum("jhp,jn->hpn", tail_inputs, in_b, preferred_element_type=jnp.float32)
    return jnp.exp(ending)[:, None, None] * state_in + fresh


def split_block(inputs_c, map_block, head_count):
    length, features = inputs_c.shape
    state_size = map_block.shape[1] // 2
    inputs_b = inputs_c.reshape(length, head_count, features // head_count)
    in_b = map_block[:, :state_size]
    out_b = map_block[:, state_size:]
    return (inputs_b, in_b, out_b)


def block_back(inputs_c, map_block, rates, grads_c, carried, state_in, weights):
    length, features = inputs_c.shape
    head_count = rates.shape[1]
    factor = 0.25 / (map_block.shape[1] // 2)
    inputs_b, in_b, out_b = split_block(inputs_c, map_block, head_count)
    grads_b = grads_c.reshape(length, head_count, features // head_count)
    grad_feats, grad_inmap, grad_outmap, carry_out = block_terms(
        inputs_b, in_b, out_b, rates, grads_b, carried, state_in, factor
    )
    grad_bc = jnp.concatenate([grad_inmap, grad_outmap], axis=1).astype(jnp.bfloat16)
    back_proj = lax.dot_general(
        grad_bc, weights, (((1,), (1,)), ((), ())), preferred_element_type=jnp.float32
    )
    summed = grads_c.astype(jnp.float32) + grad_feats.reshape(length, features) + back_proj
    return (summed.astype(jnp.bfloat16), carry_out, grad_bc)


def layer_starts(inputs_s, bc_s, rates_s):
    head_count = rates_s.shape[1]
    features = inputs_s.shape[1]
    state_size = bc_s.shape[1] // 2
    block_len = inputs_s.shape[0] // MICRO
    state_now = jnp.zeros((head_count, features // head_count, state_size), jnp.float32)
    saved = []
    for block_no in range(MICRO):
        lo_row = block_no * block_len
        inputs_b, in_b, out_b = split_block(
            inputs_s[lo_row : lo_row + block_len], bc_s[lo_row : lo_row + block_len], head_count
        )
        saved.append(state_now)
        state_now = block_end(inputs_b, in_b, rates_s[lo_row : lo_row + block_len], state_now)
    return jnp.stack(saved)


def block_consts(inputs_b, in_b, out_b, rates, factor):
    length = inputs_b.shape[0]
    cumulative = jnp.cumsum(rates, axis=0)
    ending = cumulative[-1]
    locations = jnp.arange(length)
    lower_mask = (locations[:, None] >= locations[None, :])[:, :, None]
    spread = jnp.where(lower_mask, cumulative[:, None, :] - cumulative[None, :, :], 0.0)
    decays = jnp.where(lower_mask, jnp.exp(spread), 0.0)
    tail_decay = jnp.exp(ending[None, :] - cumulative)
    leading = jnp.exp(cumulative)
    scores = jnp.dot(out_b, in_b.T, preferred_element_type=jnp.float32)
    cum_t = cumulative.T
    upper = (locations[:, None] <= locations[None, :])[None]
    spread_t = jnp.where(upper, cum_t[:, None, :] - cum_t[:, :, None], 0.0)
    decays_t = jnp.where(upper, jnp.exp(spread_t), 0.0)
    scores_t = jnp.dot(in_b, out_b.T, preferred_element_type=jnp.float32)
    weighted = (factor * decays_t * scores_t[None]).astype(jnp.bfloat16)
    return dict(
        decays=decays,
        tail=tail_decay,
        lead=leading,
        weighted=weighted,
        ending=jnp.exp(ending),
    )


def step_kernel(
    step_ref, tab_ref, wt_ref, dec_ref, inc_a_ref, inc_b_ref, top_ref, x_ref, b_ref, c_ref, tail_ref, lead_ref, xt_ref,
    sb_ref, r_ref, end_ref, w_ref, gs_ref, ms_ref, out_a_ref, out_b_ref, rnew_ref, dbc_ref, gstore_ref, mstore_ref,
    v_ref, gx_ref, tail_buf, lead_buf, xt_buf, sb_buf, r_buf, w_buf, sems, *, factor, width,
    level_pos, levels, level_no, seq_no
):
    base = (step_ref[0] * levels + level_pos) * 3
    blk = tab_ref[base]
    fetches = [
        pltpu.make_async_copy(r_ref.at[level_no, seq_no], r_buf, sems.at[0]),
        pltpu.make_async_copy(tail_ref.at[blk, level_no, seq_no], tail_buf, sems.at[1]),
        pltpu.make_async_copy(xt_ref.at[blk, level_no, seq_no], xt_buf, sems.at[2]),
        pltpu.make_async_copy(lead_ref.at[blk, level_no, seq_no], lead_buf, sems.at[3]),
        pltpu.make_async_copy(sb_ref.at[blk, level_no, seq_no], sb_buf, sems.at[4]),
        pltpu.make_async_copy(w_ref.at[level_no], w_buf, sems.at[5]),
    ]
    for fetch in fetches:
        fetch.start()
    f32 = jnp.float32
    bf16 = jnp.bfloat16
    length, features = v_ref.shape
    lanes = 128
    per_pair = lanes // width
    nt = (((1,), (1,)), ((), ()))
    tn = (((0,), (0,)), ((), ()))
    half = inc_a_ref.shape[0]
    from_top = tab_ref[base + 1] > 0
    v_ref[0:half] = jnp.where(from_top, top_ref[0:half], inc_a_ref[...])
    v_ref[half:] = jnp.where(from_top, top_ref[half:], inc_b_ref[...])
    in_map = b_ref[...]
    out_map = c_ref[...]
    lane_id = lax.broadcasted_iota(jnp.int32, (length, lanes), 1)
    masks = [(lane_id >= e * width) & (lane_id < (e + 1) * width) for e in range(per_pair)]
    mix_acc = jnp.zeros((per_pair * length, length), f32)
    for q in range(features // lanes):
        cols = slice(q * lanes, (q + 1) * lanes)
        v_q = v_ref[:, cols]
        x_q = x_ref[:, cols]
        stacked = jnp.concatenate([jnp.where(m, v_q, jnp.zeros_like(v_q)) for m in masks], axis=0)
        gx_q = jnp.dot(
            wt_ref[per_pair * q], stacked[0:length], preferred_element_type=f32
        )
        for e in range(1, per_pair):
            gx_q = gx_q + jnp.dot(
                wt_ref[per_pair * q + e],
                stacked[e * length:(e + 1) * length],
                preferred_element_type=f32,
            )
        gx_ref[:, cols] = gx_q
        pair_dots = lax.dot_general(stacked, x_q, nt, preferred_element_type=f32)
        mix_acc = mix_acc + dec_ref[q] * pair_dots
    mixing = mix_acc[0:length]
    for e in range(1, per_pair):
        mixing = mixing + mix_acc[e * length:(e + 1) * length]
    mixing = mixing.astype(bf16)
    fetches[0].wait()
    fetches[1].wait()
    rb_t = r_buf[...].astype(bf16)
    rbb = jnp.dot(in_map, rb_t, preferred_element_type=f32)
    gx_ref[...] = gx_ref[...] + tail_buf[...] * rbb
    v = v_ref[...]
    fetches[2].wait()
    grad_inmap = factor * lax.dot_general(mixing, out_map, tn, preferred_element_type=f32)
    grad_inmap = grad_inmap + lax.dot_general(xt_buf[...], rb_t, nt, preferred_element_type=f32)
    fetches[3].wait()
    fetches[4].wait()
    lead_grads = (lead_buf[...] * v.astype(f32)).astype(bf16)
    grad_outmap = factor * (
        jnp.dot(mixing, in_map, preferred_element_type=f32)
        + lax.dot_general(lead_grads, sb_buf[...], nt, preferred_element_type=f32)
    )
    carry = factor * lax.dot_general(out_map, lead_grads, tn, preferred_element_type=f32)
    rnew_ref[...] = carry + end_ref[...] * r_buf[...]
    grad_bc = jnp.concatenate([grad_inmap, grad_outmap], axis=1).astype(bf16)
    dbc_ref[...] = grad_bc
    mstore_ref[...] = jnp.where(tab_ref[base + 2] > 0, grad_bc, ms_ref[...])
    fetches[5].wait()
    back = lax.dot_general(grad_bc, w_buf[...], nt, preferred_element_type=f32)
    summed = (v.astype(f32) + gx_ref[...] + back).astype(out_a_ref.dtype)
    out_a_ref[...] = summed[0:half]
    out_b_ref[...] = summed[half:]
    gstore_ref[...] = jnp.where(tab_ref[base + 2] > 0, summed, gs_ref[...])


def fused_step(step_arr, table, level_pos, levels, per_block, incoming, top_blk, carried, w_bc, grad_store, map_store, level_no, seq_no, factor, width):
    wt2, dec2, x_flat, in_blk, out_blk, tail_full, lead_full, xt_full, states_t, end_row = per_block
    half, features = incoming[0].shape[1:]
    length = 2 * half
    state_size = in_blk.shape[-1]

    def lead_block(a):
        shape = (None, None, None) + a.shape[3:]
        tail = (0,) * (a.ndim - 3)
        return pl.BlockSpec(shape, lambda i, c, t: (t[(c[0] * levels + level_pos) * 3], level_no, seq_no) + tail)

    in_specs = [lead_block(a) for a in (wt2, dec2)]
    in_specs += [pl.BlockSpec((None, half, features), lambda i, c, t: (seq_no, 0, 0))] * 2
    in_specs.append(pl.BlockSpec((None, None, length, features), lambda i, c, t: (t[(c[0] * levels + level_pos) * 3], seq_no, 0, 0)))
    in_hbm = pl.BlockSpec(memory_space=pl.ANY)
    in_specs += [lead_block(a) for a in (x_flat, in_blk, out_blk)]
    in_specs += [in_hbm] * 5
    in_specs.append(lead_block(end_row))
    in_specs.append(in_hbm)
    store_g = pl.BlockSpec((None, None, None, length, features), lambda i, c, t: (t[(c[0] * levels + level_pos) * 3], level_no, seq_no, 0, 0))
    store_m = pl.BlockSpec((None, None, None, length, 2 * state_size), lambda i, c, t: (t[(c[0] * levels + level_pos) * 3], level_no, seq_no, 0, 0))
    in_specs += [store_g, store_m]
    out_specs = (
        pl.BlockSpec((half, features), lambda i, c, t: (0, 0)),
        pl.BlockSpec((half, features), lambda i, c, t: (0, 0)),
        pl.BlockSpec((None, None) + carried.shape[2:], lambda i, c, t: (level_no, seq_no, 0, 0)),
        pl.BlockSpec((length, 2 * state_size), lambda i, c, t: (0, 0)),
        store_g,
        store_m,
    )
    flops = 2 * length * features * (6 * state_size + 4 * length)
    moved = 2 * (4 * features * state_size * 2 + 6 * length * features) + 4 * 4 * length * features
    outs = pl.pallas_call(
        functools.partial(
            step_kernel, factor=factor, width=width, level_pos=level_pos, levels=levels,
            level_no=level_no, seq_no=seq_no,
        ),
        out_shape=(
            jax.ShapeDtypeStruct((half, features), jnp.bfloat16),
            jax.ShapeDtypeStruct((half, features), jnp.bfloat16),
            jax.ShapeDtypeStruct(carried.shape, jnp.float32),
            jax.ShapeDtypeStruct((length, 2 * state_size), jnp.bfloat16),
            jax.ShapeDtypeStruct(grad_store.shape, grad_store.dtype),
            jax.ShapeDtypeStruct(map_store.shape, map_store.dtype),
        ),
        grid_spec=pltpu.PrefetchScalarGridSpec(
            num_scalar_prefetch=2,
            grid=(1,),
            in_specs=in_specs,
            out_specs=out_specs,
            scratch_shapes=[
                pltpu.VMEM((length, features), jnp.bfloat16),
                pltpu.VMEM((length, features), jnp.float32),
                pltpu.VMEM((length, features), jnp.float32),
                pltpu.VMEM((length, features), jnp.float32),
                pltpu.VMEM((length, features), jnp.bfloat16),
                pltpu.VMEM(states_t.shape[3:], states_t.dtype),
                pltpu.VMEM(carried.shape[2:], jnp.float32),
                pltpu.VMEM(w_bc.shape[1:], w_bc.dtype),
                pltpu.SemaphoreType.DMA((6,)),
            ],
        ),
        input_output_aliases={14: 2, 17: 4, 18: 5},
        cost_estimate=pl.CostEstimate(flops=flops, bytes_accessed=moved, transcendentals=0),
    )(step_arr, table, wt2, dec2, incoming[0], incoming[1], top_blk, x_flat, in_blk, out_blk, tail_full, lead_full, xt_full, states_t, carried, end_row, w_bc, grad_store, map_store)
    return ((outs[0], outs[1]),) + tuple(outs[2:])


def shards(layer_inputs, w_bc, log_decay, top_grad):
    sections = lax.axis_size("section")
    section_id = lax.axis_index("section")
    lay_dev, seq_dev, tok_len, features = layer_inputs.shape
    head_count = log_decay.shape[-1]
    block_len = tok_len // MICRO
    state_size = w_bc.shape[-1] // 2
    factor = 0.25 / state_size
    bc_all = jnp.einsum(
        "lstd,ldc->lstc", layer_inputs, w_bc, preferred_element_type=jnp.float32
    ).astype(jnp.bfloat16)

    def blocked(a):
        split = a.reshape(a.shape[:2] + (MICRO, block_len) + a.shape[3:])
        return jnp.moveaxis(split, 2, 0)

    x_blk = blocked(layer_inputs).reshape(
        (MICRO, lay_dev, seq_dev, block_len, head_count, features // head_count)
    )
    bc_blk = blocked(bc_all)
    in_blk = bc_blk[..., :state_size]
    out_blk = bc_blk[..., state_size:]
    rates_blk = blocked(log_decay)
    consts_fn = jax.vmap(jax.vmap(jax.vmap(lambda x, b, c, r: block_consts(x, b, c, r, factor))))
    consts = consts_fn(x_blk, in_blk, out_blk, rates_blk)
    width = features // head_count
    lead_dims = consts["tail"].shape[:3]
    pairs = head_count * width // 128
    per_pair = 128 // width
    wt2 = consts["weighted"]
    dec2 = jnp.moveaxis(consts["decays"], -1, -3).reshape(
        lead_dims + (pairs, per_pair * block_len, block_len)
    )
    spread_heads = (
        jnp.arange(features)[None, :] // width == jnp.arange(head_count)[:, None]
    ).astype(jnp.float32)

    def per_lane(a):
        return jnp.einsum(
            "...h,hd->...d", a, spread_heads, precision=lax.Precision.HIGHEST,
            preferred_element_type=jnp.float32,
        )

    tail_full = per_lane(consts["tail"])
    lead_full = per_lane(consts["lead"])
    x_flat = x_blk.reshape(lead_dims + (block_len, features))
    xt_full = (tail_full * x_flat.astype(jnp.float32)).astype(jnp.bfloat16)
    end_row = per_lane(consts["ending"])[..., None, :]
    fresh_t = jnp.einsum(
        "mlsnj,mlsjd->mlsnd",
        jnp.swapaxes(in_blk[: MICRO - 1], -1, -2),
        xt_full[: MICRO - 1],
        preferred_element_type=jnp.float32,
    )
    state_now = jnp.zeros(fresh_t.shape[1:], jnp.float32)
    saved = [state_now.astype(jnp.bfloat16)[None]]
    for block_no in range(MICRO - 1):
        state_now = end_row[block_no] * state_now + fresh_t[block_no]
        saved.append(state_now.astype(jnp.bfloat16)[None])
    states_t = jnp.concatenate(saved, axis=0)
    per_block = (wt2, dec2, x_flat, in_blk, out_blk, tail_full, lead_full, xt_full, states_t, end_row)
    per_block = lax.optimization_barrier(per_block)

    top_blk = jnp.moveaxis(
        top_grad.reshape((seq_dev, MICRO, block_len, features)), 1, 0
    )
    is_top = section_id == sections - 1

    steps = MICRO + sections - 1
    counters = jnp.arange(steps, dtype=jnp.int32)[:, None]
    offsets = counters - (sections - 1 - section_id)
    valid_tab = ((offsets >= 0) & (offsets < MICRO)).astype(jnp.int32)
    block_tab = jnp.clip(MICRO - 1 - offsets, 0, MICRO - 1).astype(jnp.int32)
    top_tab = (jnp.arange(lay_dev)[None, ::-1] == lay_dev - 1) & is_top
    table = jnp.stack(
        jnp.broadcast_arrays(block_tab, top_tab.astype(jnp.int32), valid_tab), axis=-1
    ).reshape(-1).astype(jnp.int32)

    def advance(counter, loop_state, send=True):
        incoming, carried, grad_store, map_store = loop_state
        step_arr = jnp.reshape(counter, (1,)).astype(jnp.int32)
        for level_pos, level_no in enumerate(reversed(range(lay_dev))):
            level_out = []
            for seq_no in range(seq_dev):
                level_grads, carried, grad_bc, grad_store, map_store = fused_step(
                    step_arr, table, level_pos, lay_dev, per_block, incoming, top_blk, carried,
                    w_bc, grad_store, map_store, level_no, seq_no, factor, width,
                )
                level_out.append(level_grads)
            incoming = tuple(jnp.stack([g[e] for g in level_out]) for e in range(2))
        if send:
            incoming = tuple(passed_along(part, "section", -1) for part in incoming)
        return (incoming, carried, grad_store, map_store)

    initial = (
        tuple(jnp.zeros((seq_dev, block_len // 2, features), jnp.bfloat16) for _ in range(2)),
        jnp.zeros(states_t.shape[1:], jnp.float32),
        jnp.zeros((MICRO, lay_dev, seq_dev, block_len, features), jnp.bfloat16),
        jnp.zeros((MICRO, lay_dev, seq_dev, block_len, 2 * state_size), jnp.bfloat16),
    )
    final_state = lax.fori_loop(0, steps - 1, advance, initial)
    final_state = advance(steps - 1, final_state, send=False)
    grad_store = final_state[2]
    map_store = final_state[3]

    grad_inputs = jnp.moveaxis(grad_store, 0, 2).reshape(layer_inputs.shape)
    map_store = jnp.moveaxis(map_store, 0, 2).reshape(bc_all.shape)
    ways = lax.axis_size("dp")
    divisor = ways * seq_dev
    rows_here = layer_inputs.reshape(lay_dev, seq_dev * tok_len, ways, features // ways)
    rows_here = jnp.transpose(rows_here, (2, 0, 1, 3))
    rows_all = lax.all_to_all(rows_here, "dp", 0, 0, tiled=True)
    maps_here = map_store.reshape(1, lay_dev, seq_dev * tok_len, map_store.shape[-1])
    maps_all = lax.all_gather(maps_here, "dp", axis=0, tiled=True)
    grad_w = jnp.einsum(
        "glrd,glrc->ldc", rows_all, maps_all, preferred_element_type=jnp.float32
    ) / divisor
    return (grad_inputs, grad_w)


def solution(mesh):
    in_specs = (
        P("section", "dp", None, None),
        P("section", None, None),
        P("section", "dp", None, None),
        P("dp", None, None),
    )
    out_specs = (P("section", "dp", None, None), P("section", "dp", None))
    return jax.shard_map(shards, mesh=mesh, in_specs=in_specs, out_specs=out_specs, check_vma=False)
```

```python
import functools

import jax
import jax.numpy as jnp
from jax import lax
from jax.experimental import pallas as pl
from jax.experimental.pallas import tpu as pltpu
from jax.sharding import PartitionSpec as P

MICRO = 4


def shortened(value):
    return jax.tree.map(lambda a: a.astype(jnp.bfloat16) if a.dtype == jnp.float32 else a, value)


def passed_along(block, axis, distance):
    devices = range(lax.axis_size(axis))
    route = [(i - distance, i) for i in devices if i - distance in devices]
    return lax.ppermute(block, axis, route)


def block_terms(inputs_b, in_b, out_b, rates, grads_b, carried, state_in, factor):
    length = inputs_b.shape[0]
    cumulative = jnp.cumsum(rates, axis=0)
    ending = cumulative[-1]
    locations = jnp.arange(length)
    lower_mask = (locations[:, None] >= locations[None, :])[:, :, None]
    spread = jnp.where(lower_mask, cumulative[:, None, :] - cumulative[None, :, :], 0.0)
    decays = jnp.where(lower_mask, jnp.exp(spread), 0.0)
    tail_decay = jnp.exp(ending[None, :] - cumulative)
    leading = jnp.exp(cumulative)
    scores = jnp.dot(out_b, in_b.T, preferred_element_type=jnp.float32)
    weighted = (factor * decays * scores[:, :, None]).astype(jnp.bfloat16)
    carried_b = carried.astype(jnp.bfloat16)
    state_b = state_in.astype(jnp.bfloat16)
    grad_feats = jnp.einsum("kjh,khp->jhp", weighted, grads_b, preferred_element_type=jnp.float32)
    grad_feats = grad_feats + tail_decay[:, :, None] * jnp.einsum(
        "hpn,jn->jhp", carried_b, in_b, preferred_element_type=jnp.float32
    )
    pair_dots = jnp.einsum("khp,jhp->kjh", grads_b, inputs_b, preferred_element_type=jnp.float32)
    mixing = jnp.sum(decays * pair_dots, axis=2).astype(jnp.bfloat16)
    tail_inputs = (tail_decay[:, :, None] * inputs_b.astype(jnp.float32)).astype(jnp.bfloat16)
    lead_grads = (leading[:, :, None] * grads_b.astype(jnp.float32)).astype(jnp.bfloat16)
    grad_inmap = factor * jnp.dot(mixing.T, out_b, preferred_element_type=jnp.float32)
    grad_inmap = grad_inmap + jnp.einsum(
        "jhp,hpn->jn", tail_inputs, carried_b, preferred_element_type=jnp.float32
    )
    grad_outmap = factor * (
        jnp.dot(mixing, in_b, preferred_element_type=jnp.float32)
        + jnp.einsum("ihp,hpn->in", lead_grads, state_b, preferred_element_type=jnp.float32)
    )
    carry_out = factor * jnp.einsum(
        "khp,kn->hpn", lead_grads, out_b, preferred_element_type=jnp.float32
    )
    carry_out = carry_out + jnp.exp(ending)[:, None, None] * carried
    return (grad_feats, grad_inmap, grad_outmap, carry_out)


def block_end(inputs_b, in_b, rates, state_in):
    cumulative = jnp.cumsum(rates, axis=0)
    ending = cumulative[-1]
    tail_decay = jnp.exp(ending[None, :] - cumulative)
    tail_inputs = (tail_decay[:, :, None] * inputs_b.astype(jnp.float32)).astype(jnp.bfloat16)
    fresh = jnp.einsum("jhp,jn->hpn", tail_inputs, in_b, preferred_element_type=jnp.float32)
    return jnp.exp(ending)[:, None, None] * state_in + fresh


def split_block(inputs_c, map_block, head_count):
    length, features = inputs_c.shape
    state_size = map_block.shape[1] // 2
    inputs_b = inputs_c.reshape(length, head_count, features // head_count)
    in_b = map_block[:, :state_size]
    out_b = map_block[:, state_size:]
    return (inputs_b, in_b, out_b)


def block_back(inputs_c, map_block, rates, grads_c, carried, state_in, weights):
    length, features = inputs_c.shape
    head_count = rates.shape[1]
    factor = 0.25 / (map_block.shape[1] // 2)
    inputs_b, in_b, out_b = split_block(inputs_c, map_block, head_count)
    grads_b = grads_c.reshape(length, head_count, features // head_count)
    grad_feats, grad_inmap, grad_outmap, carry_out = block_terms(
        inputs_b, in_b, out_b, rates, grads_b, carried, state_in, factor
    )
    grad_bc = jnp.concatenate([grad_inmap, grad_outmap], axis=1).astype(jnp.bfloat16)
    back_proj = lax.dot_general(
        grad_bc, weights, (((1,), (1,)), ((), ())), preferred_element_type=jnp.float32
    )
    summed = grads_c.astype(jnp.float32) + grad_feats.reshape(length, features) + back_proj
    return (summed.astype(jnp.bfloat16), carry_out, grad_bc)


def layer_starts(inputs_s, bc_s, rates_s):
    head_count = rates_s.shape[1]
    features = inputs_s.shape[1]
    state_size = bc_s.shape[1] // 2
    block_len = inputs_s.shape[0] // MICRO
    state_now = jnp.zeros((head_count, features // head_count, state_size), jnp.float32)
    saved = []
    for block_no in range(MICRO):
        lo_row = block_no * block_len
        inputs_b, in_b, out_b = split_block(
            inputs_s[lo_row : lo_row + block_len], bc_s[lo_row : lo_row + block_len], head_count
        )
        saved.append(state_now)
        state_now = block_end(inputs_b, in_b, rates_s[lo_row : lo_row + block_len], state_now)
    return jnp.stack(saved)


def block_consts(inputs_b, in_b, out_b, rates, factor):
    length = inputs_b.shape[0]
    cumulative = jnp.cumsum(rates, axis=0)
    ending = cumulative[-1]
    locations = jnp.arange(length)
    lower_mask = (locations[:, None] >= locations[None, :])[:, :, None]
    spread = jnp.where(lower_mask, cumulative[:, None, :] - cumulative[None, :, :], 0.0)
    decays = jnp.where(lower_mask, jnp.exp(spread), 0.0)
    tail_decay = jnp.exp(ending[None, :] - cumulative)
    leading = jnp.exp(cumulative)
    scores = jnp.dot(out_b, in_b.T, preferred_element_type=jnp.float32)
    cum_t = cumulative.T
    upper = (locations[:, None] <= locations[None, :])[None]
    spread_t = jnp.where(upper, cum_t[:, None, :] - cum_t[:, :, None], 0.0)
    decays_t = jnp.where(upper, jnp.exp(spread_t), 0.0)
    scores_t = jnp.dot(in_b, out_b.T, preferred_element_type=jnp.float32)
    weighted = (factor * decays_t * scores_t[None]).astype(jnp.bfloat16)
    return dict(
        decays=decays,
        tail=tail_decay,
        lead=leading,
        weighted=weighted,
        ending=jnp.exp(ending),
    )


def step_kernel(
    step_ref, tab_ref, wt_ref, dec_ref, inc_ref, top_ref, x_ref, b_ref, c_ref, tail_ref, lead_ref, xt_ref,
    sb_ref, r_ref, end_ref, w_ref, gs_ref, ms_ref, out_ref, rnew_ref, dbc_ref, gstore_ref, mstore_ref,
    v_ref, gx_ref, tail_buf, lead_buf, xt_buf, sb_buf, r_buf, w_buf, sems, *, factor, width,
    level_pos, levels, level_no, seq_no
):
    base = (step_ref[0] * levels + level_pos) * 3
    blk = tab_ref[base]
    fetches = [
        pltpu.make_async_copy(r_ref.at[level_no, seq_no], r_buf, sems.at[0]),
        pltpu.make_async_copy(tail_ref.at[blk, level_no, seq_no], tail_buf, sems.at[1]),
        pltpu.make_async_copy(xt_ref.at[blk, level_no, seq_no], xt_buf, sems.at[2]),
        pltpu.make_async_copy(lead_ref.at[blk, level_no, seq_no], lead_buf, sems.at[3]),
        pltpu.make_async_copy(sb_ref.at[blk, level_no, seq_no], sb_buf, sems.at[4]),
        pltpu.make_async_copy(w_ref.at[level_no], w_buf, sems.at[5]),
    ]
    for fetch in fetches:
        fetch.start()
    f32 = jnp.float32
    bf16 = jnp.bfloat16
    length, features = v_ref.shape
    lanes = 128
    per_pair = lanes // width
    nt = (((1,), (1,)), ((), ()))
    tn = (((0,), (0,)), ((), ()))
    v_ref[...] = jnp.where(tab_ref[base + 1] > 0, top_ref[...], inc_ref[...])
    in_map = b_ref[...]
    out_map = c_ref[...]
    lane_id = lax.broadcasted_iota(jnp.int32, (length, lanes), 1)
    masks = [(lane_id >= e * width) & (lane_id < (e + 1) * width) for e in range(per_pair)]
    mix_acc = jnp.zeros((per_pair * length, length), f32)
    for q in range(features // lanes):
        cols = slice(q * lanes, (q + 1) * lanes)
        v_q = v_ref[:, cols]
        x_q = x_ref[:, cols]
        stacked = jnp.concatenate([jnp.where(m, v_q, jnp.zeros_like(v_q)) for m in masks], axis=0)
        gx_q = jnp.dot(
            wt_ref[per_pair * q], stacked[0:length], preferred_element_type=f32
        )
        for e in range(1, per_pair):
            gx_q = gx_q + jnp.dot(
                wt_ref[per_pair * q + e],
                stacked[e * length:(e + 1) * length],
                preferred_element_type=f32,
            )
        gx_ref[:, cols] = gx_q
        pair_dots = lax.dot_general(stacked, x_q, nt, preferred_element_type=f32)
        mix_acc = mix_acc + dec_ref[q] * pair_dots
    mixing = mix_acc[0:length]
    for e in range(1, per_pair):
        mixing = mixing + mix_acc[e * length:(e + 1) * length]
    mixing = mixing.astype(bf16)
    fetches[0].wait()
    fetches[1].wait()
    rb_t = r_buf[...].astype(bf16)
    rbb = jnp.dot(in_map, rb_t, preferred_element_type=f32)
    gx_ref[...] = gx_ref[...] + tail_buf[...] * rbb
    v = v_ref[...]
    fetches[2].wait()
    grad_inmap = factor * lax.dot_general(mixing, out_map, tn, preferred_element_type=f32)
    grad_inmap = grad_inmap + lax.dot_general(xt_buf[...], rb_t, nt, preferred_element_type=f32)
    fetches[3].wait()
    fetches[4].wait()
    lead_grads = (lead_buf[...] * v.astype(f32)).astype(bf16)
    grad_outmap = factor * (
        jnp.dot(mixing, in_map, preferred_element_type=f32)
        + lax.dot_general(lead_grads, sb_buf[...], nt, preferred_element_type=f32)
    )
    carry = factor * lax.dot_general(out_map, lead_grads, tn, preferred_element_type=f32)
    rnew_ref[...] = carry + end_ref[...] * r_buf[...]
    grad_bc = jnp.concatenate([grad_inmap, grad_outmap], axis=1).astype(bf16)
    dbc_ref[...] = grad_bc
    mstore_ref[...] = jnp.where(tab_ref[base + 2] > 0, grad_bc, ms_ref[...])
    fetches[5].wait()
    back = lax.dot_general(grad_bc, w_buf[...], nt, preferred_element_type=f32)
    summed = (v.astype(f32) + gx_ref[...] + back).astype(out_ref.dtype)
    out_ref[...] = summed
    gstore_ref[...] = jnp.where(tab_ref[base + 2] > 0, summed, gs_ref[...])


def fused_step(step_arr, table, level_pos, levels, per_block, incoming, top_blk, carried, w_bc, grad_store, map_store, level_no, seq_no, factor, width):
    wt2, dec2, x_flat, in_blk, out_blk, tail_full, lead_full, xt_full, states_t, end_row = per_block
    length, features = incoming.shape[1:]
    state_size = in_blk.shape[-1]

    def lead_block(a):
        shape = (None, None, None) + a.shape[3:]
        tail = (0,) * (a.ndim - 3)
        return pl.BlockSpec(shape, lambda i, c, t: (t[(c[0] * levels + level_pos) * 3], level_no, seq_no) + tail)

    in_specs = [lead_block(a) for a in (wt2, dec2)]
    in_specs.append(pl.BlockSpec((None, length, features), lambda i, c, t: (seq_no, 0, 0)))
    in_specs.append(pl.BlockSpec((None, None, length, features), lambda i, c, t: (t[(c[0] * levels + level_pos) * 3], seq_no, 0, 0)))
    in_hbm = pl.BlockSpec(memory_space=pl.ANY)
    in_specs += [lead_block(a) for a in (x_flat, in_blk, out_blk)]
    in_specs += [in_hbm] * 5
    in_specs.append(lead_block(end_row))
    in_specs.append(in_hbm)
    store_g = pl.BlockSpec((None, None, None, length, features), lambda i, c, t: (t[(c[0] * levels + level_pos) * 3], level_no, seq_no, 0, 0))
    store_m = pl.BlockSpec((None, None, None, length, 2 * state_size), lambda i, c, t: (t[(c[0] * levels + level_pos) * 3], level_no, seq_no, 0, 0))
    in_specs += [store_g, store_m]
    out_specs = (
        pl.BlockSpec((length, features), lambda i, c, t: (0, 0)),
        pl.BlockSpec((None, None) + carried.shape[2:], lambda i, c, t: (level_no, seq_no, 0, 0)),
        pl.BlockSpec((length, 2 * state_size), lambda i, c, t: (0, 0)),
        store_g,
        store_m,
    )
    flops = 2 * length * features * (6 * state_size + 4 * length)
    moved = 2 * (4 * features * state_size * 2 + 6 * length * features) + 4 * 4 * length * features
    return pl.pallas_call(
        functools.partial(
            step_kernel, factor=factor, width=width, level_pos=level_pos, levels=levels,
            level_no=level_no, seq_no=seq_no,
        ),
        out_shape=(
            jax.ShapeDtypeStruct((length, features), jnp.bfloat16),
            jax.ShapeDtypeStruct(carried.shape, jnp.float32),
            jax.ShapeDtypeStruct((length, 2 * state_size), jnp.bfloat16),
            jax.ShapeDtypeStruct(grad_store.shape, grad_store.dtype),
            jax.ShapeDtypeStruct(map_store.shape, map_store.dtype),
        ),
        grid_spec=pltpu.PrefetchScalarGridSpec(
            num_scalar_prefetch=2,
            grid=(1,),
            in_specs=in_specs,
            out_specs=out_specs,
            scratch_shapes=[
                pltpu.VMEM((length, features), jnp.bfloat16),
                pltpu.VMEM((length, features), jnp.float32),
                pltpu.VMEM((length, features), jnp.float32),
                pltpu.VMEM((length, features), jnp.float32),
                pltpu.VMEM((length, features), jnp.bfloat16),
                pltpu.VMEM(states_t.shape[3:], states_t.dtype),
                pltpu.VMEM(carried.shape[2:], jnp.float32),
                pltpu.VMEM(w_bc.shape[1:], w_bc.dtype),
                pltpu.SemaphoreType.DMA((6,)),
            ],
        ),
        input_output_aliases={13: 1, 16: 3, 17: 4},
        cost_estimate=pl.CostEstimate(flops=flops, bytes_accessed=moved, transcendentals=0),
    )(step_arr, table, wt2, dec2, incoming, top_blk, x_flat, in_blk, out_blk, tail_full, lead_full, xt_full, states_t, carried, end_row, w_bc, grad_store, map_store)


def shards(layer_inputs, w_bc, log_decay, top_grad):
    sections = lax.axis_size("section")
    section_id = lax.axis_index("section")
    lay_dev, seq_dev, tok_len, features = layer_inputs.shape
    head_count = log_decay.shape[-1]
    block_len = tok_len // MICRO
    state_size = w_bc.shape[-1] // 2
    factor = 0.25 / state_size
    bc_all = jnp.einsum(
        "lstd,ldc->lstc", layer_inputs, w_bc, preferred_element_type=jnp.float32
    ).astype(jnp.bfloat16)

    def blocked(a):
        split = a.reshape(a.shape[:2] + (MICRO, block_len) + a.shape[3:])
        return jnp.moveaxis(split, 2, 0)

    x_blk = blocked(layer_inputs).reshape(
        (MICRO, lay_dev, seq_dev, block_len, head_count, features // head_count)
    )
    bc_blk = blocked(bc_all)
    in_blk = bc_blk[..., :state_size]
    out_blk = bc_blk[..., state_size:]
    rates_blk = blocked(log_decay)
    consts_fn = jax.vmap(jax.vmap(jax.vmap(lambda x, b, c, r: block_consts(x, b, c, r, factor))))
    consts = consts_fn(x_blk, in_blk, out_blk, rates_blk)
    width = features // head_count
    lead_dims = consts["tail"].shape[:3]
    pairs = head_count * width // 128
    per_pair = 128 // width
    wt2 = consts["weighted"]
    dec2 = jnp.moveaxis(consts["decays"], -1, -3).reshape(
        lead_dims + (pairs, per_pair * block_len, block_len)
    )
    spread_heads = (
        jnp.arange(features)[None, :] // width == jnp.arange(head_count)[:, None]
    ).astype(jnp.float32)

    def per_lane(a):
        return jnp.einsum(
            "...h,hd->...d", a, spread_heads, precision=lax.Precision.HIGHEST,
            preferred_element_type=jnp.float32,
        )

    tail_full = per_lane(consts["tail"])
    lead_full = per_lane(consts["lead"])
    x_flat = x_blk.reshape(lead_dims + (block_len, features))
    xt_full = (tail_full * x_flat.astype(jnp.float32)).astype(jnp.bfloat16)
    end_row = per_lane(consts["ending"])[..., None, :]
    fresh_t = jnp.einsum(
        "mlsnj,mlsjd->mlsnd",
        jnp.swapaxes(in_blk[: MICRO - 1], -1, -2),
        xt_full[: MICRO - 1],
        preferred_element_type=jnp.float32,
    )
    state_now = jnp.zeros(fresh_t.shape[1:], jnp.float32)
    saved = [state_now.astype(jnp.bfloat16)[None]]
    for block_no in range(MICRO - 1):
        state_now = end_row[block_no] * state_now + fresh_t[block_no]
        saved.append(state_now.astype(jnp.bfloat16)[None])
    states_t = jnp.concatenate(saved, axis=0)
    per_block = (wt2, dec2, x_flat, in_blk, out_blk, tail_full, lead_full, xt_full, states_t, end_row)
    per_block = lax.optimization_barrier(per_block)

    top_blk = jnp.moveaxis(
        top_grad.reshape((seq_dev, MICRO, block_len, features)), 1, 0
    )
    is_top = section_id == sections - 1

    steps = MICRO + sections - 1
    counters = jnp.arange(steps, dtype=jnp.int32)[:, None]
    offsets = counters - (sections - 1 - section_id)
    valid_tab = ((offsets >= 0) & (offsets < MICRO)).astype(jnp.int32)
    block_tab = jnp.clip(MICRO - 1 - offsets, 0, MICRO - 1).astype(jnp.int32)
    top_tab = (jnp.arange(lay_dev)[None, ::-1] == lay_dev - 1) & is_top
    table = jnp.stack(
        jnp.broadcast_arrays(block_tab, top_tab.astype(jnp.int32), valid_tab), axis=-1
    ).reshape(-1).astype(jnp.int32)

    def advance(counter, loop_state, send=True):
        incoming, carried, grad_store, map_store = loop_state
        step_arr = jnp.reshape(counter, (1,)).astype(jnp.int32)
        for level_pos, level_no in enumerate(reversed(range(lay_dev))):
            level_out = []
            for seq_no in range(seq_dev):
                level_grads, carried, grad_bc, grad_store, map_store = fused_step(
                    step_arr, table, level_pos, lay_dev, per_block, incoming, top_blk, carried,
                    w_bc, grad_store, map_store, level_no, seq_no, factor, width,
                )
                level_out.append(level_grads)
            incoming = jnp.stack(level_out)
        if send:
            incoming = passed_along(incoming, "section", -1)
        return (incoming, carried, grad_store, map_store)

    initial = (
        jnp.zeros((seq_dev, block_len, features), jnp.bfloat16),
        jnp.zeros(states_t.shape[1:], jnp.float32),
        jnp.zeros((MICRO, lay_dev, seq_dev, block_len, features), jnp.bfloat16),
        jnp.zeros((MICRO, lay_dev, seq_dev, block_len, 2 * state_size), jnp.bfloat16),
    )
    final_state = lax.fori_loop(0, steps - 2, advance, initial)
    final_state = advance(steps - 2, final_state)
    early_all = lax.all_gather(final_state[3][None, 1:], "dp", axis=0, tiled=True)
    received, early_all = lax.optimization_barrier((final_state[0], early_all))
    final_state = advance(steps - 1, (received,) + final_state[1:], send=False)
    late_all = lax.all_gather(final_state[3][None, :1], "dp", axis=0, tiled=True)
    grad_store = final_state[2]

    grad_inputs = jnp.moveaxis(grad_store, 0, 2).reshape(layer_inputs.shape)
    ways = lax.axis_size("dp")
    divisor = ways * seq_dev
    rows_here = layer_inputs.reshape(lay_dev, seq_dev * tok_len, ways, features // ways)
    rows_here = jnp.transpose(rows_here, (2, 0, 1, 3))
    rows_all = lax.all_to_all(rows_here, "dp", 0, 0, tiled=True)
    rows_all = rows_all.reshape((ways, lay_dev, seq_dev, MICRO, block_len, features // ways))
    grad_w = jnp.einsum(
        "alsmjd,amlsjc->ldc", rows_all[:, :, :, 1:], early_all, preferred_element_type=jnp.float32
    ) + jnp.einsum(
        "alsmjd,amlsjc->ldc", rows_all[:, :, :, :1], late_all, preferred_element_type=jnp.float32
    )
    return (grad_inputs, grad_w / divisor)


def solution(mesh):
    in_specs = (
        P("section", "dp", None, None),
        P("section", None, None),
        P("section", "dp", None, None),
        P("dp", None, None),
    )
    out_specs = (P("section", "dp", None, None), P("section", "dp", None))
    return jax.shard_map(shards, mesh=mesh, in_specs=in_specs, out_specs=out_specs, check_vma=False)
```

```python
import functools

import jax
import jax.numpy as jnp
from jax import lax
from jax.experimental import pallas as pl
from jax.experimental.pallas import tpu as pltpu
from jax.sharding import PartitionSpec as P

MICRO = 4


def shortened(value):
    return jax.tree.map(lambda a: a.astype(jnp.bfloat16) if a.dtype == jnp.float32 else a, value)


def passed_along(block, axis, distance):
    devices = range(lax.axis_size(axis))
    route = [(i - distance, i) for i in devices if i - distance in devices]
    return lax.ppermute(block, axis, route)


def block_terms(inputs_b, in_b, out_b, rates, grads_b, carried, state_in, factor):
    length = inputs_b.shape[0]
    cumulative = jnp.cumsum(rates, axis=0)
    ending = cumulative[-1]
    locations = jnp.arange(length)
    lower_mask = (locations[:, None] >= locations[None, :])[:, :, None]
    spread = jnp.where(lower_mask, cumulative[:, None, :] - cumulative[None, :, :], 0.0)
    decays = jnp.where(lower_mask, jnp.exp(spread), 0.0)
    tail_decay = jnp.exp(ending[None, :] - cumulative)
    leading = jnp.exp(cumulative)
    scores = jnp.dot(out_b, in_b.T, preferred_element_type=jnp.float32)
    weighted = (factor * decays * scores[:, :, None]).astype(jnp.bfloat16)
    carried_b = carried.astype(jnp.bfloat16)
    state_b = state_in.astype(jnp.bfloat16)
    grad_feats = jnp.einsum("kjh,khp->jhp", weighted, grads_b, preferred_element_type=jnp.float32)
    grad_feats = grad_feats + tail_decay[:, :, None] * jnp.einsum(
        "hpn,jn->jhp", carried_b, in_b, preferred_element_type=jnp.float32
    )
    pair_dots = jnp.einsum("khp,jhp->kjh", grads_b, inputs_b, preferred_element_type=jnp.float32)
    mixing = jnp.sum(decays * pair_dots, axis=2).astype(jnp.bfloat16)
    tail_inputs = (tail_decay[:, :, None] * inputs_b.astype(jnp.float32)).astype(jnp.bfloat16)
    lead_grads = (leading[:, :, None] * grads_b.astype(jnp.float32)).astype(jnp.bfloat16)
    grad_inmap = factor * jnp.dot(mixing.T, out_b, preferred_element_type=jnp.float32)
    grad_inmap = grad_inmap + jnp.einsum(
        "jhp,hpn->jn", tail_inputs, carried_b, preferred_element_type=jnp.float32
    )
    grad_outmap = factor * (
        jnp.dot(mixing, in_b, preferred_element_type=jnp.float32)
        + jnp.einsum("ihp,hpn->in", lead_grads, state_b, preferred_element_type=jnp.float32)
    )
    carry_out = factor * jnp.einsum(
        "khp,kn->hpn", lead_grads, out_b, preferred_element_type=jnp.float32
    )
    carry_out = carry_out + jnp.exp(ending)[:, None, None] * carried
    return (grad_feats, grad_inmap, grad_outmap, carry_out)


def block_end(inputs_b, in_b, rates, state_in):
    cumulative = jnp.cumsum(rates, axis=0)
    ending = cumulative[-1]
    tail_decay = jnp.exp(ending[None, :] - cumulative)
    tail_inputs = (tail_decay[:, :, None] * inputs_b.astype(jnp.float32)).astype(jnp.bfloat16)
    fresh = jnp.einsum("jhp,jn->hpn", tail_inputs, in_b, preferred_element_type=jnp.float32)
    return jnp.exp(ending)[:, None, None] * state_in + fresh


def split_block(inputs_c, map_block, head_count):
    length, features = inputs_c.shape
    state_size = map_block.shape[1] // 2
    inputs_b = inputs_c.reshape(length, head_count, features // head_count)
    in_b = map_block[:, :state_size]
    out_b = map_block[:, state_size:]
    return (inputs_b, in_b, out_b)


def block_back(inputs_c, map_block, rates, grads_c, carried, state_in, weights):
    length, features = inputs_c.shape
    head_count = rates.shape[1]
    factor = 0.25 / (map_block.shape[1] // 2)
    inputs_b, in_b, out_b = split_block(inputs_c, map_block, head_count)
    grads_b = grads_c.reshape(length, head_count, features // head_count)
    grad_feats, grad_inmap, grad_outmap, carry_out = block_terms(
        inputs_b, in_b, out_b, rates, grads_b, carried, state_in, factor
    )
    grad_bc = jnp.concatenate([grad_inmap, grad_outmap], axis=1).astype(jnp.bfloat16)
    back_proj = lax.dot_general(
        grad_bc, weights, (((1,), (1,)), ((), ())), preferred_element_type=jnp.float32
    )
    summed = grads_c.astype(jnp.float32) + grad_feats.reshape(length, features) + back_proj
    return (summed.astype(jnp.bfloat16), carry_out, grad_bc)


def layer_starts(inputs_s, bc_s, rates_s):
    head_count = rates_s.shape[1]
    features = inputs_s.shape[1]
    state_size = bc_s.shape[1] // 2
    block_len = inputs_s.shape[0] // MICRO
    state_now = jnp.zeros((head_count, features // head_count, state_size), jnp.float32)
    saved = []
    for block_no in range(MICRO):
        lo_row = block_no * block_len
        inputs_b, in_b, out_b = split_block(
            inputs_s[lo_row : lo_row + block_len], bc_s[lo_row : lo_row + block_len], head_count
        )
        saved.append(state_now)
        state_now = block_end(inputs_b, in_b, rates_s[lo_row : lo_row + block_len], state_now)
    return jnp.stack(saved)


def block_consts(inputs_b, in_b, out_b, rates, factor):
    length = inputs_b.shape[0]
    cumulative = jnp.cumsum(rates, axis=0)
    ending = cumulative[-1]
    locations = jnp.arange(length)
    lower_mask = (locations[:, None] >= locations[None, :])[:, :, None]
    spread = jnp.where(lower_mask, cumulative[:, None, :] - cumulative[None, :, :], 0.0)
    decays = jnp.where(lower_mask, jnp.exp(spread), 0.0)
    tail_decay = jnp.exp(ending[None, :] - cumulative)
    leading = jnp.exp(cumulative)
    scores = jnp.dot(out_b, in_b.T, preferred_element_type=jnp.float32)
    cum_t = cumulative.T
    upper = (locations[:, None] <= locations[None, :])[None]
    spread_t = jnp.where(upper, cum_t[:, None, :] - cum_t[:, :, None], 0.0)
    decays_t = jnp.where(upper, jnp.exp(spread_t), 0.0)
    scores_t = jnp.dot(in_b, out_b.T, preferred_element_type=jnp.float32)
    weighted = (factor * decays_t * scores_t[None]).astype(jnp.bfloat16)
    return dict(
        decays=decays,
        tail=tail_decay,
        lead=leading,
        weighted=weighted,
        ending=jnp.exp(ending),
    )


def step_kernel(
    step_ref, tab_ref, wt_ref, dec_ref, inc_ref, top_ref, x_ref, b_ref, c_ref, tail_ref, lead_ref, xt_ref,
    sb_ref, r_ref, end_ref, w_ref, gs_ref, ms_ref, out_ref, rnew_ref, dbc_ref, gstore_ref, mstore_ref,
    v_ref, gx_ref, tail_buf, lead_buf, xt_buf, sb_buf, r_buf, w_buf, sems, *, factor, width,
    level_pos, levels, level_no, seq_no, need_carry
):
    base = (step_ref[0] * levels + level_pos) * 3
    blk = tab_ref[base]
    fetches = [
        pltpu.make_async_copy(r_ref.at[level_no, seq_no], r_buf, sems.at[0]),
        pltpu.make_async_copy(tail_ref.at[blk, level_no, seq_no], tail_buf, sems.at[1]),
        pltpu.make_async_copy(xt_ref.at[blk, level_no, seq_no], xt_buf, sems.at[2]),
        pltpu.make_async_copy(lead_ref.at[blk, level_no, seq_no], lead_buf, sems.at[3]),
        pltpu.make_async_copy(sb_ref.at[blk, level_no, seq_no], sb_buf, sems.at[4]),
        pltpu.make_async_copy(w_ref.at[level_no], w_buf, sems.at[5]),
    ]
    for fetch in fetches:
        fetch.start()
    f32 = jnp.float32
    bf16 = jnp.bfloat16
    length, features = v_ref.shape
    lanes = 128
    per_pair = lanes // width
    nt = (((1,), (1,)), ((), ()))
    tn = (((0,), (0,)), ((), ()))
    v_ref[...] = jnp.where(tab_ref[base + 1] > 0, top_ref[...], inc_ref[...])
    in_map = b_ref[...]
    out_map = c_ref[...]
    lane_id = lax.broadcasted_iota(jnp.int32, (length, lanes), 1)
    masks = [(lane_id >= e * width) & (lane_id < (e + 1) * width) for e in range(per_pair)]
    mix_acc = jnp.zeros((per_pair * length, length), f32)
    for q in range(features // lanes):
        cols = slice(q * lanes, (q + 1) * lanes)
        v_q = v_ref[:, cols]
        x_q = x_ref[:, cols]
        stacked = jnp.concatenate([jnp.where(m, v_q, jnp.zeros_like(v_q)) for m in masks], axis=0)
        gx_q = jnp.dot(
            wt_ref[per_pair * q], stacked[0:length], preferred_element_type=f32
        )
        for e in range(1, per_pair):
            gx_q = gx_q + jnp.dot(
                wt_ref[per_pair * q + e],
                stacked[e * length:(e + 1) * length],
                preferred_element_type=f32,
            )
        gx_ref[:, cols] = gx_q
        pair_dots = lax.dot_general(stacked, x_q, nt, preferred_element_type=f32)
        mix_acc = mix_acc + dec_ref[q] * pair_dots
    mixing = mix_acc[0:length]
    for e in range(1, per_pair):
        mixing = mixing + mix_acc[e * length:(e + 1) * length]
    mixing = mixing.astype(bf16)
    fetches[0].wait()
    fetches[1].wait()
    rb_t = r_buf[...].astype(bf16)
    rbb = jnp.dot(in_map, rb_t, preferred_element_type=f32)
    gx_ref[...] = gx_ref[...] + tail_buf[...] * rbb
    v = v_ref[...]
    fetches[2].wait()
    grad_inmap = factor * lax.dot_general(mixing, out_map, tn, preferred_element_type=f32)
    grad_inmap = grad_inmap + lax.dot_general(xt_buf[...], rb_t, nt, preferred_element_type=f32)
    fetches[3].wait()
    fetches[4].wait()
    lead_grads = (lead_buf[...] * v.astype(f32)).astype(bf16)
    grad_outmap = factor * (
        jnp.dot(mixing, in_map, preferred_element_type=f32)
        + lax.dot_general(lead_grads, sb_buf[...], nt, preferred_element_type=f32)
    )
    if need_carry:
        carry = factor * lax.dot_general(out_map, lead_grads, tn, preferred_element_type=f32)
    if need_carry:
        rnew_ref[...] = carry + end_ref[...] * r_buf[...]
    grad_bc = jnp.concatenate([grad_inmap, grad_outmap], axis=1).astype(bf16)
    dbc_ref[...] = grad_bc
    mstore_ref[...] = jnp.where(tab_ref[base + 2] > 0, grad_bc, ms_ref[...])
    fetches[5].wait()
    back = lax.dot_general(grad_bc, w_buf[...], nt, preferred_element_type=f32)
    summed = (v.astype(f32) + gx_ref[...] + back).astype(out_ref.dtype)
    out_ref[...] = summed
    gstore_ref[...] = jnp.where(tab_ref[base + 2] > 0, summed, gs_ref[...])


def fused_step(step_arr, table, level_pos, levels, per_block, incoming, top_blk, carried, w_bc, grad_store, map_store, level_no, seq_no, factor, width, need_carry=True):
    wt2, dec2, x_flat, in_blk, out_blk, tail_full, lead_full, xt_full, states_t, end_row = per_block
    length, features = incoming.shape[1:]
    state_size = in_blk.shape[-1]

    def lead_block(a):
        shape = (None, None, None) + a.shape[3:]
        tail = (0,) * (a.ndim - 3)
        return pl.BlockSpec(shape, lambda i, c, t: (t[(c[0] * levels + level_pos) * 3], level_no, seq_no) + tail)

    in_specs = [lead_block(a) for a in (wt2, dec2)]
    in_specs.append(pl.BlockSpec((None, length, features), lambda i, c, t: (seq_no, 0, 0)))
    in_specs.append(pl.BlockSpec((None, None, length, features), lambda i, c, t: (t[(c[0] * levels + level_pos) * 3], seq_no, 0, 0)))
    in_hbm = pl.BlockSpec(memory_space=pl.ANY)
    in_specs += [lead_block(a) for a in (x_flat, in_blk, out_blk)]
    in_specs += [in_hbm] * 5
    in_specs.append(lead_block(end_row))
    in_specs.append(in_hbm)
    store_g = pl.BlockSpec((None, None, None, length, features), lambda i, c, t: (t[(c[0] * levels + level_pos) * 3], level_no, seq_no, 0, 0))
    store_m = pl.BlockSpec((None, None, None, length, 2 * state_size), lambda i, c, t: (t[(c[0] * levels + level_pos) * 3], level_no, seq_no, 0, 0))
    in_specs += [store_g, store_m]
    out_specs = (
        pl.BlockSpec((length, features), lambda i, c, t: (0, 0)),
        pl.BlockSpec((None, None) + carried.shape[2:], lambda i, c, t: (level_no, seq_no, 0, 0)),
        pl.BlockSpec((length, 2 * state_size), lambda i, c, t: (0, 0)),
        store_g,
        store_m,
    )
    flops = 2 * length * features * (6 * state_size + 4 * length)
    moved = 2 * (4 * features * state_size * 2 + 6 * length * features) + 4 * 4 * length * features
    return pl.pallas_call(
        functools.partial(
            step_kernel, factor=factor, width=width, level_pos=level_pos, levels=levels,
            level_no=level_no, seq_no=seq_no, need_carry=need_carry,
        ),
        out_shape=(
            jax.ShapeDtypeStruct((length, features), jnp.bfloat16),
            jax.ShapeDtypeStruct(carried.shape, jnp.float32),
            jax.ShapeDtypeStruct((length, 2 * state_size), jnp.bfloat16),
            jax.ShapeDtypeStruct(grad_store.shape, grad_store.dtype),
            jax.ShapeDtypeStruct(map_store.shape, map_store.dtype),
        ),
        grid_spec=pltpu.PrefetchScalarGridSpec(
            num_scalar_prefetch=2,
            grid=(1,),
            in_specs=in_specs,
            out_specs=out_specs,
            scratch_shapes=[
                pltpu.VMEM((length, features), jnp.bfloat16),
                pltpu.VMEM((length, features), jnp.float32),
                pltpu.VMEM((length, features), jnp.float32),
                pltpu.VMEM((length, features), jnp.float32),
                pltpu.VMEM((length, features), jnp.bfloat16),
                pltpu.VMEM(states_t.shape[3:], states_t.dtype),
                pltpu.VMEM(carried.shape[2:], jnp.float32),
                pltpu.VMEM(w_bc.shape[1:], w_bc.dtype),
                pltpu.SemaphoreType.DMA((6,)),
            ],
        ),
        input_output_aliases={13: 1, 16: 3, 17: 4},
        cost_estimate=pl.CostEstimate(flops=flops, bytes_accessed=moved, transcendentals=0),
    )(step_arr, table, wt2, dec2, incoming, top_blk, x_flat, in_blk, out_blk, tail_full, lead_full, xt_full, states_t, carried, end_row, w_bc, grad_store, map_store)


def shards(layer_inputs, w_bc, log_decay, top_grad):
    sections = lax.axis_size("section")
    section_id = lax.axis_index("section")
    lay_dev, seq_dev, tok_len, features = layer_inputs.shape
    head_count = log_decay.shape[-1]
    block_len = tok_len // MICRO
    state_size = w_bc.shape[-1] // 2
    factor = 0.25 / state_size
    bc_all = jnp.einsum(
        "lstd,ldc->lstc", layer_inputs, w_bc, preferred_element_type=jnp.float32
    ).astype(jnp.bfloat16)

    def blocked(a):
        split = a.reshape(a.shape[:2] + (MICRO, block_len) + a.shape[3:])
        return jnp.moveaxis(split, 2, 0)

    x_blk = blocked(layer_inputs).reshape(
        (MICRO, lay_dev, seq_dev, block_len, head_count, features // head_count)
    )
    bc_blk = blocked(bc_all)
    in_blk = bc_blk[..., :state_size]
    out_blk = bc_blk[..., state_size:]
    rates_blk = blocked(log_decay)
    consts_fn = jax.vmap(jax.vmap(jax.vmap(lambda x, b, c, r: block_consts(x, b, c, r, factor))))
    consts = consts_fn(x_blk, in_blk, out_blk, rates_blk)
    width = features // head_count
    lead_dims = consts["tail"].shape[:3]
    pairs = head_count * width // 128
    per_pair = 128 // width
    wt2 = consts["weighted"]
    dec2 = jnp.moveaxis(consts["decays"], -1, -3).reshape(
        lead_dims + (pairs, per_pair * block_len, block_len)
    )
    spread_heads = (
        jnp.arange(features)[None, :] // width == jnp.arange(head_count)[:, None]
    ).astype(jnp.float32)

    def per_lane(a):
        return jnp.einsum(
            "...h,hd->...d", a, spread_heads, precision=lax.Precision.HIGHEST,
            preferred_element_type=jnp.float32,
        )

    tail_full = per_lane(consts["tail"])
    lead_full = per_lane(consts["lead"])
    x_flat = x_blk.reshape(lead_dims + (block_len, features))
    xt_full = (tail_full * x_flat.astype(jnp.float32)).astype(jnp.bfloat16)
    end_row = per_lane(consts["ending"])[..., None, :]
    fresh_t = jnp.einsum(
        "mlsnj,mlsjd->mlsnd",
        jnp.swapaxes(in_blk[: MICRO - 1], -1, -2),
        xt_full[: MICRO - 1],
        preferred_element_type=jnp.float32,
    )
    state_now = jnp.zeros(fresh_t.shape[1:], jnp.float32)
    saved = [state_now.astype(jnp.bfloat16)[None]]
    for block_no in range(MICRO - 1):
        state_now = end_row[block_no] * state_now + fresh_t[block_no]
        saved.append(state_now.astype(jnp.bfloat16)[None])
    states_t = jnp.concatenate(saved, axis=0)
    per_block = (wt2, dec2, x_flat, in_blk, out_blk, tail_full, lead_full, xt_full, states_t, end_row)
    per_block = lax.optimization_barrier(per_block)

    top_blk = jnp.moveaxis(
        top_grad.reshape((seq_dev, MICRO, block_len, features)), 1, 0
    )
    is_top = section_id == sections - 1

    steps = MICRO + sections - 1
    counters = jnp.arange(steps, dtype=jnp.int32)[:, None]
    offsets = counters - (sections - 1 - section_id)
    valid_tab = ((offsets >= 0) & (offsets < MICRO)).astype(jnp.int32)
    block_tab = jnp.clip(MICRO - 1 - offsets, 0, MICRO - 1).astype(jnp.int32)
    top_tab = (jnp.arange(lay_dev)[None, ::-1] == lay_dev - 1) & is_top
    table = jnp.stack(
        jnp.broadcast_arrays(block_tab, top_tab.astype(jnp.int32), valid_tab), axis=-1
    ).reshape(-1).astype(jnp.int32)

    def advance(counter, loop_state, send=True):
        incoming, carried, grad_store, map_store = loop_state
        step_arr = jnp.reshape(counter, (1,)).astype(jnp.int32)
        for level_pos, level_no in enumerate(reversed(range(lay_dev))):
            level_out = []
            for seq_no in range(seq_dev):
                level_grads, carried, grad_bc, grad_store, map_store = fused_step(
                    step_arr, table, level_pos, lay_dev, per_block, incoming, top_blk, carried,
                    w_bc, grad_store, map_store, level_no, seq_no, factor, width, send,
                )
                level_out.append(level_grads)
            incoming = jnp.stack(level_out)
        if send:
            incoming = passed_along(incoming, "section", -1)
        return (incoming, carried, grad_store, map_store)

    initial = (
        jnp.zeros((seq_dev, block_len, features), jnp.bfloat16),
        jnp.zeros(states_t.shape[1:], jnp.float32),
        jnp.zeros((MICRO, lay_dev, seq_dev, block_len, features), jnp.bfloat16),
        bc_all.reshape((MICRO, lay_dev, seq_dev, block_len, 2 * state_size)),
    )
    final_state = lax.fori_loop(0, steps - 1, advance, initial)
    final_state = advance(steps - 1, final_state, send=False)
    grad_store = final_state[2]
    map_store = final_state[3]

    grad_inputs = jnp.moveaxis(grad_store, 0, 2).reshape(layer_inputs.shape)
    map_store = jnp.moveaxis(map_store, 0, 2).reshape(bc_all.shape)
    ways = lax.axis_size("dp")
    divisor = ways * seq_dev
    rows_here = layer_inputs.reshape(lay_dev, seq_dev * tok_len, ways, features // ways)
    rows_here = jnp.transpose(rows_here, (2, 0, 1, 3))
    rows_all = lax.all_to_all(rows_here, "dp", 0, 0, tiled=True)
    maps_here = map_store.reshape(1, lay_dev, seq_dev * tok_len, map_store.shape[-1])
    maps_all = lax.all_gather(maps_here, "dp", axis=0, tiled=True)
    grad_w = jnp.einsum(
        "glrd,glrc->ldc", rows_all, maps_all, preferred_element_type=jnp.float32
    ) / divisor
    return (grad_inputs, grad_w)


def solution(mesh):
    in_specs = (
        P("section", "dp", None, None),
        P("section", None, None),
        P("section", "dp", None, None),
        P("dp", None, None),
    )
    out_specs = (P("section", "dp", None, None), P("section", "dp", None))
    return jax.shard_map(shards, mesh=mesh, in_specs=in_specs, out_specs=out_specs, check_vma=False)
```

```python
import functools

import jax
import jax.numpy as jnp
from jax import lax
from jax.experimental import pallas as pl
from jax.experimental.pallas import tpu as pltpu
from jax.sharding import PartitionSpec as P

MICRO = 4


def shortened(value):
    return jax.tree.map(lambda a: a.astype(jnp.bfloat16) if a.dtype == jnp.float32 else a, value)


def passed_along(block, axis, distance):
    devices = range(lax.axis_size(axis))
    route = [(i - distance, i) for i in devices if i - distance in devices]
    return lax.ppermute(block, axis, route)


def block_terms(inputs_b, in_b, out_b, rates, grads_b, carried, state_in, factor):
    length = inputs_b.shape[0]
    cumulative = jnp.cumsum(rates, axis=0)
    ending = cumulative[-1]
    locations = jnp.arange(length)
    lower_mask = (locations[:, None] >= locations[None, :])[:, :, None]
    spread = jnp.where(lower_mask, cumulative[:, None, :] - cumulative[None, :, :], 0.0)
    decays = jnp.where(lower_mask, jnp.exp(spread), 0.0)
    tail_decay = jnp.exp(ending[None, :] - cumulative)
    leading = jnp.exp(cumulative)
    scores = jnp.dot(out_b, in_b.T, preferred_element_type=jnp.float32)
    weighted = (factor * decays * scores[:, :, None]).astype(jnp.bfloat16)
    carried_b = carried.astype(jnp.bfloat16)
    state_b = state_in.astype(jnp.bfloat16)
    grad_feats = jnp.einsum("kjh,khp->jhp", weighted, grads_b, preferred_element_type=jnp.float32)
    grad_feats = grad_feats + tail_decay[:, :, None] * jnp.einsum(
        "hpn,jn->jhp", carried_b, in_b, preferred_element_type=jnp.float32
    )
    pair_dots = jnp.einsum("khp,jhp->kjh", grads_b, inputs_b, preferred_element_type=jnp.float32)
    mixing = jnp.sum(decays * pair_dots, axis=2).astype(jnp.bfloat16)
    tail_inputs = (tail_decay[:, :, None] * inputs_b.astype(jnp.float32)).astype(jnp.bfloat16)
    lead_grads = (leading[:, :, None] * grads_b.astype(jnp.float32)).astype(jnp.bfloat16)
    grad_inmap = factor * jnp.dot(mixing.T, out_b, preferred_element_type=jnp.float32)
    grad_inmap = grad_inmap + jnp.einsum(
        "jhp,hpn->jn", tail_inputs, carried_b, preferred_element_type=jnp.float32
    )
    grad_outmap = factor * (
        jnp.dot(mixing, in_b, preferred_element_type=jnp.float32)
        + jnp.einsum("ihp,hpn->in", lead_grads, state_b, preferred_element_type=jnp.float32)
    )
    carry_out = factor * jnp.einsum(
        "khp,kn->hpn", lead_grads, out_b, preferred_element_type=jnp.float32
    )
    carry_out = carry_out + jnp.exp(ending)[:, None, None] * carried
    return (grad_feats, grad_inmap, grad_outmap, carry_out)


def block_end(inputs_b, in_b, rates, state_in):
    cumulative = jnp.cumsum(rates, axis=0)
    ending = cumulative[-1]
    tail_decay = jnp.exp(ending[None, :] - cumulative)
    tail_inputs = (tail_decay[:, :, None] * inputs_b.astype(jnp.float32)).astype(jnp.bfloat16)
    fresh = jnp.einsum("jhp,jn->hpn", tail_inputs, in_b, preferred_element_type=jnp.float32)
    return jnp.exp(ending)[:, None, None] * state_in + fresh


def split_block(inputs_c, map_block, head_count):
    length, features = inputs_c.shape
    state_size = map_block.shape[1] // 2
    inputs_b = inputs_c.reshape(length, head_count, features // head_count)
    in_b = map_block[:, :state_size]
    out_b = map_block[:, state_size:]
    return (inputs_b, in_b, out_b)


def block_back(inputs_c, map_block, rates, grads_c, carried, state_in, weights):
    length, features = inputs_c.shape
    head_count = rates.shape[1]
    factor = 0.25 / (map_block.shape[1] // 2)
    inputs_b, in_b, out_b = split_block(inputs_c, map_block, head_count)
    grads_b = grads_c.reshape(length, head_count, features // head_count)
    grad_feats, grad_inmap, grad_outmap, carry_out = block_terms(
        inputs_b, in_b, out_b, rates, grads_b, carried, state_in, factor
    )
    grad_bc = jnp.concatenate([grad_inmap, grad_outmap], axis=1).astype(jnp.bfloat16)
    back_proj = lax.dot_general(
        grad_bc, weights, (((1,), (1,)), ((), ())), preferred_element_type=jnp.float32
    )
    summed = grads_c.astype(jnp.float32) + grad_feats.reshape(length, features) + back_proj
    return (summed.astype(jnp.bfloat16), carry_out, grad_bc)


def layer_starts(inputs_s, bc_s, rates_s):
    head_count = rates_s.shape[1]
    features = inputs_s.shape[1]
    state_size = bc_s.shape[1] // 2
    block_len = inputs_s.shape[0] // MICRO
    state_now = jnp.zeros((head_count, features // head_count, state_size), jnp.float32)
    saved = []
    for block_no in range(MICRO):
        lo_row = block_no * block_len
        inputs_b, in_b, out_b = split_block(
            inputs_s[lo_row : lo_row + block_len], bc_s[lo_row : lo_row + block_len], head_count
        )
        saved.append(state_now)
        state_now = block_end(inputs_b, in_b, rates_s[lo_row : lo_row + block_len], state_now)
    return jnp.stack(saved)


def block_consts(inputs_b, in_b, out_b, rates, factor):
    length = inputs_b.shape[0]
    cumulative = jnp.cumsum(rates, axis=0)
    ending = cumulative[-1]
    locations = jnp.arange(length)
    lower_mask = (locations[:, None] >= locations[None, :])[:, :, None]
    spread = jnp.where(lower_mask, cumulative[:, None, :] - cumulative[None, :, :], 0.0)
    decays = jnp.where(lower_mask, jnp.exp(spread), 0.0)
    tail_decay = jnp.exp(ending[None, :] - cumulative)
    leading = jnp.exp(cumulative)
    scores = jnp.dot(out_b, in_b.T, preferred_element_type=jnp.float32)
    cum_t = cumulative.T
    upper = (locations[:, None] <= locations[None, :])[None]
    spread_t = jnp.where(upper, cum_t[:, None, :] - cum_t[:, :, None], 0.0)
    decays_t = jnp.where(upper, jnp.exp(spread_t), 0.0)
    scores_t = jnp.dot(in_b, out_b.T, preferred_element_type=jnp.float32)
    weighted = (factor * decays_t * scores_t[None]).astype(jnp.bfloat16)
    return dict(
        decays=decays,
        tail=tail_decay,
        lead=leading,
        weighted=weighted,
        ending=jnp.exp(ending),
    )


def step_kernel(
    step_ref, tab_ref, wt_ref, dec_ref, inc_ref, top_ref, x_ref, b_ref, c_ref, tail_ref, lead_ref, xt_ref,
    sb_ref, r_ref, end_ref, w_ref, gs_ref, ms_ref, out_ref, rnew_ref, dbc_ref, gstore_ref, mstore_ref,
    v_ref, gx_ref, tail_buf, lead_buf, xt_buf, sb_buf, r_buf, w_buf, sems, wt_buf, dec_buf,
    head_sems, *, factor, width,
    level_pos, levels, level_no, seq_no
):
    base = (step_ref[0] * levels + level_pos) * 3
    blk = tab_ref[base]
    fetches = [
        pltpu.make_async_copy(r_ref.at[level_no, seq_no], r_buf, sems.at[0]),
        pltpu.make_async_copy(tail_ref.at[blk, level_no, seq_no], tail_buf, sems.at[1]),
        pltpu.make_async_copy(xt_ref.at[blk, level_no, seq_no], xt_buf, sems.at[2]),
        pltpu.make_async_copy(lead_ref.at[blk, level_no, seq_no], lead_buf, sems.at[3]),
        pltpu.make_async_copy(sb_ref.at[blk, level_no, seq_no], sb_buf, sems.at[4]),
        pltpu.make_async_copy(w_ref.at[level_no], w_buf, sems.at[5]),
    ]
    pairs = dec_buf.shape[0]
    chunks = 4 if pairs % 4 == 0 else 1
    per_chunk = pairs // chunks
    heads_chunk = per_chunk * (wt_buf.shape[0] // pairs)
    head_fetches = []
    for part in range(chunks):
        head_fetches.append((
            pltpu.make_async_copy(
                wt_ref.at[blk, level_no, seq_no, pl.ds(part * heads_chunk, heads_chunk)],
                wt_buf.at[pl.ds(part * heads_chunk, heads_chunk)],
                head_sems.at[2 * part],
            ),
            pltpu.make_async_copy(
                dec_ref.at[blk, level_no, seq_no, pl.ds(part * per_chunk, per_chunk)],
                dec_buf.at[pl.ds(part * per_chunk, per_chunk)],
                head_sems.at[2 * part + 1],
            ),
        ))
    for pair_fetch in head_fetches:
        for fetch in pair_fetch:
            fetch.start()
    for fetch in fetches:
        fetch.start()
    f32 = jnp.float32
    bf16 = jnp.bfloat16
    length, features = v_ref.shape
    lanes = 128
    per_pair = lanes // width
    nt = (((1,), (1,)), ((), ()))
    tn = (((0,), (0,)), ((), ()))
    v_ref[...] = jnp.where(tab_ref[base + 1] > 0, top_ref[...], inc_ref[...])
    in_map = b_ref[...]
    out_map = c_ref[...]
    lane_id = lax.broadcasted_iota(jnp.int32, (length, lanes), 1)
    masks = [(lane_id >= e * width) & (lane_id < (e + 1) * width) for e in range(per_pair)]
    mix_acc = jnp.zeros((per_pair * length, length), f32)
    for q in range(features // lanes):
        cols = slice(q * lanes, (q + 1) * lanes)
        if q % per_chunk == 0:
            for fetch in head_fetches[q // per_chunk]:
                fetch.wait()
        v_q = v_ref[:, cols]
        x_q = x_ref[:, cols]
        stacked = jnp.concatenate([jnp.where(m, v_q, jnp.zeros_like(v_q)) for m in masks], axis=0)
        gx_q = jnp.dot(
            wt_buf[per_pair * q], stacked[0:length], preferred_element_type=f32
        )
        for e in range(1, per_pair):
            gx_q = gx_q + jnp.dot(
                wt_buf[per_pair * q + e],
                stacked[e * length:(e + 1) * length],
                preferred_element_type=f32,
            )
        gx_ref[:, cols] = gx_q
        pair_dots = lax.dot_general(stacked, x_q, nt, preferred_element_type=f32)
        mix_acc = mix_acc + dec_buf[q] * pair_dots
    mixing = mix_acc[0:length]
    for e in range(1, per_pair):
        mixing = mixing + mix_acc[e * length:(e + 1) * length]
    mixing = mixing.astype(bf16)
    fetches[0].wait()
    fetches[1].wait()
    rb_t = r_buf[...].astype(bf16)
    rbb = jnp.dot(in_map, rb_t, preferred_element_type=f32)
    gx_ref[...] = gx_ref[...] + tail_buf[...] * rbb
    v = v_ref[...]
    fetches[2].wait()
    grad_inmap = factor * lax.dot_general(mixing, out_map, tn, preferred_element_type=f32)
    grad_inmap = grad_inmap + lax.dot_general(xt_buf[...], rb_t, nt, preferred_element_type=f32)
    fetches[3].wait()
    fetches[4].wait()
    lead_grads = (lead_buf[...] * v.astype(f32)).astype(bf16)
    grad_outmap = factor * (
        jnp.dot(mixing, in_map, preferred_element_type=f32)
        + lax.dot_general(lead_grads, sb_buf[...], nt, preferred_element_type=f32)
    )
    carry = factor * lax.dot_general(out_map, lead_grads, tn, preferred_element_type=f32)
    rnew_ref[...] = carry + end_ref[...] * r_buf[...]
    grad_bc = jnp.concatenate([grad_inmap, grad_outmap], axis=1).astype(bf16)
    dbc_ref[...] = grad_bc
    mstore_ref[...] = jnp.where(tab_ref[base + 2] > 0, grad_bc, ms_ref[...])
    fetches[5].wait()
    back = lax.dot_general(grad_bc, w_buf[...], nt, preferred_element_type=f32)
    summed = (v.astype(f32) + gx_ref[...] + back).astype(out_ref.dtype)
    out_ref[...] = summed
    gstore_ref[...] = jnp.where(tab_ref[base + 2] > 0, summed, gs_ref[...])


def fused_step(step_arr, table, level_pos, levels, per_block, incoming, top_blk, carried, w_bc, grad_store, map_store, level_no, seq_no, factor, width):
    wt2, dec2, x_flat, in_blk, out_blk, tail_full, lead_full, xt_full, states_t, end_row = per_block
    length, features = incoming.shape[1:]
    state_size = in_blk.shape[-1]

    def lead_block(a):
        shape = (None, None, None) + a.shape[3:]
        tail = (0,) * (a.ndim - 3)
        return pl.BlockSpec(shape, lambda i, c, t: (t[(c[0] * levels + level_pos) * 3], level_no, seq_no) + tail)

    in_specs = [pl.BlockSpec(memory_space=pl.ANY)] * 2
    in_specs.append(pl.BlockSpec((None, length, features), lambda i, c, t: (seq_no, 0, 0)))
    in_specs.append(pl.BlockSpec((None, None, length, features), lambda i, c, t: (t[(c[0] * levels + level_pos) * 3], seq_no, 0, 0)))
    in_hbm = pl.BlockSpec(memory_space=pl.ANY)
    in_specs += [lead_block(a) for a in (x_flat, in_blk, out_blk)]
    in_specs += [in_hbm] * 5
    in_specs.append(lead_block(end_row))
    in_specs.append(in_hbm)
    store_g = pl.BlockSpec((None, None, None, length, features), lambda i, c, t: (t[(c[0] * levels + level_pos) * 3], level_no, seq_no, 0, 0))
    store_m = pl.BlockSpec((None, None, None, length, 2 * state_size), lambda i, c, t: (t[(c[0] * levels + level_pos) * 3], level_no, seq_no, 0, 0))
    in_specs += [store_g, store_m]
    out_specs = (
        pl.BlockSpec((length, features), lambda i, c, t: (0, 0)),
        pl.BlockSpec((None, None) + carried.shape[2:], lambda i, c, t: (level_no, seq_no, 0, 0)),
        pl.BlockSpec((length, 2 * state_size), lambda i, c, t: (0, 0)),
        store_g,
        store_m,
    )
    flops = 2 * length * features * (6 * state_size + 4 * length)
    moved = 2 * (4 * features * state_size * 2 + 6 * length * features) + 4 * 4 * length * features
    return pl.pallas_call(
        functools.partial(
            step_kernel, factor=factor, width=width, level_pos=level_pos, levels=levels,
            level_no=level_no, seq_no=seq_no,
        ),
        out_shape=(
            jax.ShapeDtypeStruct((length, features), jnp.bfloat16),
            jax.ShapeDtypeStruct(carried.shape, jnp.float32),
            jax.ShapeDtypeStruct((length, 2 * state_size), jnp.bfloat16),
            jax.ShapeDtypeStruct(grad_store.shape, grad_store.dtype),
            jax.ShapeDtypeStruct(map_store.shape, map_store.dtype),
        ),
        grid_spec=pltpu.PrefetchScalarGridSpec(
            num_scalar_prefetch=2,
            grid=(1,),
            in_specs=in_specs,
            out_specs=out_specs,
            scratch_shapes=[
                pltpu.VMEM((length, features), jnp.bfloat16),
                pltpu.VMEM((length, features), jnp.float32),
                pltpu.VMEM((length, features), jnp.float32),
                pltpu.VMEM((length, features), jnp.float32),
                pltpu.VMEM((length, features), jnp.bfloat16),
                pltpu.VMEM(states_t.shape[3:], states_t.dtype),
                pltpu.VMEM(carried.shape[2:], jnp.float32),
                pltpu.VMEM(w_bc.shape[1:], w_bc.dtype),
                pltpu.SemaphoreType.DMA((6,)),
                pltpu.VMEM(wt2.shape[3:], wt2.dtype),
                pltpu.VMEM(dec2.shape[3:], dec2.dtype),
                pltpu.SemaphoreType.DMA((8,)),
            ],
        ),
        input_output_aliases={13: 1, 16: 3, 17: 4},
        cost_estimate=pl.CostEstimate(flops=flops, bytes_accessed=moved, transcendentals=0),
    )(step_arr, table, wt2, dec2, incoming, top_blk, x_flat, in_blk, out_blk, tail_full, lead_full, xt_full, states_t, carried, end_row, w_bc, grad_store, map_store)


def shards(layer_inputs, w_bc, log_decay, top_grad):
    sections = lax.axis_size("section")
    section_id = lax.axis_index("section")
    lay_dev, seq_dev, tok_len, features = layer_inputs.shape
    head_count = log_decay.shape[-1]
    block_len = tok_len // MICRO
    state_size = w_bc.shape[-1] // 2
    factor = 0.25 / state_size
    bc_all = jnp.einsum(
        "lstd,ldc->lstc", layer_inputs, w_bc, preferred_element_type=jnp.float32
    ).astype(jnp.bfloat16)

    def blocked(a):
        split = a.reshape(a.shape[:2] + (MICRO, block_len) + a.shape[3:])
        return jnp.moveaxis(split, 2, 0)

    x_blk = blocked(layer_inputs).reshape(
        (MICRO, lay_dev, seq_dev, block_len, head_count, features // head_count)
    )
    bc_blk = blocked(bc_all)
    in_blk = bc_blk[..., :state_size]
    out_blk = bc_blk[..., state_size:]
    rates_blk = blocked(log_decay)
    consts_fn = jax.vmap(jax.vmap(jax.vmap(lambda x, b, c, r: block_consts(x, b, c, r, factor))))
    consts = consts_fn(x_blk, in_blk, out_blk, rates_blk)
    width = features // head_count
    lead_dims = consts["tail"].shape[:3]
    pairs = head_count * width // 128
    per_pair = 128 // width
    wt2 = consts["weighted"]
    dec2 = jnp.moveaxis(consts["decays"], -1, -3).reshape(
        lead_dims + (pairs, per_pair * block_len, block_len)
    )
    spread_heads = (
        jnp.arange(features)[None, :] // width == jnp.arange(head_count)[:, None]
    ).astype(jnp.float32)

    def per_lane(a):
        return jnp.einsum(
            "...h,hd->...d", a, spread_heads, precision=lax.Precision.HIGHEST,
            preferred_element_type=jnp.float32,
        )

    tail_full = per_lane(consts["tail"])
    lead_full = per_lane(consts["lead"])
    x_flat = x_blk.reshape(lead_dims + (block_len, features))
    xt_full = (tail_full * x_flat.astype(jnp.float32)).astype(jnp.bfloat16)
    end_row = per_lane(consts["ending"])[..., None, :]
    fresh_t = jnp.einsum(
        "mlsnj,mlsjd->mlsnd",
        jnp.swapaxes(in_blk[: MICRO - 1], -1, -2),
        xt_full[: MICRO - 1],
        preferred_element_type=jnp.float32,
    )
    state_now = jnp.zeros(fresh_t.shape[1:], jnp.float32)
    saved = [state_now.astype(jnp.bfloat16)[None]]
    for block_no in range(MICRO - 1):
        state_now = end_row[block_no] * state_now + fresh_t[block_no]
        saved.append(state_now.astype(jnp.bfloat16)[None])
    states_t = jnp.concatenate(saved, axis=0)
    per_block = (wt2, dec2, x_flat, in_blk, out_blk, tail_full, lead_full, xt_full, states_t, end_row)
    per_block = lax.optimization_barrier(per_block)

    top_blk = jnp.moveaxis(
        top_grad.reshape((seq_dev, MICRO, block_len, features)), 1, 0
    )
    is_top = section_id == sections - 1

    steps = MICRO + sections - 1
    counters = jnp.arange(steps, dtype=jnp.int32)[:, None]
    offsets = counters - (sections - 1 - section_id)
    valid_tab = ((offsets >= 0) & (offsets < MICRO)).astype(jnp.int32)
    block_tab = jnp.clip(MICRO - 1 - offsets, 0, MICRO - 1).astype(jnp.int32)
    top_tab = (jnp.arange(lay_dev)[None, ::-1] == lay_dev - 1) & is_top
    table = jnp.stack(
        jnp.broadcast_arrays(block_tab, top_tab.astype(jnp.int32), valid_tab), axis=-1
    ).reshape(-1).astype(jnp.int32)

    def advance(counter, loop_state, send=True):
        incoming, carried, grad_store, map_store = loop_state
        step_arr = jnp.reshape(counter, (1,)).astype(jnp.int32)
        for level_pos, level_no in enumerate(reversed(range(lay_dev))):
            level_out = []
            for seq_no in range(seq_dev):
                level_grads, carried, grad_bc, grad_store, map_store = fused_step(
                    step_arr, table, level_pos, lay_dev, per_block, incoming, top_blk, carried,
                    w_bc, grad_store, map_store, level_no, seq_no, factor, width,
                )
                level_out.append(level_grads)
            incoming = jnp.stack(level_out)
        if send:
            incoming = passed_along(incoming, "section", -1)
        return (incoming, carried, grad_store, map_store)

    initial = (
        jnp.zeros((seq_dev, block_len, features), jnp.bfloat16),
        jnp.zeros(states_t.shape[1:], jnp.float32),
        jnp.zeros((MICRO, lay_dev, seq_dev, block_len, features), jnp.bfloat16),
        jnp.zeros((MICRO, lay_dev, seq_dev, block_len, 2 * state_size), jnp.bfloat16),
    )
    final_state = lax.fori_loop(0, steps - 1, advance, initial)
    final_state = advance(steps - 1, final_state, send=False)
    grad_store = final_state[2]
    map_store = final_state[3]

    grad_inputs = jnp.moveaxis(grad_store, 0, 2).reshape(layer_inputs.shape)
    map_store = jnp.moveaxis(map_store, 0, 2).reshape(bc_all.shape)
    ways = lax.axis_size("dp")
    divisor = ways * seq_dev
    rows_here = layer_inputs.reshape(lay_dev, seq_dev * tok_len, ways, features // ways)
    rows_here = jnp.transpose(rows_here, (2, 0, 1, 3))
    rows_all = lax.all_to_all(rows_here, "dp", 0, 0, tiled=True)
    maps_here = map_store.reshape(1, lay_dev, seq_dev * tok_len, map_store.shape[-1])
    maps_all = lax.all_gather(maps_here, "dp", axis=0, tiled=True)
    grad_w = jnp.einsum(
        "glrd,glrc->ldc", rows_all, maps_all, preferred_element_type=jnp.float32
    ) / divisor
    return (grad_inputs, grad_w)


def solution(mesh):
    in_specs = (
        P("section", "dp", None, None),
        P("section", None, None),
        P("section", "dp", None, None),
        P("dp", None, None),
    )
    out_specs = (P("section", "dp", None, None), P("section", "dp", None))
    return jax.shard_map(shards, mesh=mesh, in_specs=in_specs, out_specs=out_specs, check_vma=False)
```

```python
import functools

import jax
import jax.numpy as jnp
from jax import lax
from jax.experimental import pallas as pl
from jax.experimental.pallas import tpu as pltpu
from jax.sharding import PartitionSpec as P

MICRO = 4


def shortened(value):
    return jax.tree.map(lambda a: a.astype(jnp.bfloat16) if a.dtype == jnp.float32 else a, value)


def passed_along(block, axis, distance):
    devices = range(lax.axis_size(axis))
    route = [(i - distance, i) for i in devices if i - distance in devices]
    return lax.ppermute(block, axis, route)


def block_terms(inputs_b, in_b, out_b, rates, grads_b, carried, state_in, factor):
    length = inputs_b.shape[0]
    cumulative = jnp.cumsum(rates, axis=0)
    ending = cumulative[-1]
    locations = jnp.arange(length)
    lower_mask = (locations[:, None] >= locations[None, :])[:, :, None]
    spread = jnp.where(lower_mask, cumulative[:, None, :] - cumulative[None, :, :], 0.0)
    decays = jnp.where(lower_mask, jnp.exp(spread), 0.0)
    tail_decay = jnp.exp(ending[None, :] - cumulative)
    leading = jnp.exp(cumulative)
    scores = jnp.dot(out_b, in_b.T, preferred_element_type=jnp.float32)
    weighted = (factor * decays * scores[:, :, None]).astype(jnp.bfloat16)
    carried_b = carried.astype(jnp.bfloat16)
    state_b = state_in.astype(jnp.bfloat16)
    grad_feats = jnp.einsum("kjh,khp->jhp", weighted, grads_b, preferred_element_type=jnp.float32)
    grad_feats = grad_feats + tail_decay[:, :, None] * jnp.einsum(
        "hpn,jn->jhp", carried_b, in_b, preferred_element_type=jnp.float32
    )
    pair_dots = jnp.einsum("khp,jhp->kjh", grads_b, inputs_b, preferred_element_type=jnp.float32)
    mixing = jnp.sum(decays * pair_dots, axis=2).astype(jnp.bfloat16)
    tail_inputs = (tail_decay[:, :, None] * inputs_b.astype(jnp.float32)).astype(jnp.bfloat16)
    lead_grads = (leading[:, :, None] * grads_b.astype(jnp.float32)).astype(jnp.bfloat16)
    grad_inmap = factor * jnp.dot(mixing.T, out_b, preferred_element_type=jnp.float32)
    grad_inmap = grad_inmap + jnp.einsum(
        "jhp,hpn->jn", tail_inputs, carried_b, preferred_element_type=jnp.float32
    )
    grad_outmap = factor * (
        jnp.dot(mixing, in_b, preferred_element_type=jnp.float32)
        + jnp.einsum("ihp,hpn->in", lead_grads, state_b, preferred_element_type=jnp.float32)
    )
    carry_out = factor * jnp.einsum(
        "khp,kn->hpn", lead_grads, out_b, preferred_element_type=jnp.float32
    )
    carry_out = carry_out + jnp.exp(ending)[:, None, None] * carried
    return (grad_feats, grad_inmap, grad_outmap, carry_out)


def block_end(inputs_b, in_b, rates, state_in):
    cumulative = jnp.cumsum(rates, axis=0)
    ending = cumulative[-1]
    tail_decay = jnp.exp(ending[None, :] - cumulative)
    tail_inputs = (tail_decay[:, :, None] * inputs_b.astype(jnp.float32)).astype(jnp.bfloat16)
    fresh = jnp.einsum("jhp,jn->hpn", tail_inputs, in_b, preferred_element_type=jnp.float32)
    return jnp.exp(ending)[:, None, None] * state_in + fresh


def split_block(inputs_c, map_block, head_count):
    length, features = inputs_c.shape
    state_size = map_block.shape[1] // 2
    inputs_b = inputs_c.reshape(length, head_count, features // head_count)
    in_b = map_block[:, :state_size]
    out_b = map_block[:, state_size:]
    return (inputs_b, in_b, out_b)


def block_back(inputs_c, map_block, rates, grads_c, carried, state_in, weights):
    length, features = inputs_c.shape
    head_count = rates.shape[1]
    factor = 0.25 / (map_block.shape[1] // 2)
    inputs_b, in_b, out_b = split_block(inputs_c, map_block, head_count)
    grads_b = grads_c.reshape(length, head_count, features // head_count)
    grad_feats, grad_inmap, grad_outmap, carry_out = block_terms(
        inputs_b, in_b, out_b, rates, grads_b, carried, state_in, factor
    )
    grad_bc = jnp.concatenate([grad_inmap, grad_outmap], axis=1).astype(jnp.bfloat16)
    back_proj = lax.dot_general(
        grad_bc, weights, (((1,), (1,)), ((), ())), preferred_element_type=jnp.float32
    )
    summed = grads_c.astype(jnp.float32) + grad_feats.reshape(length, features) + back_proj
    return (summed.astype(jnp.bfloat16), carry_out, grad_bc)


def layer_starts(inputs_s, bc_s, rates_s):
    head_count = rates_s.shape[1]
    features = inputs_s.shape[1]
    state_size = bc_s.shape[1] // 2
    block_len = inputs_s.shape[0] // MICRO
    state_now = jnp.zeros((head_count, features // head_count, state_size), jnp.float32)
    saved = []
    for block_no in range(MICRO):
        lo_row = block_no * block_len
        inputs_b, in_b, out_b = split_block(
            inputs_s[lo_row : lo_row + block_len], bc_s[lo_row : lo_row + block_len], head_count
        )
        saved.append(state_now)
        state_now = block_end(inputs_b, in_b, rates_s[lo_row : lo_row + block_len], state_now)
    return jnp.stack(saved)


def block_consts(inputs_b, in_b, out_b, rates, factor):
    length = inputs_b.shape[0]
    cumulative = jnp.cumsum(rates, axis=0)
    ending = cumulative[-1]
    locations = jnp.arange(length)
    lower_mask = (locations[:, None] >= locations[None, :])[:, :, None]
    spread = jnp.where(lower_mask, cumulative[:, None, :] - cumulative[None, :, :], 0.0)
    decays = jnp.where(lower_mask, jnp.exp(spread), 0.0)
    tail_decay = jnp.exp(ending[None, :] - cumulative)
    leading = jnp.exp(cumulative)
    scores = jnp.dot(out_b, in_b.T, preferred_element_type=jnp.float32)
    cum_t = cumulative.T
    upper = (locations[:, None] <= locations[None, :])[None]
    spread_t = jnp.where(upper, cum_t[:, None, :] - cum_t[:, :, None], 0.0)
    decays_t = jnp.where(upper, jnp.exp(spread_t), 0.0)
    scores_t = jnp.dot(in_b, out_b.T, preferred_element_type=jnp.float32)
    weighted = (factor * decays_t * scores_t[None]).astype(jnp.bfloat16)
    return dict(
        decays=decays,
        tail=tail_decay,
        lead=leading,
        weighted=weighted,
        ending=jnp.exp(ending),
    )


def step_kernel(
    step_ref, tab_ref, wt_ref, dec_ref, inc_ref, top_ref, x_ref, b_ref, c_ref, tail_ref, lead_ref, xt_ref,
    sb_ref, r_ref, end_ref, w_ref, gs_ref, ms_ref, out_ref, rnew_ref, dbc_ref, gstore_ref, mstore_ref,
    v_ref, gx_ref, *, factor, width, level_pos, levels
):
    base = (step_ref[0] * levels + level_pos) * 3
    f32 = jnp.float32
    bf16 = jnp.bfloat16
    length, features = v_ref.shape
    lanes = 128
    per_pair = lanes // width
    nt = (((1,), (1,)), ((), ()))
    tn = (((0,), (0,)), ((), ()))
    v_ref[...] = jnp.where(tab_ref[base + 1] > 0, top_ref[...], inc_ref[...])
    rb_t = r_ref[...].astype(bf16)
    in_map = b_ref[...]
    out_map = c_ref[...]
    lane_id = lax.broadcasted_iota(jnp.int32, (length, lanes), 1)
    masks = [(lane_id >= e * width) & (lane_id < (e + 1) * width) for e in range(per_pair)]
    mix_acc = jnp.zeros((per_pair * length, length), f32)
    for q in range(features // lanes):
        cols = slice(q * lanes, (q + 1) * lanes)
        v_q = v_ref[:, cols]
        x_q = x_ref[:, cols]
        stacked = jnp.concatenate([jnp.where(m, v_q, jnp.zeros_like(v_q)) for m in masks], axis=0)
        gx_q = jnp.dot(
            wt_ref[per_pair * q], stacked[0:length], preferred_element_type=f32
        )
        for e in range(1, per_pair):
            gx_q = gx_q + jnp.dot(
                wt_ref[per_pair * q + e],
                stacked[e * length:(e + 1) * length],
                preferred_element_type=f32,
            )
        rbb_q = jnp.dot(in_map, rb_t[:, cols], preferred_element_type=f32)
        gx_ref[:, cols] = gx_q + tail_ref[:, cols] * rbb_q
        pair_dots = lax.dot_general(stacked, x_q, nt, preferred_element_type=f32)
        mix_acc = mix_acc + dec_ref[q] * pair_dots
    mixing = mix_acc[0:length]
    for e in range(1, per_pair):
        mixing = mixing + mix_acc[e * length:(e + 1) * length]
    mixing = mixing.astype(bf16)
    v = v_ref[...]
    lead_grads = (lead_ref[...] * v.astype(f32)).astype(bf16)
    grad_inmap = factor * lax.dot_general(mixing, out_map, tn, preferred_element_type=f32)
    grad_inmap = grad_inmap + lax.dot_general(xt_ref[...], rb_t, nt, preferred_element_type=f32)
    grad_outmap = factor * (
        jnp.dot(mixing, in_map, preferred_element_type=f32)
        + lax.dot_general(lead_grads, sb_ref[...], nt, preferred_element_type=f32)
    )
    carry = factor * lax.dot_general(out_map, lead_grads, tn, preferred_element_type=f32)
    rnew_ref[...] = carry + end_ref[...] * r_ref[...]
    grad_bc = jnp.concatenate([grad_inmap, grad_outmap], axis=1).astype(bf16)
    dbc_ref[...] = grad_bc
    mstore_ref[...] = jnp.where(tab_ref[base + 2] > 0, grad_bc, ms_ref[...])
    back = lax.dot_general(grad_bc, w_ref[...], nt, preferred_element_type=f32)
    summed = (v.astype(f32) + gx_ref[...] + back).astype(out_ref.dtype)
    out_ref[...] = summed
    gstore_ref[...] = jnp.where(tab_ref[base + 2] > 0, summed, gs_ref[...])


def fused_step(step_arr, table, level_pos, levels, per_block, incoming, top_blk, carried, w_bc, grad_store, map_store, level_no, seq_no, factor, width):
    wt2, dec2, x_flat, in_blk, out_blk, tail_full, lead_full, xt_full, states_t, end_row = per_block
    length, features = incoming.shape[1:]
    state_size = in_blk.shape[-1]

    def lead_block(a):
        shape = (None, None, None) + a.shape[3:]
        tail = (0,) * (a.ndim - 3)
        return pl.BlockSpec(shape, lambda i, c, t: (t[(c[0] * levels + level_pos) * 3], level_no, seq_no) + tail)

    in_specs = [lead_block(a) for a in (wt2, dec2)]
    in_specs.append(pl.BlockSpec((None, length, features), lambda i, c, t: (seq_no, 0, 0)))
    in_specs.append(pl.BlockSpec((None, None, length, features), lambda i, c, t: (t[(c[0] * levels + level_pos) * 3], seq_no, 0, 0)))
    in_specs += [lead_block(a) for a in (x_flat, in_blk, out_blk, tail_full, lead_full, xt_full, states_t)]
    in_specs.append(pl.BlockSpec((None, None) + carried.shape[2:], lambda i, c, t: (level_no, seq_no, 0, 0)))
    in_specs.append(lead_block(end_row))
    in_specs.append(pl.BlockSpec((None,) + w_bc.shape[1:], lambda i, c, t: (level_no, 0, 0)))
    store_g = pl.BlockSpec((None, None, None, length, features), lambda i, c, t: (t[(c[0] * levels + level_pos) * 3], level_no, seq_no, 0, 0))
    store_m = pl.BlockSpec((None, None, None, length, 2 * state_size), lambda i, c, t: (t[(c[0] * levels + level_pos) * 3], level_no, seq_no, 0, 0))
    in_specs += [store_g, store_m]
    out_specs = (
        pl.BlockSpec((length, features), lambda i, c, t: (0, 0)),
        pl.BlockSpec((None, None) + carried.shape[2:], lambda i, c, t: (level_no, seq_no, 0, 0)),
        pl.BlockSpec((length, 2 * state_size), lambda i, c, t: (0, 0)),
        store_g,
        store_m,
    )
    flops = 2 * length * features * (6 * state_size + 4 * length)
    moved = 2 * (4 * features * state_size * 2 + 6 * length * features) + 4 * 4 * length * features
    return pl.pallas_call(
        functools.partial(
            step_kernel, factor=factor, width=width, level_pos=level_pos, levels=levels
        ),
        out_shape=(
            jax.ShapeDtypeStruct((length, features), jnp.bfloat16),
            jax.ShapeDtypeStruct(carried.shape, jnp.float32),
            jax.ShapeDtypeStruct((length, 2 * state_size), jnp.bfloat16),
            jax.ShapeDtypeStruct(grad_store.shape, grad_store.dtype),
            jax.ShapeDtypeStruct(map_store.shape, map_store.dtype),
        ),
        grid_spec=pltpu.PrefetchScalarGridSpec(
            num_scalar_prefetch=2,
            grid=(1,),
            in_specs=in_specs,
            out_specs=out_specs,
            scratch_shapes=[
                pltpu.VMEM((length, features), jnp.bfloat16),
                pltpu.VMEM((length, features), jnp.float32),
            ],
        ),
        input_output_aliases={13: 1, 16: 3, 17: 4},
        cost_estimate=pl.CostEstimate(flops=flops, bytes_accessed=moved, transcendentals=0),
    )(step_arr, table, wt2, dec2, incoming, top_blk, x_flat, in_blk, out_blk, tail_full, lead_full, xt_full, states_t, carried, end_row, w_bc, grad_store, map_store)


def shards(layer_inputs, w_bc, log_decay, top_grad):
    sections = lax.axis_size("section")
    section_id = lax.axis_index("section")
    lay_dev, seq_dev, tok_len, features = layer_inputs.shape
    head_count = log_decay.shape[-1]
    block_len = tok_len // MICRO
    state_size = w_bc.shape[-1] // 2
    factor = 0.25 / state_size
    bc_all = jnp.einsum(
        "lstd,ldc->lstc", layer_inputs, w_bc, preferred_element_type=jnp.float32
    ).astype(jnp.bfloat16)

    def blocked(a):
        split = a.reshape(a.shape[:2] + (MICRO, block_len) + a.shape[3:])
        return jnp.moveaxis(split, 2, 0)

    x_blk = blocked(layer_inputs).reshape(
        (MICRO, lay_dev, seq_dev, block_len, head_count, features // head_count)
    )
    bc_blk = blocked(bc_all)
    in_blk = bc_blk[..., :state_size]
    out_blk = bc_blk[..., state_size:]
    rates_blk = blocked(log_decay)
    consts_fn = jax.vmap(jax.vmap(jax.vmap(lambda x, b, c, r: block_consts(x, b, c, r, factor))))
    consts = consts_fn(x_blk, in_blk, out_blk, rates_blk)
    width = features // head_count
    lead_dims = consts["tail"].shape[:3]
    pairs = head_count * width // 128
    per_pair = 128 // width
    wt2 = consts["weighted"]
    dec2 = jnp.moveaxis(consts["decays"], -1, -3).reshape(
        lead_dims + (pairs, per_pair * block_len, block_len)
    )
    spread_heads = (
        jnp.arange(features)[None, :] // width == jnp.arange(head_count)[:, None]
    ).astype(jnp.float32)

    def per_lane(a):
        return jnp.einsum(
            "...h,hd->...d", a, spread_heads, precision=lax.Precision.HIGHEST,
            preferred_element_type=jnp.float32,
        )

    tail_full = per_lane(consts["tail"])
    lead_full = per_lane(consts["lead"])
    x_flat = x_blk.reshape(lead_dims + (block_len, features))
    xt_full = (tail_full * x_flat.astype(jnp.float32)).astype(jnp.bfloat16)
    end_row = per_lane(consts["ending"])[..., None, :]
    fresh_t = jnp.einsum(
        "mlsnj,mlsjd->mlsnd",
        jnp.swapaxes(in_blk[: MICRO - 1], -1, -2),
        xt_full[: MICRO - 1],
        preferred_element_type=jnp.float32,
    )
    state_now = jnp.zeros(fresh_t.shape[1:], jnp.float32)
    saved = [state_now.astype(jnp.bfloat16)[None]]
    for block_no in range(MICRO - 1):
        state_now = end_row[block_no] * state_now + fresh_t[block_no]
        saved.append(state_now.astype(jnp.bfloat16)[None])
    states_t = jnp.concatenate(saved, axis=0)
    per_block = (wt2, dec2, x_flat, in_blk, out_blk, tail_full, lead_full, xt_full, states_t, end_row)
    per_block = lax.optimization_barrier(per_block)

    top_blk = jnp.moveaxis(
        top_grad.reshape((seq_dev, MICRO, block_len, features)), 1, 0
    )
    is_top = section_id == sections - 1

    steps = MICRO + sections - 1
    counters = jnp.arange(steps, dtype=jnp.int32)[:, None]
    offsets = counters - (sections - 1 - section_id)
    valid_tab = ((offsets >= 0) & (offsets < MICRO)).astype(jnp.int32)
    block_tab = jnp.clip(MICRO - 1 - offsets, 0, MICRO - 1).astype(jnp.int32)
    top_tab = (jnp.arange(lay_dev)[None, ::-1] == lay_dev - 1) & is_top
    table = jnp.stack(
        jnp.broadcast_arrays(block_tab, top_tab.astype(jnp.int32), valid_tab), axis=-1
    ).reshape(-1).astype(jnp.int32)

    def advance(counter, loop_state, send=True):
        incoming, carried, grad_store, map_store = loop_state
        step_arr = jnp.reshape(counter, (1,)).astype(jnp.int32)
        for level_pos, level_no in enumerate(reversed(range(lay_dev))):
            level_out = []
            for seq_no in range(seq_dev):
                level_grads, carried, grad_bc, grad_store, map_store = fused_step(
                    step_arr, table, level_pos, lay_dev, per_block, incoming, top_blk, carried,
                    w_bc, grad_store, map_store, level_no, seq_no, factor, width,
                )
                level_out.append(level_grads)
            incoming = jnp.stack(level_out)
        if send:
            incoming = passed_along(incoming, "section", -1)
        return (incoming, carried, grad_store, map_store)

    initial = (
        jnp.zeros((seq_dev, block_len, features), jnp.bfloat16),
        jnp.zeros(states_t.shape[1:], jnp.float32),
        jnp.zeros((MICRO, lay_dev, seq_dev, block_len, features), jnp.bfloat16),
        jnp.zeros((MICRO, lay_dev, seq_dev, block_len, 2 * state_size), jnp.bfloat16),
    )
    final_state = lax.fori_loop(0, steps - 1, advance, initial)
    final_state = advance(steps - 1, final_state, send=False)
    grad_store = final_state[2]
    map_store = final_state[3]

    grad_inputs = jnp.moveaxis(grad_store, 0, 2).reshape(layer_inputs.shape)
    map_store = jnp.moveaxis(map_store, 0, 2).reshape(bc_all.shape)
    ways = lax.axis_size("dp")
    divisor = ways * seq_dev
    rows_here = layer_inputs.reshape(lay_dev, seq_dev * tok_len, ways, features // ways)
    rows_here = jnp.transpose(rows_here, (2, 0, 1, 3))
    rows_all = lax.all_to_all(rows_here, "dp", 0, 0, tiled=True)
    maps_here = map_store.reshape(1, lay_dev, seq_dev * tok_len, map_store.shape[-1])
    maps_all = lax.all_gather(maps_here, "dp", axis=0, tiled=True)
    grad_w = jnp.einsum(
        "glrd,glrc->ldc", rows_all, maps_all, preferred_element_type=jnp.float32
    ) / divisor
    return (grad_inputs, grad_w)


def solution(mesh):
    in_specs = (
        P("section", "dp", None, None),
        P("section", None, None),
        P("section", "dp", None, None),
        P("dp", None, None),
    )
    out_specs = (P("section", "dp", None, None), P("section", "dp", None))
    return jax.shard_map(shards, mesh=mesh, in_specs=in_specs, out_specs=out_specs, check_vma=False)
```

```python
import functools

import jax
import jax.numpy as jnp
from jax import lax
from jax.experimental import pallas as pl
from jax.experimental.pallas import tpu as pltpu
from jax.sharding import PartitionSpec as P

MICRO = 4


def shortened(value):
    return jax.tree.map(lambda a: a.astype(jnp.bfloat16) if a.dtype == jnp.float32 else a, value)


def passed_along(block, axis, distance):
    devices = range(lax.axis_size(axis))
    route = [(i - distance, i) for i in devices if i - distance in devices]
    return lax.ppermute(block, axis, route)


def block_terms(inputs_b, in_b, out_b, rates, grads_b, carried, state_in, factor):
    length = inputs_b.shape[0]
    cumulative = jnp.cumsum(rates, axis=0)
    ending = cumulative[-1]
    locations = jnp.arange(length)
    lower_mask = (locations[:, None] >= locations[None, :])[:, :, None]
    spread = jnp.where(lower_mask, cumulative[:, None, :] - cumulative[None, :, :], 0.0)
    decays = jnp.where(lower_mask, jnp.exp(spread), 0.0)
    tail_decay = jnp.exp(ending[None, :] - cumulative)
    leading = jnp.exp(cumulative)
    scores = jnp.dot(out_b, in_b.T, preferred_element_type=jnp.float32)
    weighted = (factor * decays * scores[:, :, None]).astype(jnp.bfloat16)
    carried_b = carried.astype(jnp.bfloat16)
    state_b = state_in.astype(jnp.bfloat16)
    grad_feats = jnp.einsum("kjh,khp->jhp", weighted, grads_b, preferred_element_type=jnp.float32)
    grad_feats = grad_feats + tail_decay[:, :, None] * jnp.einsum(
        "hpn,jn->jhp", carried_b, in_b, preferred_element_type=jnp.float32
    )
    pair_dots = jnp.einsum("khp,jhp->kjh", grads_b, inputs_b, preferred_element_type=jnp.float32)
    mixing = jnp.sum(decays * pair_dots, axis=2).astype(jnp.bfloat16)
    tail_inputs = (tail_decay[:, :, None] * inputs_b.astype(jnp.float32)).astype(jnp.bfloat16)
    lead_grads = (leading[:, :, None] * grads_b.astype(jnp.float32)).astype(jnp.bfloat16)
    grad_inmap = factor * jnp.dot(mixing.T, out_b, preferred_element_type=jnp.float32)
    grad_inmap = grad_inmap + jnp.einsum(
        "jhp,hpn->jn", tail_inputs, carried_b, preferred_element_type=jnp.float32
    )
    grad_outmap = factor * (
        jnp.dot(mixing, in_b, preferred_element_type=jnp.float32)
        + jnp.einsum("ihp,hpn->in", lead_grads, state_b, preferred_element_type=jnp.float32)
    )
    carry_out = factor * jnp.einsum(
        "khp,kn->hpn", lead_grads, out_b, preferred_element_type=jnp.float32
    )
    carry_out = carry_out + jnp.exp(ending)[:, None, None] * carried
    return (grad_feats, grad_inmap, grad_outmap, carry_out)


def block_end(inputs_b, in_b, rates, state_in):
    cumulative = jnp.cumsum(rates, axis=0)
    ending = cumulative[-1]
    tail_decay = jnp.exp(ending[None, :] - cumulative)
    tail_inputs = (tail_decay[:, :, None] * inputs_b.astype(jnp.float32)).astype(jnp.bfloat16)
    fresh = jnp.einsum("jhp,jn->hpn", tail_inputs, in_b, preferred_element_type=jnp.float32)
    return jnp.exp(ending)[:, None, None] * state_in + fresh


def split_block(inputs_c, map_block, head_count):
    length, features = inputs_c.shape
    state_size = map_block.shape[1] // 2
    inputs_b = inputs_c.reshape(length, head_count, features // head_count)
    in_b = map_block[:, :state_size]
    out_b = map_block[:, state_size:]
    return (inputs_b, in_b, out_b)


def block_back(inputs_c, map_block, rates, grads_c, carried, state_in, weights):
    length, features = inputs_c.shape
    head_count = rates.shape[1]
    factor = 0.25 / (map_block.shape[1] // 2)
    inputs_b, in_b, out_b = split_block(inputs_c, map_block, head_count)
    grads_b = grads_c.reshape(length, head_count, features // head_count)
    grad_feats, grad_inmap, grad_outmap, carry_out = block_terms(
        inputs_b, in_b, out_b, rates, grads_b, carried, state_in, factor
    )
    grad_bc = jnp.concatenate([grad_inmap, grad_outmap], axis=1).astype(jnp.bfloat16)
    back_proj = lax.dot_general(
        grad_bc, weights, (((1,), (1,)), ((), ())), preferred_element_type=jnp.float32
    )
    summed = grads_c.astype(jnp.float32) + grad_feats.reshape(length, features) + back_proj
    return (summed.astype(jnp.bfloat16), carry_out, grad_bc)


def layer_starts(inputs_s, bc_s, rates_s):
    head_count = rates_s.shape[1]
    features = inputs_s.shape[1]
    state_size = bc_s.shape[1] // 2
    block_len = inputs_s.shape[0] // MICRO
    state_now = jnp.zeros((head_count, features // head_count, state_size), jnp.float32)
    saved = []
    for block_no in range(MICRO):
        lo_row = block_no * block_len
        inputs_b, in_b, out_b = split_block(
            inputs_s[lo_row : lo_row + block_len], bc_s[lo_row : lo_row + block_len], head_count
        )
        saved.append(state_now)
        state_now = block_end(inputs_b, in_b, rates_s[lo_row : lo_row + block_len], state_now)
    return jnp.stack(saved)


def block_consts(inputs_b, in_b, out_b, rates, factor):
    length = inputs_b.shape[0]
    cumulative = jnp.cumsum(rates, axis=0)
    ending = cumulative[-1]
    locations = jnp.arange(length)
    lower_mask = (locations[:, None] >= locations[None, :])[:, :, None]
    spread = jnp.where(lower_mask, cumulative[:, None, :] - cumulative[None, :, :], 0.0)
    decays = jnp.where(lower_mask, jnp.exp(spread), 0.0)
    tail_decay = jnp.exp(ending[None, :] - cumulative)
    leading = jnp.exp(cumulative)
    scores = jnp.dot(out_b, in_b.T, preferred_element_type=jnp.float32)
    cum_t = cumulative.T
    upper = (locations[:, None] <= locations[None, :])[None]
    spread_t = jnp.where(upper, cum_t[:, None, :] - cum_t[:, :, None], 0.0)
    decays_t = jnp.where(upper, jnp.exp(spread_t), 0.0)
    scores_t = jnp.dot(in_b, out_b.T, preferred_element_type=jnp.float32)
    weighted = (factor * decays_t * scores_t[None]).astype(jnp.bfloat16)
    return dict(
        decays=decays,
        tail=tail_decay,
        lead=leading,
        weighted=weighted,
        ending=jnp.exp(ending),
    )


def step_kernel(
    step_ref, tab_ref, wt_ref, dec_ref, inc_ref, top_ref, x_ref, b_ref, c_ref, tail_ref, lead_ref, xt_ref,
    sb_ref, r_ref, end_ref, w_ref, gs_ref, ms_ref, out_ref, rnew_ref, dbc_ref, gstore_ref, mstore_ref,
    v_ref, gx_ref, *, factor, width, level_pos, levels
):
    base = (step_ref[0] * levels + level_pos) * 3
    f32 = jnp.float32
    bf16 = jnp.bfloat16
    length, features = v_ref.shape
    lanes = 128
    per_pair = lanes // width
    nt = (((1,), (1,)), ((), ()))
    tn = (((0,), (0,)), ((), ()))
    v_ref[...] = jnp.where(tab_ref[base + 1] > 0, top_ref[...], inc_ref[...])
    rb_t = r_ref[...].astype(bf16)
    in_map = b_ref[...]
    out_map = c_ref[...]
    lane_id = lax.broadcasted_iota(jnp.int32, (length, lanes), 1)
    masks = [(lane_id >= e * width) & (lane_id < (e + 1) * width) for e in range(per_pair)]
    mix_acc = jnp.zeros((per_pair * length, length), f32)
    for q in range(features // lanes):
        cols = slice(q * lanes, (q + 1) * lanes)
        v_q = v_ref[:, cols]
        x_q = x_ref[:, cols]
        stacked = jnp.concatenate([jnp.where(m, v_q, jnp.zeros_like(v_q)) for m in masks], axis=0)
        gx_q = jnp.dot(
            wt_ref[per_pair * q], stacked[0:length], preferred_element_type=f32
        )
        for e in range(1, per_pair):
            gx_q = gx_q + jnp.dot(
                wt_ref[per_pair * q + e],
                stacked[e * length:(e + 1) * length],
                preferred_element_type=f32,
            )
        gx_ref[:, cols] = gx_q
        pair_dots = lax.dot_general(stacked, x_q, nt, preferred_element_type=f32)
        mix_acc = mix_acc + dec_ref[q] * pair_dots
    mixing = mix_acc[0:length]
    for e in range(1, per_pair):
        mixing = mixing + mix_acc[e * length:(e + 1) * length]
    mixing = mixing.astype(bf16)
    rbb = jnp.dot(in_map, rb_t, preferred_element_type=f32)
    gx_ref[...] = gx_ref[...] + tail_ref[...] * rbb
    v = v_ref[...]
    lead_grads = (lead_ref[...] * v.astype(f32)).astype(bf16)
    grad_inmap = factor * lax.dot_general(mixing, out_map, tn, preferred_element_type=f32)
    grad_inmap = grad_inmap + lax.dot_general(xt_ref[...], rb_t, nt, preferred_element_type=f32)
    grad_outmap = factor * (
        jnp.dot(mixing, in_map, preferred_element_type=f32)
        + lax.dot_general(lead_grads, sb_ref[...], nt, preferred_element_type=f32)
    )
    carry = factor * lax.dot_general(out_map, lead_grads, tn, preferred_element_type=f32)
    rnew_ref[...] = carry + end_ref[...] * r_ref[...]
    grad_bc = jnp.concatenate([grad_inmap, grad_outmap], axis=1).astype(bf16)
    dbc_ref[...] = grad_bc
    mstore_ref[...] = jnp.where(tab_ref[base + 2] > 0, grad_bc, ms_ref[...])
    back = lax.dot_general(grad_bc, w_ref[...], nt, preferred_element_type=f32)
    summed = (v.astype(f32) + gx_ref[...] + back).astype(out_ref.dtype)
    out_ref[...] = summed
    gstore_ref[...] = jnp.where(tab_ref[base + 2] > 0, summed, gs_ref[...])


def fused_step(step_arr, table, level_pos, levels, per_block, incoming, top_blk, carried, w_bc, grad_store, map_store, level_no, seq_no, factor, width):
    wt2, dec2, x_flat, in_blk, out_blk, tail_full, lead_full, xt_full, states_t, end_row = per_block
    length, features = incoming.shape[1:]
    state_size = in_blk.shape[-1]

    def lead_block(a):
        shape = (None, None, None) + a.shape[3:]
        tail = (0,) * (a.ndim - 3)
        return pl.BlockSpec(shape, lambda i, c, t: (t[(c[0] * levels + level_pos) * 3], level_no, seq_no) + tail)

    in_specs = [lead_block(a) for a in (wt2, dec2)]
    in_specs.append(pl.BlockSpec((None, length, features), lambda i, c, t: (seq_no, 0, 0)))
    in_specs.append(pl.BlockSpec((None, None, length, features), lambda i, c, t: (t[(c[0] * levels + level_pos) * 3], seq_no, 0, 0)))
    in_specs += [lead_block(a) for a in (x_flat, in_blk, out_blk, tail_full, lead_full, xt_full, states_t)]
    in_specs.append(pl.BlockSpec((None, None) + carried.shape[2:], lambda i, c, t: (level_no, seq_no, 0, 0)))
    in_specs.append(lead_block(end_row))
    in_specs.append(pl.BlockSpec((None,) + w_bc.shape[1:], lambda i, c, t: (level_no, 0, 0)))
    store_g = pl.BlockSpec((None, None, None, length, features), lambda i, c, t: (t[(c[0] * levels + level_pos) * 3], level_no, seq_no, 0, 0))
    store_m = pl.BlockSpec((None, None, None, length, 2 * state_size), lambda i, c, t: (t[(c[0] * levels + level_pos) * 3], level_no, seq_no, 0, 0))
    in_specs += [store_g, store_m]
    out_specs = (
        pl.BlockSpec((length, features), lambda i, c, t: (0, 0)),
        pl.BlockSpec((None, None) + carried.shape[2:], lambda i, c, t: (level_no, seq_no, 0, 0)),
        pl.BlockSpec((length, 2 * state_size), lambda i, c, t: (0, 0)),
        store_g,
        store_m,
    )
    flops = 2 * length * features * (6 * state_size + 4 * length)
    moved = 2 * (4 * features * state_size * 2 + 6 * length * features) + 4 * 4 * length * features
    return pl.pallas_call(
        functools.partial(
            step_kernel, factor=factor, width=width, level_pos=level_pos, levels=levels
        ),
        out_shape=(
            jax.ShapeDtypeStruct((length, features), jnp.bfloat16),
            jax.ShapeDtypeStruct(carried.shape, jnp.float32),
            jax.ShapeDtypeStruct((length, 2 * state_size), jnp.bfloat16),
            jax.ShapeDtypeStruct(grad_store.shape, grad_store.dtype),
            jax.ShapeDtypeStruct(map_store.shape, map_store.dtype),
        ),
        grid_spec=pltpu.PrefetchScalarGridSpec(
            num_scalar_prefetch=2,
            grid=(1,),
            in_specs=in_specs,
            out_specs=out_specs,
            scratch_shapes=[
                pltpu.VMEM((length, features), jnp.bfloat16),
                pltpu.VMEM((length, features), jnp.float32),
            ],
        ),
        input_output_aliases={13: 1, 16: 3, 17: 4},
        cost_estimate=pl.CostEstimate(flops=flops, bytes_accessed=moved, transcendentals=0),
    )(step_arr, table, wt2, dec2, incoming, top_blk, x_flat, in_blk, out_blk, tail_full, lead_full, xt_full, states_t, carried, end_row, w_bc, grad_store, map_store)


def shards(layer_inputs, w_bc, log_decay, top_grad):
    sections = lax.axis_size("section")
    section_id = lax.axis_index("section")
    lay_dev, seq_dev, tok_len, features = layer_inputs.shape
    head_count = log_decay.shape[-1]
    block_len = tok_len // MICRO
    state_size = w_bc.shape[-1] // 2
    factor = 0.25 / state_size
    bc_all = jnp.einsum(
        "lstd,ldc->lstc", layer_inputs, w_bc, preferred_element_type=jnp.float32
    ).astype(jnp.bfloat16)

    def blocked(a):
        split = a.reshape(a.shape[:2] + (MICRO, block_len) + a.shape[3:])
        return jnp.moveaxis(split, 2, 0)

    x_blk = blocked(layer_inputs).reshape(
        (MICRO, lay_dev, seq_dev, block_len, head_count, features // head_count)
    )
    bc_blk = blocked(bc_all)
    in_blk = bc_blk[..., :state_size]
    out_blk = bc_blk[..., state_size:]
    rates_blk = blocked(log_decay)
    consts_fn = jax.vmap(jax.vmap(jax.vmap(lambda x, b, c, r: block_consts(x, b, c, r, factor))))
    consts = consts_fn(x_blk, in_blk, out_blk, rates_blk)
    width = features // head_count
    lead_dims = consts["tail"].shape[:3]
    pairs = head_count * width // 128
    per_pair = 128 // width
    wt2 = consts["weighted"]
    dec2 = jnp.moveaxis(consts["decays"], -1, -3).reshape(
        lead_dims + (pairs, per_pair * block_len, block_len)
    )
    spread_heads = (
        jnp.arange(features)[None, :] // width == jnp.arange(head_count)[:, None]
    ).astype(jnp.float32)

    def per_lane(a):
        return jnp.einsum(
            "...h,hd->...d", a, spread_heads, precision=lax.Precision.HIGHEST,
            preferred_element_type=jnp.float32,
        )

    tail_full = per_lane(consts["tail"])
    lead_full = per_lane(consts["lead"])
    x_flat = x_blk.reshape(lead_dims + (block_len, features))
    xt_full = (tail_full * x_flat.astype(jnp.float32)).astype(jnp.bfloat16)
    end_row = per_lane(consts["ending"])[..., None, :]
    fresh_t = jnp.einsum(
        "mlsnj,mlsjd->mlsnd",
        jnp.swapaxes(in_blk[: MICRO - 1], -1, -2),
        xt_full[: MICRO - 1],
        preferred_element_type=jnp.float32,
    )
    state_now = jnp.zeros(fresh_t.shape[1:], jnp.float32)
    saved = [state_now.astype(jnp.bfloat16)[None]]
    for block_no in range(MICRO - 1):
        state_now = end_row[block_no] * state_now + fresh_t[block_no]
        saved.append(state_now.astype(jnp.bfloat16)[None])
    states_t = jnp.concatenate(saved, axis=0)
    per_block = (wt2, dec2, x_flat, in_blk, out_blk, tail_full, lead_full, xt_full, states_t, end_row)
    per_block = lax.optimization_barrier(per_block)

    top_blk = jnp.moveaxis(
        top_grad.reshape((seq_dev, MICRO, block_len, features)), 1, 0
    )
    is_top = section_id == sections - 1

    steps = MICRO + sections - 1
    counters = jnp.arange(steps, dtype=jnp.int32)[:, None]
    offsets = counters - (sections - 1 - section_id)
    valid_tab = ((offsets >= 0) & (offsets < MICRO)).astype(jnp.int32)
    block_tab = jnp.clip(MICRO - 1 - offsets, 0, MICRO - 1).astype(jnp.int32)
    top_tab = (jnp.arange(lay_dev)[None, ::-1] == lay_dev - 1) & is_top
    table = jnp.stack(
        jnp.broadcast_arrays(block_tab, top_tab.astype(jnp.int32), valid_tab), axis=-1
    ).reshape(-1).astype(jnp.int32)

    def advance(counter, loop_state, send=True):
        incoming, carried, grad_store, map_store = loop_state
        step_arr = jnp.reshape(counter, (1,)).astype(jnp.int32)
        for level_pos, level_no in enumerate(reversed(range(lay_dev))):
            level_out = []
            for seq_no in range(seq_dev):
                level_grads, carried, grad_bc, grad_store, map_store = fused_step(
                    step_arr, table, level_pos, lay_dev, per_block, incoming, top_blk, carried,
                    w_bc, grad_store, map_store, level_no, seq_no, factor, width,
                )
                level_out.append(level_grads)
            incoming = jnp.stack(level_out)
        if send:
            incoming = passed_along(incoming, "section", -1)
        return (incoming, carried, grad_store, map_store)

    initial = (
        jnp.zeros((seq_dev, block_len, features), jnp.bfloat16),
        jnp.zeros(states_t.shape[1:], jnp.float32),
        jnp.zeros((MICRO, lay_dev, seq_dev, block_len, features), jnp.bfloat16),
        jnp.zeros((MICRO, lay_dev, seq_dev, block_len, 2 * state_size), jnp.bfloat16),
    )
    final_state = lax.fori_loop(0, steps - 1, advance, initial)
    final_state = advance(steps - 1, final_state, send=False)
    grad_store = final_state[2]
    map_store = final_state[3]

    grad_inputs = jnp.moveaxis(grad_store, 0, 2).reshape(layer_inputs.shape)
    map_store = jnp.moveaxis(map_store, 0, 2).reshape(bc_all.shape)
    ways = lax.axis_size("dp")
    divisor = ways * seq_dev
    rows_here = layer_inputs.reshape(lay_dev, seq_dev * tok_len, ways, features // ways)
    rows_here = jnp.transpose(rows_here, (2, 0, 1, 3))
    rows_all = lax.all_to_all(rows_here, "dp", 0, 0, tiled=True)
    maps_here = map_store.reshape(1, lay_dev, seq_dev * tok_len, map_store.shape[-1])
    maps_all = lax.all_gather(maps_here, "dp", axis=0, tiled=True)
    grad_w = jnp.einsum(
        "glrd,glrc->ldc", rows_all, maps_all, preferred_element_type=jnp.float32
    ) / divisor
    return (grad_inputs, grad_w)


def solution(mesh):
    in_specs = (
        P("section", "dp", None, None),
        P("section", None, None),
        P("section", "dp", None, None),
        P("dp", None, None),
    )
    out_specs = (P("section", "dp", None, None), P("section", "dp", None))
    return jax.shard_map(shards, mesh=mesh, in_specs=in_specs, out_specs=out_specs, check_vma=False)
```
